128 devices in a mesh: gx: 8 (over y, x_lo), gy: 16 (over x_hi, z, core).
Axes of the slice: x: 4 (x_hi: 2, x_lo: 2; x = x_hi * 2 + x_lo), y: 4, z: 4, core: 2. Of those that a mesh axis runs over, the one named last changes fastest.
Arguments:
- sources: float32 [2, 2, 1024, 2048], P(None, None, 'gx', 'gy'), may hold values from -9 to 9
- wavenumber: float32 [1024, 2048], P('gx', 'gy'), may hold values from 0.2 to 0.8
- row_inverse: float32 [32, 2, 64, 64], P('gy'), may hold values from -0.3 to 0.3
- col_inverse: float32 [16, 2, 64, 64], P('gx'), may hold values from -0.3 to 0.3
- reach_steps: int32 [8, 16, 4], P('gx', 'gy'), may hold values from 1 to 4, as said below
Outputs:
- fields: float32 [2, 2, 1024, 2048], P(None, None, 'gx', 'gy')
The draws below stay inside these ranges and needn't reach their ends.
Inputs may be any that keep to these rules, and one draw needn't show every extreme that they name: `reach_steps`: every value occurs somewhere in every draw.
All inputs are finite; a program needn't handle non-finite values.
Results may differ from the reference program's by a relative error of at most 0.0003.
Values sent between devices are 32-bit elements; how exact they have to be, the bound alone decides.
No kernel may reach another device: no remote copies, remote signals or barrier semaphores. Data moves between devices by JAX's collectives and lax.ppermute only.
A program may use at most 64 MiB of HBM per device.

```python
import math
import jax
import jax.numpy as jnp
from jax import lax

BLK = 64
ITERS = 2
SWEEPS = 4
NX = 1024
NY = 2048
N_GX = 8
N_GY = 16


def draw_sources(key, part):
    return 1.5 * jax.random.truncated_normal(jax.random.fold_in(key, 11), -6.0, 6.0, (2, 2, NX, NY), jnp.float32)


def inverse_blocks(key, block_count):
    identity = (lax.broadcasted_iota(jnp.int32, (BLK, BLK), 0) == lax.broadcasted_iota(jnp.int32, (BLK, BLK), 1)).astype(jnp.float32)
    first_key, second_key = jax.random.split(key)
    scatter = jax.random.truncated_normal(first_key, -3.0, 3.0, (block_count, 2, BLK, BLK), jnp.float32)
    spread = jnp.array([0.08, 0.04], dtype=jnp.float32).reshape(1, 2, 1, 1) / BLK ** 0.5
    centre = jnp.array([0.2, 0.05], dtype=jnp.float32).reshape(1, 2, 1, 1)
    wobble = jnp.array([0.04, 0.02], dtype=jnp.float32).reshape(1, 2, 1, 1) * jax.random.uniform(second_key, (block_count, 2, 1, BLK), jnp.float32, -1.0, 1.0)
    return identity * (centre + wobble) + (1.0 - identity) * spread * scatter


def draw_row_inverse(key, part):
    return inverse_blocks(jax.random.fold_in(key, 21), NY // BLK)


def draw_col_inverse(key, part):
    return inverse_blocks(jax.random.fold_in(key, 31), NX // BLK)


def draw_reach_steps(key, part):
    drawn_steps = jax.random.randint(jax.random.fold_in(key, 41), (N_GX, N_GY, 4), 1, 5)
    drawn_steps = drawn_steps.at[0, 0, 1].set(4)
    drawn_steps = drawn_steps.at[0, 0, 3].set(1)
    return drawn_steps.astype(jnp.int32)


def block_scale(key, dims, cuts, low, top_value):
    level, own = 1.0, jax.random.fold_in(key, 6)
    for axis_at, parts in cuts:
        draws = jnp.exp(jax.random.uniform(jax.random.fold_in(own, axis_at), (parts,), jnp.float32, low / len(cuts), top_value / len(cuts)))
        level = level * jnp.repeat(draws, dims[axis_at] // parts).reshape([-1 if axis == axis_at else 1 for axis in range(len(dims))])
    return level


def setup_inputs(seed: int = 0) -> dict:
    keys = jax.random.split(jax.random.key(seed), 6)
    sources = draw_sources(jax.random.fold_in(keys[5], 71), 0)
    wavenumber = jnp.clip(jnp.exp(math.log(0.8) - 1.3862944 * jax.random.uniform(keys[1], (NX, NY), jnp.float32) ** block_scale(keys[1], (NX, NY), ((0, 8), (1, 16)), -0.2, 0.2)), 0.2, 0.8)
    row_inverse = draw_row_inverse(jax.random.fold_in(keys[5], 71), 0)
    col_inverse = draw_col_inverse(jax.random.fold_in(keys[5], 71), 0)
    reach_steps = draw_reach_steps(jax.random.fold_in(keys[5], 71), 0)
    return dict(sources=sources, wavenumber=wavenumber, row_inverse=row_inverse, col_inverse=col_inverse, reach_steps=reach_steps)


DAMPING = 0.5
ROBIN_COEF = 0.5


def to_index(value):
    return jnp.asarray(value).astype(jnp.int32)


def slice_line(values, start, axis):
    starts = [to_index(0) for _ in range(values.ndim)]
    starts[axis] = to_index(start)
    sizes = list(values.shape)
    sizes[axis] = 1
    return lax.dynamic_slice(values, starts, sizes)


def fill_ghost(values, upper, lower, left, right, signs):
    upper, lower, left, right = to_index(upper), to_index(lower), to_index(left), to_index(right)
    height, breadth = values.shape[2], values.shape[3]
    row_ids = lax.broadcasted_iota(jnp.int32, (height, 1), 0)
    col_ids = lax.broadcasted_iota(jnp.int32, (1, breadth), 1)
    upper_row = slice_line(values, upper, 2)
    lower_row = slice_line(values, lower - 1, 2)
    values = jnp.where(row_ids < upper, upper_row, jnp.where(row_ids >= lower, lower_row, values))
    left_col = slice_line(values, left, 3)
    right_col = slice_line(values, right - 1, 3)
    values = jnp.where(col_ids < left, left_col, jnp.where(col_ids >= right, right_col, values))
    inside = (row_ids >= upper) & (row_ids < lower) & (col_ids >= left) & (col_ids < right)
    real_part = values[:, 0]
    imag_part = values[:, 1]
    ghost_cycle = jnp.stack([real_part + signs * ROBIN_COEF * imag_part, imag_part - signs * ROBIN_COEF * real_part], axis=1)
    return jnp.where(inside, values, ghost_cycle)


def apply_operator(padded, wave_cells, signs):
    centre = padded[:, :, 1:-1, 1:-1]
    edge_sum = padded[:, :, :-2, 1:-1] + padded[:, :, 2:, 1:-1] + padded[:, :, 1:-1, :-2] + padded[:, :, 1:-1, 2:]
    corner_sum = padded[:, :, :-2, :-2] + padded[:, :, :-2, 2:] + padded[:, :, 2:, :-2] + padded[:, :, 2:, 2:]
    laplace = (4.0 * edge_sum + corner_sum - 20.0 * centre) / 6.0
    real_part = centre[:, 0]
    imag_part = centre[:, 1]
    mass_term = jnp.stack([real_part - signs * DAMPING * imag_part, imag_part + signs * DAMPING * real_part], axis=1)
    return -laplace - wave_cells * mass_term


def combine_parts(products, signs, shape):
    real_out = products[0][:, 0] - signs[..., None] * products[1][:, 1]
    imag_out = products[0][:, 1] + signs[..., None] * products[1][:, 0]
    return jnp.stack([real_out, imag_out], axis=1).reshape(shape)


def along_rows(values, inverse, signs):
    block = inverse.shape[-1]
    blocked = values.reshape(values.shape[0], 2, values.shape[2], values.shape[3] // block, block)
    products = jnp.einsum("qmok,fchqk->mfchqo", inverse, blocked, precision=lax.Precision.HIGHEST)
    return combine_parts(products, signs, values.shape)


def along_cols(values, inverse, signs):
    block = inverse.shape[-1]
    blocked = values.reshape(values.shape[0], 2, values.shape[2] // block, block, values.shape[3])
    products = jnp.einsum("qmok,fcqkw->mfcqow", inverse, blocked, precision=lax.Precision.HIGHEST)
    return combine_parts(products, signs, values.shape)


def solve_local(resid_ext, wave_ext, row_blocks, col_blocks, live_rect, signs):
    upper, lower, left, right = [to_index(v) for v in live_rect]
    height, breadth = resid_ext.shape[2], resid_ext.shape[3]
    row_ids = lax.broadcasted_iota(jnp.int32, (height, 1), 0)
    col_ids = lax.broadcasted_iota(jnp.int32, (1, breadth), 1)
    live_mask = ((row_ids >= upper) & (row_ids < lower) & (col_ids >= left) & (col_ids < right)).astype(resid_ext.dtype)
    local_res = resid_ext * live_mask
    correction = jnp.zeros_like(resid_ext)
    for sweep_index in range(SWEEPS):
        if sweep_index > 0:
            padded = jnp.pad(correction, ((0, 0), (0, 0), (1, 1), (1, 1)))
            padded = fill_ghost(padded, upper + 1, lower + 1, left + 1, right + 1, signs)
            local_res = live_mask * (resid_ext - apply_operator(padded, wave_ext, signs))
        if sweep_index % 2 == 0:
            update = along_rows(local_res, row_blocks, signs)
        else:
            update = along_cols(local_res, col_blocks, signs)
        correction = correction + live_mask * update
    return correction


def reference(sources, wavenumber, row_inverse, col_inverse, reach_steps):
    grid_rows, grid_cols = sources.shape[2], sources.shape[3]
    own_rows = grid_rows // N_GX
    own_cols = grid_cols // N_GY
    block = BLK
    step_cells = BLK // 4
    signs = jnp.array([1.0, -1.0], dtype=sources.dtype).reshape(2, 1, 1)
    wave_pad = jnp.pad(wavenumber, block)
    row_pad = jnp.pad(row_inverse, ((1, 1), (0, 0), (0, 0), (0, 0)))
    col_pad = jnp.pad(col_inverse, ((1, 1), (0, 0), (0, 0), (0, 0)))
    solution = jnp.zeros_like(sources)
    zero = to_index(0)
    for iteration in range(ITERS):
        padded = jnp.pad(solution, ((0, 0), (0, 0), (1, 1), (1, 1)))
        padded = fill_ghost(padded, 1, grid_rows + 1, 1, grid_cols + 1, signs)
        residual = sources - apply_operator(padded, wavenumber, signs)
        resid_pad = jnp.pad(residual, ((0, 0), (0, 0), (block, block), (block, block)))

        def solve_one(sub_index):
            row_rank = to_index(sub_index // N_GY)
            col_rank = to_index(sub_index % N_GY)
            widths = (reach_steps[row_rank, col_rank] * step_cells).astype(jnp.int32)
            upper_w = jnp.where(row_rank > 0, widths[0], zero)
            lower_w = jnp.where(row_rank < N_GX - 1, widths[1], zero)
            left_w = jnp.where(col_rank > 0, widths[2], zero)
            right_w = jnp.where(col_rank < N_GY - 1, widths[3], zero)
            live_rect = (block - upper_w, block + own_rows + lower_w, block - left_w, block + own_cols + right_w)
            row_start = to_index(row_rank * own_rows)
            col_start = to_index(col_rank * own_cols)
            resid_ext = lax.dynamic_slice(resid_pad, (zero, zero, row_start, col_start), (2, 2, own_rows + 2 * block, own_cols + 2 * block))
            wave_ext = lax.dynamic_slice(wave_pad, (row_start, col_start), (own_rows + 2 * block, own_cols + 2 * block))
            row_blocks = lax.dynamic_slice(row_pad, (to_index(col_rank * (own_cols // block)), zero, zero, zero), (own_cols // block + 2, 2, block, block))
            col_blocks = lax.dynamic_slice(col_pad, (to_index(row_rank * (own_rows // block)), zero, zero, zero), (own_rows // block + 2, 2, block, block))
            correction = solve_local(resid_ext, wave_ext, row_blocks, col_blocks, live_rect, signs)
            return correction[:, :, block:block + own_rows, block:block + own_cols]

        pieces = lax.map(solve_one, jnp.arange(N_GX * N_GY, dtype=jnp.int32))
        pieces = pieces.reshape(N_GX, N_GY, 2, 2, own_rows, own_cols).transpose(2, 3, 0, 4, 1, 5).reshape(2, 2, grid_rows, grid_cols)
        solution = solution + pieces
    return solution
```

```python
import jax
import jax.numpy as jnp
from jax import lax
from jax.sharding import PartitionSpec as P

ITERS = 2
SWEEPS = 4


DAMPING = 0.5
ROBIN_COEF = 0.5


def with_halo(shard, sides, width):
    for axis, dim in sides:
        peers, length = (lax.axis_size(axis), shard.shape[dim])
        up = [(i, (i + 1) % peers) for i in range(peers - 1)]
        down = [(j, i) for i, j in up]
        last = lax.slice_in_dim(shard, length - width, length, axis=dim)
        first = lax.slice_in_dim(shard, 0, width, axis=dim)
        before = lax.ppermute(last, axis, up)
        after = lax.ppermute(first, axis, down)
        shard = jnp.concatenate([before, shard, after], axis=dim)
    return shard


def to_index(value):
    return jnp.asarray(value).astype(jnp.int32)


def slice_line(values, start, axis):
    starts = [to_index(0) for _ in range(values.ndim)]
    starts[axis] = to_index(start)
    sizes = list(values.shape)
    sizes[axis] = 1
    return lax.dynamic_slice(values, starts, sizes)


def fill_ghost(values, upper, lower, left, right, signs):
    upper, lower, left, right = (to_index(upper), to_index(lower), to_index(left), to_index(right))
    height, breadth = (values.shape[2], values.shape[3])
    row_ids = lax.broadcasted_iota(jnp.int32, (height, 1), 0)
    col_ids = lax.broadcasted_iota(jnp.int32, (1, breadth), 1)
    upper_row = slice_line(values, upper, 2)
    lower_row = slice_line(values, lower - 1, 2)
    values = jnp.where(row_ids < upper, upper_row, jnp.where(row_ids >= lower, lower_row, values))
    left_col = slice_line(values, left, 3)
    right_col = slice_line(values, right - 1, 3)
    values = jnp.where(col_ids < left, left_col, jnp.where(col_ids >= right, right_col, values))
    inside = (row_ids >= upper) & (row_ids < lower) & (col_ids >= left) & (col_ids < right)
    real_part = values[:, 0]
    imag_part = values[:, 1]
    ghost_cycle = jnp.stack(
        [real_part + signs * ROBIN_COEF * imag_part, imag_part - signs * ROBIN_COEF * real_part],
        axis=1,
    )
    return jnp.where(inside, values, ghost_cycle)


def apply_operator(padded, wave_cells, signs):
    centre = padded[:, :, 1:-1, 1:-1]
    edge_sum = (
        padded[:, :, :-2, 1:-1]
        + padded[:, :, 2:, 1:-1]
        + padded[:, :, 1:-1, :-2]
        + padded[:, :, 1:-1, 2:]
    )
    corner_sum = (
        padded[:, :, :-2, :-2]
        + padded[:, :, :-2, 2:]
        + padded[:, :, 2:, :-2]
        + padded[:, :, 2:, 2:]
    )
    laplace = (4.0 * edge_sum + corner_sum - 20.0 * centre) / 6.0
    real_part = centre[:, 0]
    imag_part = centre[:, 1]
    mass_term = jnp.stack(
        [real_part - signs * DAMPING * imag_part, imag_part + signs * DAMPING * real_part], axis=1
    )
    return -laplace - wave_cells * mass_term


def combine_parts(products, signs, shape):
    real_out = products[0][:, 0] - signs[..., None] * products[1][:, 1]
    imag_out = products[0][:, 1] + signs[..., None] * products[1][:, 0]
    return jnp.stack([real_out, imag_out], axis=1).reshape(shape)


def along_rows(values, inverse, signs):
    block = inverse.shape[-1]
    blocked = values.reshape(values.shape[0], 2, values.shape[2], values.shape[3] // block, block)
    products = jnp.einsum("qmok,fchqk->mfchqo", inverse, blocked, precision=lax.Precision.HIGHEST)
    return combine_parts(products, signs, values.shape)


def along_cols(values, inverse, signs):
    block = inverse.shape[-1]
    blocked = values.reshape(values.shape[0], 2, values.shape[2] // block, block, values.shape[3])
    products = jnp.einsum("qmok,fcqkw->mfcqow", inverse, blocked, precision=lax.Precision.HIGHEST)
    return combine_parts(products, signs, values.shape)


def solve_local(resid_ext, wave_ext, row_blocks, col_blocks, live_rect, signs):
    upper, lower, left, right = [to_index(v) for v in live_rect]
    height, breadth = (resid_ext.shape[2], resid_ext.shape[3])
    row_ids = lax.broadcasted_iota(jnp.int32, (height, 1), 0)
    col_ids = lax.broadcasted_iota(jnp.int32, (1, breadth), 1)
    live_mask = (
        (row_ids >= upper) & (row_ids < lower) & (col_ids >= left) & (col_ids < right)
    ).astype(resid_ext.dtype)
    local_res = resid_ext * live_mask
    correction = jnp.zeros_like(resid_ext)
    for sweep_index in range(SWEEPS):
        if sweep_index > 0:
            padded = jnp.pad(correction, ((0, 0), (0, 0), (1, 1), (1, 1)))
            padded = fill_ghost(padded, upper + 1, lower + 1, left + 1, right + 1, signs)
            local_res = live_mask * (resid_ext - apply_operator(padded, wave_ext, signs))
        if sweep_index % 2 == 0:
            update = along_rows(local_res, row_blocks, signs)
        else:
            update = along_cols(local_res, col_blocks, signs)
        correction = correction + live_mask * update
    return correction


def exchange(x, row_width, col_width, extra=None):
    row_count = lax.axis_size("gx")
    col_count = lax.axis_size("gy")
    height, breadth = (x.shape[-2], x.shape[-1])
    pieces = {}
    for dr in (-1, 0, 1):
        for dc in (-1, 0, 1):
            if dr == 0 and dc == 0:
                continue
            slab = x
            if dr == -1:
                slab = lax.slice_in_dim(slab, height - row_width, height, axis=x.ndim - 2)
            elif dr == 1:
                slab = lax.slice_in_dim(slab, 0, row_width, axis=x.ndim - 2)
            if dc == -1:
                slab = lax.slice_in_dim(slab, breadth - col_width, breadth, axis=x.ndim - 1)
            elif dc == 1:
                slab = lax.slice_in_dim(slab, 0, col_width, axis=x.ndim - 1)
            if extra is not None and (dr, dc) in extra:
                slab = jnp.concatenate([slab, extra[(dr, dc)]], axis=0)
            perm = []
            for r in range(row_count):
                for c in range(col_count):
                    rr, cc = (r - dr, c - dc)
                    if 0 <= rr < row_count and 0 <= cc < col_count:
                        perm.append((r * col_count + c, rr * col_count + cc))
            pieces[(dr, dc)] = lax.ppermute(slab, ("gx", "gy"), perm)
    return pieces


def assemble(pieces, centre, lead):
    rows = []
    for dr in (-1, 0, 1):
        row = []
        for dc in (-1, 0, 1):
            part = centre if (dr == 0 and dc == 0) else pieces[(dr, dc)][:lead]
            row.append(part)
        rows.append(jnp.concatenate(row, axis=-1))
    return jnp.concatenate(rows, axis=-2)


def shards(sources, wavenumber, row_inverse, col_inverse, reach_steps):
    own_rows, own_cols = (sources.shape[2], sources.shape[3])
    block = row_inverse.shape[-1]
    step_cells = block // 4
    signs = jnp.array([1.0, -1.0], dtype=sources.dtype).reshape(2, 1, 1)
    row_rank = to_index(lax.axis_index("gx"))
    col_rank = to_index(lax.axis_index("gy"))
    row_count = lax.axis_size("gx")
    col_count = lax.axis_size("gy")
    zero = to_index(0)
    widths = reach_steps.reshape(4) * step_cells
    upper_w = jnp.where(row_rank > 0, widths[0], zero)
    lower_w = jnp.where(row_rank < row_count - 1, widths[1], zero)
    left_w = jnp.where(col_rank > 0, widths[2], zero)
    right_w = jnp.where(col_rank < col_count - 1, widths[3], zero)
    live_rect = (
        block - upper_w,
        block + own_rows + lower_w,
        block - left_w,
        block + own_cols + right_w,
    )
    stacked = jnp.concatenate([sources.reshape(4, own_rows, own_cols), wavenumber[None]], axis=0)
    row_pair = row_inverse.shape[0]
    col_pair = col_inverse.shape[0]
    extra = {
        (0, -1): row_inverse[row_pair - 1].reshape(1, own_rows, block),
        (0, 1): row_inverse[0].reshape(1, own_rows, block),
        (-1, 0): col_inverse[col_pair - 1].reshape(1, block, own_cols),
        (1, 0): col_inverse[0].reshape(1, block, own_cols),
    }
    pieces = exchange(stacked, block, block, extra)
    stacked_ext = assemble(pieces, stacked, 5)
    sources_ext = stacked_ext[:4].reshape(2, 2, own_rows + 2 * block, own_cols + 2 * block)
    wave_ext = stacked_ext[4]
    inv_shape = (1,) + row_inverse.shape[1:]
    row_blocks = jnp.concatenate(
        [pieces[(0, -1)][5:].reshape(inv_shape), row_inverse, pieces[(0, 1)][5:].reshape(inv_shape)], axis=0
    )
    col_blocks = jnp.concatenate(
        [pieces[(-1, 0)][5:].reshape(inv_shape), col_inverse, pieces[(1, 0)][5:].reshape(inv_shape)], axis=0
    )
    width = block + 1
    grid_upper = to_index(jnp.where(row_rank == 0, width, 0))
    grid_lower = to_index(jnp.where(row_rank == row_count - 1, width + own_rows, own_rows + 2 * width))
    grid_left = to_index(jnp.where(col_rank == 0, width, 0))
    grid_right = to_index(jnp.where(col_rank == col_count - 1, width + own_cols, own_cols + 2 * width))
    solution = None
    for iteration in range(ITERS):
        if iteration == 0:
            resid_ext = sources_ext
        else:
            padded = assemble(exchange(solution, width, width), solution, 2)
            padded = fill_ghost(padded, grid_upper, grid_lower, grid_left, grid_right, signs)
            resid_ext = sources_ext - apply_operator(padded, wave_ext, signs)
        correction = solve_local(resid_ext, wave_ext, row_blocks, col_blocks, live_rect, signs)
        own = correction[:, :, block : block + own_rows, block : block + own_cols]
        solution = own if solution is None else solution + own
    return solution


def solution(mesh):
    return jax.shard_map(
        shards,
        mesh=mesh,
        in_specs=(
            P(None, None, "gx", "gy"),
            P("gx", "gy"),
            P("gy", None, None, None),
            P("gx", None, None, None),
            P("gx", "gy", None),
        ),
        out_specs=P(None, None, "gx", "gy"),
        check_vma=False,
    )
```

```python
import jax
import jax.numpy as jnp
from jax import lax
from jax.sharding import PartitionSpec as P
from jax.experimental import pallas as pl
from jax.experimental.pallas import tpu as pltpu

ITERS = 2
SWEEPS = 4


DAMPING = 0.5
ROBIN_COEF = 0.5


def with_halo(shard, sides, width):
    for axis, dim in sides:
        peers, length = (lax.axis_size(axis), shard.shape[dim])
        up = [(i, (i + 1) % peers) for i in range(peers - 1)]
        down = [(j, i) for i, j in up]
        last = lax.slice_in_dim(shard, length - width, length, axis=dim)
        first = lax.slice_in_dim(shard, 0, width, axis=dim)
        before = lax.ppermute(last, axis, up)
        after = lax.ppermute(first, axis, down)
        shard = jnp.concatenate([before, shard, after], axis=dim)
    return shard


def to_index(value):
    return jnp.asarray(value).astype(jnp.int32)


def slice_line(values, start, axis):
    starts = [to_index(0) for _ in range(values.ndim)]
    starts[axis] = to_index(start)
    sizes = list(values.shape)
    sizes[axis] = 1
    return lax.dynamic_slice(values, starts, sizes)


def fill_ghost(values, upper, lower, left, right, signs):
    upper, lower, left, right = (to_index(upper), to_index(lower), to_index(left), to_index(right))
    height, breadth = (values.shape[2], values.shape[3])
    row_ids = lax.broadcasted_iota(jnp.int32, (height, 1), 0)
    col_ids = lax.broadcasted_iota(jnp.int32, (1, breadth), 1)
    upper_row = slice_line(values, upper, 2)
    lower_row = slice_line(values, lower - 1, 2)
    values = jnp.where(row_ids < upper, upper_row, jnp.where(row_ids >= lower, lower_row, values))
    left_col = slice_line(values, left, 3)
    right_col = slice_line(values, right - 1, 3)
    values = jnp.where(col_ids < left, left_col, jnp.where(col_ids >= right, right_col, values))
    inside = (row_ids >= upper) & (row_ids < lower) & (col_ids >= left) & (col_ids < right)
    real_part = values[:, 0]
    imag_part = values[:, 1]
    ghost_cycle = jnp.stack(
        [real_part + signs * ROBIN_COEF * imag_part, imag_part - signs * ROBIN_COEF * real_part],
        axis=1,
    )
    return jnp.where(inside, values, ghost_cycle)


def apply_operator(padded, wave_cells, signs):
    centre = padded[:, :, 1:-1, 1:-1]
    edge_sum = (
        padded[:, :, :-2, 1:-1]
        + padded[:, :, 2:, 1:-1]
        + padded[:, :, 1:-1, :-2]
        + padded[:, :, 1:-1, 2:]
    )
    corner_sum = (
        padded[:, :, :-2, :-2]
        + padded[:, :, :-2, 2:]
        + padded[:, :, 2:, :-2]
        + padded[:, :, 2:, 2:]
    )
    laplace = (4.0 * edge_sum + corner_sum - 20.0 * centre) / 6.0
    real_part = centre[:, 0]
    imag_part = centre[:, 1]
    mass_term = jnp.stack(
        [real_part - signs * DAMPING * imag_part, imag_part + signs * DAMPING * real_part], axis=1
    )
    return -laplace - wave_cells * mass_term


def combine_parts(products, signs, shape):
    real_out = products[0][:, 0] - signs[..., None] * products[1][:, 1]
    imag_out = products[0][:, 1] + signs[..., None] * products[1][:, 0]
    return jnp.stack([real_out, imag_out], axis=1).reshape(shape)


def along_rows(values, inverse, signs):
    block = inverse.shape[-1]
    blocked = values.reshape(values.shape[0], 2, values.shape[2], values.shape[3] // block, block)
    products = jnp.einsum("qmok,fchqk->mfchqo", inverse, blocked, precision=lax.Precision.HIGHEST)
    return combine_parts(products, signs, values.shape)


def along_cols(values, inverse, signs):
    block = inverse.shape[-1]
    blocked = values.reshape(values.shape[0], 2, values.shape[2] // block, block, values.shape[3])
    products = jnp.einsum("qmok,fcqkw->mfcqow", inverse, blocked, precision=lax.Precision.HIGHEST)
    return combine_parts(products, signs, values.shape)


def solve_local(resid_ext, wave_ext, row_blocks, col_blocks, live_rect, signs):
    upper, lower, left, right = [to_index(v) for v in live_rect]
    height, breadth = (resid_ext.shape[2], resid_ext.shape[3])
    row_ids = lax.broadcasted_iota(jnp.int32, (height, 1), 0)
    col_ids = lax.broadcasted_iota(jnp.int32, (1, breadth), 1)
    live_mask = (
        (row_ids >= upper) & (row_ids < lower) & (col_ids >= left) & (col_ids < right)
    ).astype(resid_ext.dtype)
    local_res = resid_ext * live_mask
    correction = jnp.zeros_like(resid_ext)
    for sweep_index in range(SWEEPS):
        if sweep_index > 0:
            padded = jnp.pad(correction, ((0, 0), (0, 0), (1, 1), (1, 1)))
            padded = fill_ghost(padded, upper + 1, lower + 1, left + 1, right + 1, signs)
            local_res = live_mask * (resid_ext - apply_operator(padded, wave_ext, signs))
        if sweep_index % 2 == 0:
            update = along_rows(local_res, row_blocks, signs)
        else:
            update = along_cols(local_res, col_blocks, signs)
        correction = correction + live_mask * update
    return correction


def exchange(x, row_width, col_width, extra=None):
    row_count = lax.axis_size("gx")
    col_count = lax.axis_size("gy")
    height, breadth = (x.shape[-2], x.shape[-1])
    pieces = {}
    for dr in (-1, 0, 1):
        for dc in (-1, 0, 1):
            if dr == 0 and dc == 0:
                continue
            slab = x
            if dr == -1:
                slab = lax.slice_in_dim(slab, height - row_width, height, axis=x.ndim - 2)
            elif dr == 1:
                slab = lax.slice_in_dim(slab, 0, row_width, axis=x.ndim - 2)
            if dc == -1:
                slab = lax.slice_in_dim(slab, breadth - col_width, breadth, axis=x.ndim - 1)
            elif dc == 1:
                slab = lax.slice_in_dim(slab, 0, col_width, axis=x.ndim - 1)
            if extra is not None and (dr, dc) in extra:
                slab = jnp.concatenate([slab, extra[(dr, dc)]], axis=0)
            perm = []
            for r in range(row_count):
                for c in range(col_count):
                    rr, cc = (r - dr, c - dc)
                    if 0 <= rr < row_count and 0 <= cc < col_count:
                        perm.append((r * col_count + c, rr * col_count + cc))
            pieces[(dr, dc)] = lax.ppermute(slab, ("gx", "gy"), perm)
    return pieces


def assemble(pieces, centre, lead):
    rows = []
    for dr in (-1, 0, 1):
        row = []
        for dc in (-1, 0, 1):
            part = centre if (dr == 0 and dc == 0) else pieces[(dr, dc)][:lead]
            row.append(part)
        rows.append(jnp.concatenate(row, axis=-1))
    return jnp.concatenate(rows, axis=-2)


def shift_rows(x, step):
    return pltpu.roll(x, step % x.shape[0], 0)


def shift_cols(x, step):
    return pltpu.roll(x, step % x.shape[1], 1)


def solve_kernel(rect_ref, resid_ref, wave_ref, wrow_ref, wcol_ref, out_ref):
    height, breadth = (resid_ref.shape[2], resid_ref.shape[3])
    half = height // 2
    upper, lower, left, right = (rect_ref[0], rect_ref[1], rect_ref[2], rect_ref[3])
    row_ids = lax.broadcasted_iota(jnp.int32, (height, breadth), 0)
    col_ids = lax.broadcasted_iota(jnp.int32, (height, breadth), 1)
    live = (row_ids >= upper) & (row_ids < lower) & (col_ids >= left) & (col_ids < right)
    top, bottom = (row_ids == upper, row_ids == lower - 1)
    first, last = (col_ids == left, col_ids == right - 1)
    wave = wave_ref[...]
    zero = jnp.zeros((height, breadth), jnp.float32)

    def mask(x):
        return jnp.where(live, x, zero)

    def neighbours(x):
        up = jnp.where(top, x, shift_rows(x, 1))
        down = jnp.where(bottom, x, shift_rows(x, -1))
        edge, edge_ghost, corner, corner_ghost = (zero, zero, zero, zero)
        for line, line_flag in ((up, top), (x, None), (down, bottom)):
            lft = jnp.where(first, line, shift_cols(line, 1))
            rgt = jnp.where(last, line, shift_cols(line, -1))
            lft_flag = first if line_flag is None else (first | line_flag)
            rgt_flag = last if line_flag is None else (last | line_flag)
            if line_flag is None:
                edge = edge + lft + rgt
                edge_ghost = edge_ghost + jnp.where(lft_flag, lft, zero) + jnp.where(rgt_flag, rgt, zero)
            else:
                edge = edge + line
                edge_ghost = edge_ghost + jnp.where(line_flag, line, zero)
                corner = corner + lft + rgt
                corner_ghost = corner_ghost + jnp.where(lft_flag, lft, zero) + jnp.where(rgt_flag, rgt, zero)
        return edge, edge_ghost, corner, corner_ghost

    def operator(real_part, imag_part, sign):
        er, egr, cr, cgr = neighbours(real_part)
        ei, egi, ci, cgi = neighbours(imag_part)
        edge_r = er + sign * ROBIN_COEF * egi
        edge_i = ei - sign * ROBIN_COEF * egr
        corner_r = cr + sign * ROBIN_COEF * cgi
        corner_i = ci - sign * ROBIN_COEF * cgr
        lap_r = (4.0 * edge_r + corner_r - 20.0 * real_part) / 6.0
        lap_i = (4.0 * edge_i + corner_i - 20.0 * imag_part) / 6.0
        mass_r = real_part - sign * DAMPING * imag_part
        mass_i = imag_part + sign * DAMPING * real_part
        return (-lap_r - wave * mass_r, -lap_i - wave * mass_i)

    def dot(a, b):
        return jnp.dot(a, b, precision=lax.Precision.HIGHEST, preferred_element_type=jnp.float32)

    def rows_apply(real_part, imag_part, sign):
        outs_r, outs_i = ([], [])
        for h in range(breadth // half):
            cols = slice(h * half, (h + 1) * half)
            stacked = jnp.concatenate([real_part[:, cols], imag_part[:, cols]], axis=0)
            prod = dot(stacked, wrow_ref[h])
            outs_r.append(prod[:height, :half] - sign * prod[height:, half:])
            outs_i.append(prod[height:, :half] + sign * prod[:height, half:])
        return (jnp.concatenate(outs_r, axis=1), jnp.concatenate(outs_i, axis=1))

    def cols_apply(real_part, imag_part, sign):
        outs_r, outs_i = ([], [])
        for h in range(height // half):
            rows = slice(h * half, (h + 1) * half)
            stacked = jnp.concatenate([real_part[rows, :], imag_part[rows, :]], axis=1)
            prod = dot(wcol_ref[h], stacked)
            outs_r.append(prod[:half, :breadth] - sign * prod[half:, breadth:])
            outs_i.append(prod[:half, breadth:] + sign * prod[half:, :breadth])
        return (jnp.concatenate(outs_r, axis=0), jnp.concatenate(outs_i, axis=0))

    for problem in range(resid_ref.shape[0]):
        sign = 1.0 - 2.0 * problem
        res_r = resid_ref[problem, 0]
        res_i = resid_ref[problem, 1]
        loc_r, loc_i = (mask(res_r), mask(res_i))
        cor_r, cor_i = (zero, zero)
        for sweep_index in range(SWEEPS):
            if sweep_index > 0:
                op_r, op_i = operator(cor_r, cor_i, sign)
                loc_r, loc_i = (mask(res_r - op_r), mask(res_i - op_i))
            if sweep_index % 2 == 0:
                up_r, up_i = rows_apply(loc_r, loc_i, sign)
            else:
                up_r, up_i = cols_apply(loc_r, loc_i, sign)
            cor_r, cor_i = (cor_r + mask(up_r), cor_i + mask(up_i))
        out_ref[problem, 0] = cor_r
        out_ref[problem, 1] = cor_i


def line_matrices(row_blocks, col_blocks):
    block = row_blocks.shape[-1]
    eye = jnp.eye(2, dtype=row_blocks.dtype)

    def pair_diag(mats):
        return jnp.einsum("qp,qok->qopk", eye, mats).reshape(2 * block, 2 * block)

    row_mats, col_mats = ([], [])
    for h in range(row_blocks.shape[0] // 2):
        pair = row_blocks[2 * h : 2 * h + 2]
        parts = [pair_diag(jnp.swapaxes(pair[:, m], 1, 2)) for m in range(2)]
        row_mats.append(jnp.concatenate(parts, axis=1))
    for h in range(col_blocks.shape[0] // 2):
        pair = col_blocks[2 * h : 2 * h + 2]
        parts = [pair_diag(pair[:, m]) for m in range(2)]
        col_mats.append(jnp.concatenate(parts, axis=0))
    return jnp.stack(row_mats), jnp.stack(col_mats)


def solve_local_kernel(resid_ext, wave_ext, row_mats, col_mats, live_rect, interpret=False):
    rect = jnp.stack([to_index(v) for v in live_rect])
    vmem = pltpu.MemorySpace.VMEM if hasattr(pltpu, "MemorySpace") else pltpu.VMEM
    return pl.pallas_call(
        solve_kernel,
        out_shape=jax.ShapeDtypeStruct(resid_ext.shape, resid_ext.dtype),
        in_specs=[pl.BlockSpec(memory_space=pltpu.SMEM)] + [pl.BlockSpec(memory_space=vmem)] * 4,
        out_specs=pl.BlockSpec(memory_space=vmem),
        interpret=interpret,
    )(rect, resid_ext, wave_ext, row_mats, col_mats)


def shards(sources, wavenumber, row_inverse, col_inverse, reach_steps):
    own_rows, own_cols = (sources.shape[2], sources.shape[3])
    block = row_inverse.shape[-1]
    step_cells = block // 4
    signs = jnp.array([1.0, -1.0], dtype=sources.dtype).reshape(2, 1, 1)
    row_rank = to_index(lax.axis_index("gx"))
    col_rank = to_index(lax.axis_index("gy"))
    row_count = lax.axis_size("gx")
    col_count = lax.axis_size("gy")
    zero = to_index(0)
    widths = reach_steps.reshape(4) * step_cells
    upper_w = jnp.where(row_rank > 0, widths[0], zero)
    lower_w = jnp.where(row_rank < row_count - 1, widths[1], zero)
    left_w = jnp.where(col_rank > 0, widths[2], zero)
    right_w = jnp.where(col_rank < col_count - 1, widths[3], zero)
    live_rect = (
        block - upper_w,
        block + own_rows + lower_w,
        block - left_w,
        block + own_cols + right_w,
    )
    stacked = jnp.concatenate([sources.reshape(4, own_rows, own_cols), wavenumber[None]], axis=0)
    row_pair = row_inverse.shape[0]
    col_pair = col_inverse.shape[0]
    extra = {
        (0, -1): row_inverse[row_pair - 1].reshape(1, own_rows, block),
        (0, 1): row_inverse[0].reshape(1, own_rows, block),
        (-1, 0): col_inverse[col_pair - 1].reshape(1, block, own_cols),
        (1, 0): col_inverse[0].reshape(1, block, own_cols),
    }
    pieces = exchange(stacked, block, block, extra)
    stacked_ext = assemble(pieces, stacked, 5)
    sources_ext = stacked_ext[:4].reshape(2, 2, own_rows + 2 * block, own_cols + 2 * block)
    wave_ext = stacked_ext[4]
    inv_shape = (1,) + row_inverse.shape[1:]
    row_blocks = jnp.concatenate(
        [pieces[(0, -1)][5:].reshape(inv_shape), row_inverse, pieces[(0, 1)][5:].reshape(inv_shape)], axis=0
    )
    col_blocks = jnp.concatenate(
        [pieces[(-1, 0)][5:].reshape(inv_shape), col_inverse, pieces[(1, 0)][5:].reshape(inv_shape)], axis=0
    )
    row_mats, col_mats = line_matrices(row_blocks, col_blocks)
    width = block + 1
    grid_upper = to_index(jnp.where(row_rank == 0, width, 0))
    grid_lower = to_index(jnp.where(row_rank == row_count - 1, width + own_rows, own_rows + 2 * width))
    grid_left = to_index(jnp.where(col_rank == 0, width, 0))
    grid_right = to_index(jnp.where(col_rank == col_count - 1, width + own_cols, own_cols + 2 * width))
    solution = None
    for iteration in range(ITERS):
        if iteration == 0:
            resid_ext = sources_ext
        else:
            padded = assemble(exchange(solution, width, width), solution, 2)
            padded = fill_ghost(padded, grid_upper, grid_lower, grid_left, grid_right, signs)
            resid_ext = sources_ext - apply_operator(padded, wave_ext, signs)
        correction = solve_local_kernel(resid_ext, wave_ext, row_mats, col_mats, live_rect)
        own = correction[:, :, block : block + own_rows, block : block + own_cols]
        solution = own if solution is None else solution + own
    return solution


def solution(mesh):
    return jax.shard_map(
        shards,
        mesh=mesh,
        in_specs=(
            P(None, None, "gx", "gy"),
            P("gx", "gy"),
            P("gy", None, None, None),
            P("gx", None, None, None),
            P("gx", "gy", None),
        ),
        out_specs=P(None, None, "gx", "gy"),
        check_vma=False,
    )
```

```python
import jax
import jax.numpy as jnp
from jax import lax
from jax.sharding import PartitionSpec as P
from jax.experimental import pallas as pl
from jax.experimental.pallas import tpu as pltpu

ITERS = 2
SWEEPS = 4


DAMPING = 0.5
ROBIN_COEF = 0.5


def with_halo(shard, sides, width):
    for axis, dim in sides:
        peers, length = (lax.axis_size(axis), shard.shape[dim])
        up = [(i, (i + 1) % peers) for i in range(peers - 1)]
        down = [(j, i) for i, j in up]
        last = lax.slice_in_dim(shard, length - width, length, axis=dim)
        first = lax.slice_in_dim(shard, 0, width, axis=dim)
        before = lax.ppermute(last, axis, up)
        after = lax.ppermute(first, axis, down)
        shard = jnp.concatenate([before, shard, after], axis=dim)
    return shard


def to_index(value):
    return jnp.asarray(value).astype(jnp.int32)


def slice_line(values, start, axis):
    starts = [to_index(0) for _ in range(values.ndim)]
    starts[axis] = to_index(start)
    sizes = list(values.shape)
    sizes[axis] = 1
    return lax.dynamic_slice(values, starts, sizes)


def fill_ghost(values, upper, lower, left, right, signs):
    upper, lower, left, right = (to_index(upper), to_index(lower), to_index(left), to_index(right))
    height, breadth = (values.shape[2], values.shape[3])
    row_ids = lax.broadcasted_iota(jnp.int32, (height, 1), 0)
    col_ids = lax.broadcasted_iota(jnp.int32, (1, breadth), 1)
    upper_row = slice_line(values, upper, 2)
    lower_row = slice_line(values, lower - 1, 2)
    values = jnp.where(row_ids < upper, upper_row, jnp.where(row_ids >= lower, lower_row, values))
    left_col = slice_line(values, left, 3)
    right_col = slice_line(values, right - 1, 3)
    values = jnp.where(col_ids < left, left_col, jnp.where(col_ids >= right, right_col, values))
    inside = (row_ids >= upper) & (row_ids < lower) & (col_ids >= left) & (col_ids < right)
    real_part = values[:, 0]
    imag_part = values[:, 1]
    ghost_cycle = jnp.stack(
        [real_part + signs * ROBIN_COEF * imag_part, imag_part - signs * ROBIN_COEF * real_part],
        axis=1,
    )
    return jnp.where(inside, values, ghost_cycle)


def apply_operator(padded, wave_cells, signs):
    centre = padded[:, :, 1:-1, 1:-1]
    edge_sum = (
        padded[:, :, :-2, 1:-1]
        + padded[:, :, 2:, 1:-1]
        + padded[:, :, 1:-1, :-2]
        + padded[:, :, 1:-1, 2:]
    )
    corner_sum = (
        padded[:, :, :-2, :-2]
        + padded[:, :, :-2, 2:]
        + padded[:, :, 2:, :-2]
        + padded[:, :, 2:, 2:]
    )
    laplace = (4.0 * edge_sum + corner_sum - 20.0 * centre) / 6.0
    real_part = centre[:, 0]
    imag_part = centre[:, 1]
    mass_term = jnp.stack(
        [real_part - signs * DAMPING * imag_part, imag_part + signs * DAMPING * real_part], axis=1
    )
    return -laplace - wave_cells * mass_term


def combine_parts(products, signs, shape):
    real_out = products[0][:, 0] - signs[..., None] * products[1][:, 1]
    imag_out = products[0][:, 1] + signs[..., None] * products[1][:, 0]
    return jnp.stack([real_out, imag_out], axis=1).reshape(shape)


def along_rows(values, inverse, signs):
    block = inverse.shape[-1]
    blocked = values.reshape(values.shape[0], 2, values.shape[2], values.shape[3] // block, block)
    products = jnp.einsum("qmok,fchqk->mfchqo", inverse, blocked, precision=lax.Precision.HIGHEST)
    return combine_parts(products, signs, values.shape)


def along_cols(values, inverse, signs):
    block = inverse.shape[-1]
    blocked = values.reshape(values.shape[0], 2, values.shape[2] // block, block, values.shape[3])
    products = jnp.einsum("qmok,fcqkw->mfcqow", inverse, blocked, precision=lax.Precision.HIGHEST)
    return combine_parts(products, signs, values.shape)


def solve_local(resid_ext, wave_ext, row_blocks, col_blocks, live_rect, signs):
    upper, lower, left, right = [to_index(v) for v in live_rect]
    height, breadth = (resid_ext.shape[2], resid_ext.shape[3])
    row_ids = lax.broadcasted_iota(jnp.int32, (height, 1), 0)
    col_ids = lax.broadcasted_iota(jnp.int32, (1, breadth), 1)
    live_mask = (
        (row_ids >= upper) & (row_ids < lower) & (col_ids >= left) & (col_ids < right)
    ).astype(resid_ext.dtype)
    local_res = resid_ext * live_mask
    correction = jnp.zeros_like(resid_ext)
    for sweep_index in range(SWEEPS):
        if sweep_index > 0:
            padded = jnp.pad(correction, ((0, 0), (0, 0), (1, 1), (1, 1)))
            padded = fill_ghost(padded, upper + 1, lower + 1, left + 1, right + 1, signs)
            local_res = live_mask * (resid_ext - apply_operator(padded, wave_ext, signs))
        if sweep_index % 2 == 0:
            update = along_rows(local_res, row_blocks, signs)
        else:
            update = along_cols(local_res, col_blocks, signs)
        correction = correction + live_mask * update
    return correction


def exchange(x, row_width, col_width, extra=None):
    row_count = lax.axis_size("gx")
    col_count = lax.axis_size("gy")
    height, breadth = (x.shape[-2], x.shape[-1])
    pieces = {}
    for dr in (-1, 0, 1):
        for dc in (-1, 0, 1):
            if dr == 0 and dc == 0:
                continue
            slab = x
            if dr == -1:
                slab = lax.slice_in_dim(slab, height - row_width, height, axis=x.ndim - 2)
            elif dr == 1:
                slab = lax.slice_in_dim(slab, 0, row_width, axis=x.ndim - 2)
            if dc == -1:
                slab = lax.slice_in_dim(slab, breadth - col_width, breadth, axis=x.ndim - 1)
            elif dc == 1:
                slab = lax.slice_in_dim(slab, 0, col_width, axis=x.ndim - 1)
            if extra is not None and (dr, dc) in extra:
                slab = jnp.concatenate([slab, extra[(dr, dc)]], axis=0)
            perm = []
            for r in range(row_count):
                for c in range(col_count):
                    rr, cc = (r - dr, c - dc)
                    if 0 <= rr < row_count and 0 <= cc < col_count:
                        perm.append((r * col_count + c, rr * col_count + cc))
            pieces[(dr, dc)] = lax.ppermute(slab, ("gx", "gy"), perm)
    return pieces


def exchange_axis(x, axis, dim, width, extra_lo=None, extra_hi=None):
    peers, length = (lax.axis_size(axis), x.shape[dim])
    up = [(i, i + 1) for i in range(peers - 1)]
    down = [(j, i) for i, j in up]
    last = lax.slice_in_dim(x, length - width, length, axis=dim)
    first = lax.slice_in_dim(x, 0, width, axis=dim)
    if extra_lo is not None:
        last = jnp.concatenate([last, extra_lo], axis=0)
        first = jnp.concatenate([first, extra_hi], axis=0)
    return lax.ppermute(last, axis, up), lax.ppermute(first, axis, down)


def assemble(pieces, centre, lead):
    rows = []
    for dr in (-1, 0, 1):
        row = []
        for dc in (-1, 0, 1):
            part = centre if (dr == 0 and dc == 0) else pieces[(dr, dc)][:lead]
            row.append(part)
        rows.append(jnp.concatenate(row, axis=-1))
    return jnp.concatenate(rows, axis=-2)


def shift_rows(x, step):
    return pltpu.roll(x, step % x.shape[0], 0)


def shift_cols(x, step):
    return pltpu.roll(x, step % x.shape[1], 1)


def solve_kernel(rect_ref, resid_ref, wave_ref, wrow_ref, wcol_ref, out_ref):
    height, breadth = (resid_ref.shape[2], resid_ref.shape[3])
    half = height // 2
    upper, lower, left, right = (rect_ref[0], rect_ref[1], rect_ref[2], rect_ref[3])
    row_ids = lax.broadcasted_iota(jnp.int32, (height, breadth), 0)
    col_ids = lax.broadcasted_iota(jnp.int32, (height, breadth), 1)
    live = (row_ids >= upper) & (row_ids < lower) & (col_ids >= left) & (col_ids < right)
    top, bottom = (row_ids == upper, row_ids == lower - 1)
    first, last = (col_ids == left, col_ids == right - 1)
    wave = wave_ref[...]
    zero = jnp.zeros((height, breadth), jnp.float32)

    def mask(x):
        return jnp.where(live, x, zero)

    def neighbours(x):
        up = jnp.where(top, x, shift_rows(x, 1))
        down = jnp.where(bottom, x, shift_rows(x, -1))
        edge, edge_ghost, corner, corner_ghost = (zero, zero, zero, zero)
        for line, line_flag in ((up, top), (x, None), (down, bottom)):
            lft = jnp.where(first, line, shift_cols(line, 1))
            rgt = jnp.where(last, line, shift_cols(line, -1))
            lft_flag = first if line_flag is None else (first | line_flag)
            rgt_flag = last if line_flag is None else (last | line_flag)
            if line_flag is None:
                edge = edge + lft + rgt
                edge_ghost = edge_ghost + jnp.where(lft_flag, lft, zero) + jnp.where(rgt_flag, rgt, zero)
            else:
                edge = edge + line
                edge_ghost = edge_ghost + jnp.where(line_flag, line, zero)
                corner = corner + lft + rgt
                corner_ghost = corner_ghost + jnp.where(lft_flag, lft, zero) + jnp.where(rgt_flag, rgt, zero)
        return edge, edge_ghost, corner, corner_ghost

    def operator(real_part, imag_part, sign):
        er, egr, cr, cgr = neighbours(real_part)
        ei, egi, ci, cgi = neighbours(imag_part)
        edge_r = er + sign * ROBIN_COEF * egi
        edge_i = ei - sign * ROBIN_COEF * egr
        corner_r = cr + sign * ROBIN_COEF * cgi
        corner_i = ci - sign * ROBIN_COEF * cgr
        lap_r = (4.0 * edge_r + corner_r - 20.0 * real_part) / 6.0
        lap_i = (4.0 * edge_i + corner_i - 20.0 * imag_part) / 6.0
        mass_r = real_part - sign * DAMPING * imag_part
        mass_i = imag_part + sign * DAMPING * real_part
        return (-lap_r - wave * mass_r, -lap_i - wave * mass_i)

    def dot(a, b):
        return jnp.dot(a, b, precision=lax.Precision.HIGHEST, preferred_element_type=jnp.float32)

    def rows_apply(real_part, imag_part, sign):
        outs_r, outs_i = ([], [])
        for h in range(breadth // half):
            cols = slice(h * half, (h + 1) * half)
            stacked = jnp.concatenate([real_part[:, cols], imag_part[:, cols]], axis=0)
            prod = dot(stacked, wrow_ref[h])
            outs_r.append(prod[:height, :half] - sign * prod[height:, half:])
            outs_i.append(prod[height:, :half] + sign * prod[:height, half:])
        return (jnp.concatenate(outs_r, axis=1), jnp.concatenate(outs_i, axis=1))

    def cols_apply(real_part, imag_part, sign):
        outs_r, outs_i = ([], [])
        for h in range(height // half):
            rows = slice(h * half, (h + 1) * half)
            stacked = jnp.concatenate([real_part[rows, :], imag_part[rows, :]], axis=1)
            prod = dot(wcol_ref[h], stacked)
            outs_r.append(prod[:half, :breadth] - sign * prod[half:, breadth:])
            outs_i.append(prod[:half, breadth:] + sign * prod[half:, :breadth])
        return (jnp.concatenate(outs_r, axis=0), jnp.concatenate(outs_i, axis=0))

    for problem in range(resid_ref.shape[0]):
        sign = 1.0 - 2.0 * problem
        res_r = resid_ref[problem, 0]
        res_i = resid_ref[problem, 1]
        loc_r, loc_i = (mask(res_r), mask(res_i))
        cor_r, cor_i = (zero, zero)
        for sweep_index in range(SWEEPS):
            if sweep_index > 0:
                op_r, op_i = operator(cor_r, cor_i, sign)
                loc_r, loc_i = (mask(res_r - op_r), mask(res_i - op_i))
            if sweep_index % 2 == 0:
                up_r, up_i = rows_apply(loc_r, loc_i, sign)
            else:
                up_r, up_i = cols_apply(loc_r, loc_i, sign)
            cor_r, cor_i = (cor_r + mask(up_r), cor_i + mask(up_i))
        out_ref[problem, 0] = cor_r
        out_ref[problem, 1] = cor_i


def line_matrices(row_blocks, col_blocks):
    block = row_blocks.shape[-1]
    eye = jnp.eye(2, dtype=row_blocks.dtype)

    def pair_diag(mats):
        return jnp.einsum("qp,qok->qopk", eye, mats).reshape(2 * block, 2 * block)

    row_mats, col_mats = ([], [])
    for h in range(row_blocks.shape[0] // 2):
        pair = row_blocks[2 * h : 2 * h + 2]
        parts = [pair_diag(jnp.swapaxes(pair[:, m], 1, 2)) for m in range(2)]
        row_mats.append(jnp.concatenate(parts, axis=1))
    for h in range(col_blocks.shape[0] // 2):
        pair = col_blocks[2 * h : 2 * h + 2]
        parts = [pair_diag(pair[:, m]) for m in range(2)]
        col_mats.append(jnp.concatenate(parts, axis=0))
    return jnp.stack(row_mats), jnp.stack(col_mats)


def solve_local_kernel(resid_ext, wave_ext, row_mats, col_mats, live_rect, interpret=False):
    rect = jnp.stack([to_index(v) for v in live_rect])
    vmem = pltpu.MemorySpace.VMEM if hasattr(pltpu, "MemorySpace") else pltpu.VMEM
    return pl.pallas_call(
        solve_kernel,
        out_shape=jax.ShapeDtypeStruct(resid_ext.shape, resid_ext.dtype),
        in_specs=[pl.BlockSpec(memory_space=pltpu.SMEM)] + [pl.BlockSpec(memory_space=vmem)] * 4,
        out_specs=pl.BlockSpec(memory_space=vmem),
        interpret=interpret,
    )(rect, resid_ext, wave_ext, row_mats, col_mats)


def shards(sources, wavenumber, row_inverse, col_inverse, reach_steps):
    own_rows, own_cols = (sources.shape[2], sources.shape[3])
    block = row_inverse.shape[-1]
    step_cells = block // 4
    signs = jnp.array([1.0, -1.0], dtype=sources.dtype).reshape(2, 1, 1)
    row_rank = to_index(lax.axis_index("gx"))
    col_rank = to_index(lax.axis_index("gy"))
    row_count = lax.axis_size("gx")
    col_count = lax.axis_size("gy")
    zero = to_index(0)
    widths = reach_steps.reshape(4) * step_cells
    upper_w = jnp.where(row_rank > 0, widths[0], zero)
    lower_w = jnp.where(row_rank < row_count - 1, widths[1], zero)
    left_w = jnp.where(col_rank > 0, widths[2], zero)
    right_w = jnp.where(col_rank < col_count - 1, widths[3], zero)
    live_rect = (
        block - upper_w,
        block + own_rows + lower_w,
        block - left_w,
        block + own_cols + right_w,
    )
    stacked = jnp.concatenate([sources.reshape(4, own_rows, own_cols), wavenumber[None]], axis=0)
    lead = stacked.shape[0]
    col_pair = col_inverse.shape[0]
    row_pair = row_inverse.shape[0]
    inv_rows = col_inverse.shape[1] * block * block // own_cols
    before, after = exchange_axis(
        stacked, "gx", 1, block,
        col_inverse[col_pair - 1].reshape(1, inv_rows, own_cols), col_inverse[0].reshape(1, inv_rows, own_cols),
    )
    tall = jnp.concatenate([before[:lead, :block], stacked, after[:lead, :block]], axis=1)
    def inv_slab(mats):
        flat = mats.reshape(1, -1, block)
        return jnp.pad(flat, ((0, 0), (0, tall.shape[1] - flat.shape[1]), (0, 0)))
    left, right = exchange_axis(tall, "gy", 2, block, inv_slab(row_inverse[row_pair - 1]), inv_slab(row_inverse[0]))
    stacked_ext = jnp.concatenate([left[:lead], tall, right[:lead]], axis=2)
    sources_ext = stacked_ext[:4].reshape(2, 2, own_rows + 2 * block, own_cols + 2 * block)
    wave_ext = stacked_ext[4]
    inv_shape = (1,) + row_inverse.shape[1:]
    inv_size = row_inverse.shape[1] * block * block // block
    col_blocks = jnp.concatenate(
        [before[lead:].reshape(inv_shape), col_inverse, after[lead:].reshape(inv_shape)], axis=0
    )
    row_blocks = jnp.concatenate(
        [left[lead:, :inv_size].reshape(inv_shape), row_inverse, right[lead:, :inv_size].reshape(inv_shape)], axis=0
    )
    row_mats, col_mats = line_matrices(row_blocks, col_blocks)
    width = block + 1
    grid_upper = to_index(jnp.where(row_rank == 0, width, 0))
    grid_lower = to_index(jnp.where(row_rank == row_count - 1, width + own_rows, own_rows + 2 * width))
    grid_left = to_index(jnp.where(col_rank == 0, width, 0))
    grid_right = to_index(jnp.where(col_rank == col_count - 1, width + own_cols, own_cols + 2 * width))
    solution = None
    for iteration in range(ITERS):
        if iteration == 0:
            resid_ext = sources_ext
        else:
            before, after = exchange_axis(solution, "gx", 2, width)
            tall = jnp.concatenate([before, solution, after], axis=2)
            left, right = exchange_axis(tall, "gy", 3, width)
            padded = jnp.concatenate([left, tall, right], axis=3)
            padded = fill_ghost(padded, grid_upper, grid_lower, grid_left, grid_right, signs)
            resid_ext = sources_ext - apply_operator(padded, wave_ext, signs)
        correction = solve_local_kernel(resid_ext, wave_ext, row_mats, col_mats, live_rect)
        own = correction[:, :, block : block + own_rows, block : block + own_cols]
        solution = own if solution is None else solution + own
    return solution


def solution(mesh):
    return jax.shard_map(
        shards,
        mesh=mesh,
        in_specs=(
            P(None, None, "gx", "gy"),
            P("gx", "gy"),
            P("gy", None, None, None),
            P("gx", None, None, None),
            P("gx", "gy", None),
        ),
        out_specs=P(None, None, "gx", "gy"),
        check_vma=False,
    )
```

```python
import jax
import jax.numpy as jnp
from jax import lax
from jax.sharding import PartitionSpec as P
from jax.experimental import pallas as pl
from jax.experimental.pallas import tpu as pltpu

ITERS = 2
SWEEPS = 4


DAMPING = 0.5
ROBIN_COEF = 0.5


def with_halo(shard, sides, width):
    for axis, dim in sides:
        peers, length = (lax.axis_size(axis), shard.shape[dim])
        up = [(i, (i + 1) % peers) for i in range(peers - 1)]
        down = [(j, i) for i, j in up]
        last = lax.slice_in_dim(shard, length - width, length, axis=dim)
        first = lax.slice_in_dim(shard, 0, width, axis=dim)
        before = lax.ppermute(last, axis, up)
        after = lax.ppermute(first, axis, down)
        shard = jnp.concatenate([before, shard, after], axis=dim)
    return shard


def to_index(value):
    return jnp.asarray(value).astype(jnp.int32)


def slice_line(values, start, axis):
    starts = [to_index(0) for _ in range(values.ndim)]
    starts[axis] = to_index(start)
    sizes = list(values.shape)
    sizes[axis] = 1
    return lax.dynamic_slice(values, starts, sizes)


def fill_ghost(values, upper, lower, left, right, signs):
    upper, lower, left, right = (to_index(upper), to_index(lower), to_index(left), to_index(right))
    height, breadth = (values.shape[2], values.shape[3])
    row_ids = lax.broadcasted_iota(jnp.int32, (height, 1), 0)
    col_ids = lax.broadcasted_iota(jnp.int32, (1, breadth), 1)
    upper_row = slice_line(values, upper, 2)
    lower_row = slice_line(values, lower - 1, 2)
    values = jnp.where(row_ids < upper, upper_row, jnp.where(row_ids >= lower, lower_row, values))
    left_col = slice_line(values, left, 3)
    right_col = slice_line(values, right - 1, 3)
    values = jnp.where(col_ids < left, left_col, jnp.where(col_ids >= right, right_col, values))
    inside = (row_ids >= upper) & (row_ids < lower) & (col_ids >= left) & (col_ids < right)
    real_part = values[:, 0]
    imag_part = values[:, 1]
    ghost_cycle = jnp.stack(
        [real_part + signs * ROBIN_COEF * imag_part, imag_part - signs * ROBIN_COEF * real_part],
        axis=1,
    )
    return jnp.where(inside, values, ghost_cycle)


def apply_operator(padded, wave_cells, signs):
    centre = padded[:, :, 1:-1, 1:-1]
    edge_sum = (
        padded[:, :, :-2, 1:-1]
        + padded[:, :, 2:, 1:-1]
        + padded[:, :, 1:-1, :-2]
        + padded[:, :, 1:-1, 2:]
    )
    corner_sum = (
        padded[:, :, :-2, :-2]
        + padded[:, :, :-2, 2:]
        + padded[:, :, 2:, :-2]
        + padded[:, :, 2:, 2:]
    )
    laplace = (4.0 * edge_sum + corner_sum - 20.0 * centre) / 6.0
    real_part = centre[:, 0]
    imag_part = centre[:, 1]
    mass_term = jnp.stack(
        [real_part - signs * DAMPING * imag_part, imag_part + signs * DAMPING * real_part], axis=1
    )
    return -laplace - wave_cells * mass_term


def combine_parts(products, signs, shape):
    real_out = products[0][:, 0] - signs[..., None] * products[1][:, 1]
    imag_out = products[0][:, 1] + signs[..., None] * products[1][:, 0]
    return jnp.stack([real_out, imag_out], axis=1).reshape(shape)


def along_rows(values, inverse, signs):
    block = inverse.shape[-1]
    blocked = values.reshape(values.shape[0], 2, values.shape[2], values.shape[3] // block, block)
    products = jnp.einsum("qmok,fchqk->mfchqo", inverse, blocked, precision=lax.Precision.HIGHEST)
    return combine_parts(products, signs, values.shape)


def along_cols(values, inverse, signs):
    block = inverse.shape[-1]
    blocked = values.reshape(values.shape[0], 2, values.shape[2] // block, block, values.shape[3])
    products = jnp.einsum("qmok,fcqkw->mfcqow", inverse, blocked, precision=lax.Precision.HIGHEST)
    return combine_parts(products, signs, values.shape)


def solve_local(resid_ext, wave_ext, row_blocks, col_blocks, live_rect, signs):
    upper, lower, left, right = [to_index(v) for v in live_rect]
    height, breadth = (resid_ext.shape[2], resid_ext.shape[3])
    row_ids = lax.broadcasted_iota(jnp.int32, (height, 1), 0)
    col_ids = lax.broadcasted_iota(jnp.int32, (1, breadth), 1)
    live_mask = (
        (row_ids >= upper) & (row_ids < lower) & (col_ids >= left) & (col_ids < right)
    ).astype(resid_ext.dtype)
    local_res = resid_ext * live_mask
    correction = jnp.zeros_like(resid_ext)
    for sweep_index in range(SWEEPS):
        if sweep_index > 0:
            padded = jnp.pad(correction, ((0, 0), (0, 0), (1, 1), (1, 1)))
            padded = fill_ghost(padded, upper + 1, lower + 1, left + 1, right + 1, signs)
            local_res = live_mask * (resid_ext - apply_operator(padded, wave_ext, signs))
        if sweep_index % 2 == 0:
            update = along_rows(local_res, row_blocks, signs)
        else:
            update = along_cols(local_res, col_blocks, signs)
        correction = correction + live_mask * update
    return correction


def exchange(x, row_width, col_width, extra=None):
    row_count = lax.axis_size("gx")
    col_count = lax.axis_size("gy")
    height, breadth = (x.shape[-2], x.shape[-1])
    pieces = {}
    for dr in (-1, 0, 1):
        for dc in (-1, 0, 1):
            if dr == 0 and dc == 0:
                continue
            slab = x
            if dr == -1:
                slab = lax.slice_in_dim(slab, height - row_width, height, axis=x.ndim - 2)
            elif dr == 1:
                slab = lax.slice_in_dim(slab, 0, row_width, axis=x.ndim - 2)
            if dc == -1:
                slab = lax.slice_in_dim(slab, breadth - col_width, breadth, axis=x.ndim - 1)
            elif dc == 1:
                slab = lax.slice_in_dim(slab, 0, col_width, axis=x.ndim - 1)
            if extra is not None and (dr, dc) in extra:
                slab = jnp.concatenate([slab, extra[(dr, dc)]], axis=0)
            perm = []
            for r in range(row_count):
                for c in range(col_count):
                    rr, cc = (r - dr, c - dc)
                    if 0 <= rr < row_count and 0 <= cc < col_count:
                        perm.append((r * col_count + c, rr * col_count + cc))
            pieces[(dr, dc)] = lax.ppermute(slab, ("gx", "gy"), perm)
    return pieces


def exchange_axis(x, axis, dim, width, extra_lo=None, extra_hi=None):
    peers, length = (lax.axis_size(axis), x.shape[dim])
    up = [(i, i + 1) for i in range(peers - 1)]
    down = [(j, i) for i, j in up]
    last = lax.slice_in_dim(x, length - width, length, axis=dim)
    first = lax.slice_in_dim(x, 0, width, axis=dim)
    if extra_lo is not None:
        last = jnp.concatenate([last, extra_lo], axis=0)
        first = jnp.concatenate([first, extra_hi], axis=0)
    return lax.ppermute(last, axis, up), lax.ppermute(first, axis, down)


def assemble(pieces, centre, lead):
    rows = []
    for dr in (-1, 0, 1):
        row = []
        for dc in (-1, 0, 1):
            part = centre if (dr == 0 and dc == 0) else pieces[(dr, dc)][:lead]
            row.append(part)
        rows.append(jnp.concatenate(row, axis=-1))
    return jnp.concatenate(rows, axis=-2)


def shift_rows(x, step):
    return pltpu.roll(x, step % x.shape[0], 0)


def shift_cols(x, step):
    return pltpu.roll(x, step % x.shape[1], 1)


def solve_kernel(rect_ref, resid_ref, data_ref, wrow_ref, wcol_ref, out_ref):
    height, breadth = (resid_ref.shape[1], resid_ref.shape[2])
    half = height // 2
    upper, lower, left, right = (rect_ref[0], rect_ref[1], rect_ref[2], rect_ref[3])
    row_ids = lax.broadcasted_iota(jnp.int32, (height, breadth), 0)
    col_ids = lax.broadcasted_iota(jnp.int32, (height, breadth), 1)
    live = (row_ids >= upper) & (row_ids < lower) & (col_ids >= left) & (col_ids < right)
    top, bottom = (row_ids == upper, row_ids == lower - 1)
    first, last = (col_ids == left, col_ids == right - 1)
    wave = data_ref[4]
    zero = jnp.zeros((height, breadth), jnp.float32)

    def mask(x):
        return jnp.where(live, x, zero)

    def neighbours(x):
        up = jnp.where(top, x, shift_rows(x, 1))
        down = jnp.where(bottom, x, shift_rows(x, -1))
        edge, edge_ghost, corner, corner_ghost = (zero, zero, zero, zero)
        for line, line_flag in ((up, top), (x, None), (down, bottom)):
            lft = jnp.where(first, line, shift_cols(line, 1))
            rgt = jnp.where(last, line, shift_cols(line, -1))
            lft_flag = first if line_flag is None else (first | line_flag)
            rgt_flag = last if line_flag is None else (last | line_flag)
            if line_flag is None:
                edge = edge + lft + rgt
                edge_ghost = edge_ghost + jnp.where(lft_flag, lft, zero) + jnp.where(rgt_flag, rgt, zero)
            else:
                edge = edge + line
                edge_ghost = edge_ghost + jnp.where(line_flag, line, zero)
                corner = corner + lft + rgt
                corner_ghost = corner_ghost + jnp.where(lft_flag, lft, zero) + jnp.where(rgt_flag, rgt, zero)
        return edge, edge_ghost, corner, corner_ghost

    def operator(real_part, imag_part, sign):
        er, egr, cr, cgr = neighbours(real_part)
        ei, egi, ci, cgi = neighbours(imag_part)
        edge_r = er + sign * ROBIN_COEF * egi
        edge_i = ei - sign * ROBIN_COEF * egr
        corner_r = cr + sign * ROBIN_COEF * cgi
        corner_i = ci - sign * ROBIN_COEF * cgr
        lap_r = (4.0 * edge_r + corner_r - 20.0 * real_part) / 6.0
        lap_i = (4.0 * edge_i + corner_i - 20.0 * imag_part) / 6.0
        mass_r = real_part - sign * DAMPING * imag_part
        mass_i = imag_part + sign * DAMPING * real_part
        return (-lap_r - wave * mass_r, -lap_i - wave * mass_i)

    def dot(a, b):
        return jnp.dot(a, b, precision=lax.Precision.HIGHEST, preferred_element_type=jnp.float32)

    def rows_apply(real_part, imag_part, sign):
        outs_r, outs_i = ([], [])
        for h in range(breadth // half):
            cols = slice(h * half, (h + 1) * half)
            stacked = jnp.concatenate([real_part[:, cols], imag_part[:, cols]], axis=0)
            prod = dot(stacked, wrow_ref[h])
            outs_r.append(prod[:height, :half] - sign * prod[height:, half:])
            outs_i.append(prod[height:, :half] + sign * prod[:height, half:])
        return (jnp.concatenate(outs_r, axis=1), jnp.concatenate(outs_i, axis=1))

    def cols_apply(real_part, imag_part, sign):
        outs_r, outs_i = ([], [])
        for h in range(height // half):
            rows = slice(h * half, (h + 1) * half)
            stacked = jnp.concatenate([real_part[rows, :], imag_part[rows, :]], axis=1)
            prod = dot(wcol_ref[h], stacked)
            outs_r.append(prod[:half, :breadth] - sign * prod[half:, breadth:])
            outs_i.append(prod[:half, breadth:] + sign * prod[half:, :breadth])
        return (jnp.concatenate(outs_r, axis=0), jnp.concatenate(outs_i, axis=0))

    for problem in range(out_ref.shape[0]):
        sign = 1.0 - 2.0 * problem
        res_r = resid_ref[2 * problem]
        res_i = resid_ref[2 * problem + 1]
        loc_r, loc_i = (mask(res_r), mask(res_i))
        cor_r, cor_i = (zero, zero)
        for sweep_index in range(SWEEPS):
            if sweep_index > 0:
                op_r, op_i = operator(cor_r, cor_i, sign)
                loc_r, loc_i = (mask(res_r - op_r), mask(res_i - op_i))
            if sweep_index % 2 == 0:
                up_r, up_i = rows_apply(loc_r, loc_i, sign)
            else:
                up_r, up_i = cols_apply(loc_r, loc_i, sign)
            cor_r, cor_i = (cor_r + mask(up_r), cor_i + mask(up_i))
        out_ref[problem, 0] = cor_r
        out_ref[problem, 1] = cor_i


def line_matrices(row_blocks, col_blocks):
    block = row_blocks.shape[-1]
    eye = jnp.eye(2, dtype=row_blocks.dtype)
    halves = row_blocks.shape[0] // 2
    rows_t = jnp.transpose(row_blocks, (0, 3, 1, 2)).reshape(halves, 2, block, 2, block)
    row_mats = jnp.einsum("hakmo,ab->hakmbo", rows_t, eye).reshape(halves, 2 * block, 4 * block)
    cols = col_blocks.reshape(halves, 2, 2, block, block)
    col_mats = jnp.einsum("hamok,ab->hmaobk", cols, eye).reshape(halves, 4 * block, 2 * block)
    return row_mats, col_mats


def solve_local_kernel(resid_planes, data_ext, row_mats, col_mats, live_rect, interpret=False):
    rect = jnp.stack([to_index(v) for v in live_rect])
    out_shape = (2, 2) + resid_planes.shape[1:]
    vmem = pltpu.MemorySpace.VMEM if hasattr(pltpu, "MemorySpace") else pltpu.VMEM
    return pl.pallas_call(
        solve_kernel,
        out_shape=jax.ShapeDtypeStruct(out_shape, resid_planes.dtype),
        in_specs=[pl.BlockSpec(memory_space=pltpu.SMEM)] + [pl.BlockSpec(memory_space=vmem)] * 4,
        out_specs=pl.BlockSpec(memory_space=vmem),
        interpret=interpret,
    )(rect, resid_planes, data_ext, row_mats, col_mats)


def shards(sources, wavenumber, row_inverse, col_inverse, reach_steps):
    own_rows, own_cols = (sources.shape[2], sources.shape[3])
    block = row_inverse.shape[-1]
    step_cells = block // 4
    signs = jnp.array([1.0, -1.0], dtype=sources.dtype).reshape(2, 1, 1)
    row_rank = to_index(lax.axis_index("gx"))
    col_rank = to_index(lax.axis_index("gy"))
    row_count = lax.axis_size("gx")
    col_count = lax.axis_size("gy")
    zero = to_index(0)
    widths = reach_steps.reshape(4) * step_cells
    upper_w = jnp.where(row_rank > 0, widths[0], zero)
    lower_w = jnp.where(row_rank < row_count - 1, widths[1], zero)
    left_w = jnp.where(col_rank > 0, widths[2], zero)
    right_w = jnp.where(col_rank < col_count - 1, widths[3], zero)
    live_rect = (
        block - upper_w,
        block + own_rows + lower_w,
        block - left_w,
        block + own_cols + right_w,
    )
    stacked = jnp.concatenate([sources.reshape(4, own_rows, own_cols), wavenumber[None]], axis=0)
    lead = stacked.shape[0]
    col_pair = col_inverse.shape[0]
    row_pair = row_inverse.shape[0]
    inv_rows = col_inverse.shape[1] * block * block // own_cols
    before, after = exchange_axis(
        stacked, "gx", 1, block,
        col_inverse[col_pair - 1].reshape(1, inv_rows, own_cols), col_inverse[0].reshape(1, inv_rows, own_cols),
    )
    tall = jnp.concatenate([before[:lead, :block], stacked, after[:lead, :block]], axis=1)
    def inv_slab(mats):
        flat = mats.reshape(1, -1, block)
        return jnp.pad(flat, ((0, 0), (0, tall.shape[1] - flat.shape[1]), (0, 0)))
    left, right = exchange_axis(tall, "gy", 2, block, inv_slab(row_inverse[row_pair - 1]), inv_slab(row_inverse[0]))
    stacked_ext = jnp.concatenate([left[:lead], tall, right[:lead]], axis=2)
    sources_ext = stacked_ext[:4].reshape(2, 2, own_rows + 2 * block, own_cols + 2 * block)
    wave_ext = stacked_ext[4]
    inv_shape = (1,) + row_inverse.shape[1:]
    inv_size = row_inverse.shape[1] * block * block // block
    col_blocks = jnp.concatenate(
        [before[lead:].reshape(inv_shape), col_inverse, after[lead:].reshape(inv_shape)], axis=0
    )
    row_blocks = jnp.concatenate(
        [left[lead:, :inv_size].reshape(inv_shape), row_inverse, right[lead:, :inv_size].reshape(inv_shape)], axis=0
    )
    row_mats, col_mats = line_matrices(row_blocks, col_blocks)
    width = block + 1
    grid_upper = to_index(jnp.where(row_rank == 0, width, 0))
    grid_lower = to_index(jnp.where(row_rank == row_count - 1, width + own_rows, own_rows + 2 * width))
    grid_left = to_index(jnp.where(col_rank == 0, width, 0))
    grid_right = to_index(jnp.where(col_rank == col_count - 1, width + own_cols, own_cols + 2 * width))
    solution = None
    for iteration in range(ITERS):
        if iteration == 0:
            resid_planes = stacked_ext
        else:
            before, after = exchange_axis(solution, "gx", 2, width)
            tall = jnp.concatenate([before, solution, after], axis=2)
            left, right = exchange_axis(tall, "gy", 3, width)
            padded = jnp.concatenate([left, tall, right], axis=3)
            padded = fill_ghost(padded, grid_upper, grid_lower, grid_left, grid_right, signs)
            resid_ext = sources_ext - apply_operator(padded, wave_ext, signs)
            resid_planes = resid_ext.reshape((4,) + resid_ext.shape[2:])
        correction = solve_local_kernel(resid_planes, stacked_ext, row_mats, col_mats, live_rect)
        own = correction[:, :, block : block + own_rows, block : block + own_cols]
        solution = own if solution is None else solution + own
    return solution


def solution(mesh):
    return jax.shard_map(
        shards,
        mesh=mesh,
        in_specs=(
            P(None, None, "gx", "gy"),
            P("gx", "gy"),
            P("gy", None, None, None),
            P("gx", None, None, None),
            P("gx", "gy", None),
        ),
        out_specs=P(None, None, "gx", "gy"),
        check_vma=False,
    )
```

```python
import jax
import jax.numpy as jnp
from jax import lax
from jax.sharding import PartitionSpec as P
from jax.experimental import pallas as pl
from jax.experimental.pallas import tpu as pltpu

ITERS = 2
SWEEPS = 4


DAMPING = 0.5
ROBIN_COEF = 0.5


def with_halo(shard, sides, width):
    for axis, dim in sides:
        peers, length = (lax.axis_size(axis), shard.shape[dim])
        up = [(i, (i + 1) % peers) for i in range(peers - 1)]
        down = [(j, i) for i, j in up]
        last = lax.slice_in_dim(shard, length - width, length, axis=dim)
        first = lax.slice_in_dim(shard, 0, width, axis=dim)
        before = lax.ppermute(last, axis, up)
        after = lax.ppermute(first, axis, down)
        shard = jnp.concatenate([before, shard, after], axis=dim)
    return shard


def to_index(value):
    return jnp.asarray(value).astype(jnp.int32)


def slice_line(values, start, axis):
    starts = [to_index(0) for _ in range(values.ndim)]
    starts[axis] = to_index(start)
    sizes = list(values.shape)
    sizes[axis] = 1
    return lax.dynamic_slice(values, starts, sizes)


def fill_ghost(values, upper, lower, left, right, signs):
    upper, lower, left, right = (to_index(upper), to_index(lower), to_index(left), to_index(right))
    height, breadth = (values.shape[2], values.shape[3])
    row_ids = lax.broadcasted_iota(jnp.int32, (height, 1), 0)
    col_ids = lax.broadcasted_iota(jnp.int32, (1, breadth), 1)
    upper_row = slice_line(values, upper, 2)
    lower_row = slice_line(values, lower - 1, 2)
    values = jnp.where(row_ids < upper, upper_row, jnp.where(row_ids >= lower, lower_row, values))
    left_col = slice_line(values, left, 3)
    right_col = slice_line(values, right - 1, 3)
    values = jnp.where(col_ids < left, left_col, jnp.where(col_ids >= right, right_col, values))
    inside = (row_ids >= upper) & (row_ids < lower) & (col_ids >= left) & (col_ids < right)
    real_part = values[:, 0]
    imag_part = values[:, 1]
    ghost_cycle = jnp.stack(
        [real_part + signs * ROBIN_COEF * imag_part, imag_part - signs * ROBIN_COEF * real_part],
        axis=1,
    )
    return jnp.where(inside, values, ghost_cycle)


def apply_operator(padded, wave_cells, signs):
    centre = padded[:, :, 1:-1, 1:-1]
    edge_sum = (
        padded[:, :, :-2, 1:-1]
        + padded[:, :, 2:, 1:-1]
        + padded[:, :, 1:-1, :-2]
        + padded[:, :, 1:-1, 2:]
    )
    corner_sum = (
        padded[:, :, :-2, :-2]
        + padded[:, :, :-2, 2:]
        + padded[:, :, 2:, :-2]
        + padded[:, :, 2:, 2:]
    )
    laplace = (4.0 * edge_sum + corner_sum - 20.0 * centre) / 6.0
    real_part = centre[:, 0]
    imag_part = centre[:, 1]
    mass_term = jnp.stack(
        [real_part - signs * DAMPING * imag_part, imag_part + signs * DAMPING * real_part], axis=1
    )
    return -laplace - wave_cells * mass_term


def combine_parts(products, signs, shape):
    real_out = products[0][:, 0] - signs[..., None] * products[1][:, 1]
    imag_out = products[0][:, 1] + signs[..., None] * products[1][:, 0]
    return jnp.stack([real_out, imag_out], axis=1).reshape(shape)


def along_rows(values, inverse, signs):
    block = inverse.shape[-1]
    blocked = values.reshape(values.shape[0], 2, values.shape[2], values.shape[3] // block, block)
    products = jnp.einsum("qmok,fchqk->mfchqo", inverse, blocked, precision=lax.Precision.HIGHEST)
    return combine_parts(products, signs, values.shape)


def along_cols(values, inverse, signs):
    block = inverse.shape[-1]
    blocked = values.reshape(values.shape[0], 2, values.shape[2] // block, block, values.shape[3])
    products = jnp.einsum("qmok,fcqkw->mfcqow", inverse, blocked, precision=lax.Precision.HIGHEST)
    return combine_parts(products, signs, values.shape)


def solve_local(resid_ext, wave_ext, row_blocks, col_blocks, live_rect, signs):
    upper, lower, left, right = [to_index(v) for v in live_rect]
    height, breadth = (resid_ext.shape[2], resid_ext.shape[3])
    row_ids = lax.broadcasted_iota(jnp.int32, (height, 1), 0)
    col_ids = lax.broadcasted_iota(jnp.int32, (1, breadth), 1)
    live_mask = (
        (row_ids >= upper) & (row_ids < lower) & (col_ids >= left) & (col_ids < right)
    ).astype(resid_ext.dtype)
    local_res = resid_ext * live_mask
    correction = jnp.zeros_like(resid_ext)
    for sweep_index in range(SWEEPS):
        if sweep_index > 0:
            padded = jnp.pad(correction, ((0, 0), (0, 0), (1, 1), (1, 1)))
            padded = fill_ghost(padded, upper + 1, lower + 1, left + 1, right + 1, signs)
            local_res = live_mask * (resid_ext - apply_operator(padded, wave_ext, signs))
        if sweep_index % 2 == 0:
            update = along_rows(local_res, row_blocks, signs)
        else:
            update = along_cols(local_res, col_blocks, signs)
        correction = correction + live_mask * update
    return correction


def exchange(x, row_width, col_width, extra=None):
    row_count = lax.axis_size("gx")
    col_count = lax.axis_size("gy")
    height, breadth = (x.shape[-2], x.shape[-1])
    pieces = {}
    for dr in (-1, 0, 1):
        for dc in (-1, 0, 1):
            if dr == 0 and dc == 0:
                continue
            slab = x
            if dr == -1:
                slab = lax.slice_in_dim(slab, height - row_width, height, axis=x.ndim - 2)
            elif dr == 1:
                slab = lax.slice_in_dim(slab, 0, row_width, axis=x.ndim - 2)
            if dc == -1:
                slab = lax.slice_in_dim(slab, breadth - col_width, breadth, axis=x.ndim - 1)
            elif dc == 1:
                slab = lax.slice_in_dim(slab, 0, col_width, axis=x.ndim - 1)
            if extra is not None and (dr, dc) in extra:
                slab = jnp.concatenate([slab, extra[(dr, dc)]], axis=0)
            perm = []
            for r in range(row_count):
                for c in range(col_count):
                    rr, cc = (r - dr, c - dc)
                    if 0 <= rr < row_count and 0 <= cc < col_count:
                        perm.append((r * col_count + c, rr * col_count + cc))
            pieces[(dr, dc)] = lax.ppermute(slab, ("gx", "gy"), perm)
    return pieces


def exchange_axis(x, axis, dim, width, extra_lo=None, extra_hi=None):
    peers, length = (lax.axis_size(axis), x.shape[dim])
    up = [(i, i + 1) for i in range(peers - 1)]
    down = [(j, i) for i, j in up]
    last = lax.slice_in_dim(x, length - width, length, axis=dim)
    first = lax.slice_in_dim(x, 0, width, axis=dim)
    if extra_lo is not None:
        last = jnp.concatenate([last, extra_lo], axis=0)
        first = jnp.concatenate([first, extra_hi], axis=0)
    return lax.ppermute(last, axis, up), lax.ppermute(first, axis, down)


def assemble(pieces, centre, lead):
    rows = []
    for dr in (-1, 0, 1):
        row = []
        for dc in (-1, 0, 1):
            part = centre if (dr == 0 and dc == 0) else pieces[(dr, dc)][:lead]
            row.append(part)
        rows.append(jnp.concatenate(row, axis=-1))
    return jnp.concatenate(rows, axis=-2)


def shift_rows(x, step):
    return pltpu.roll(x, step % x.shape[0], 0)


def shift_cols(x, step):
    return pltpu.roll(x, step % x.shape[1], 1)


def solve_kernel(rect_ref, resid_ref, data_ref, wrow_ref, wcol_ref, out_ref):
    height, breadth = (resid_ref.shape[1], resid_ref.shape[2])
    half = height // 2
    upper, lower, left, right = (rect_ref[0], rect_ref[1], rect_ref[2], rect_ref[3])
    row_ids = lax.broadcasted_iota(jnp.int32, (height, breadth), 0)
    col_ids = lax.broadcasted_iota(jnp.int32, (height, breadth), 1)
    live = (row_ids >= upper) & (row_ids < lower) & (col_ids >= left) & (col_ids < right)
    top, bottom = (row_ids == upper, row_ids == lower - 1)
    first, last = (col_ids == left, col_ids == right - 1)
    wave = data_ref[4]
    zero = jnp.zeros((height, breadth), jnp.float32)

    def mask(x):
        return jnp.where(live, x, zero)

    def neighbours(x):
        up = jnp.where(top, x, shift_rows(x, 1))
        down = jnp.where(bottom, x, shift_rows(x, -1))
        edge, edge_ghost, corner, corner_ghost = (zero, zero, zero, zero)
        for line, line_flag in ((up, top), (x, None), (down, bottom)):
            lft = jnp.where(first, line, shift_cols(line, 1))
            rgt = jnp.where(last, line, shift_cols(line, -1))
            lft_flag = first if line_flag is None else (first | line_flag)
            rgt_flag = last if line_flag is None else (last | line_flag)
            if line_flag is None:
                edge = edge + lft + rgt
                edge_ghost = edge_ghost + jnp.where(lft_flag, lft, zero) + jnp.where(rgt_flag, rgt, zero)
            else:
                edge = edge + line
                edge_ghost = edge_ghost + jnp.where(line_flag, line, zero)
                corner = corner + lft + rgt
                corner_ghost = corner_ghost + jnp.where(lft_flag, lft, zero) + jnp.where(rgt_flag, rgt, zero)
        return edge, edge_ghost, corner, corner_ghost

    def operator(real_part, imag_part, sign):
        er, egr, cr, cgr = neighbours(real_part)
        ei, egi, ci, cgi = neighbours(imag_part)
        edge_r = er + sign * ROBIN_COEF * egi
        edge_i = ei - sign * ROBIN_COEF * egr
        corner_r = cr + sign * ROBIN_COEF * cgi
        corner_i = ci - sign * ROBIN_COEF * cgr
        lap_r = (4.0 * edge_r + corner_r - 20.0 * real_part) / 6.0
        lap_i = (4.0 * edge_i + corner_i - 20.0 * imag_part) / 6.0
        mass_r = real_part - sign * DAMPING * imag_part
        mass_i = imag_part + sign * DAMPING * real_part
        return (-lap_r - wave * mass_r, -lap_i - wave * mass_i)

    def dot(a, b):
        return jnp.dot(a, b, precision=lax.Precision.HIGHEST, preferred_element_type=jnp.float32)

    def rows_apply(real_part, imag_part, sign):
        outs_r, outs_i = ([], [])
        for h in range(breadth // half):
            cols = slice(h * half, (h + 1) * half)
            stacked = jnp.concatenate([real_part[:, cols], imag_part[:, cols]], axis=0)
            prod = dot(stacked, wrow_ref[h])
            outs_r.append(prod[:height, :half] - sign * prod[height:, half:])
            outs_i.append(prod[height:, :half] + sign * prod[:height, half:])
        return (jnp.concatenate(outs_r, axis=1), jnp.concatenate(outs_i, axis=1))

    def cols_apply(real_part, imag_part, sign):
        outs_r, outs_i = ([], [])
        for h in range(height // half):
            rows = slice(h * half, (h + 1) * half)
            stacked = jnp.concatenate([real_part[rows, :], imag_part[rows, :]], axis=1)
            prod = dot(wcol_ref[h], stacked)
            outs_r.append(prod[:half, :breadth] - sign * prod[half:, breadth:])
            outs_i.append(prod[:half, breadth:] + sign * prod[half:, :breadth])
        return (jnp.concatenate(outs_r, axis=0), jnp.concatenate(outs_i, axis=0))

    def problem_body(problem, carry):
        sign = 1.0 - 2.0 * problem.astype(jnp.float32)
        res_r = resid_ref[2 * problem]
        res_i = resid_ref[2 * problem + 1]
        up_r, up_i = rows_apply(mask(res_r), mask(res_i), sign)
        out_ref[problem, 0] = mask(up_r)
        out_ref[problem, 1] = mask(up_i)

        def sweep_body(step, inner):
            cor_r = out_ref[problem, 0]
            cor_i = out_ref[problem, 1]
            op_r, op_i = operator(cor_r, cor_i, sign)
            loc_r, loc_i = (mask(resid_ref[2 * problem] - op_r), mask(resid_ref[2 * problem + 1] - op_i))
            up_r, up_i = lax.cond(
                step % 2 == 0,
                lambda: cols_apply(loc_r, loc_i, sign),
                lambda: rows_apply(loc_r, loc_i, sign),
            )
            out_ref[problem, 0] = cor_r + mask(up_r)
            out_ref[problem, 1] = cor_i + mask(up_i)
            return inner

        lax.fori_loop(0, SWEEPS - 1, sweep_body, 0)
        return carry

    lax.fori_loop(0, out_ref.shape[0], problem_body, 0)


def line_matrices(row_blocks, col_blocks):
    block = row_blocks.shape[-1]
    eye = jnp.eye(2, dtype=row_blocks.dtype)
    halves = row_blocks.shape[0] // 2
    rows_t = jnp.transpose(row_blocks, (0, 3, 1, 2)).reshape(halves, 2, block, 2, block)
    row_mats = jnp.einsum("hakmo,ab->hakmbo", rows_t, eye).reshape(halves, 2 * block, 4 * block)
    cols = col_blocks.reshape(halves, 2, 2, block, block)
    col_mats = jnp.einsum("hamok,ab->hmaobk", cols, eye).reshape(halves, 4 * block, 2 * block)
    return row_mats, col_mats


def solve_local_kernel(resid_planes, data_ext, row_mats, col_mats, live_rect, interpret=False):
    rect = jnp.stack([to_index(v) for v in live_rect])
    out_shape = (2, 2) + resid_planes.shape[1:]
    vmem = pltpu.MemorySpace.VMEM if hasattr(pltpu, "MemorySpace") else pltpu.VMEM
    return pl.pallas_call(
        solve_kernel,
        out_shape=jax.ShapeDtypeStruct(out_shape, resid_planes.dtype),
        in_specs=[pl.BlockSpec(memory_space=pltpu.SMEM)] + [pl.BlockSpec(memory_space=vmem)] * 4,
        out_specs=pl.BlockSpec(memory_space=vmem),
        interpret=interpret,
    )(rect, resid_planes, data_ext, row_mats, col_mats)


def shards(sources, wavenumber, row_inverse, col_inverse, reach_steps):
    own_rows, own_cols = (sources.shape[2], sources.shape[3])
    block = row_inverse.shape[-1]
    step_cells = block // 4
    signs = jnp.array([1.0, -1.0], dtype=sources.dtype).reshape(2, 1, 1)
    row_rank = to_index(lax.axis_index("gx"))
    col_rank = to_index(lax.axis_index("gy"))
    row_count = lax.axis_size("gx")
    col_count = lax.axis_size("gy")
    zero = to_index(0)
    widths = reach_steps.reshape(4) * step_cells
    upper_w = jnp.where(row_rank > 0, widths[0], zero)
    lower_w = jnp.where(row_rank < row_count - 1, widths[1], zero)
    left_w = jnp.where(col_rank > 0, widths[2], zero)
    right_w = jnp.where(col_rank < col_count - 1, widths[3], zero)
    live_rect = (
        block - upper_w,
        block + own_rows + lower_w,
        block - left_w,
        block + own_cols + right_w,
    )
    stacked = jnp.concatenate([sources.reshape(4, own_rows, own_cols), wavenumber[None]], axis=0)
    lead = stacked.shape[0]
    col_pair = col_inverse.shape[0]
    row_pair = row_inverse.shape[0]
    inv_rows = col_inverse.shape[1] * block * block // own_cols
    before, after = exchange_axis(
        stacked, "gx", 1, block,
        col_inverse[col_pair - 1].reshape(1, inv_rows, own_cols), col_inverse[0].reshape(1, inv_rows, own_cols),
    )
    tall = jnp.concatenate([before[:lead, :block], stacked, after[:lead, :block]], axis=1)
    def inv_slab(mats):
        flat = mats.reshape(1, -1, block)
        return jnp.pad(flat, ((0, 0), (0, tall.shape[1] - flat.shape[1]), (0, 0)))
    left, right = exchange_axis(tall, "gy", 2, block, inv_slab(row_inverse[row_pair - 1]), inv_slab(row_inverse[0]))
    stacked_ext = jnp.concatenate([left[:lead], tall, right[:lead]], axis=2)
    sources_ext = stacked_ext[:4].reshape(2, 2, own_rows + 2 * block, own_cols + 2 * block)
    wave_ext = stacked_ext[4]
    inv_shape = (1,) + row_inverse.shape[1:]
    inv_size = row_inverse.shape[1] * block * block // block
    col_blocks = jnp.concatenate(
        [before[lead:].reshape(inv_shape), col_inverse, after[lead:].reshape(inv_shape)], axis=0
    )
    row_blocks = jnp.concatenate(
        [left[lead:, :inv_size].reshape(inv_shape), row_inverse, right[lead:, :inv_size].reshape(inv_shape)], axis=0
    )
    row_mats, col_mats = line_matrices(row_blocks, col_blocks)
    width = block + 1
    grid_upper = to_index(jnp.where(row_rank == 0, width, 0))
    grid_lower = to_index(jnp.where(row_rank == row_count - 1, width + own_rows, own_rows + 2 * width))
    grid_left = to_index(jnp.where(col_rank == 0, width, 0))
    grid_right = to_index(jnp.where(col_rank == col_count - 1, width + own_cols, own_cols + 2 * width))
    solution = None
    for iteration in range(ITERS):
        if iteration == 0:
            resid_planes = stacked_ext
        else:
            before, after = exchange_axis(solution, "gx", 2, width)
            tall = jnp.concatenate([before, solution, after], axis=2)
            left, right = exchange_axis(tall, "gy", 3, width)
            padded = jnp.concatenate([left, tall, right], axis=3)
            padded = fill_ghost(padded, grid_upper, grid_lower, grid_left, grid_right, signs)
            resid_ext = sources_ext - apply_operator(padded, wave_ext, signs)
            resid_planes = resid_ext.reshape((4,) + resid_ext.shape[2:])
        correction = solve_local_kernel(resid_planes, stacked_ext, row_mats, col_mats, live_rect)
        own = correction[:, :, block : block + own_rows, block : block + own_cols]
        solution = own if solution is None else solution + own
    return solution


def solution(mesh):
    return jax.shard_map(
        shards,
        mesh=mesh,
        in_specs=(
            P(None, None, "gx", "gy"),
            P("gx", "gy"),
            P("gy", None, None, None),
            P("gx", None, None, None),
            P("gx", "gy", None),
        ),
        out_specs=P(None, None, "gx", "gy"),
        check_vma=False,
    )
```

```python
import jax
import jax.numpy as jnp
from jax import lax
from jax.sharding import PartitionSpec as P
from jax.experimental import pallas as pl
from jax.experimental.pallas import tpu as pltpu

ITERS = 2
SWEEPS = 4


DAMPING = 0.5
ROBIN_COEF = 0.5


def with_halo(shard, sides, width):
    for axis, dim in sides:
        peers, length = (lax.axis_size(axis), shard.shape[dim])
        up = [(i, (i + 1) % peers) for i in range(peers - 1)]
        down = [(j, i) for i, j in up]
        last = lax.slice_in_dim(shard, length - width, length, axis=dim)
        first = lax.slice_in_dim(shard, 0, width, axis=dim)
        before = lax.ppermute(last, axis, up)
        after = lax.ppermute(first, axis, down)
        shard = jnp.concatenate([before, shard, after], axis=dim)
    return shard


def to_index(value):
    return jnp.asarray(value).astype(jnp.int32)


def slice_line(values, start, axis):
    starts = [to_index(0) for _ in range(values.ndim)]
    starts[axis] = to_index(start)
    sizes = list(values.shape)
    sizes[axis] = 1
    return lax.dynamic_slice(values, starts, sizes)


def fill_ghost(values, upper, lower, left, right, signs):
    upper, lower, left, right = (to_index(upper), to_index(lower), to_index(left), to_index(right))
    height, breadth = (values.shape[2], values.shape[3])
    row_ids = lax.broadcasted_iota(jnp.int32, (height, 1), 0)
    col_ids = lax.broadcasted_iota(jnp.int32, (1, breadth), 1)
    upper_row = slice_line(values, upper, 2)
    lower_row = slice_line(values, lower - 1, 2)
    values = jnp.where(row_ids < upper, upper_row, jnp.where(row_ids >= lower, lower_row, values))
    left_col = slice_line(values, left, 3)
    right_col = slice_line(values, right - 1, 3)
    values = jnp.where(col_ids < left, left_col, jnp.where(col_ids >= right, right_col, values))
    inside = (row_ids >= upper) & (row_ids < lower) & (col_ids >= left) & (col_ids < right)
    real_part = values[:, 0]
    imag_part = values[:, 1]
    ghost_cycle = jnp.stack(
        [real_part + signs * ROBIN_COEF * imag_part, imag_part - signs * ROBIN_COEF * real_part],
        axis=1,
    )
    return jnp.where(inside, values, ghost_cycle)


def apply_operator(padded, wave_cells, signs):
    centre = padded[:, :, 1:-1, 1:-1]
    edge_sum = (
        padded[:, :, :-2, 1:-1]
        + padded[:, :, 2:, 1:-1]
        + padded[:, :, 1:-1, :-2]
        + padded[:, :, 1:-1, 2:]
    )
    corner_sum = (
        padded[:, :, :-2, :-2]
        + padded[:, :, :-2, 2:]
        + padded[:, :, 2:, :-2]
        + padded[:, :, 2:, 2:]
    )
    laplace = (4.0 * edge_sum + corner_sum - 20.0 * centre) / 6.0
    real_part = centre[:, 0]
    imag_part = centre[:, 1]
    mass_term = jnp.stack(
        [real_part - signs * DAMPING * imag_part, imag_part + signs * DAMPING * real_part], axis=1
    )
    return -laplace - wave_cells * mass_term


def combine_parts(products, signs, shape):
    real_out = products[0][:, 0] - signs[..., None] * products[1][:, 1]
    imag_out = products[0][:, 1] + signs[..., None] * products[1][:, 0]
    return jnp.stack([real_out, imag_out], axis=1).reshape(shape)


def along_rows(values, inverse, signs):
    block = inverse.shape[-1]
    blocked = values.reshape(values.shape[0], 2, values.shape[2], values.shape[3] // block, block)
    products = jnp.einsum("qmok,fchqk->mfchqo", inverse, blocked, precision=lax.Precision.HIGHEST)
    return combine_parts(products, signs, values.shape)


def along_cols(values, inverse, signs):
    block = inverse.shape[-1]
    blocked = values.reshape(values.shape[0], 2, values.shape[2] // block, block, values.shape[3])
    products = jnp.einsum("qmok,fcqkw->mfcqow", inverse, blocked, precision=lax.Precision.HIGHEST)
    return combine_parts(products, signs, values.shape)


def solve_local(resid_ext, wave_ext, row_blocks, col_blocks, live_rect, signs):
    upper, lower, left, right = [to_index(v) for v in live_rect]
    height, breadth = (resid_ext.shape[2], resid_ext.shape[3])
    row_ids = lax.broadcasted_iota(jnp.int32, (height, 1), 0)
    col_ids = lax.broadcasted_iota(jnp.int32, (1, breadth), 1)
    live_mask = (
        (row_ids >= upper) & (row_ids < lower) & (col_ids >= left) & (col_ids < right)
    ).astype(resid_ext.dtype)
    local_res = resid_ext * live_mask
    correction = jnp.zeros_like(resid_ext)
    for sweep_index in range(SWEEPS):
        if sweep_index > 0:
            padded = jnp.pad(correction, ((0, 0), (0, 0), (1, 1), (1, 1)))
            padded = fill_ghost(padded, upper + 1, lower + 1, left + 1, right + 1, signs)
            local_res = live_mask * (resid_ext - apply_operator(padded, wave_ext, signs))
        if sweep_index % 2 == 0:
            update = along_rows(local_res, row_blocks, signs)
        else:
            update = along_cols(local_res, col_blocks, signs)
        correction = correction + live_mask * update
    return correction


def exchange(x, row_width, col_width, extra=None):
    row_count = lax.axis_size("gx")
    col_count = lax.axis_size("gy")
    height, breadth = (x.shape[-2], x.shape[-1])
    pieces = {}
    for dr in (-1, 0, 1):
        for dc in (-1, 0, 1):
            if dr == 0 and dc == 0:
                continue
            slab = x
            if dr == -1:
                slab = lax.slice_in_dim(slab, height - row_width, height, axis=x.ndim - 2)
            elif dr == 1:
                slab = lax.slice_in_dim(slab, 0, row_width, axis=x.ndim - 2)
            if dc == -1:
                slab = lax.slice_in_dim(slab, breadth - col_width, breadth, axis=x.ndim - 1)
            elif dc == 1:
                slab = lax.slice_in_dim(slab, 0, col_width, axis=x.ndim - 1)
            if extra is not None and (dr, dc) in extra:
                slab = jnp.concatenate([slab, extra[(dr, dc)]], axis=0)
            perm = []
            for r in range(row_count):
                for c in range(col_count):
                    rr, cc = (r - dr, c - dc)
                    if 0 <= rr < row_count and 0 <= cc < col_count:
                        perm.append((r * col_count + c, rr * col_count + cc))
            pieces[(dr, dc)] = lax.ppermute(slab, ("gx", "gy"), perm)
    return pieces


def exchange_axis(x, axis, dim, width, extra_lo=None, extra_hi=None):
    peers, length = (lax.axis_size(axis), x.shape[dim])
    up = [(i, i + 1) for i in range(peers - 1)]
    down = [(j, i) for i, j in up]
    last = lax.slice_in_dim(x, length - width, length, axis=dim)
    first = lax.slice_in_dim(x, 0, width, axis=dim)
    if extra_lo is not None:
        last = jnp.concatenate([last, extra_lo], axis=0)
        first = jnp.concatenate([first, extra_hi], axis=0)
    return lax.ppermute(last, axis, up), lax.ppermute(first, axis, down)


def assemble(pieces, centre, lead):
    rows = []
    for dr in (-1, 0, 1):
        row = []
        for dc in (-1, 0, 1):
            part = centre if (dr == 0 and dc == 0) else pieces[(dr, dc)][:lead]
            row.append(part)
        rows.append(jnp.concatenate(row, axis=-1))
    return jnp.concatenate(rows, axis=-2)


def shift_rows(x, step):
    return pltpu.roll(x, step % x.shape[0], 0)


def shift_cols(x, step):
    return pltpu.roll(x, step % x.shape[1], 1)


def solve_kernel(rect_ref, resid_ref, data_ref, wrow_ref, wcol_ref, out_ref):
    height, breadth = (resid_ref.shape[1], resid_ref.shape[2])
    half = height // 2
    upper, lower, left, right = (rect_ref[0], rect_ref[1], rect_ref[2], rect_ref[3])
    row_ids = lax.broadcasted_iota(jnp.int32, (height, breadth), 0)
    col_ids = lax.broadcasted_iota(jnp.int32, (height, breadth), 1)
    live = (row_ids >= upper) & (row_ids < lower) & (col_ids >= left) & (col_ids < right)
    top, bottom = (row_ids == upper, row_ids == lower - 1)
    first, last = (col_ids == left, col_ids == right - 1)
    wave = data_ref[4]
    zero = jnp.zeros((height, breadth), jnp.float32)

    def mask(x):
        return jnp.where(live, x, zero)

    def neighbours(x):
        up = jnp.where(top, x, shift_rows(x, 1))
        down = jnp.where(bottom, x, shift_rows(x, -1))
        edge, edge_ghost, corner, corner_ghost = (zero, zero, zero, zero)
        for line, line_flag in ((up, top), (x, None), (down, bottom)):
            lft = jnp.where(first, line, shift_cols(line, 1))
            rgt = jnp.where(last, line, shift_cols(line, -1))
            lft_flag = first if line_flag is None else (first | line_flag)
            rgt_flag = last if line_flag is None else (last | line_flag)
            if line_flag is None:
                edge = edge + lft + rgt
                edge_ghost = edge_ghost + jnp.where(lft_flag, lft, zero) + jnp.where(rgt_flag, rgt, zero)
            else:
                edge = edge + line
                edge_ghost = edge_ghost + jnp.where(line_flag, line, zero)
                corner = corner + lft + rgt
                corner_ghost = corner_ghost + jnp.where(lft_flag, lft, zero) + jnp.where(rgt_flag, rgt, zero)
        return edge, edge_ghost, corner, corner_ghost

    def operator(real_part, imag_part, sign):
        er, egr, cr, cgr = neighbours(real_part)
        ei, egi, ci, cgi = neighbours(imag_part)
        edge_r = er + sign * ROBIN_COEF * egi
        edge_i = ei - sign * ROBIN_COEF * egr
        corner_r = cr + sign * ROBIN_COEF * cgi
        corner_i = ci - sign * ROBIN_COEF * cgr
        lap_r = (4.0 * edge_r + corner_r - 20.0 * real_part) / 6.0
        lap_i = (4.0 * edge_i + corner_i - 20.0 * imag_part) / 6.0
        mass_r = real_part - sign * DAMPING * imag_part
        mass_i = imag_part + sign * DAMPING * real_part
        return (-lap_r - wave * mass_r, -lap_i - wave * mass_i)

    def dot(a, b):
        return jnp.dot(a, b, precision=lax.Precision.HIGH, preferred_element_type=jnp.float32)

    def rows_apply(real_part, imag_part, sign):
        outs_r, outs_i = ([], [])
        for h in range(breadth // half):
            cols = slice(h * half, (h + 1) * half)
            stacked = jnp.concatenate([real_part[:, cols], imag_part[:, cols]], axis=0)
            prod = dot(stacked, wrow_ref[h])
            outs_r.append(prod[:height, :half] - sign * prod[height:, half:])
            outs_i.append(prod[height:, :half] + sign * prod[:height, half:])
        return (jnp.concatenate(outs_r, axis=1), jnp.concatenate(outs_i, axis=1))

    def cols_apply(real_part, imag_part, sign):
        outs_r, outs_i = ([], [])
        for h in range(height // half):
            rows = slice(h * half, (h + 1) * half)
            stacked = jnp.concatenate([real_part[rows, :], imag_part[rows, :]], axis=1)
            prod = dot(wcol_ref[h], stacked)
            outs_r.append(prod[:half, :breadth] - sign * prod[half:, breadth:])
            outs_i.append(prod[:half, breadth:] + sign * prod[half:, :breadth])
        return (jnp.concatenate(outs_r, axis=0), jnp.concatenate(outs_i, axis=0))

    def problem_body(problem, carry):
        sign = 1.0 - 2.0 * problem.astype(jnp.float32)
        res_r = resid_ref[2 * problem]
        res_i = resid_ref[2 * problem + 1]
        up_r, up_i = rows_apply(mask(res_r), mask(res_i), sign)
        out_ref[problem, 0] = mask(up_r)
        out_ref[problem, 1] = mask(up_i)

        def sweep_body(step, inner):
            cor_r = out_ref[problem, 0]
            cor_i = out_ref[problem, 1]
            op_r, op_i = operator(cor_r, cor_i, sign)
            loc_r, loc_i = (mask(resid_ref[2 * problem] - op_r), mask(resid_ref[2 * problem + 1] - op_i))
            up_r, up_i = lax.cond(
                step % 2 == 0,
                lambda: cols_apply(loc_r, loc_i, sign),
                lambda: rows_apply(loc_r, loc_i, sign),
            )
            out_ref[problem, 0] = cor_r + mask(up_r)
            out_ref[problem, 1] = cor_i + mask(up_i)
            return inner

        lax.fori_loop(0, SWEEPS - 1, sweep_body, 0)
        return carry

    lax.fori_loop(0, out_ref.shape[0], problem_body, 0)


def line_matrices(row_blocks, col_blocks):
    block = row_blocks.shape[-1]
    eye = jnp.eye(2, dtype=row_blocks.dtype)
    halves = row_blocks.shape[0] // 2
    rows_t = jnp.transpose(row_blocks, (0, 3, 1, 2)).reshape(halves, 2, block, 2, block)
    row_mats = jnp.einsum("hakmo,ab->hakmbo", rows_t, eye).reshape(halves, 2 * block, 4 * block)
    cols = col_blocks.reshape(halves, 2, 2, block, block)
    col_mats = jnp.einsum("hamok,ab->hmaobk", cols, eye).reshape(halves, 4 * block, 2 * block)
    return row_mats, col_mats


def solve_local_kernel(resid_planes, data_ext, row_mats, col_mats, live_rect, interpret=False):
    rect = jnp.stack([to_index(v) for v in live_rect])
    out_shape = (2, 2) + resid_planes.shape[1:]
    vmem = pltpu.MemorySpace.VMEM if hasattr(pltpu, "MemorySpace") else pltpu.VMEM
    return pl.pallas_call(
        solve_kernel,
        out_shape=jax.ShapeDtypeStruct(out_shape, resid_planes.dtype),
        in_specs=[pl.BlockSpec(memory_space=pltpu.SMEM)] + [pl.BlockSpec(memory_space=vmem)] * 4,
        out_specs=pl.BlockSpec(memory_space=vmem),
        interpret=interpret,
    )(rect, resid_planes, data_ext, row_mats, col_mats)


def shards(sources, wavenumber, row_inverse, col_inverse, reach_steps):
    own_rows, own_cols = (sources.shape[2], sources.shape[3])
    block = row_inverse.shape[-1]
    step_cells = block // 4
    signs = jnp.array([1.0, -1.0], dtype=sources.dtype).reshape(2, 1, 1)
    row_rank = to_index(lax.axis_index("gx"))
    col_rank = to_index(lax.axis_index("gy"))
    row_count = lax.axis_size("gx")
    col_count = lax.axis_size("gy")
    zero = to_index(0)
    widths = reach_steps.reshape(4) * step_cells
    upper_w = jnp.where(row_rank > 0, widths[0], zero)
    lower_w = jnp.where(row_rank < row_count - 1, widths[1], zero)
    left_w = jnp.where(col_rank > 0, widths[2], zero)
    right_w = jnp.where(col_rank < col_count - 1, widths[3], zero)
    live_rect = (
        block - upper_w,
        block + own_rows + lower_w,
        block - left_w,
        block + own_cols + right_w,
    )
    stacked = jnp.concatenate([sources.reshape(4, own_rows, own_cols), wavenumber[None]], axis=0)
    lead = stacked.shape[0]
    col_pair = col_inverse.shape[0]
    row_pair = row_inverse.shape[0]
    inv_rows = col_inverse.shape[1] * block * block // own_cols
    before, after = exchange_axis(
        stacked, "gx", 1, block,
        col_inverse[col_pair - 1].reshape(1, inv_rows, own_cols), col_inverse[0].reshape(1, inv_rows, own_cols),
    )
    tall = jnp.concatenate([before[:lead, :block], stacked, after[:lead, :block]], axis=1)
    def inv_slab(mats):
        flat = mats.reshape(1, -1, block)
        return jnp.pad(flat, ((0, 0), (0, tall.shape[1] - flat.shape[1]), (0, 0)))
    left, right = exchange_axis(tall, "gy", 2, block, inv_slab(row_inverse[row_pair - 1]), inv_slab(row_inverse[0]))
    stacked_ext = jnp.concatenate([left[:lead], tall, right[:lead]], axis=2)
    sources_ext = stacked_ext[:4].reshape(2, 2, own_rows + 2 * block, own_cols + 2 * block)
    wave_ext = stacked_ext[4]
    inv_shape = (1,) + row_inverse.shape[1:]
    inv_size = row_inverse.shape[1] * block * block // block
    col_blocks = jnp.concatenate(
        [before[lead:].reshape(inv_shape), col_inverse, after[lead:].reshape(inv_shape)], axis=0
    )
    row_blocks = jnp.concatenate(
        [left[lead:, :inv_size].reshape(inv_shape), row_inverse, right[lead:, :inv_size].reshape(inv_shape)], axis=0
    )
    row_mats, col_mats = line_matrices(row_blocks, col_blocks)
    width = block + 1
    grid_upper = to_index(jnp.where(row_rank == 0, width, 0))
    grid_lower = to_index(jnp.where(row_rank == row_count - 1, width + own_rows, own_rows + 2 * width))
    grid_left = to_index(jnp.where(col_rank == 0, width, 0))
    grid_right = to_index(jnp.where(col_rank == col_count - 1, width + own_cols, own_cols + 2 * width))
    solution = None
    for iteration in range(ITERS):
        if iteration == 0:
            resid_planes = stacked_ext
        else:
            before, after = exchange_axis(solution, "gx", 2, width)
            tall = jnp.concatenate([before, solution, after], axis=2)
            left, right = exchange_axis(tall, "gy", 3, width)
            padded = jnp.concatenate([left, tall, right], axis=3)
            padded = fill_ghost(padded, grid_upper, grid_lower, grid_left, grid_right, signs)
            resid_ext = sources_ext - apply_operator(padded, wave_ext, signs)
            resid_planes = resid_ext.reshape((4,) + resid_ext.shape[2:])
        correction = solve_local_kernel(resid_planes, stacked_ext, row_mats, col_mats, live_rect)
        own = correction[:, :, block : block + own_rows, block : block + own_cols]
        solution = own if solution is None else solution + own
    return solution


def solution(mesh):
    return jax.shard_map(
        shards,
        mesh=mesh,
        in_specs=(
            P(None, None, "gx", "gy"),
            P("gx", "gy"),
            P("gy", None, None, None),
            P("gx", None, None, None),
            P("gx", "gy", None),
        ),
        out_specs=P(None, None, "gx", "gy"),
        check_vma=False,
    )
```

```python
import jax
import jax.numpy as jnp
from jax import lax
from jax.sharding import PartitionSpec as P
from jax.experimental import pallas as pl
from jax.experimental.pallas import tpu as pltpu

ITERS = 2
SWEEPS = 4


DAMPING = 0.5
ROBIN_COEF = 0.5


def with_halo(shard, sides, width):
    for axis, dim in sides:
        peers, length = (lax.axis_size(axis), shard.shape[dim])
        up = [(i, (i + 1) % peers) for i in range(peers - 1)]
        down = [(j, i) for i, j in up]
        last = lax.slice_in_dim(shard, length - width, length, axis=dim)
        first = lax.slice_in_dim(shard, 0, width, axis=dim)
        before = lax.ppermute(last, axis, up)
        after = lax.ppermute(first, axis, down)
        shard = jnp.concatenate([before, shard, after], axis=dim)
    return shard


def to_index(value):
    return jnp.asarray(value).astype(jnp.int32)


def slice_line(values, start, axis):
    starts = [to_index(0) for _ in range(values.ndim)]
    starts[axis] = to_index(start)
    sizes = list(values.shape)
    sizes[axis] = 1
    return lax.dynamic_slice(values, starts, sizes)


def fill_ghost(values, upper, lower, left, right, signs):
    upper, lower, left, right = (to_index(upper), to_index(lower), to_index(left), to_index(right))
    height, breadth = (values.shape[2], values.shape[3])
    row_ids = lax.broadcasted_iota(jnp.int32, (height, 1), 0)
    col_ids = lax.broadcasted_iota(jnp.int32, (1, breadth), 1)
    upper_row = slice_line(values, upper, 2)
    lower_row = slice_line(values, lower - 1, 2)
    values = jnp.where(row_ids < upper, upper_row, jnp.where(row_ids >= lower, lower_row, values))
    left_col = slice_line(values, left, 3)
    right_col = slice_line(values, right - 1, 3)
    values = jnp.where(col_ids < left, left_col, jnp.where(col_ids >= right, right_col, values))
    inside = (row_ids >= upper) & (row_ids < lower) & (col_ids >= left) & (col_ids < right)
    real_part = values[:, 0]
    imag_part = values[:, 1]
    ghost_cycle = jnp.stack(
        [real_part + signs * ROBIN_COEF * imag_part, imag_part - signs * ROBIN_COEF * real_part],
        axis=1,
    )
    return jnp.where(inside, values, ghost_cycle)


def apply_operator(padded, wave_cells, signs):
    centre = padded[:, :, 1:-1, 1:-1]
    edge_sum = (
        padded[:, :, :-2, 1:-1]
        + padded[:, :, 2:, 1:-1]
        + padded[:, :, 1:-1, :-2]
        + padded[:, :, 1:-1, 2:]
    )
    corner_sum = (
        padded[:, :, :-2, :-2]
        + padded[:, :, :-2, 2:]
        + padded[:, :, 2:, :-2]
        + padded[:, :, 2:, 2:]
    )
    laplace = (4.0 * edge_sum + corner_sum - 20.0 * centre) / 6.0
    real_part = centre[:, 0]
    imag_part = centre[:, 1]
    mass_term = jnp.stack(
        [real_part - signs * DAMPING * imag_part, imag_part + signs * DAMPING * real_part], axis=1
    )
    return -laplace - wave_cells * mass_term


def combine_parts(products, signs, shape):
    real_out = products[0][:, 0] - signs[..., None] * products[1][:, 1]
    imag_out = products[0][:, 1] + signs[..., None] * products[1][:, 0]
    return jnp.stack([real_out, imag_out], axis=1).reshape(shape)


def along_rows(values, inverse, signs):
    block = inverse.shape[-1]
    blocked = values.reshape(values.shape[0], 2, values.shape[2], values.shape[3] // block, block)
    products = jnp.einsum("qmok,fchqk->mfchqo", inverse, blocked, precision=lax.Precision.HIGHEST)
    return combine_parts(products, signs, values.shape)


def along_cols(values, inverse, signs):
    block = inverse.shape[-1]
    blocked = values.reshape(values.shape[0], 2, values.shape[2] // block, block, values.shape[3])
    products = jnp.einsum("qmok,fcqkw->mfcqow", inverse, blocked, precision=lax.Precision.HIGHEST)
    return combine_parts(products, signs, values.shape)


def solve_local(resid_ext, wave_ext, row_blocks, col_blocks, live_rect, signs):
    upper, lower, left, right = [to_index(v) for v in live_rect]
    height, breadth = (resid_ext.shape[2], resid_ext.shape[3])
    row_ids = lax.broadcasted_iota(jnp.int32, (height, 1), 0)
    col_ids = lax.broadcasted_iota(jnp.int32, (1, breadth), 1)
    live_mask = (
        (row_ids >= upper) & (row_ids < lower) & (col_ids >= left) & (col_ids < right)
    ).astype(resid_ext.dtype)
    local_res = resid_ext * live_mask
    correction = jnp.zeros_like(resid_ext)
    for sweep_index in range(SWEEPS):
        if sweep_index > 0:
            padded = jnp.pad(correction, ((0, 0), (0, 0), (1, 1), (1, 1)))
            padded = fill_ghost(padded, upper + 1, lower + 1, left + 1, right + 1, signs)
            local_res = live_mask * (resid_ext - apply_operator(padded, wave_ext, signs))
        if sweep_index % 2 == 0:
            update = along_rows(local_res, row_blocks, signs)
        else:
            update = along_cols(local_res, col_blocks, signs)
        correction = correction + live_mask * update
    return correction


def exchange(x, row_width, col_width, extra=None):
    row_count = lax.axis_size("gx")
    col_count = lax.axis_size("gy")
    height, breadth = (x.shape[-2], x.shape[-1])
    pieces = {}
    for dr in (-1, 0, 1):
        for dc in (-1, 0, 1):
            if dr == 0 and dc == 0:
                continue
            slab = x
            if dr == -1:
                slab = lax.slice_in_dim(slab, height - row_width, height, axis=x.ndim - 2)
            elif dr == 1:
                slab = lax.slice_in_dim(slab, 0, row_width, axis=x.ndim - 2)
            if dc == -1:
                slab = lax.slice_in_dim(slab, breadth - col_width, breadth, axis=x.ndim - 1)
            elif dc == 1:
                slab = lax.slice_in_dim(slab, 0, col_width, axis=x.ndim - 1)
            if extra is not None and (dr, dc) in extra:
                slab = jnp.concatenate([slab, extra[(dr, dc)]], axis=0)
            perm = []
            for r in range(row_count):
                for c in range(col_count):
                    rr, cc = (r - dr, c - dc)
                    if 0 <= rr < row_count and 0 <= cc < col_count:
                        perm.append((r * col_count + c, rr * col_count + cc))
            pieces[(dr, dc)] = lax.ppermute(slab, ("gx", "gy"), perm)
    return pieces


def exchange_axis(x, axis, dim, width, extra_lo=None, extra_hi=None):
    peers, length = (lax.axis_size(axis), x.shape[dim])
    up = [(i, i + 1) for i in range(peers - 1)]
    down = [(j, i) for i, j in up]
    last = lax.slice_in_dim(x, length - width, length, axis=dim)
    first = lax.slice_in_dim(x, 0, width, axis=dim)
    if extra_lo is not None:
        last = jnp.concatenate([last, extra_lo], axis=0)
        first = jnp.concatenate([first, extra_hi], axis=0)
    return lax.ppermute(last, axis, up), lax.ppermute(first, axis, down)


def assemble(pieces, centre, lead):
    rows = []
    for dr in (-1, 0, 1):
        row = []
        for dc in (-1, 0, 1):
            part = centre if (dr == 0 and dc == 0) else pieces[(dr, dc)][:lead]
            row.append(part)
        rows.append(jnp.concatenate(row, axis=-1))
    return jnp.concatenate(rows, axis=-2)


def solve_kernel(rect_ref, resid_ref, data_ref, wrow_ref, wcol_ref, out_ref):
    height, breadth = (resid_ref.shape[1], resid_ref.shape[2])
    half = height // 2
    upper, lower, left, right = (rect_ref[0], rect_ref[1], rect_ref[2], rect_ref[3])
    row_ids = lax.broadcasted_iota(jnp.int32, (height, breadth), 0)
    col_ids = lax.broadcasted_iota(jnp.int32, (height, breadth), 1)
    live = (row_ids >= upper) & (row_ids < lower) & (col_ids >= left) & (col_ids < right)
    top, bottom = (row_ids == upper, row_ids == lower - 1)
    first, last = (col_ids == left, col_ids == right - 1)
    row_flag = top.astype(jnp.float32) + bottom.astype(jnp.float32)
    col_flag = first.astype(jnp.float32) + last.astype(jnp.float32)
    edge_flag = 4.0 * (row_flag + col_flag)
    zero = jnp.zeros((height, breadth), jnp.float32)

    def mask(x):
        return jnp.where(live, x, zero)

    def rows_sum(x):
        up = jnp.where(top, x, pltpu.roll(x, 1, 0))
        down = jnp.where(bottom, x, pltpu.roll(x, height - 1, 0))
        return up + down

    def cols_sum(x):
        lft = jnp.where(first, x, pltpu.roll(x, 1, 1))
        rgt = jnp.where(last, x, pltpu.roll(x, breadth - 1, 1))
        return lft + rgt

    def stencil(x):
        vertical = rows_sum(x)
        ghost_rows = row_flag * x
        total = 4.0 * (vertical + cols_sum(x)) + cols_sum(vertical)
        ghost = edge_flag * x + cols_sum(ghost_rows) + col_flag * (vertical - ghost_rows)
        return total, ghost

    def operator(real_part, imag_part, sign):
        wave = data_ref[4]
        total_r, ghost_r = stencil(real_part)
        total_i, ghost_i = stencil(imag_part)
        lap_r = (total_r + sign * ROBIN_COEF * ghost_i - 20.0 * real_part) / 6.0
        lap_i = (total_i - sign * ROBIN_COEF * ghost_r - 20.0 * imag_part) / 6.0
        mass_r = real_part - sign * DAMPING * imag_part
        mass_i = imag_part + sign * DAMPING * real_part
        return (-lap_r - wave * mass_r, -lap_i - wave * mass_i)

    def dot(a, b):
        return jnp.dot(a, b, precision=lax.Precision.HIGH, preferred_element_type=jnp.float32)

    def rows_apply(real_part, imag_part, sign):
        outs_r, outs_i = ([], [])
        for h in range(breadth // half):
            cols = slice(h * half, (h + 1) * half)
            prod_r = dot(real_part[:, cols], wrow_ref[h])
            prod_i = dot(imag_part[:, cols], wrow_ref[h])
            outs_r.append(prod_r[:, :half] - sign * prod_i[:, half:])
            outs_i.append(prod_i[:, :half] + sign * prod_r[:, half:])
        return (jnp.concatenate(outs_r, axis=1), jnp.concatenate(outs_i, axis=1))

    def cols_apply(real_part, imag_part, sign):
        outs_r, outs_i = ([], [])
        for h in range(height // half):
            rows = slice(h * half, (h + 1) * half)
            prod_r = dot(wcol_ref[h], real_part[rows, :])
            prod_i = dot(wcol_ref[h], imag_part[rows, :])
            outs_r.append(prod_r[:half] - sign * prod_i[half:])
            outs_i.append(prod_i[:half] + sign * prod_r[half:])
        return (jnp.concatenate(outs_r, axis=0), jnp.concatenate(outs_i, axis=0))

    def problem_body(problem, carry):
        sign = 1.0 - 2.0 * problem.astype(jnp.float32)
        up_r, up_i = rows_apply(mask(resid_ref[2 * problem]), mask(resid_ref[2 * problem + 1]), sign)
        out_ref[problem, 0] = mask(up_r)
        out_ref[problem, 1] = mask(up_i)

        def sweep_body(step, inner):
            cor_r = out_ref[problem, 0]
            cor_i = out_ref[problem, 1]
            op_r, op_i = operator(cor_r, cor_i, sign)
            loc_r, loc_i = (mask(resid_ref[2 * problem] - op_r), mask(resid_ref[2 * problem + 1] - op_i))
            up_r, up_i = lax.cond(
                step % 2 == 0,
                lambda: cols_apply(loc_r, loc_i, sign),
                lambda: rows_apply(loc_r, loc_i, sign),
            )
            out_ref[problem, 0] = cor_r + mask(up_r)
            out_ref[problem, 1] = cor_i + mask(up_i)
            return inner

        lax.fori_loop(0, SWEEPS - 1, sweep_body, 0)
        return carry

    lax.fori_loop(0, out_ref.shape[0], problem_body, 0)


def line_matrices(row_blocks, col_blocks):
    block = row_blocks.shape[-1]
    eye = jnp.eye(2, dtype=row_blocks.dtype)
    halves = row_blocks.shape[0] // 2
    rows_t = jnp.transpose(row_blocks, (0, 3, 1, 2)).reshape(halves, 2, block, 2, block)
    row_mats = jnp.einsum("hakmo,ab->hakmbo", rows_t, eye).reshape(halves, 2 * block, 4 * block)
    cols = col_blocks.reshape(halves, 2, 2, block, block)
    col_mats = jnp.einsum("hamok,ab->hmaobk", cols, eye).reshape(halves, 4 * block, 2 * block)
    return row_mats, col_mats


def solve_local_kernel(resid_planes, data_ext, row_mats, col_mats, live_rect, interpret=False):
    rect = jnp.stack([to_index(v) for v in live_rect])
    out_shape = (2, 2) + resid_planes.shape[1:]
    vmem = pltpu.MemorySpace.VMEM if hasattr(pltpu, "MemorySpace") else pltpu.VMEM
    return pl.pallas_call(
        solve_kernel,
        out_shape=jax.ShapeDtypeStruct(out_shape, resid_planes.dtype),
        in_specs=[pl.BlockSpec(memory_space=pltpu.SMEM)] + [pl.BlockSpec(memory_space=vmem)] * 4,
        out_specs=pl.BlockSpec(memory_space=vmem),
        interpret=interpret,
    )(rect, resid_planes, data_ext, row_mats, col_mats)


def shards(sources, wavenumber, row_inverse, col_inverse, reach_steps):
    own_rows, own_cols = (sources.shape[2], sources.shape[3])
    block = row_inverse.shape[-1]
    step_cells = block // 4
    signs = jnp.array([1.0, -1.0], dtype=sources.dtype).reshape(2, 1, 1)
    row_rank = to_index(lax.axis_index("gx"))
    col_rank = to_index(lax.axis_index("gy"))
    row_count = lax.axis_size("gx")
    col_count = lax.axis_size("gy")
    zero = to_index(0)
    widths = reach_steps.reshape(4) * step_cells
    upper_w = jnp.where(row_rank > 0, widths[0], zero)
    lower_w = jnp.where(row_rank < row_count - 1, widths[1], zero)
    left_w = jnp.where(col_rank > 0, widths[2], zero)
    right_w = jnp.where(col_rank < col_count - 1, widths[3], zero)
    live_rect = (
        block - upper_w,
        block + own_rows + lower_w,
        block - left_w,
        block + own_cols + right_w,
    )
    stacked = jnp.concatenate([sources.reshape(4, own_rows, own_cols), wavenumber[None]], axis=0)
    lead = stacked.shape[0]
    col_pair = col_inverse.shape[0]
    row_pair = row_inverse.shape[0]
    inv_rows = col_inverse.shape[1] * block * block // own_cols
    before, after = exchange_axis(
        stacked, "gx", 1, block,
        col_inverse[col_pair - 1].reshape(1, inv_rows, own_cols), col_inverse[0].reshape(1, inv_rows, own_cols),
    )
    tall = jnp.concatenate([before[:lead, :block], stacked, after[:lead, :block]], axis=1)
    def inv_slab(mats):
        flat = mats.reshape(1, -1, block)
        return jnp.pad(flat, ((0, 0), (0, tall.shape[1] - flat.shape[1]), (0, 0)))
    left, right = exchange_axis(tall, "gy", 2, block, inv_slab(row_inverse[row_pair - 1]), inv_slab(row_inverse[0]))
    stacked_ext = jnp.concatenate([left[:lead], tall, right[:lead]], axis=2)
    sources_ext = stacked_ext[:4].reshape(2, 2, own_rows + 2 * block, own_cols + 2 * block)
    wave_ext = stacked_ext[4]
    inv_shape = (1,) + row_inverse.shape[1:]
    inv_size = row_inverse.shape[1] * block * block // block
    col_blocks = jnp.concatenate(
        [before[lead:].reshape(inv_shape), col_inverse, after[lead:].reshape(inv_shape)], axis=0
    )
    row_blocks = jnp.concatenate(
        [left[lead:, :inv_size].reshape(inv_shape), row_inverse, right[lead:, :inv_size].reshape(inv_shape)], axis=0
    )
    row_mats, col_mats = line_matrices(row_blocks, col_blocks)
    width = block + 1
    grid_upper = to_index(jnp.where(row_rank == 0, width, 0))
    grid_lower = to_index(jnp.where(row_rank == row_count - 1, width + own_rows, own_rows + 2 * width))
    grid_left = to_index(jnp.where(col_rank == 0, width, 0))
    grid_right = to_index(jnp.where(col_rank == col_count - 1, width + own_cols, own_cols + 2 * width))
    solution = None
    for iteration in range(ITERS):
        if iteration == 0:
            resid_planes = stacked_ext
        else:
            before, after = exchange_axis(solution, "gx", 2, width)
            tall = jnp.concatenate([before, solution, after], axis=2)
            left, right = exchange_axis(tall, "gy", 3, width)
            padded = jnp.concatenate([left, tall, right], axis=3)
            padded = fill_ghost(padded, grid_upper, grid_lower, grid_left, grid_right, signs)
            resid_ext = sources_ext - apply_operator(padded, wave_ext, signs)
            resid_planes = resid_ext.reshape((4,) + resid_ext.shape[2:])
        correction = solve_local_kernel(resid_planes, stacked_ext, row_mats, col_mats, live_rect)
        own = correction[:, :, block : block + own_rows, block : block + own_cols]
        solution = own if solution is None else solution + own
    return solution


def solution(mesh):
    return jax.shard_map(
        shards,
        mesh=mesh,
        in_specs=(
            P(None, None, "gx", "gy"),
            P("gx", "gy"),
            P("gy", None, None, None),
            P("gx", None, None, None),
            P("gx", "gy", None),
        ),
        out_specs=P(None, None, "gx", "gy"),
        check_vma=False,
    )
```

```python
import jax
import jax.numpy as jnp
from jax import lax
from jax.sharding import PartitionSpec as P
from jax.experimental import pallas as pl
from jax.experimental.pallas import tpu as pltpu

ITERS = 2
SWEEPS = 4


DAMPING = 0.5
ROBIN_COEF = 0.5


def with_halo(shard, sides, width):
    for axis, dim in sides:
        peers, length = (lax.axis_size(axis), shard.shape[dim])
        up = [(i, (i + 1) % peers) for i in range(peers - 1)]
        down = [(j, i) for i, j in up]
        last = lax.slice_in_dim(shard, length - width, length, axis=dim)
        first = lax.slice_in_dim(shard, 0, width, axis=dim)
        before = lax.ppermute(last, axis, up)
        after = lax.ppermute(first, axis, down)
        shard = jnp.concatenate([before, shard, after], axis=dim)
    return shard


def to_index(value):
    return jnp.asarray(value).astype(jnp.int32)


def slice_line(values, start, axis):
    starts = [to_index(0) for _ in range(values.ndim)]
    starts[axis] = to_index(start)
    sizes = list(values.shape)
    sizes[axis] = 1
    return lax.dynamic_slice(values, starts, sizes)


def fill_ghost(values, upper, lower, left, right, signs):
    upper, lower, left, right = (to_index(upper), to_index(lower), to_index(left), to_index(right))
    height, breadth = (values.shape[2], values.shape[3])
    row_ids = lax.broadcasted_iota(jnp.int32, (height, 1), 0)
    col_ids = lax.broadcasted_iota(jnp.int32, (1, breadth), 1)
    upper_row = slice_line(values, upper, 2)
    lower_row = slice_line(values, lower - 1, 2)
    values = jnp.where(row_ids < upper, upper_row, jnp.where(row_ids >= lower, lower_row, values))
    left_col = slice_line(values, left, 3)
    right_col = slice_line(values, right - 1, 3)
    values = jnp.where(col_ids < left, left_col, jnp.where(col_ids >= right, right_col, values))
    inside = (row_ids >= upper) & (row_ids < lower) & (col_ids >= left) & (col_ids < right)
    real_part = values[:, 0]
    imag_part = values[:, 1]
    ghost_cycle = jnp.stack(
        [real_part + signs * ROBIN_COEF * imag_part, imag_part - signs * ROBIN_COEF * real_part],
        axis=1,
    )
    return jnp.where(inside, values, ghost_cycle)


def apply_operator(padded, wave_cells, signs):
    centre = padded[:, :, 1:-1, 1:-1]
    edge_sum = (
        padded[:, :, :-2, 1:-1]
        + padded[:, :, 2:, 1:-1]
        + padded[:, :, 1:-1, :-2]
        + padded[:, :, 1:-1, 2:]
    )
    corner_sum = (
        padded[:, :, :-2, :-2]
        + padded[:, :, :-2, 2:]
        + padded[:, :, 2:, :-2]
        + padded[:, :, 2:, 2:]
    )
    laplace = (4.0 * edge_sum + corner_sum - 20.0 * centre) / 6.0
    real_part = centre[:, 0]
    imag_part = centre[:, 1]
    mass_term = jnp.stack(
        [real_part - signs * DAMPING * imag_part, imag_part + signs * DAMPING * real_part], axis=1
    )
    return -laplace - wave_cells * mass_term


def combine_parts(products, signs, shape):
    real_out = products[0][:, 0] - signs[..., None] * products[1][:, 1]
    imag_out = products[0][:, 1] + signs[..., None] * products[1][:, 0]
    return jnp.stack([real_out, imag_out], axis=1).reshape(shape)


def along_rows(values, inverse, signs):
    block = inverse.shape[-1]
    blocked = values.reshape(values.shape[0], 2, values.shape[2], values.shape[3] // block, block)
    products = jnp.einsum("qmok,fchqk->mfchqo", inverse, blocked, precision=lax.Precision.HIGHEST)
    return combine_parts(products, signs, values.shape)


def along_cols(values, inverse, signs):
    block = inverse.shape[-1]
    blocked = values.reshape(values.shape[0], 2, values.shape[2] // block, block, values.shape[3])
    products = jnp.einsum("qmok,fcqkw->mfcqow", inverse, blocked, precision=lax.Precision.HIGHEST)
    return combine_parts(products, signs, values.shape)


def solve_local(resid_ext, wave_ext, row_blocks, col_blocks, live_rect, signs):
    upper, lower, left, right = [to_index(v) for v in live_rect]
    height, breadth = (resid_ext.shape[2], resid_ext.shape[3])
    row_ids = lax.broadcasted_iota(jnp.int32, (height, 1), 0)
    col_ids = lax.broadcasted_iota(jnp.int32, (1, breadth), 1)
    live_mask = (
        (row_ids >= upper) & (row_ids < lower) & (col_ids >= left) & (col_ids < right)
    ).astype(resid_ext.dtype)
    local_res = resid_ext * live_mask
    correction = jnp.zeros_like(resid_ext)
    for sweep_index in range(SWEEPS):
        if sweep_index > 0:
            padded = jnp.pad(correction, ((0, 0), (0, 0), (1, 1), (1, 1)))
            padded = fill_ghost(padded, upper + 1, lower + 1, left + 1, right + 1, signs)
            local_res = live_mask * (resid_ext - apply_operator(padded, wave_ext, signs))
        if sweep_index % 2 == 0:
            update = along_rows(local_res, row_blocks, signs)
        else:
            update = along_cols(local_res, col_blocks, signs)
        correction = correction + live_mask * update
    return correction


def exchange(x, row_width, col_width, extra=None):
    row_count = lax.axis_size("gx")
    col_count = lax.axis_size("gy")
    height, breadth = (x.shape[-2], x.shape[-1])
    pieces = {}
    for dr in (-1, 0, 1):
        for dc in (-1, 0, 1):
            if dr == 0 and dc == 0:
                continue
            slab = x
            if dr == -1:
                slab = lax.slice_in_dim(slab, height - row_width, height, axis=x.ndim - 2)
            elif dr == 1:
                slab = lax.slice_in_dim(slab, 0, row_width, axis=x.ndim - 2)
            if dc == -1:
                slab = lax.slice_in_dim(slab, breadth - col_width, breadth, axis=x.ndim - 1)
            elif dc == 1:
                slab = lax.slice_in_dim(slab, 0, col_width, axis=x.ndim - 1)
            if extra is not None and (dr, dc) in extra:
                slab = jnp.concatenate([slab, extra[(dr, dc)]], axis=0)
            perm = []
            for r in range(row_count):
                for c in range(col_count):
                    rr, cc = (r - dr, c - dc)
                    if 0 <= rr < row_count and 0 <= cc < col_count:
                        perm.append((r * col_count + c, rr * col_count + cc))
            pieces[(dr, dc)] = lax.ppermute(slab, ("gx", "gy"), perm)
    return pieces


def exchange_axis(x, axis, dim, width, extra_lo=None, extra_hi=None):
    peers, length = (lax.axis_size(axis), x.shape[dim])
    up = [(i, i + 1) for i in range(peers - 1)]
    down = [(j, i) for i, j in up]
    last = lax.slice_in_dim(x, length - width, length, axis=dim)
    first = lax.slice_in_dim(x, 0, width, axis=dim)
    if extra_lo is not None:
        last = jnp.concatenate([last, extra_lo], axis=0)
        first = jnp.concatenate([first, extra_hi], axis=0)
    return lax.ppermute(last, axis, up), lax.ppermute(first, axis, down)


def assemble(pieces, centre, lead):
    rows = []
    for dr in (-1, 0, 1):
        row = []
        for dc in (-1, 0, 1):
            part = centre if (dr == 0 and dc == 0) else pieces[(dr, dc)][:lead]
            row.append(part)
        rows.append(jnp.concatenate(row, axis=-1))
    return jnp.concatenate(rows, axis=-2)


def solve_kernel(rect_ref, resid_ref, data_ref, wrow_ref, wcol_ref, out_ref):
    height, breadth = (resid_ref.shape[1], resid_ref.shape[2])
    half = height // 2
    upper, lower, left, right = (rect_ref[0], rect_ref[1], rect_ref[2], rect_ref[3])
    row_ids = lax.broadcasted_iota(jnp.int32, (height, breadth), 0)
    col_ids = lax.broadcasted_iota(jnp.int32, (height, breadth), 1)
    live = (row_ids >= upper) & (row_ids < lower) & (col_ids >= left) & (col_ids < right)
    top, bottom = (row_ids == upper, row_ids == lower - 1)
    first, last = (col_ids == left, col_ids == right - 1)
    row_flag = top.astype(jnp.float32) + bottom.astype(jnp.float32)
    col_flag = first.astype(jnp.float32) + last.astype(jnp.float32)
    edge_flag = 4.0 * (row_flag + col_flag)
    zero = jnp.zeros((height, breadth), jnp.float32)

    def mask(x):
        return jnp.where(live, x, zero)

    def rows_sum(x):
        up = jnp.where(top, x, pltpu.roll(x, 1, 0))
        down = jnp.where(bottom, x, pltpu.roll(x, height - 1, 0))
        return up + down

    def cols_sum(x):
        lft = jnp.where(first, x, pltpu.roll(x, 1, 1))
        rgt = jnp.where(last, x, pltpu.roll(x, breadth - 1, 1))
        return lft + rgt

    def stencil(x):
        vertical = rows_sum(x)
        ghost_rows = row_flag * x
        total = 4.0 * (vertical + cols_sum(x)) + cols_sum(vertical)
        ghost = edge_flag * x + cols_sum(ghost_rows) + col_flag * (vertical - ghost_rows)
        return total, ghost

    def operator(real_part, imag_part, sign):
        wave = data_ref[4]
        total_r, ghost_r = stencil(real_part)
        total_i, ghost_i = stencil(imag_part)
        lap_r = (total_r + sign * ROBIN_COEF * ghost_i - 20.0 * real_part) / 6.0
        lap_i = (total_i - sign * ROBIN_COEF * ghost_r - 20.0 * imag_part) / 6.0
        mass_r = real_part - sign * DAMPING * imag_part
        mass_i = imag_part + sign * DAMPING * real_part
        return (-lap_r - wave * mass_r, -lap_i - wave * mass_i)

    def dot(a, b):
        return jnp.dot(a, b, precision=lax.Precision.HIGH, preferred_element_type=jnp.float32)

    def rows_apply(real_part, imag_part, sign):
        outs_r, outs_i = ([], [])
        for h in range(breadth // half):
            cols = slice(h * half, (h + 1) * half)
            prod_r = dot(real_part[:, cols], wrow_ref[h])
            prod_i = dot(imag_part[:, cols], wrow_ref[h])
            outs_r.append(prod_r[:, :half] - sign * prod_i[:, half:])
            outs_i.append(prod_i[:, :half] + sign * prod_r[:, half:])
        return (jnp.concatenate(outs_r, axis=1), jnp.concatenate(outs_i, axis=1))

    def cols_apply(real_part, imag_part, sign):
        outs_r, outs_i = ([], [])
        for h in range(height // half):
            rows = slice(h * half, (h + 1) * half)
            prod_r = dot(wcol_ref[h], real_part[rows, :])
            prod_i = dot(wcol_ref[h], imag_part[rows, :])
            outs_r.append(prod_r[:half] - sign * prod_i[half:])
            outs_i.append(prod_i[:half] + sign * prod_r[half:])
        return (jnp.concatenate(outs_r, axis=0), jnp.concatenate(outs_i, axis=0))

    def problem_body(problem, carry):
        sign = 1.0 - 2.0 * problem.astype(jnp.float32)
        up_r, up_i = rows_apply(mask(resid_ref[2 * problem]), mask(resid_ref[2 * problem + 1]), sign)
        out_ref[problem, 0] = mask(up_r)
        out_ref[problem, 1] = mask(up_i)

        cor_r, cor_i = (mask(up_r), mask(up_i))
        for step in range(SWEEPS - 1):
            op_r, op_i = operator(cor_r, cor_i, sign)
            loc_r, loc_i = (mask(resid_ref[2 * problem] - op_r), mask(resid_ref[2 * problem + 1] - op_i))
            apply = cols_apply if step % 2 == 0 else rows_apply
            up_r, up_i = apply(loc_r, loc_i, sign)
            cor_r, cor_i = (cor_r + mask(up_r), cor_i + mask(up_i))
        out_ref[problem, 0] = cor_r
        out_ref[problem, 1] = cor_i
        return carry

    lax.fori_loop(0, out_ref.shape[0], problem_body, 0)


def line_matrices(row_blocks, col_blocks):
    block = row_blocks.shape[-1]
    eye = jnp.eye(2, dtype=row_blocks.dtype)
    halves = row_blocks.shape[0] // 2
    rows_t = jnp.transpose(row_blocks, (0, 3, 1, 2)).reshape(halves, 2, block, 2, block)
    row_mats = jnp.einsum("hakmo,ab->hakmbo", rows_t, eye).reshape(halves, 2 * block, 4 * block)
    cols = col_blocks.reshape(halves, 2, 2, block, block)
    col_mats = jnp.einsum("hamok,ab->hmaobk", cols, eye).reshape(halves, 4 * block, 2 * block)
    return row_mats, col_mats


def solve_local_kernel(resid_planes, data_ext, row_mats, col_mats, live_rect, interpret=False):
    rect = jnp.stack([to_index(v) for v in live_rect])
    out_shape = (2, 2) + resid_planes.shape[1:]
    vmem = pltpu.MemorySpace.VMEM if hasattr(pltpu, "MemorySpace") else pltpu.VMEM
    return pl.pallas_call(
        solve_kernel,
        out_shape=jax.ShapeDtypeStruct(out_shape, resid_planes.dtype),
        in_specs=[pl.BlockSpec(memory_space=pltpu.SMEM)] + [pl.BlockSpec(memory_space=vmem)] * 4,
        out_specs=pl.BlockSpec(memory_space=vmem),
        interpret=interpret,
    )(rect, resid_planes, data_ext, row_mats, col_mats)


def shards(sources, wavenumber, row_inverse, col_inverse, reach_steps):
    own_rows, own_cols = (sources.shape[2], sources.shape[3])
    block = row_inverse.shape[-1]
    step_cells = block // 4
    signs = jnp.array([1.0, -1.0], dtype=sources.dtype).reshape(2, 1, 1)
    row_rank = to_index(lax.axis_index("gx"))
    col_rank = to_index(lax.axis_index("gy"))
    row_count = lax.axis_size("gx")
    col_count = lax.axis_size("gy")
    zero = to_index(0)
    widths = reach_steps.reshape(4) * step_cells
    upper_w = jnp.where(row_rank > 0, widths[0], zero)
    lower_w = jnp.where(row_rank < row_count - 1, widths[1], zero)
    left_w = jnp.where(col_rank > 0, widths[2], zero)
    right_w = jnp.where(col_rank < col_count - 1, widths[3], zero)
    live_rect = (
        block - upper_w,
        block + own_rows + lower_w,
        block - left_w,
        block + own_cols + right_w,
    )
    stacked = jnp.concatenate([sources.reshape(4, own_rows, own_cols), wavenumber[None]], axis=0)
    lead = stacked.shape[0]
    col_pair = col_inverse.shape[0]
    row_pair = row_inverse.shape[0]
    inv_rows = col_inverse.shape[1] * block * block // own_cols
    before, after = exchange_axis(
        stacked, "gx", 1, block,
        col_inverse[col_pair - 1].reshape(1, inv_rows, own_cols), col_inverse[0].reshape(1, inv_rows, own_cols),
    )
    tall = jnp.concatenate([before[:lead, :block], stacked, after[:lead, :block]], axis=1)
    def inv_slab(mats):
        flat = mats.reshape(1, -1, block)
        return jnp.pad(flat, ((0, 0), (0, tall.shape[1] - flat.shape[1]), (0, 0)))
    left, right = exchange_axis(tall, "gy", 2, block, inv_slab(row_inverse[row_pair - 1]), inv_slab(row_inverse[0]))
    stacked_ext = jnp.concatenate([left[:lead], tall, right[:lead]], axis=2)
    sources_ext = stacked_ext[:4].reshape(2, 2, own_rows + 2 * block, own_cols + 2 * block)
    wave_ext = stacked_ext[4]
    inv_shape = (1,) + row_inverse.shape[1:]
    inv_size = row_inverse.shape[1] * block * block // block
    col_blocks = jnp.concatenate(
        [before[lead:].reshape(inv_shape), col_inverse, after[lead:].reshape(inv_shape)], axis=0
    )
    row_blocks = jnp.concatenate(
        [left[lead:, :inv_size].reshape(inv_shape), row_inverse, right[lead:, :inv_size].reshape(inv_shape)], axis=0
    )
    row_mats, col_mats = line_matrices(row_blocks, col_blocks)
    width = block + 1
    grid_upper = to_index(jnp.where(row_rank == 0, width, 0))
    grid_lower = to_index(jnp.where(row_rank == row_count - 1, width + own_rows, own_rows + 2 * width))
    grid_left = to_index(jnp.where(col_rank == 0, width, 0))
    grid_right = to_index(jnp.where(col_rank == col_count - 1, width + own_cols, own_cols + 2 * width))
    solution = None
    for iteration in range(ITERS):
        if iteration == 0:
            resid_planes = stacked_ext
        else:
            before, after = exchange_axis(solution, "gx", 2, width)
            tall = jnp.concatenate([before, solution, after], axis=2)
            left, right = exchange_axis(tall, "gy", 3, width)
            padded = jnp.concatenate([left, tall, right], axis=3)
            padded = fill_ghost(padded, grid_upper, grid_lower, grid_left, grid_right, signs)
            resid_ext = sources_ext - apply_operator(padded, wave_ext, signs)
            resid_planes = resid_ext.reshape((4,) + resid_ext.shape[2:])
        correction = solve_local_kernel(resid_planes, stacked_ext, row_mats, col_mats, live_rect)
        own = correction[:, :, block : block + own_rows, block : block + own_cols]
        solution = own if solution is None else solution + own
    return solution


def solution(mesh):
    return jax.shard_map(
        shards,
        mesh=mesh,
        in_specs=(
            P(None, None, "gx", "gy"),
            P("gx", "gy"),
            P("gy", None, None, None),
            P("gx", None, None, None),
            P("gx", "gy", None),
        ),
        out_specs=P(None, None, "gx", "gy"),
        check_vma=False,
    )
```

```python
import jax
import jax.numpy as jnp
from jax import lax
from jax.sharding import PartitionSpec as P
from jax.experimental import pallas as pl
from jax.experimental.pallas import tpu as pltpu

ITERS = 2
SWEEPS = 4


DAMPING = 0.5
ROBIN_COEF = 0.5


def with_halo(shard, sides, width):
    for axis, dim in sides:
        peers, length = (lax.axis_size(axis), shard.shape[dim])
        up = [(i, (i + 1) % peers) for i in range(peers - 1)]
        down = [(j, i) for i, j in up]
        last = lax.slice_in_dim(shard, length - width, length, axis=dim)
        first = lax.slice_in_dim(shard, 0, width, axis=dim)
        before = lax.ppermute(last, axis, up)
        after = lax.ppermute(first, axis, down)
        shard = jnp.concatenate([before, shard, after], axis=dim)
    return shard


def to_index(value):
    return jnp.asarray(value).astype(jnp.int32)


def slice_line(values, start, axis):
    starts = [to_index(0) for _ in range(values.ndim)]
    starts[axis] = to_index(start)
    sizes = list(values.shape)
    sizes[axis] = 1
    return lax.dynamic_slice(values, starts, sizes)


def fill_ghost(values, upper, lower, left, right, signs):
    upper, lower, left, right = (to_index(upper), to_index(lower), to_index(left), to_index(right))
    height, breadth = (values.shape[2], values.shape[3])
    row_ids = lax.broadcasted_iota(jnp.int32, (height, 1), 0)
    col_ids = lax.broadcasted_iota(jnp.int32, (1, breadth), 1)
    upper_row = slice_line(values, upper, 2)
    lower_row = slice_line(values, lower - 1, 2)
    values = jnp.where(row_ids < upper, upper_row, jnp.where(row_ids >= lower, lower_row, values))
    left_col = slice_line(values, left, 3)
    right_col = slice_line(values, right - 1, 3)
    values = jnp.where(col_ids < left, left_col, jnp.where(col_ids >= right, right_col, values))
    inside = (row_ids >= upper) & (row_ids < lower) & (col_ids >= left) & (col_ids < right)
    real_part = values[:, 0]
    imag_part = values[:, 1]
    ghost_cycle = jnp.stack(
        [real_part + signs * ROBIN_COEF * imag_part, imag_part - signs * ROBIN_COEF * real_part],
        axis=1,
    )
    return jnp.where(inside, values, ghost_cycle)


def grid_ghost(values, width, edges, signs):
    at_top, at_bottom, at_left, at_right = edges
    height, breadth = (values.shape[2], values.shape[3])
    row_ids = lax.broadcasted_iota(jnp.int32, (height, 1), 0)
    col_ids = lax.broadcasted_iota(jnp.int32, (1, breadth), 1)
    above = at_top & (row_ids < width)
    below = at_bottom & (row_ids >= height - width)
    values = jnp.where(
        above, values[:, :, width : width + 1], jnp.where(below, values[:, :, height - width - 1 : height - width], values)
    )
    before = at_left & (col_ids < width)
    after = at_right & (col_ids >= breadth - width)
    values = jnp.where(
        before, values[:, :, :, width : width + 1],
        jnp.where(after, values[:, :, :, breadth - width - 1 : breadth - width], values),
    )
    outside = above | below | before | after
    real_part = values[:, 0]
    imag_part = values[:, 1]
    ghost_cycle = jnp.stack(
        [real_part + signs * ROBIN_COEF * imag_part, imag_part - signs * ROBIN_COEF * real_part],
        axis=1,
    )
    return jnp.where(outside, ghost_cycle, values)


def apply_operator(padded, wave_cells, signs):
    centre = padded[:, :, 1:-1, 1:-1]
    edge_sum = (
        padded[:, :, :-2, 1:-1]
        + padded[:, :, 2:, 1:-1]
        + padded[:, :, 1:-1, :-2]
        + padded[:, :, 1:-1, 2:]
    )
    corner_sum = (
        padded[:, :, :-2, :-2]
        + padded[:, :, :-2, 2:]
        + padded[:, :, 2:, :-2]
        + padded[:, :, 2:, 2:]
    )
    laplace = (4.0 * edge_sum + corner_sum - 20.0 * centre) / 6.0
    real_part = centre[:, 0]
    imag_part = centre[:, 1]
    mass_term = jnp.stack(
        [real_part - signs * DAMPING * imag_part, imag_part + signs * DAMPING * real_part], axis=1
    )
    return -laplace - wave_cells * mass_term


def combine_parts(products, signs, shape):
    real_out = products[0][:, 0] - signs[..., None] * products[1][:, 1]
    imag_out = products[0][:, 1] + signs[..., None] * products[1][:, 0]
    return jnp.stack([real_out, imag_out], axis=1).reshape(shape)


def along_rows(values, inverse, signs):
    block = inverse.shape[-1]
    blocked = values.reshape(values.shape[0], 2, values.shape[2], values.shape[3] // block, block)
    products = jnp.einsum("qmok,fchqk->mfchqo", inverse, blocked, precision=lax.Precision.HIGHEST)
    return combine_parts(products, signs, values.shape)


def along_cols(values, inverse, signs):
    block = inverse.shape[-1]
    blocked = values.reshape(values.shape[0], 2, values.shape[2] // block, block, values.shape[3])
    products = jnp.einsum("qmok,fcqkw->mfcqow", inverse, blocked, precision=lax.Precision.HIGHEST)
    return combine_parts(products, signs, values.shape)


def solve_local(resid_ext, wave_ext, row_blocks, col_blocks, live_rect, signs):
    upper, lower, left, right = [to_index(v) for v in live_rect]
    height, breadth = (resid_ext.shape[2], resid_ext.shape[3])
    row_ids = lax.broadcasted_iota(jnp.int32, (height, 1), 0)
    col_ids = lax.broadcasted_iota(jnp.int32, (1, breadth), 1)
    live_mask = (
        (row_ids >= upper) & (row_ids < lower) & (col_ids >= left) & (col_ids < right)
    ).astype(resid_ext.dtype)
    local_res = resid_ext * live_mask
    correction = jnp.zeros_like(resid_ext)
    for sweep_index in range(SWEEPS):
        if sweep_index > 0:
            padded = jnp.pad(correction, ((0, 0), (0, 0), (1, 1), (1, 1)))
            padded = fill_ghost(padded, upper + 1, lower + 1, left + 1, right + 1, signs)
            local_res = live_mask * (resid_ext - apply_operator(padded, wave_ext, signs))
        if sweep_index % 2 == 0:
            update = along_rows(local_res, row_blocks, signs)
        else:
            update = along_cols(local_res, col_blocks, signs)
        correction = correction + live_mask * update
    return correction


def exchange(x, row_width, col_width, extra=None):
    row_count = lax.axis_size("gx")
    col_count = lax.axis_size("gy")
    height, breadth = (x.shape[-2], x.shape[-1])
    pieces = {}
    for dr in (-1, 0, 1):
        for dc in (-1, 0, 1):
            if dr == 0 and dc == 0:
                continue
            slab = x
            if dr == -1:
                slab = lax.slice_in_dim(slab, height - row_width, height, axis=x.ndim - 2)
            elif dr == 1:
                slab = lax.slice_in_dim(slab, 0, row_width, axis=x.ndim - 2)
            if dc == -1:
                slab = lax.slice_in_dim(slab, breadth - col_width, breadth, axis=x.ndim - 1)
            elif dc == 1:
                slab = lax.slice_in_dim(slab, 0, col_width, axis=x.ndim - 1)
            if extra is not None and (dr, dc) in extra:
                slab = jnp.concatenate([slab, extra[(dr, dc)]], axis=0)
            perm = []
            for r in range(row_count):
                for c in range(col_count):
                    rr, cc = (r - dr, c - dc)
                    if 0 <= rr < row_count and 0 <= cc < col_count:
                        perm.append((r * col_count + c, rr * col_count + cc))
            pieces[(dr, dc)] = lax.ppermute(slab, ("gx", "gy"), perm)
    return pieces


def exchange_axis(x, axis, dim, width, extra_lo=None, extra_hi=None):
    peers, length = (lax.axis_size(axis), x.shape[dim])
    up = [(i, i + 1) for i in range(peers - 1)]
    down = [(j, i) for i, j in up]
    last = lax.slice_in_dim(x, length - width, length, axis=dim)
    first = lax.slice_in_dim(x, 0, width, axis=dim)
    if extra_lo is not None:
        last = jnp.concatenate([last, extra_lo], axis=0)
        first = jnp.concatenate([first, extra_hi], axis=0)
    return lax.ppermute(last, axis, up), lax.ppermute(first, axis, down)


def assemble(pieces, centre, lead):
    rows = []
    for dr in (-1, 0, 1):
        row = []
        for dc in (-1, 0, 1):
            part = centre if (dr == 0 and dc == 0) else pieces[(dr, dc)][:lead]
            row.append(part)
        rows.append(jnp.concatenate(row, axis=-1))
    return jnp.concatenate(rows, axis=-2)


def solve_kernel(rect_ref, resid_ref, data_ref, wrow_ref, wcol_ref, *refs):
    out_ref = refs[-1]
    base_ref = refs[0] if len(refs) > 1 else None
    height, breadth = (resid_ref.shape[1], resid_ref.shape[2])
    half = height // 2
    upper, lower, left, right = (rect_ref[0], rect_ref[1], rect_ref[2], rect_ref[3])
    row_ids = lax.broadcasted_iota(jnp.int32, (height, breadth), 0)
    col_ids = lax.broadcasted_iota(jnp.int32, (height, breadth), 1)
    live = (row_ids >= upper) & (row_ids < lower) & (col_ids >= left) & (col_ids < right)
    top, bottom = (row_ids == upper, row_ids == lower - 1)
    first, last = (col_ids == left, col_ids == right - 1)
    row_flag = top.astype(jnp.float32) + bottom.astype(jnp.float32)
    col_flag = first.astype(jnp.float32) + last.astype(jnp.float32)
    edge_flag = 4.0 * (row_flag + col_flag)
    zero = jnp.zeros((height, breadth), jnp.float32)

    def mask(x):
        return jnp.where(live, x, zero)

    def rows_sum(x):
        up = jnp.where(top, x, pltpu.roll(x, 1, 0))
        down = jnp.where(bottom, x, pltpu.roll(x, height - 1, 0))
        return up + down

    def cols_sum(x):
        lft = jnp.where(first, x, pltpu.roll(x, 1, 1))
        rgt = jnp.where(last, x, pltpu.roll(x, breadth - 1, 1))
        return lft + rgt

    def stencil(x):
        vertical = rows_sum(x)
        ghost_rows = row_flag * x
        total = 4.0 * (vertical + cols_sum(x)) + cols_sum(vertical)
        ghost = edge_flag * x + cols_sum(ghost_rows) + col_flag * (vertical - ghost_rows)
        return total, ghost

    def operator(real_part, imag_part, sign):
        wave = data_ref[4]
        total_r, ghost_r = stencil(real_part)
        total_i, ghost_i = stencil(imag_part)
        lap_r = (total_r + sign * ROBIN_COEF * ghost_i - 20.0 * real_part) / 6.0
        lap_i = (total_i - sign * ROBIN_COEF * ghost_r - 20.0 * imag_part) / 6.0
        mass_r = real_part - sign * DAMPING * imag_part
        mass_i = imag_part + sign * DAMPING * real_part
        return (-lap_r - wave * mass_r, -lap_i - wave * mass_i)

    def dot(a, b):
        return jnp.dot(a, b, precision=lax.Precision.HIGH, preferred_element_type=jnp.float32)

    def rows_apply(real_part, imag_part, sign):
        outs_r, outs_i = ([], [])
        for h in range(breadth // half):
            cols = slice(h * half, (h + 1) * half)
            prod_r = dot(real_part[:, cols], wrow_ref[h])
            prod_i = dot(imag_part[:, cols], wrow_ref[h])
            outs_r.append(prod_r[:, :half] - sign * prod_i[:, half:])
            outs_i.append(prod_i[:, :half] + sign * prod_r[:, half:])
        return (jnp.concatenate(outs_r, axis=1), jnp.concatenate(outs_i, axis=1))

    def cols_apply(real_part, imag_part, sign):
        outs_r, outs_i = ([], [])
        for h in range(height // half):
            rows = slice(h * half, (h + 1) * half)
            prod_r = dot(wcol_ref[h], real_part[rows, :])
            prod_i = dot(wcol_ref[h], imag_part[rows, :])
            outs_r.append(prod_r[:half] - sign * prod_i[half:])
            outs_i.append(prod_i[:half] + sign * prod_r[half:])
        return (jnp.concatenate(outs_r, axis=0), jnp.concatenate(outs_i, axis=0))

    def problem_body(problem, carry):
        sign = 1.0 - 2.0 * problem.astype(jnp.float32)
        up_r, up_i = rows_apply(mask(resid_ref[2 * problem]), mask(resid_ref[2 * problem + 1]), sign)
        cor_r, cor_i = (mask(up_r), mask(up_i))
        for step in range(SWEEPS - 1):
            op_r, op_i = operator(cor_r, cor_i, sign)
            loc_r, loc_i = (mask(resid_ref[2 * problem] - op_r), mask(resid_ref[2 * problem + 1] - op_i))
            apply = cols_apply if step % 2 == 0 else rows_apply
            up_r, up_i = apply(loc_r, loc_i, sign)
            cor_r, cor_i = (cor_r + mask(up_r), cor_i + mask(up_i))
        if base_ref is not None:
            cor_r, cor_i = (cor_r + base_ref[problem, 0], cor_i + base_ref[problem, 1])
        out_ref[problem, 0] = cor_r
        out_ref[problem, 1] = cor_i
        return carry

    lax.fori_loop(0, out_ref.shape[0], problem_body, 0)


def line_matrices(row_blocks, col_blocks):
    block = row_blocks.shape[-1]
    eye = jnp.eye(2, dtype=row_blocks.dtype)
    halves = row_blocks.shape[0] // 2
    rows_t = jnp.transpose(row_blocks, (0, 3, 1, 2)).reshape(halves, 2, block, 2, block)
    row_mats = jnp.einsum("hakmo,ab->hakmbo", rows_t, eye).reshape(halves, 2 * block, 4 * block)
    cols = col_blocks.reshape(halves, 2, 2, block, block)
    col_mats = jnp.einsum("hamok,ab->hmaobk", cols, eye).reshape(halves, 4 * block, 2 * block)
    return row_mats, col_mats


def solve_local_kernel(resid_planes, data_ext, row_mats, col_mats, live_rect, base=None, interpret=False):
    extra = [] if base is None else [base]
    rect = jnp.stack([to_index(v) for v in live_rect])
    out_shape = (2, 2) + resid_planes.shape[1:]
    vmem = pltpu.MemorySpace.VMEM if hasattr(pltpu, "MemorySpace") else pltpu.VMEM
    return pl.pallas_call(
        solve_kernel,
        out_shape=jax.ShapeDtypeStruct(out_shape, resid_planes.dtype),
        in_specs=[pl.BlockSpec(memory_space=pltpu.SMEM)] + [pl.BlockSpec(memory_space=vmem)] * (4 + len(extra)),
        out_specs=pl.BlockSpec(memory_space=vmem),
        interpret=interpret,
    )(rect, resid_planes, data_ext, row_mats, col_mats, *extra)


def shards(sources, wavenumber, row_inverse, col_inverse, reach_steps):
    own_rows, own_cols = (sources.shape[2], sources.shape[3])
    block = row_inverse.shape[-1]
    step_cells = block // 4
    signs = jnp.array([1.0, -1.0], dtype=sources.dtype).reshape(2, 1, 1)
    row_rank = to_index(lax.axis_index("gx"))
    col_rank = to_index(lax.axis_index("gy"))
    row_count = lax.axis_size("gx")
    col_count = lax.axis_size("gy")
    zero = to_index(0)
    widths = reach_steps.reshape(4) * step_cells
    upper_w = jnp.where(row_rank > 0, widths[0], zero)
    lower_w = jnp.where(row_rank < row_count - 1, widths[1], zero)
    left_w = jnp.where(col_rank > 0, widths[2], zero)
    right_w = jnp.where(col_rank < col_count - 1, widths[3], zero)
    live_rect = (
        block - upper_w,
        block + own_rows + lower_w,
        block - left_w,
        block + own_cols + right_w,
    )
    stacked = jnp.concatenate([sources.reshape(4, own_rows, own_cols), wavenumber[None]], axis=0)
    lead = stacked.shape[0]
    col_pair = col_inverse.shape[0]
    row_pair = row_inverse.shape[0]
    inv_rows = col_inverse.shape[1] * block * block // own_cols
    before, after = exchange_axis(
        stacked, "gx", 1, block,
        col_inverse[col_pair - 1].reshape(1, inv_rows, own_cols), col_inverse[0].reshape(1, inv_rows, own_cols),
    )
    tall = jnp.concatenate([before[:lead, :block], stacked, after[:lead, :block]], axis=1)
    def inv_slab(mats):
        flat = mats.reshape(1, -1, block)
        return jnp.pad(flat, ((0, 0), (0, tall.shape[1] - flat.shape[1]), (0, 0)))
    left, right = exchange_axis(tall, "gy", 2, block, inv_slab(row_inverse[row_pair - 1]), inv_slab(row_inverse[0]))
    stacked_ext = jnp.concatenate([left[:lead], tall, right[:lead]], axis=2)
    sources_ext = stacked_ext[:4].reshape(2, 2, own_rows + 2 * block, own_cols + 2 * block)
    wave_ext = stacked_ext[4]
    inv_shape = (1,) + row_inverse.shape[1:]
    inv_size = row_inverse.shape[1] * block * block // block
    col_blocks = jnp.concatenate(
        [before[lead:].reshape(inv_shape), col_inverse, after[lead:].reshape(inv_shape)], axis=0
    )
    row_blocks = jnp.concatenate(
        [left[lead:, :inv_size].reshape(inv_shape), row_inverse, right[lead:, :inv_size].reshape(inv_shape)], axis=0
    )
    row_mats, col_mats = line_matrices(row_blocks, col_blocks)
    width = block + 1
    edges = (row_rank == 0, row_rank == row_count - 1, col_rank == 0, col_rank == col_count - 1)
    solution = None
    base = None
    for iteration in range(ITERS):
        if iteration == 0:
            resid_planes = stacked_ext
        else:
            before, after = exchange_axis(solution, "gx", 2, width)
            tall = jnp.concatenate([before, solution, after], axis=2)
            left, right = exchange_axis(tall, "gy", 3, width)
            padded = jnp.concatenate([left, tall, right], axis=3)
            padded = grid_ghost(padded, width, edges, signs)
            resid_ext = sources_ext - apply_operator(padded, wave_ext, signs)
            resid_planes = resid_ext.reshape((4,) + resid_ext.shape[2:])
        correction = solve_local_kernel(resid_planes, stacked_ext, row_mats, col_mats, live_rect, base=base)
        base = correction
        solution = correction[:, :, block : block + own_rows, block : block + own_cols]
    return solution


def solution(mesh):
    return jax.shard_map(
        shards,
        mesh=mesh,
        in_specs=(
            P(None, None, "gx", "gy"),
            P("gx", "gy"),
            P("gy", None, None, None),
            P("gx", None, None, None),
            P("gx", "gy", None),
        ),
        out_specs=P(None, None, "gx", "gy"),
        check_vma=False,
    )
```

```python
import functools

import jax
import jax.numpy as jnp
from jax import lax
from jax.sharding import PartitionSpec as P
from jax.experimental import pallas as pl
from jax.experimental.pallas import tpu as pltpu

ITERS = 2
SWEEPS = 4


DAMPING = 0.5
ROBIN_COEF = 0.5


def with_halo(shard, sides, width):
    for axis, dim in sides:
        peers, length = (lax.axis_size(axis), shard.shape[dim])
        up = [(i, (i + 1) % peers) for i in range(peers - 1)]
        down = [(j, i) for i, j in up]
        last = lax.slice_in_dim(shard, length - width, length, axis=dim)
        first = lax.slice_in_dim(shard, 0, width, axis=dim)
        before = lax.ppermute(last, axis, up)
        after = lax.ppermute(first, axis, down)
        shard = jnp.concatenate([before, shard, after], axis=dim)
    return shard


def to_index(value):
    return jnp.asarray(value).astype(jnp.int32)


def slice_line(values, start, axis):
    starts = [to_index(0) for _ in range(values.ndim)]
    starts[axis] = to_index(start)
    sizes = list(values.shape)
    sizes[axis] = 1
    return lax.dynamic_slice(values, starts, sizes)


def fill_ghost(values, upper, lower, left, right, signs):
    upper, lower, left, right = (to_index(upper), to_index(lower), to_index(left), to_index(right))
    height, breadth = (values.shape[2], values.shape[3])
    row_ids = lax.broadcasted_iota(jnp.int32, (height, 1), 0)
    col_ids = lax.broadcasted_iota(jnp.int32, (1, breadth), 1)
    upper_row = slice_line(values, upper, 2)
    lower_row = slice_line(values, lower - 1, 2)
    values = jnp.where(row_ids < upper, upper_row, jnp.where(row_ids >= lower, lower_row, values))
    left_col = slice_line(values, left, 3)
    right_col = slice_line(values, right - 1, 3)
    values = jnp.where(col_ids < left, left_col, jnp.where(col_ids >= right, right_col, values))
    inside = (row_ids >= upper) & (row_ids < lower) & (col_ids >= left) & (col_ids < right)
    real_part = values[:, 0]
    imag_part = values[:, 1]
    ghost_cycle = jnp.stack(
        [real_part + signs * ROBIN_COEF * imag_part, imag_part - signs * ROBIN_COEF * real_part],
        axis=1,
    )
    return jnp.where(inside, values, ghost_cycle)


def grid_ghost(values, width, edges, signs):
    at_top, at_bottom, at_left, at_right = edges
    height, breadth = (values.shape[2], values.shape[3])
    row_ids = lax.broadcasted_iota(jnp.int32, (height, 1), 0)
    col_ids = lax.broadcasted_iota(jnp.int32, (1, breadth), 1)
    above = at_top & (row_ids < width)
    below = at_bottom & (row_ids >= height - width)
    values = jnp.where(
        above, values[:, :, width : width + 1], jnp.where(below, values[:, :, height - width - 1 : height - width], values)
    )
    before = at_left & (col_ids < width)
    after = at_right & (col_ids >= breadth - width)
    values = jnp.where(
        before, values[:, :, :, width : width + 1],
        jnp.where(after, values[:, :, :, breadth - width - 1 : breadth - width], values),
    )
    outside = above | below | before | after
    real_part = values[:, 0]
    imag_part = values[:, 1]
    ghost_cycle = jnp.stack(
        [real_part + signs * ROBIN_COEF * imag_part, imag_part - signs * ROBIN_COEF * real_part],
        axis=1,
    )
    return jnp.where(outside, ghost_cycle, values)


def apply_operator(padded, wave_cells, signs):
    centre = padded[:, :, 1:-1, 1:-1]
    edge_sum = (
        padded[:, :, :-2, 1:-1]
        + padded[:, :, 2:, 1:-1]
        + padded[:, :, 1:-1, :-2]
        + padded[:, :, 1:-1, 2:]
    )
    corner_sum = (
        padded[:, :, :-2, :-2]
        + padded[:, :, :-2, 2:]
        + padded[:, :, 2:, :-2]
        + padded[:, :, 2:, 2:]
    )
    laplace = (4.0 * edge_sum + corner_sum - 20.0 * centre) / 6.0
    real_part = centre[:, 0]
    imag_part = centre[:, 1]
    mass_term = jnp.stack(
        [real_part - signs * DAMPING * imag_part, imag_part + signs * DAMPING * real_part], axis=1
    )
    return -laplace - wave_cells * mass_term


def combine_parts(products, signs, shape):
    real_out = products[0][:, 0] - signs[..., None] * products[1][:, 1]
    imag_out = products[0][:, 1] + signs[..., None] * products[1][:, 0]
    return jnp.stack([real_out, imag_out], axis=1).reshape(shape)


def along_rows(values, inverse, signs):
    block = inverse.shape[-1]
    blocked = values.reshape(values.shape[0], 2, values.shape[2], values.shape[3] // block, block)
    products = jnp.einsum("qmok,fchqk->mfchqo", inverse, blocked, precision=lax.Precision.HIGHEST)
    return combine_parts(products, signs, values.shape)


def along_cols(values, inverse, signs):
    block = inverse.shape[-1]
    blocked = values.reshape(values.shape[0], 2, values.shape[2] // block, block, values.shape[3])
    products = jnp.einsum("qmok,fcqkw->mfcqow", inverse, blocked, precision=lax.Precision.HIGHEST)
    return combine_parts(products, signs, values.shape)


def solve_local(resid_ext, wave_ext, row_blocks, col_blocks, live_rect, signs):
    upper, lower, left, right = [to_index(v) for v in live_rect]
    height, breadth = (resid_ext.shape[2], resid_ext.shape[3])
    row_ids = lax.broadcasted_iota(jnp.int32, (height, 1), 0)
    col_ids = lax.broadcasted_iota(jnp.int32, (1, breadth), 1)
    live_mask = (
        (row_ids >= upper) & (row_ids < lower) & (col_ids >= left) & (col_ids < right)
    ).astype(resid_ext.dtype)
    local_res = resid_ext * live_mask
    correction = jnp.zeros_like(resid_ext)
    for sweep_index in range(SWEEPS):
        if sweep_index > 0:
            padded = jnp.pad(correction, ((0, 0), (0, 0), (1, 1), (1, 1)))
            padded = fill_ghost(padded, upper + 1, lower + 1, left + 1, right + 1, signs)
            local_res = live_mask * (resid_ext - apply_operator(padded, wave_ext, signs))
        if sweep_index % 2 == 0:
            update = along_rows(local_res, row_blocks, signs)
        else:
            update = along_cols(local_res, col_blocks, signs)
        correction = correction + live_mask * update
    return correction


def exchange(x, row_width, col_width, extra=None):
    row_count = lax.axis_size("gx")
    col_count = lax.axis_size("gy")
    height, breadth = (x.shape[-2], x.shape[-1])
    pieces = {}
    for dr in (-1, 0, 1):
        for dc in (-1, 0, 1):
            if dr == 0 and dc == 0:
                continue
            slab = x
            if dr == -1:
                slab = lax.slice_in_dim(slab, height - row_width, height, axis=x.ndim - 2)
            elif dr == 1:
                slab = lax.slice_in_dim(slab, 0, row_width, axis=x.ndim - 2)
            if dc == -1:
                slab = lax.slice_in_dim(slab, breadth - col_width, breadth, axis=x.ndim - 1)
            elif dc == 1:
                slab = lax.slice_in_dim(slab, 0, col_width, axis=x.ndim - 1)
            if extra is not None and (dr, dc) in extra:
                slab = jnp.concatenate([slab, extra[(dr, dc)]], axis=0)
            perm = []
            for r in range(row_count):
                for c in range(col_count):
                    rr, cc = (r - dr, c - dc)
                    if 0 <= rr < row_count and 0 <= cc < col_count:
                        perm.append((r * col_count + c, rr * col_count + cc))
            pieces[(dr, dc)] = lax.ppermute(slab, ("gx", "gy"), perm)
    return pieces


def exchange_axis(x, axis, dim, width, extra_lo=None, extra_hi=None):
    peers, length = (lax.axis_size(axis), x.shape[dim])
    up = [(i, i + 1) for i in range(peers - 1)]
    down = [(j, i) for i, j in up]
    last = lax.slice_in_dim(x, length - width, length, axis=dim)
    first = lax.slice_in_dim(x, 0, width, axis=dim)
    if extra_lo is not None:
        last = jnp.concatenate([last, extra_lo], axis=0)
        first = jnp.concatenate([first, extra_hi], axis=0)
    return lax.ppermute(last, axis, up), lax.ppermute(first, axis, down)


def assemble(pieces, centre, lead):
    rows = []
    for dr in (-1, 0, 1):
        row = []
        for dc in (-1, 0, 1):
            part = centre if (dr == 0 and dc == 0) else pieces[(dr, dc)][:lead]
            row.append(part)
        rows.append(jnp.concatenate(row, axis=-1))
    return jnp.concatenate(rows, axis=-2)


def solve_kernel(rect_ref, resid_ref, data_ref, wrow_ref, wcol_ref, *refs, has_base, last, own_rows, own_cols, slab):
    base_ref = refs[0] if has_base else None
    outs = refs[1:] if has_base else refs
    full_ref = None if last else outs[0]
    own_ref = outs[-1] if last else outs[1]
    top_ref, bottom_ref = (None, None) if last else outs[2:4]
    height, breadth = (resid_ref.shape[1], resid_ref.shape[2])
    half = height // 2
    upper, lower, left, right = (rect_ref[0], rect_ref[1], rect_ref[2], rect_ref[3])
    row_ids = lax.broadcasted_iota(jnp.int32, (height, breadth), 0)
    col_ids = lax.broadcasted_iota(jnp.int32, (height, breadth), 1)
    live = (row_ids >= upper) & (row_ids < lower) & (col_ids >= left) & (col_ids < right)
    top, bottom = (row_ids == upper, row_ids == lower - 1)
    first, last = (col_ids == left, col_ids == right - 1)
    row_flag = top.astype(jnp.float32) + bottom.astype(jnp.float32)
    col_flag = first.astype(jnp.float32) + last.astype(jnp.float32)
    edge_flag = 4.0 * (row_flag + col_flag)
    zero = jnp.zeros((height, breadth), jnp.float32)

    def mask(x):
        return jnp.where(live, x, zero)

    def rows_sum(x):
        up = jnp.where(top, x, pltpu.roll(x, 1, 0))
        down = jnp.where(bottom, x, pltpu.roll(x, height - 1, 0))
        return up + down

    def cols_sum(x):
        lft = jnp.where(first, x, pltpu.roll(x, 1, 1))
        rgt = jnp.where(last, x, pltpu.roll(x, breadth - 1, 1))
        return lft + rgt

    def stencil(x):
        vertical = rows_sum(x)
        ghost_rows = row_flag * x
        total = 4.0 * (vertical + cols_sum(x)) + cols_sum(vertical)
        ghost = edge_flag * x + cols_sum(ghost_rows) + col_flag * (vertical - ghost_rows)
        return total, ghost

    def operator(real_part, imag_part, sign):
        wave = data_ref[4]
        total_r, ghost_r = stencil(real_part)
        total_i, ghost_i = stencil(imag_part)
        lap_r = (total_r + sign * ROBIN_COEF * ghost_i - 20.0 * real_part) / 6.0
        lap_i = (total_i - sign * ROBIN_COEF * ghost_r - 20.0 * imag_part) / 6.0
        mass_r = real_part - sign * DAMPING * imag_part
        mass_i = imag_part + sign * DAMPING * real_part
        return (-lap_r - wave * mass_r, -lap_i - wave * mass_i)

    def dot(a, b):
        return jnp.dot(a, b, precision=lax.Precision.HIGH, preferred_element_type=jnp.float32)

    def rows_apply(real_part, imag_part, sign):
        outs_r, outs_i = ([], [])
        for h in range(breadth // half):
            cols = slice(h * half, (h + 1) * half)
            prod_r = dot(real_part[:, cols], wrow_ref[h])
            prod_i = dot(imag_part[:, cols], wrow_ref[h])
            outs_r.append(prod_r[:, :half] - sign * prod_i[:, half:])
            outs_i.append(prod_i[:, :half] + sign * prod_r[:, half:])
        return (jnp.concatenate(outs_r, axis=1), jnp.concatenate(outs_i, axis=1))

    def cols_apply(real_part, imag_part, sign):
        outs_r, outs_i = ([], [])
        for h in range(height // half):
            rows = slice(h * half, (h + 1) * half)
            prod_r = dot(wcol_ref[h], real_part[rows, :])
            prod_i = dot(wcol_ref[h], imag_part[rows, :])
            outs_r.append(prod_r[:half] - sign * prod_i[half:])
            outs_i.append(prod_i[:half] + sign * prod_r[half:])
        return (jnp.concatenate(outs_r, axis=0), jnp.concatenate(outs_i, axis=0))

    def problem_body(problem, carry):
        sign = 1.0 - 2.0 * problem.astype(jnp.float32)
        up_r, up_i = rows_apply(mask(resid_ref[2 * problem]), mask(resid_ref[2 * problem + 1]), sign)
        cor_r, cor_i = (mask(up_r), mask(up_i))
        for step in range(SWEEPS - 1):
            op_r, op_i = operator(cor_r, cor_i, sign)
            loc_r, loc_i = (mask(resid_ref[2 * problem] - op_r), mask(resid_ref[2 * problem + 1] - op_i))
            apply = cols_apply if step % 2 == 0 else rows_apply
            up_r, up_i = apply(loc_r, loc_i, sign)
            cor_r, cor_i = (cor_r + mask(up_r), cor_i + mask(up_i))
        if base_ref is not None:
            cor_r, cor_i = (cor_r + base_ref[problem, 0], cor_i + base_ref[problem, 1])
        first_row = (height - own_rows) // 2
        for part, value in ((0, cor_r), (1, cor_i)):
            if full_ref is not None:
                full_ref[problem, part] = value
            own = pltpu.roll(value, breadth - (breadth - own_cols) // 2, 1)[first_row : first_row + own_rows, :own_cols]
            own_ref[problem, part] = own
            if top_ref is not None:
                top_ref[problem, part] = own[:slab]
                bottom_ref[problem, part] = own[own_rows - slab :]
        return carry

    lax.fori_loop(0, resid_ref.shape[0] // 2, problem_body, 0)


def line_matrices(row_blocks, col_blocks):
    block = row_blocks.shape[-1]
    eye = jnp.eye(2, dtype=row_blocks.dtype)
    halves = row_blocks.shape[0] // 2
    rows_t = jnp.transpose(row_blocks, (0, 3, 1, 2)).reshape(halves, 2, block, 2, block)
    row_mats = jnp.einsum("hakmo,ab->hakmbo", rows_t, eye).reshape(halves, 2 * block, 4 * block)
    cols = col_blocks.reshape(halves, 2, 2, block, block)
    col_mats = jnp.einsum("hamok,ab->hmaobk", cols, eye).reshape(halves, 4 * block, 2 * block)
    return row_mats, col_mats


def solve_local_kernel(resid_planes, data_ext, row_mats, col_mats, live_rect, own_shape, slab, base=None, last=False,
                       interpret=False):
    extra = [] if base is None else [base]
    rect = jnp.stack([to_index(v) for v in live_rect])
    dtype = resid_planes.dtype
    shapes = [] if last else [(2, 2) + resid_planes.shape[1:]]
    shapes.append((2, 2) + own_shape)
    if not last:
        shapes += [(2, 2, slab, own_shape[1])] * 2
    vmem = pltpu.MemorySpace.VMEM if hasattr(pltpu, "MemorySpace") else pltpu.VMEM
    kernel = functools.partial(
        solve_kernel, has_base=base is not None, last=last, own_rows=own_shape[0], own_cols=own_shape[1], slab=slab
    )
    return pl.pallas_call(
        kernel,
        out_shape=[jax.ShapeDtypeStruct(s, dtype) for s in shapes],
        in_specs=[pl.BlockSpec(memory_space=pltpu.SMEM)] + [pl.BlockSpec(memory_space=vmem)] * (4 + len(extra)),
        out_specs=[pl.BlockSpec(memory_space=vmem)] * len(shapes),
        interpret=interpret,
    )(rect, resid_planes, data_ext, row_mats, col_mats, *extra)


def shards(sources, wavenumber, row_inverse, col_inverse, reach_steps):
    own_rows, own_cols = (sources.shape[2], sources.shape[3])
    block = row_inverse.shape[-1]
    step_cells = block // 4
    signs = jnp.array([1.0, -1.0], dtype=sources.dtype).reshape(2, 1, 1)
    row_rank = to_index(lax.axis_index("gx"))
    col_rank = to_index(lax.axis_index("gy"))
    row_count = lax.axis_size("gx")
    col_count = lax.axis_size("gy")
    zero = to_index(0)
    widths = reach_steps.reshape(4) * step_cells
    upper_w = jnp.where(row_rank > 0, widths[0], zero)
    lower_w = jnp.where(row_rank < row_count - 1, widths[1], zero)
    left_w = jnp.where(col_rank > 0, widths[2], zero)
    right_w = jnp.where(col_rank < col_count - 1, widths[3], zero)
    live_rect = (
        block - upper_w,
        block + own_rows + lower_w,
        block - left_w,
        block + own_cols + right_w,
    )
    stacked = jnp.concatenate([sources.reshape(4, own_rows, own_cols), wavenumber[None]], axis=0)
    lead = stacked.shape[0]
    col_pair = col_inverse.shape[0]
    row_pair = row_inverse.shape[0]
    inv_rows = col_inverse.shape[1] * block * block // own_cols
    before, after = exchange_axis(
        stacked, "gx", 1, block,
        col_inverse[col_pair - 1].reshape(1, inv_rows, own_cols), col_inverse[0].reshape(1, inv_rows, own_cols),
    )
    tall = jnp.concatenate([before[:lead, :block], stacked, after[:lead, :block]], axis=1)
    def inv_slab(mats):
        flat = mats.reshape(1, -1, block)
        return jnp.pad(flat, ((0, 0), (0, tall.shape[1] - flat.shape[1]), (0, 0)))
    left, right = exchange_axis(tall, "gy", 2, block, inv_slab(row_inverse[row_pair - 1]), inv_slab(row_inverse[0]))
    stacked_ext = jnp.concatenate([left[:lead], tall, right[:lead]], axis=2)
    sources_ext = stacked_ext[:4].reshape(2, 2, own_rows + 2 * block, own_cols + 2 * block)
    wave_ext = stacked_ext[4]
    inv_shape = (1,) + row_inverse.shape[1:]
    inv_size = row_inverse.shape[1] * block * block // block
    col_blocks = jnp.concatenate(
        [before[lead:].reshape(inv_shape), col_inverse, after[lead:].reshape(inv_shape)], axis=0
    )
    row_blocks = jnp.concatenate(
        [left[lead:, :inv_size].reshape(inv_shape), row_inverse, right[lead:, :inv_size].reshape(inv_shape)], axis=0
    )
    row_mats, col_mats = line_matrices(row_blocks, col_blocks)
    width = block + 1
    edges = (row_rank == 0, row_rank == row_count - 1, col_rank == 0, col_rank == col_count - 1)
    slab = -(-width // 8) * 8
    solution = None
    base = None
    for iteration in range(ITERS):
        last = iteration == ITERS - 1
        if iteration == 0:
            resid_planes = stacked_ext
        else:
            peers = lax.axis_size("gx")
            up = [(i, i + 1) for i in range(peers - 1)]
            down = [(j, i) for i, j in up]
            before = lax.ppermute(bottom, "gx", up)[:, :, slab - width :]
            after = lax.ppermute(top, "gx", down)[:, :, :width]
            tall = jnp.concatenate([before, solution, after], axis=2)
            left, right = exchange_axis(tall, "gy", 3, width)
            padded = jnp.concatenate([left, tall, right], axis=3)
            padded = grid_ghost(padded, width, edges, signs)
            resid_ext = sources_ext - apply_operator(padded, wave_ext, signs)
            resid_planes = resid_ext.reshape((4,) + resid_ext.shape[2:])
        outs = solve_local_kernel(
            resid_planes, stacked_ext, row_mats, col_mats, live_rect, (own_rows, own_cols), slab, base=base, last=last
        )
        if last:
            solution = outs[0]
        else:
            base, solution, top, bottom = outs
    return solution


def solution(mesh):
    return jax.shard_map(
        shards,
        mesh=mesh,
        in_specs=(
            P(None, None, "gx", "gy"),
            P("gx", "gy"),
            P("gy", None, None, None),
            P("gx", None, None, None),
            P("gx", "gy", None),
        ),
        out_specs=P(None, None, "gx", "gy"),
        check_vma=False,
    )
```

```python
import functools

import jax
import jax.numpy as jnp
from jax import lax
from jax.sharding import PartitionSpec as P
from jax.experimental import pallas as pl
from jax.experimental.pallas import tpu as pltpu

ITERS = 2
SWEEPS = 4


DAMPING = 0.5
ROBIN_COEF = 0.5


def with_halo(shard, sides, width):
    for axis, dim in sides:
        peers, length = (lax.axis_size(axis), shard.shape[dim])
        up = [(i, (i + 1) % peers) for i in range(peers - 1)]
        down = [(j, i) for i, j in up]
        last = lax.slice_in_dim(shard, length - width, length, axis=dim)
        first = lax.slice_in_dim(shard, 0, width, axis=dim)
        before = lax.ppermute(last, axis, up)
        after = lax.ppermute(first, axis, down)
        shard = jnp.concatenate([before, shard, after], axis=dim)
    return shard


def to_index(value):
    return jnp.asarray(value).astype(jnp.int32)


def slice_line(values, start, axis):
    starts = [to_index(0) for _ in range(values.ndim)]
    starts[axis] = to_index(start)
    sizes = list(values.shape)
    sizes[axis] = 1
    return lax.dynamic_slice(values, starts, sizes)


def fill_ghost(values, upper, lower, left, right, signs):
    upper, lower, left, right = (to_index(upper), to_index(lower), to_index(left), to_index(right))
    height, breadth = (values.shape[2], values.shape[3])
    row_ids = lax.broadcasted_iota(jnp.int32, (height, 1), 0)
    col_ids = lax.broadcasted_iota(jnp.int32, (1, breadth), 1)
    upper_row = slice_line(values, upper, 2)
    lower_row = slice_line(values, lower - 1, 2)
    values = jnp.where(row_ids < upper, upper_row, jnp.where(row_ids >= lower, lower_row, values))
    left_col = slice_line(values, left, 3)
    right_col = slice_line(values, right - 1, 3)
    values = jnp.where(col_ids < left, left_col, jnp.where(col_ids >= right, right_col, values))
    inside = (row_ids >= upper) & (row_ids < lower) & (col_ids >= left) & (col_ids < right)
    real_part = values[:, 0]
    imag_part = values[:, 1]
    ghost_cycle = jnp.stack(
        [real_part + signs * ROBIN_COEF * imag_part, imag_part - signs * ROBIN_COEF * real_part],
        axis=1,
    )
    return jnp.where(inside, values, ghost_cycle)


def grid_ghost(values, width, edges, signs):
    at_top, at_bottom, at_left, at_right = edges
    height, breadth = (values.shape[2], values.shape[3])
    row_ids = lax.broadcasted_iota(jnp.int32, (height, 1), 0)
    col_ids = lax.broadcasted_iota(jnp.int32, (1, breadth), 1)
    above = at_top & (row_ids < width)
    below = at_bottom & (row_ids >= height - width)
    values = jnp.where(
        above, values[:, :, width : width + 1], jnp.where(below, values[:, :, height - width - 1 : height - width], values)
    )
    before = at_left & (col_ids < width)
    after = at_right & (col_ids >= breadth - width)
    values = jnp.where(
        before, values[:, :, :, width : width + 1],
        jnp.where(after, values[:, :, :, breadth - width - 1 : breadth - width], values),
    )
    outside = above | below | before | after
    real_part = values[:, 0]
    imag_part = values[:, 1]
    ghost_cycle = jnp.stack(
        [real_part + signs * ROBIN_COEF * imag_part, imag_part - signs * ROBIN_COEF * real_part],
        axis=1,
    )
    return jnp.where(outside, ghost_cycle, values)


def apply_operator(padded, wave_cells, signs):
    centre = padded[:, :, 1:-1, 1:-1]
    edge_sum = (
        padded[:, :, :-2, 1:-1]
        + padded[:, :, 2:, 1:-1]
        + padded[:, :, 1:-1, :-2]
        + padded[:, :, 1:-1, 2:]
    )
    corner_sum = (
        padded[:, :, :-2, :-2]
        + padded[:, :, :-2, 2:]
        + padded[:, :, 2:, :-2]
        + padded[:, :, 2:, 2:]
    )
    laplace = (4.0 * edge_sum + corner_sum - 20.0 * centre) / 6.0
    real_part = centre[:, 0]
    imag_part = centre[:, 1]
    mass_term = jnp.stack(
        [real_part - signs * DAMPING * imag_part, imag_part + signs * DAMPING * real_part], axis=1
    )
    return -laplace - wave_cells * mass_term


def combine_parts(products, signs, shape):
    real_out = products[0][:, 0] - signs[..., None] * products[1][:, 1]
    imag_out = products[0][:, 1] + signs[..., None] * products[1][:, 0]
    return jnp.stack([real_out, imag_out], axis=1).reshape(shape)


def along_rows(values, inverse, signs):
    block = inverse.shape[-1]
    blocked = values.reshape(values.shape[0], 2, values.shape[2], values.shape[3] // block, block)
    products = jnp.einsum("qmok,fchqk->mfchqo", inverse, blocked, precision=lax.Precision.HIGHEST)
    return combine_parts(products, signs, values.shape)


def along_cols(values, inverse, signs):
    block = inverse.shape[-1]
    blocked = values.reshape(values.shape[0], 2, values.shape[2] // block, block, values.shape[3])
    products = jnp.einsum("qmok,fcqkw->mfcqow", inverse, blocked, precision=lax.Precision.HIGHEST)
    return combine_parts(products, signs, values.shape)


def solve_local(resid_ext, wave_ext, row_blocks, col_blocks, live_rect, signs):
    upper, lower, left, right = [to_index(v) for v in live_rect]
    height, breadth = (resid_ext.shape[2], resid_ext.shape[3])
    row_ids = lax.broadcasted_iota(jnp.int32, (height, 1), 0)
    col_ids = lax.broadcasted_iota(jnp.int32, (1, breadth), 1)
    live_mask = (
        (row_ids >= upper) & (row_ids < lower) & (col_ids >= left) & (col_ids < right)
    ).astype(resid_ext.dtype)
    local_res = resid_ext * live_mask
    correction = jnp.zeros_like(resid_ext)
    for sweep_index in range(SWEEPS):
        if sweep_index > 0:
            padded = jnp.pad(correction, ((0, 0), (0, 0), (1, 1), (1, 1)))
            padded = fill_ghost(padded, upper + 1, lower + 1, left + 1, right + 1, signs)
            local_res = live_mask * (resid_ext - apply_operator(padded, wave_ext, signs))
        if sweep_index % 2 == 0:
            update = along_rows(local_res, row_blocks, signs)
        else:
            update = along_cols(local_res, col_blocks, signs)
        correction = correction + live_mask * update
    return correction


def exchange(x, row_width, col_width, extra=None):
    row_count = lax.axis_size("gx")
    col_count = lax.axis_size("gy")
    height, breadth = (x.shape[-2], x.shape[-1])
    pieces = {}
    for dr in (-1, 0, 1):
        for dc in (-1, 0, 1):
            if dr == 0 and dc == 0:
                continue
            slab = x
            if dr == -1:
                slab = lax.slice_in_dim(slab, height - row_width, height, axis=x.ndim - 2)
            elif dr == 1:
                slab = lax.slice_in_dim(slab, 0, row_width, axis=x.ndim - 2)
            if dc == -1:
                slab = lax.slice_in_dim(slab, breadth - col_width, breadth, axis=x.ndim - 1)
            elif dc == 1:
                slab = lax.slice_in_dim(slab, 0, col_width, axis=x.ndim - 1)
            if extra is not None and (dr, dc) in extra:
                slab = jnp.concatenate([slab, extra[(dr, dc)]], axis=0)
            perm = []
            for r in range(row_count):
                for c in range(col_count):
                    rr, cc = (r - dr, c - dc)
                    if 0 <= rr < row_count and 0 <= cc < col_count:
                        perm.append((r * col_count + c, rr * col_count + cc))
            pieces[(dr, dc)] = lax.ppermute(slab, ("gx", "gy"), perm)
    return pieces


def exchange_axis(x, axis, dim, width, extra_lo=None, extra_hi=None):
    peers, length = (lax.axis_size(axis), x.shape[dim])
    up = [(i, i + 1) for i in range(peers - 1)]
    down = [(j, i) for i, j in up]
    last = lax.slice_in_dim(x, length - width, length, axis=dim)
    first = lax.slice_in_dim(x, 0, width, axis=dim)
    if extra_lo is not None:
        last = jnp.concatenate([last, extra_lo], axis=0)
        first = jnp.concatenate([first, extra_hi], axis=0)
    return lax.ppermute(last, axis, up), lax.ppermute(first, axis, down)


def assemble(pieces, centre, lead):
    rows = []
    for dr in (-1, 0, 1):
        row = []
        for dc in (-1, 0, 1):
            part = centre if (dr == 0 and dc == 0) else pieces[(dr, dc)][:lead]
            row.append(part)
        rows.append(jnp.concatenate(row, axis=-1))
    return jnp.concatenate(rows, axis=-2)


def grid_residual(fields_ref, data_ref, res_ref):
    height, breadth = (res_ref.shape[1], res_ref.shape[2])

    def ahead(x, step, axis):
        return pltpu.roll(x, x.shape[axis] - step, axis)

    for problem in range(res_ref.shape[0] // 2):
        sign = 1.0 - 2.0 * problem
        totals, centres = ([], [])
        for part in range(2):
            padded = fields_ref[2 * problem + part]
            outer = padded + ahead(padded, 2, 0)
            middle = ahead(padded, 1, 0)
            edge = ahead(outer, 1, 1) + middle + ahead(middle, 2, 1)
            corner = outer + ahead(outer, 2, 1)
            totals.append((4.0 * edge + corner)[:height, :breadth])
            centres.append(ahead(middle, 1, 1)[:height, :breadth])
        real_part, imag_part = centres
        wave = data_ref[4]
        lap_r = (totals[0] - 20.0 * real_part) / 6.0
        lap_i = (totals[1] - 20.0 * imag_part) / 6.0
        mass_r = real_part - sign * DAMPING * imag_part
        mass_i = imag_part + sign * DAMPING * real_part
        res_ref[2 * problem] = data_ref[2 * problem] - (-lap_r - wave * mass_r)
        res_ref[2 * problem + 1] = data_ref[2 * problem + 1] - (-lap_i - wave * mass_i)


def solve_kernel(rect_ref, resid_ref, data_ref, wrow_ref, wcol_ref, *refs, has_base, last, own_rows, own_cols, slab,
                 from_fields):
    if from_fields:
        grid_residual(resid_ref, data_ref, refs[-1])
        resid_ref = refs[-1]
        refs = refs[:-1]
    base_ref = refs[0] if has_base else None
    outs = refs[1:] if has_base else refs
    full_ref = None if last else outs[0]
    own_ref = outs[-1] if last else outs[1]
    top_ref, bottom_ref = (None, None) if last else outs[2:4]
    height, breadth = (resid_ref.shape[1], resid_ref.shape[2])
    half = height // 2
    upper, lower, left, right = (rect_ref[0], rect_ref[1], rect_ref[2], rect_ref[3])
    row_ids = lax.broadcasted_iota(jnp.int32, (height, breadth), 0)
    col_ids = lax.broadcasted_iota(jnp.int32, (height, breadth), 1)
    live = (row_ids >= upper) & (row_ids < lower) & (col_ids >= left) & (col_ids < right)
    top, bottom = (row_ids == upper, row_ids == lower - 1)
    first, last = (col_ids == left, col_ids == right - 1)
    row_flag = top.astype(jnp.float32) + bottom.astype(jnp.float32)
    col_flag = first.astype(jnp.float32) + last.astype(jnp.float32)
    edge_flag = 4.0 * (row_flag + col_flag)
    zero = jnp.zeros((height, breadth), jnp.float32)

    def mask(x):
        return jnp.where(live, x, zero)

    def rows_sum(x):
        up = jnp.where(top, x, pltpu.roll(x, 1, 0))
        down = jnp.where(bottom, x, pltpu.roll(x, height - 1, 0))
        return up + down

    def cols_sum(x):
        lft = jnp.where(first, x, pltpu.roll(x, 1, 1))
        rgt = jnp.where(last, x, pltpu.roll(x, breadth - 1, 1))
        return lft + rgt

    def stencil(x):
        vertical = rows_sum(x)
        ghost_rows = row_flag * x
        total = 4.0 * (vertical + cols_sum(x)) + cols_sum(vertical)
        ghost = edge_flag * x + cols_sum(ghost_rows) + col_flag * (vertical - ghost_rows)
        return total, ghost

    def operator(real_part, imag_part, sign):
        wave = data_ref[4]
        total_r, ghost_r = stencil(real_part)
        total_i, ghost_i = stencil(imag_part)
        lap_r = (total_r + sign * ROBIN_COEF * ghost_i - 20.0 * real_part) / 6.0
        lap_i = (total_i - sign * ROBIN_COEF * ghost_r - 20.0 * imag_part) / 6.0
        mass_r = real_part - sign * DAMPING * imag_part
        mass_i = imag_part + sign * DAMPING * real_part
        return (-lap_r - wave * mass_r, -lap_i - wave * mass_i)

    def dot(a, b):
        return jnp.dot(a, b, precision=lax.Precision.HIGH, preferred_element_type=jnp.float32)

    def rows_apply(real_part, imag_part, sign):
        outs_r, outs_i = ([], [])
        for h in range(breadth // half):
            cols = slice(h * half, (h + 1) * half)
            prod_r = dot(real_part[:, cols], wrow_ref[h])
            prod_i = dot(imag_part[:, cols], wrow_ref[h])
            outs_r.append(prod_r[:, :half] - sign * prod_i[:, half:])
            outs_i.append(prod_i[:, :half] + sign * prod_r[:, half:])
        return (jnp.concatenate(outs_r, axis=1), jnp.concatenate(outs_i, axis=1))

    def cols_apply(real_part, imag_part, sign):
        outs_r, outs_i = ([], [])
        for h in range(height // half):
            rows = slice(h * half, (h + 1) * half)
            prod_r = dot(wcol_ref[h], real_part[rows, :])
            prod_i = dot(wcol_ref[h], imag_part[rows, :])
            outs_r.append(prod_r[:half] - sign * prod_i[half:])
            outs_i.append(prod_i[:half] + sign * prod_r[half:])
        return (jnp.concatenate(outs_r, axis=0), jnp.concatenate(outs_i, axis=0))

    def problem_body(problem, carry):
        sign = 1.0 - 2.0 * problem.astype(jnp.float32)
        up_r, up_i = rows_apply(mask(resid_ref[2 * problem]), mask(resid_ref[2 * problem + 1]), sign)
        cor_r, cor_i = (mask(up_r), mask(up_i))
        for step in range(SWEEPS - 1):
            op_r, op_i = operator(cor_r, cor_i, sign)
            loc_r, loc_i = (mask(resid_ref[2 * problem] - op_r), mask(resid_ref[2 * problem + 1] - op_i))
            apply = cols_apply if step % 2 == 0 else rows_apply
            up_r, up_i = apply(loc_r, loc_i, sign)
            cor_r, cor_i = (cor_r + mask(up_r), cor_i + mask(up_i))
        if base_ref is not None:
            cor_r, cor_i = (cor_r + base_ref[problem, 0], cor_i + base_ref[problem, 1])
        first_row = (height - own_rows) // 2
        for part, value in ((0, cor_r), (1, cor_i)):
            if full_ref is not None:
                full_ref[problem, part] = value
            own = pltpu.roll(value, breadth - (breadth - own_cols) // 2, 1)[first_row : first_row + own_rows, :own_cols]
            own_ref[problem, part] = own
            if top_ref is not None:
                top_ref[problem, part] = own[:slab]
                bottom_ref[problem, part] = own[own_rows - slab :]
        return carry

    lax.fori_loop(0, resid_ref.shape[0] // 2, problem_body, 0)


def line_matrices(row_blocks, col_blocks):
    block = row_blocks.shape[-1]
    eye = jnp.eye(2, dtype=row_blocks.dtype)
    halves = row_blocks.shape[0] // 2
    rows_t = jnp.transpose(row_blocks, (0, 3, 1, 2)).reshape(halves, 2, block, 2, block)
    row_mats = jnp.einsum("hakmo,ab->hakmbo", rows_t, eye).reshape(halves, 2 * block, 4 * block)
    cols = col_blocks.reshape(halves, 2, 2, block, block)
    col_mats = jnp.einsum("hamok,ab->hmaobk", cols, eye).reshape(halves, 4 * block, 2 * block)
    return row_mats, col_mats


def solve_local_kernel(resid_planes, data_ext, row_mats, col_mats, live_rect, own_shape, slab, base=None, last=False,
                       from_fields=False, interpret=False):
    extra = [] if base is None else [base]
    rect = jnp.stack([to_index(v) for v in live_rect])
    dtype = resid_planes.dtype
    ext_shape = data_ext.shape[1:]
    shapes = [] if last else [(2, 2) + ext_shape]
    shapes.append((2, 2) + own_shape)
    if not last:
        shapes += [(2, 2, slab, own_shape[1])] * 2
    vmem = pltpu.MemorySpace.VMEM if hasattr(pltpu, "MemorySpace") else pltpu.VMEM
    kernel = functools.partial(
        solve_kernel, has_base=base is not None, last=last, own_rows=own_shape[0], own_cols=own_shape[1], slab=slab,
        from_fields=from_fields,
    )
    scratch = [pltpu.VMEM((4,) + ext_shape, jnp.float32)] if from_fields else []
    return pl.pallas_call(
        kernel,
        out_shape=[jax.ShapeDtypeStruct(s, dtype) for s in shapes],
        in_specs=[pl.BlockSpec(memory_space=pltpu.SMEM)] + [pl.BlockSpec(memory_space=vmem)] * (4 + len(extra)),
        out_specs=[pl.BlockSpec(memory_space=vmem)] * len(shapes),
        scratch_shapes=scratch,
        interpret=interpret,
    )(rect, resid_planes, data_ext, row_mats, col_mats, *extra)


def shards(sources, wavenumber, row_inverse, col_inverse, reach_steps):
    own_rows, own_cols = (sources.shape[2], sources.shape[3])
    block = row_inverse.shape[-1]
    step_cells = block // 4
    signs = jnp.array([1.0, -1.0], dtype=sources.dtype).reshape(2, 1, 1)
    row_rank = to_index(lax.axis_index("gx"))
    col_rank = to_index(lax.axis_index("gy"))
    row_count = lax.axis_size("gx")
    col_count = lax.axis_size("gy")
    zero = to_index(0)
    widths = reach_steps.reshape(4) * step_cells
    upper_w = jnp.where(row_rank > 0, widths[0], zero)
    lower_w = jnp.where(row_rank < row_count - 1, widths[1], zero)
    left_w = jnp.where(col_rank > 0, widths[2], zero)
    right_w = jnp.where(col_rank < col_count - 1, widths[3], zero)
    live_rect = (
        block - upper_w,
        block + own_rows + lower_w,
        block - left_w,
        block + own_cols + right_w,
    )
    stacked = jnp.concatenate([sources.reshape(4, own_rows, own_cols), wavenumber[None]], axis=0)
    lead = stacked.shape[0]
    col_pair = col_inverse.shape[0]
    row_pair = row_inverse.shape[0]
    inv_rows = col_inverse.shape[1] * block * block // own_cols
    before, after = exchange_axis(
        stacked, "gx", 1, block,
        col_inverse[col_pair - 1].reshape(1, inv_rows, own_cols), col_inverse[0].reshape(1, inv_rows, own_cols),
    )
    tall = jnp.concatenate([before[:lead, :block], stacked, after[:lead, :block]], axis=1)
    def inv_slab(mats):
        flat = mats.reshape(1, -1, block)
        return jnp.pad(flat, ((0, 0), (0, tall.shape[1] - flat.shape[1]), (0, 0)))
    left, right = exchange_axis(tall, "gy", 2, block, inv_slab(row_inverse[row_pair - 1]), inv_slab(row_inverse[0]))
    stacked_ext = jnp.concatenate([left[:lead], tall, right[:lead]], axis=2)
    sources_ext = stacked_ext[:4].reshape(2, 2, own_rows + 2 * block, own_cols + 2 * block)
    wave_ext = stacked_ext[4]
    inv_shape = (1,) + row_inverse.shape[1:]
    inv_size = row_inverse.shape[1] * block * block // block
    col_blocks = jnp.concatenate(
        [before[lead:].reshape(inv_shape), col_inverse, after[lead:].reshape(inv_shape)], axis=0
    )
    row_blocks = jnp.concatenate(
        [left[lead:, :inv_size].reshape(inv_shape), row_inverse, right[lead:, :inv_size].reshape(inv_shape)], axis=0
    )
    row_mats, col_mats = line_matrices(row_blocks, col_blocks)
    width = block + 1
    edges = (row_rank == 0, row_rank == row_count - 1, col_rank == 0, col_rank == col_count - 1)
    slab = -(-width // 8) * 8
    solution = None
    base = None
    for iteration in range(ITERS):
        last = iteration == ITERS - 1
        if iteration == 0:
            resid_planes = stacked_ext
        else:
            peers = lax.axis_size("gx")
            up = [(i, i + 1) for i in range(peers - 1)]
            down = [(j, i) for i, j in up]
            before = lax.ppermute(bottom, "gx", up)[:, :, slab - width :]
            after = lax.ppermute(top, "gx", down)[:, :, :width]
            tall = jnp.concatenate([before, solution, after], axis=2)
            left, right = exchange_axis(tall, "gy", 3, width)
            padded = jnp.concatenate([left, tall, right], axis=3)
            padded = grid_ghost(padded, width, edges, signs)
            tile_rows = -(-padded.shape[2] // 8) * 8 - padded.shape[2]
            tile_cols = -(-padded.shape[3] // 128) * 128 - padded.shape[3]
            padded = jnp.pad(padded, ((0, 0), (0, 0), (0, tile_rows), (0, tile_cols)))
            resid_planes = padded.reshape((4,) + padded.shape[2:])
        outs = solve_local_kernel(
            resid_planes, stacked_ext, row_mats, col_mats, live_rect, (own_rows, own_cols), slab, base=base, last=last,
            from_fields=iteration > 0,
        )
        if last:
            solution = outs[0]
        else:
            base, solution, top, bottom = outs
    return solution


def solution(mesh):
    return jax.shard_map(
        shards,
        mesh=mesh,
        in_specs=(
            P(None, None, "gx", "gy"),
            P("gx", "gy"),
            P("gy", None, None, None),
            P("gx", None, None, None),
            P("gx", "gy", None),
        ),
        out_specs=P(None, None, "gx", "gy"),
        check_vma=False,
    )
```

```python
import functools

import jax
import jax.numpy as jnp
from jax import lax
from jax.sharding import PartitionSpec as P
from jax.experimental import pallas as pl
from jax.experimental.pallas import tpu as pltpu

ITERS = 2
SWEEPS = 4


DAMPING = 0.5
ROBIN_COEF = 0.5


def with_halo(shard, sides, width):
    for axis, dim in sides:
        peers, length = (lax.axis_size(axis), shard.shape[dim])
        up = [(i, (i + 1) % peers) for i in range(peers - 1)]
        down = [(j, i) for i, j in up]
        last = lax.slice_in_dim(shard, length - width, length, axis=dim)
        first = lax.slice_in_dim(shard, 0, width, axis=dim)
        before = lax.ppermute(last, axis, up)
        after = lax.ppermute(first, axis, down)
        shard = jnp.concatenate([before, shard, after], axis=dim)
    return shard


def to_index(value):
    return jnp.asarray(value).astype(jnp.int32)


def slice_line(values, start, axis):
    starts = [to_index(0) for _ in range(values.ndim)]
    starts[axis] = to_index(start)
    sizes = list(values.shape)
    sizes[axis] = 1
    return lax.dynamic_slice(values, starts, sizes)


def fill_ghost(values, upper, lower, left, right, signs):
    upper, lower, left, right = (to_index(upper), to_index(lower), to_index(left), to_index(right))
    height, breadth = (values.shape[2], values.shape[3])
    row_ids = lax.broadcasted_iota(jnp.int32, (height, 1), 0)
    col_ids = lax.broadcasted_iota(jnp.int32, (1, breadth), 1)
    upper_row = slice_line(values, upper, 2)
    lower_row = slice_line(values, lower - 1, 2)
    values = jnp.where(row_ids < upper, upper_row, jnp.where(row_ids >= lower, lower_row, values))
    left_col = slice_line(values, left, 3)
    right_col = slice_line(values, right - 1, 3)
    values = jnp.where(col_ids < left, left_col, jnp.where(col_ids >= right, right_col, values))
    inside = (row_ids >= upper) & (row_ids < lower) & (col_ids >= left) & (col_ids < right)
    real_part = values[:, 0]
    imag_part = values[:, 1]
    ghost_cycle = jnp.stack(
        [real_part + signs * ROBIN_COEF * imag_part, imag_part - signs * ROBIN_COEF * real_part],
        axis=1,
    )
    return jnp.where(inside, values, ghost_cycle)


def grid_ghost(values, width, edges, signs):
    at_top, at_bottom, at_left, at_right = edges
    height, breadth = (values.shape[2], values.shape[3])
    row_ids = lax.broadcasted_iota(jnp.int32, (height, 1), 0)
    col_ids = lax.broadcasted_iota(jnp.int32, (1, breadth), 1)
    above = at_top & (row_ids < width)
    below = at_bottom & (row_ids >= height - width)
    values = jnp.where(
        above, values[:, :, width : width + 1], jnp.where(below, values[:, :, height - width - 1 : height - width], values)
    )
    before = at_left & (col_ids < width)
    after = at_right & (col_ids >= breadth - width)
    values = jnp.where(
        before, values[:, :, :, width : width + 1],
        jnp.where(after, values[:, :, :, breadth - width - 1 : breadth - width], values),
    )
    outside = above | below | before | after
    real_part = values[:, 0]
    imag_part = values[:, 1]
    ghost_cycle = jnp.stack(
        [real_part + signs * ROBIN_COEF * imag_part, imag_part - signs * ROBIN_COEF * real_part],
        axis=1,
    )
    return jnp.where(outside, ghost_cycle, values)


def apply_operator(padded, wave_cells, signs):
    centre = padded[:, :, 1:-1, 1:-1]
    edge_sum = (
        padded[:, :, :-2, 1:-1]
        + padded[:, :, 2:, 1:-1]
        + padded[:, :, 1:-1, :-2]
        + padded[:, :, 1:-1, 2:]
    )
    corner_sum = (
        padded[:, :, :-2, :-2]
        + padded[:, :, :-2, 2:]
        + padded[:, :, 2:, :-2]
        + padded[:, :, 2:, 2:]
    )
    laplace = (4.0 * edge_sum + corner_sum - 20.0 * centre) / 6.0
    real_part = centre[:, 0]
    imag_part = centre[:, 1]
    mass_term = jnp.stack(
        [real_part - signs * DAMPING * imag_part, imag_part + signs * DAMPING * real_part], axis=1
    )
    return -laplace - wave_cells * mass_term


def combine_parts(products, signs, shape):
    real_out = products[0][:, 0] - signs[..., None] * products[1][:, 1]
    imag_out = products[0][:, 1] + signs[..., None] * products[1][:, 0]
    return jnp.stack([real_out, imag_out], axis=1).reshape(shape)


def along_rows(values, inverse, signs):
    block = inverse.shape[-1]
    blocked = values.reshape(values.shape[0], 2, values.shape[2], values.shape[3] // block, block)
    products = jnp.einsum("qmok,fchqk->mfchqo", inverse, blocked, precision=lax.Precision.HIGHEST)
    return combine_parts(products, signs, values.shape)


def along_cols(values, inverse, signs):
    block = inverse.shape[-1]
    blocked = values.reshape(values.shape[0], 2, values.shape[2] // block, block, values.shape[3])
    products = jnp.einsum("qmok,fcqkw->mfcqow", inverse, blocked, precision=lax.Precision.HIGHEST)
    return combine_parts(products, signs, values.shape)


def solve_local(resid_ext, wave_ext, row_blocks, col_blocks, live_rect, signs):
    upper, lower, left, right = [to_index(v) for v in live_rect]
    height, breadth = (resid_ext.shape[2], resid_ext.shape[3])
    row_ids = lax.broadcasted_iota(jnp.int32, (height, 1), 0)
    col_ids = lax.broadcasted_iota(jnp.int32, (1, breadth), 1)
    live_mask = (
        (row_ids >= upper) & (row_ids < lower) & (col_ids >= left) & (col_ids < right)
    ).astype(resid_ext.dtype)
    local_res = resid_ext * live_mask
    correction = jnp.zeros_like(resid_ext)
    for sweep_index in range(SWEEPS):
        if sweep_index > 0:
            padded = jnp.pad(correction, ((0, 0), (0, 0), (1, 1), (1, 1)))
            padded = fill_ghost(padded, upper + 1, lower + 1, left + 1, right + 1, signs)
            local_res = live_mask * (resid_ext - apply_operator(padded, wave_ext, signs))
        if sweep_index % 2 == 0:
            update = along_rows(local_res, row_blocks, signs)
        else:
            update = along_cols(local_res, col_blocks, signs)
        correction = correction + live_mask * update
    return correction


def exchange(x, row_width, col_width, extra=None):
    row_count = lax.axis_size("gx")
    col_count = lax.axis_size("gy")
    height, breadth = (x.shape[-2], x.shape[-1])
    pieces = {}
    for dr in (-1, 0, 1):
        for dc in (-1, 0, 1):
            if dr == 0 and dc == 0:
                continue
            slab = x
            if dr == -1:
                slab = lax.slice_in_dim(slab, height - row_width, height, axis=x.ndim - 2)
            elif dr == 1:
                slab = lax.slice_in_dim(slab, 0, row_width, axis=x.ndim - 2)
            if dc == -1:
                slab = lax.slice_in_dim(slab, breadth - col_width, breadth, axis=x.ndim - 1)
            elif dc == 1:
                slab = lax.slice_in_dim(slab, 0, col_width, axis=x.ndim - 1)
            if extra is not None and (dr, dc) in extra:
                slab = jnp.concatenate([slab, extra[(dr, dc)]], axis=0)
            perm = []
            for r in range(row_count):
                for c in range(col_count):
                    rr, cc = (r - dr, c - dc)
                    if 0 <= rr < row_count and 0 <= cc < col_count:
                        perm.append((r * col_count + c, rr * col_count + cc))
            pieces[(dr, dc)] = lax.ppermute(slab, ("gx", "gy"), perm)
    return pieces


def exchange_axis(x, axis, dim, width, extra_lo=None, extra_hi=None):
    peers, length = (lax.axis_size(axis), x.shape[dim])
    up = [(i, i + 1) for i in range(peers - 1)]
    down = [(j, i) for i, j in up]
    last = lax.slice_in_dim(x, length - width, length, axis=dim)
    first = lax.slice_in_dim(x, 0, width, axis=dim)
    if extra_lo is not None:
        last = jnp.concatenate([last, extra_lo], axis=0)
        first = jnp.concatenate([first, extra_hi], axis=0)
    return lax.ppermute(last, axis, up), lax.ppermute(first, axis, down)


def assemble(pieces, centre, lead):
    rows = []
    for dr in (-1, 0, 1):
        row = []
        for dc in (-1, 0, 1):
            part = centre if (dr == 0 and dc == 0) else pieces[(dr, dc)][:lead]
            row.append(part)
        rows.append(jnp.concatenate(row, axis=-1))
    return jnp.concatenate(rows, axis=-2)


def grid_residual(fields_ref, data_ref, res_ref):
    height, breadth = (res_ref.shape[1], res_ref.shape[2])

    def ahead(x, step, axis):
        return pltpu.roll(x, x.shape[axis] - step, axis)

    for problem in range(res_ref.shape[0] // 2):
        sign = 1.0 - 2.0 * problem
        totals, centres = ([], [])
        for part in range(2):
            padded = fields_ref[2 * problem + part]
            outer = padded + ahead(padded, 2, 0)
            middle = ahead(padded, 1, 0)
            edge = ahead(outer, 1, 1) + middle + ahead(middle, 2, 1)
            corner = outer + ahead(outer, 2, 1)
            totals.append((4.0 * edge + corner)[:height, :breadth])
            centres.append(ahead(middle, 1, 1)[:height, :breadth])
        real_part, imag_part = centres
        wave = data_ref[4]
        lap_r = (totals[0] - 20.0 * real_part) / 6.0
        lap_i = (totals[1] - 20.0 * imag_part) / 6.0
        mass_r = real_part - sign * DAMPING * imag_part
        mass_i = imag_part + sign * DAMPING * real_part
        res_ref[2 * problem] = data_ref[2 * problem] - (-lap_r - wave * mass_r)
        res_ref[2 * problem + 1] = data_ref[2 * problem + 1] - (-lap_i - wave * mass_i)


def solve_kernel(rect_ref, resid_ref, data_ref, wrow_ref, wcol_ref, *refs, has_base, last, own_rows, own_cols, slab,
                 from_fields):
    if from_fields:
        grid_residual(resid_ref, data_ref, refs[-1])
        resid_ref = refs[-1]
        refs = refs[:-1]
    base_ref = refs[0] if has_base else None
    outs = refs[1:] if has_base else refs
    full_ref = None if last else outs[0]
    own_ref = outs[-1] if last else outs[1]
    top_ref, bottom_ref = (None, None) if last else outs[2:4]
    height, breadth = (resid_ref.shape[1], resid_ref.shape[2])
    half = height // 2
    upper, lower, left, right = (rect_ref[0], rect_ref[1], rect_ref[2], rect_ref[3])
    row_ids = lax.broadcasted_iota(jnp.int32, (height, breadth), 0)
    col_ids = lax.broadcasted_iota(jnp.int32, (height, breadth), 1)
    live = (row_ids >= upper) & (row_ids < lower) & (col_ids >= left) & (col_ids < right)
    top, bottom = (row_ids == upper, row_ids == lower - 1)
    first, last = (col_ids == left, col_ids == right - 1)
    row_flag = top.astype(jnp.float32) + bottom.astype(jnp.float32)
    col_flag = first.astype(jnp.float32) + last.astype(jnp.float32)
    edge_flag = 4.0 * (row_flag + col_flag)
    zero = jnp.zeros((height, breadth), jnp.float32)

    def mask(x):
        return jnp.where(live, x, zero)

    def rows_sum(x):
        up = jnp.where(top, x, pltpu.roll(x, 1, 0))
        down = jnp.where(bottom, x, pltpu.roll(x, height - 1, 0))
        return up + down

    def cols_sum(x):
        lft = jnp.where(first, x, pltpu.roll(x, 1, 1))
        rgt = jnp.where(last, x, pltpu.roll(x, breadth - 1, 1))
        return lft + rgt

    def stencil(x):
        vertical = rows_sum(x)
        ghost_rows = row_flag * x
        total = 4.0 * (vertical + cols_sum(x)) + cols_sum(vertical)
        ghost = edge_flag * x + cols_sum(ghost_rows) + col_flag * (vertical - ghost_rows)
        return total, ghost

    def operator(real_part, imag_part, sign):
        wave = data_ref[4]
        total_r, ghost_r = stencil(real_part)
        total_i, ghost_i = stencil(imag_part)
        lap_r = (total_r + sign * ROBIN_COEF * ghost_i - 20.0 * real_part) / 6.0
        lap_i = (total_i - sign * ROBIN_COEF * ghost_r - 20.0 * imag_part) / 6.0
        mass_r = real_part - sign * DAMPING * imag_part
        mass_i = imag_part + sign * DAMPING * real_part
        return (-lap_r - wave * mass_r, -lap_i - wave * mass_i)

    def dot(a, b):
        return jnp.dot(a, b, precision=lax.Precision.HIGH, preferred_element_type=jnp.float32)

    def dot_t(a, b):
        return lax.dot_general(
            a, b, (((1,), (1,)), ((), ())), precision=lax.Precision.HIGH, preferred_element_type=jnp.float32
        )

    def rows_apply(real_part, imag_part, sign):
        outs_r, outs_i = ([], [])
        for h in range(breadth // half):
            cols = slice(h * half, (h + 1) * half)
            prod_r = dot_t(real_part[:, cols], wrow_ref[h])
            prod_i = dot_t(imag_part[:, cols], wrow_ref[h])
            outs_r.append(prod_r[:, :half] - sign * prod_i[:, half:])
            outs_i.append(prod_i[:, :half] + sign * prod_r[:, half:])
        return (jnp.concatenate(outs_r, axis=1), jnp.concatenate(outs_i, axis=1))

    def cols_apply(real_part, imag_part, sign):
        outs_r, outs_i = ([], [])
        for h in range(height // half):
            rows = slice(h * half, (h + 1) * half)
            prod_r = dot(wcol_ref[h], real_part[rows, :])
            prod_i = dot(wcol_ref[h], imag_part[rows, :])
            outs_r.append(prod_r[:half] - sign * prod_i[half:])
            outs_i.append(prod_i[:half] + sign * prod_r[half:])
        return (jnp.concatenate(outs_r, axis=0), jnp.concatenate(outs_i, axis=0))

    def problem_body(problem, carry):
        sign = 1.0 - 2.0 * problem.astype(jnp.float32)
        up_r, up_i = rows_apply(mask(resid_ref[2 * problem]), mask(resid_ref[2 * problem + 1]), sign)
        cor_r, cor_i = (mask(up_r), mask(up_i))
        for step in range(SWEEPS - 1):
            op_r, op_i = operator(cor_r, cor_i, sign)
            loc_r, loc_i = (mask(resid_ref[2 * problem] - op_r), mask(resid_ref[2 * problem + 1] - op_i))
            apply = cols_apply if step % 2 == 0 else rows_apply
            up_r, up_i = apply(loc_r, loc_i, sign)
            cor_r, cor_i = (cor_r + mask(up_r), cor_i + mask(up_i))
        if base_ref is not None:
            cor_r, cor_i = (cor_r + base_ref[problem, 0], cor_i + base_ref[problem, 1])
        first_row = (height - own_rows) // 2
        for part, value in ((0, cor_r), (1, cor_i)):
            if full_ref is not None:
                full_ref[problem, part] = value
            own = pltpu.roll(value, breadth - (breadth - own_cols) // 2, 1)[first_row : first_row + own_rows, :own_cols]
            own_ref[problem, part] = own
            if top_ref is not None:
                top_ref[problem, part] = own[:slab]
                bottom_ref[problem, part] = own[own_rows - slab :]
        return carry

    lax.fori_loop(0, resid_ref.shape[0] // 2, problem_body, 0)


def line_matrices(row_blocks, col_blocks):
    block = row_blocks.shape[-1]

    def pairs(blocks):
        mats = []
        for h in range(blocks.shape[0] // 2):
            parts = []
            for m in range(2):
                for a in range(2):
                    parts.append(jnp.pad(blocks[2 * h + a, m], ((0, 0), (a * block, (1 - a) * block))))
            mats.append(jnp.concatenate(parts, axis=0))
        return jnp.stack(mats)

    return pairs(row_blocks), pairs(col_blocks)


def solve_local_kernel(resid_planes, data_ext, row_mats, col_mats, live_rect, own_shape, slab, base=None, last=False,
                       from_fields=False, interpret=False):
    extra = [] if base is None else [base]
    rect = jnp.stack([to_index(v) for v in live_rect])
    dtype = resid_planes.dtype
    ext_shape = data_ext.shape[1:]
    shapes = [] if last else [(2, 2) + ext_shape]
    shapes.append((2, 2) + own_shape)
    if not last:
        shapes += [(2, 2, slab, own_shape[1])] * 2
    vmem = pltpu.MemorySpace.VMEM if hasattr(pltpu, "MemorySpace") else pltpu.VMEM
    kernel = functools.partial(
        solve_kernel, has_base=base is not None, last=last, own_rows=own_shape[0], own_cols=own_shape[1], slab=slab,
        from_fields=from_fields,
    )
    scratch = [pltpu.VMEM((4,) + ext_shape, jnp.float32)] if from_fields else []
    return pl.pallas_call(
        kernel,
        out_shape=[jax.ShapeDtypeStruct(s, dtype) for s in shapes],
        in_specs=[pl.BlockSpec(memory_space=pltpu.SMEM)] + [pl.BlockSpec(memory_space=vmem)] * (4 + len(extra)),
        out_specs=[pl.BlockSpec(memory_space=vmem)] * len(shapes),
        scratch_shapes=scratch,
        interpret=interpret,
    )(rect, resid_planes, data_ext, row_mats, col_mats, *extra)


def shards(sources, wavenumber, row_inverse, col_inverse, reach_steps):
    own_rows, own_cols = (sources.shape[2], sources.shape[3])
    block = row_inverse.shape[-1]
    step_cells = block // 4
    signs = jnp.array([1.0, -1.0], dtype=sources.dtype).reshape(2, 1, 1)
    row_rank = to_index(lax.axis_index("gx"))
    col_rank = to_index(lax.axis_index("gy"))
    row_count = lax.axis_size("gx")
    col_count = lax.axis_size("gy")
    zero = to_index(0)
    widths = reach_steps.reshape(4) * step_cells
    upper_w = jnp.where(row_rank > 0, widths[0], zero)
    lower_w = jnp.where(row_rank < row_count - 1, widths[1], zero)
    left_w = jnp.where(col_rank > 0, widths[2], zero)
    right_w = jnp.where(col_rank < col_count - 1, widths[3], zero)
    live_rect = (
        block - upper_w,
        block + own_rows + lower_w,
        block - left_w,
        block + own_cols + right_w,
    )
    stacked = jnp.concatenate([sources.reshape(4, own_rows, own_cols), wavenumber[None]], axis=0)
    lead = stacked.shape[0]
    col_pair = col_inverse.shape[0]
    row_pair = row_inverse.shape[0]
    inv_rows = col_inverse.shape[1] * block * block // own_cols
    before, after = exchange_axis(
        stacked, "gx", 1, block,
        col_inverse[col_pair - 1].reshape(1, inv_rows, own_cols), col_inverse[0].reshape(1, inv_rows, own_cols),
    )
    tall = jnp.concatenate([before[:lead, :block], stacked, after[:lead, :block]], axis=1)
    def inv_slab(mats):
        flat = mats.reshape(1, -1, block)
        return jnp.pad(flat, ((0, 0), (0, tall.shape[1] - flat.shape[1]), (0, 0)))
    left, right = exchange_axis(tall, "gy", 2, block, inv_slab(row_inverse[row_pair - 1]), inv_slab(row_inverse[0]))
    stacked_ext = jnp.concatenate([left[:lead], tall, right[:lead]], axis=2)
    sources_ext = stacked_ext[:4].reshape(2, 2, own_rows + 2 * block, own_cols + 2 * block)
    wave_ext = stacked_ext[4]
    inv_shape = (1,) + row_inverse.shape[1:]
    inv_size = row_inverse.shape[1] * block * block // block
    col_blocks = jnp.concatenate(
        [before[lead:].reshape(inv_shape), col_inverse, after[lead:].reshape(inv_shape)], axis=0
    )
    row_blocks = jnp.concatenate(
        [left[lead:, :inv_size].reshape(inv_shape), row_inverse, right[lead:, :inv_size].reshape(inv_shape)], axis=0
    )
    row_mats, col_mats = line_matrices(row_blocks, col_blocks)
    width = block + 1
    edges = (row_rank == 0, row_rank == row_count - 1, col_rank == 0, col_rank == col_count - 1)
    slab = -(-width // 8) * 8
    solution = None
    base = None
    for iteration in range(ITERS):
        last = iteration == ITERS - 1
        if iteration == 0:
            resid_planes = stacked_ext
        else:
            peers = lax.axis_size("gx")
            up = [(i, i + 1) for i in range(peers - 1)]
            down = [(j, i) for i, j in up]
            before = lax.ppermute(bottom, "gx", up)[:, :, slab - width :]
            after = lax.ppermute(top, "gx", down)[:, :, :width]
            tall = jnp.concatenate([before, solution, after], axis=2)
            left, right = exchange_axis(tall, "gy", 3, width)
            padded = jnp.concatenate([left, tall, right], axis=3)
            padded = grid_ghost(padded, width, edges, signs)
            tile_rows = -(-padded.shape[2] // 8) * 8 - padded.shape[2]
            tile_cols = -(-padded.shape[3] // 128) * 128 - padded.shape[3]
            padded = jnp.pad(padded, ((0, 0), (0, 0), (0, tile_rows), (0, tile_cols)))
            resid_planes = padded.reshape((4,) + padded.shape[2:])
        outs = solve_local_kernel(
            resid_planes, stacked_ext, row_mats, col_mats, live_rect, (own_rows, own_cols), slab, base=base, last=last,
            from_fields=iteration > 0,
        )
        if last:
            solution = outs[0]
        else:
            base, solution, top, bottom = outs
    return solution


def solution(mesh):
    return jax.shard_map(
        shards,
        mesh=mesh,
        in_specs=(
            P(None, None, "gx", "gy"),
            P("gx", "gy"),
            P("gy", None, None, None),
            P("gx", None, None, None),
            P("gx", "gy", None),
        ),
        out_specs=P(None, None, "gx", "gy"),
        check_vma=False,
    )
```

```python
import functools

import jax
import jax.numpy as jnp
from jax import lax
from jax.sharding import PartitionSpec as P
from jax.experimental import pallas as pl
from jax.experimental.pallas import tpu as pltpu

ITERS = 2
SWEEPS = 4


DAMPING = 0.5
ROBIN_COEF = 0.5


def with_halo(shard, sides, width):
    for axis, dim in sides:
        peers, length = (lax.axis_size(axis), shard.shape[dim])
        up = [(i, (i + 1) % peers) for i in range(peers - 1)]
        down = [(j, i) for i, j in up]
        last = lax.slice_in_dim(shard, length - width, length, axis=dim)
        first = lax.slice_in_dim(shard, 0, width, axis=dim)
        before = lax.ppermute(last, axis, up)
        after = lax.ppermute(first, axis, down)
        shard = jnp.concatenate([before, shard, after], axis=dim)
    return shard


def to_index(value):
    return jnp.asarray(value).astype(jnp.int32)


def slice_line(values, start, axis):
    starts = [to_index(0) for _ in range(values.ndim)]
    starts[axis] = to_index(start)
    sizes = list(values.shape)
    sizes[axis] = 1
    return lax.dynamic_slice(values, starts, sizes)


def fill_ghost(values, upper, lower, left, right, signs):
    upper, lower, left, right = (to_index(upper), to_index(lower), to_index(left), to_index(right))
    height, breadth = (values.shape[2], values.shape[3])
    row_ids = lax.broadcasted_iota(jnp.int32, (height, 1), 0)
    col_ids = lax.broadcasted_iota(jnp.int32, (1, breadth), 1)
    upper_row = slice_line(values, upper, 2)
    lower_row = slice_line(values, lower - 1, 2)
    values = jnp.where(row_ids < upper, upper_row, jnp.where(row_ids >= lower, lower_row, values))
    left_col = slice_line(values, left, 3)
    right_col = slice_line(values, right - 1, 3)
    values = jnp.where(col_ids < left, left_col, jnp.where(col_ids >= right, right_col, values))
    inside = (row_ids >= upper) & (row_ids < lower) & (col_ids >= left) & (col_ids < right)
    real_part = values[:, 0]
    imag_part = values[:, 1]
    ghost_cycle = jnp.stack(
        [real_part + signs * ROBIN_COEF * imag_part, imag_part - signs * ROBIN_COEF * real_part],
        axis=1,
    )
    return jnp.where(inside, values, ghost_cycle)


def grid_ghost(values, width, extent, edges, signs):
    at_top, at_bottom, at_left, at_right = edges
    height, breadth = extent
    row_ids = lax.broadcasted_iota(jnp.int32, (values.shape[2], 1), 0)
    col_ids = lax.broadcasted_iota(jnp.int32, (1, values.shape[3]), 1)
    above = at_top & (row_ids < width)
    below = at_bottom & (row_ids >= height - width)
    before = at_left & (col_ids < width)
    after = at_right & (col_ids >= breadth - width)
    first_row, last_row = (width, height - width - 1)
    first_col, last_col = (width, breadth - width - 1)

    def rows_filled(part):
        return jnp.where(
            above, part[:, :, first_row : first_row + 1], jnp.where(below, part[:, :, last_row : last_row + 1], part)
        )

    filled = rows_filled(values)
    left_col = rows_filled(values[:, :, :, first_col : first_col + 1])
    right_col = rows_filled(values[:, :, :, last_col : last_col + 1])
    values = jnp.where(before, left_col, jnp.where(after, right_col, filled))
    outside = above | below | before | after
    real_part = values[:, 0]
    imag_part = values[:, 1]
    ghost_cycle = jnp.stack(
        [real_part + signs * ROBIN_COEF * imag_part, imag_part - signs * ROBIN_COEF * real_part],
        axis=1,
    )
    return jnp.where(outside, ghost_cycle, values)


def apply_operator(padded, wave_cells, signs):
    centre = padded[:, :, 1:-1, 1:-1]
    edge_sum = (
        padded[:, :, :-2, 1:-1]
        + padded[:, :, 2:, 1:-1]
        + padded[:, :, 1:-1, :-2]
        + padded[:, :, 1:-1, 2:]
    )
    corner_sum = (
        padded[:, :, :-2, :-2]
        + padded[:, :, :-2, 2:]
        + padded[:, :, 2:, :-2]
        + padded[:, :, 2:, 2:]
    )
    laplace = (4.0 * edge_sum + corner_sum - 20.0 * centre) / 6.0
    real_part = centre[:, 0]
    imag_part = centre[:, 1]
    mass_term = jnp.stack(
        [real_part - signs * DAMPING * imag_part, imag_part + signs * DAMPING * real_part], axis=1
    )
    return -laplace - wave_cells * mass_term


def combine_parts(products, signs, shape):
    real_out = products[0][:, 0] - signs[..., None] * products[1][:, 1]
    imag_out = products[0][:, 1] + signs[..., None] * products[1][:, 0]
    return jnp.stack([real_out, imag_out], axis=1).reshape(shape)


def along_rows(values, inverse, signs):
    block = inverse.shape[-1]
    blocked = values.reshape(values.shape[0], 2, values.shape[2], values.shape[3] // block, block)
    products = jnp.einsum("qmok,fchqk->mfchqo", inverse, blocked, precision=lax.Precision.HIGHEST)
    return combine_parts(products, signs, values.shape)


def along_cols(values, inverse, signs):
    block = inverse.shape[-1]
    blocked = values.reshape(values.shape[0], 2, values.shape[2] // block, block, values.shape[3])
    products = jnp.einsum("qmok,fcqkw->mfcqow", inverse, blocked, precision=lax.Precision.HIGHEST)
    return combine_parts(products, signs, values.shape)


def solve_local(resid_ext, wave_ext, row_blocks, col_blocks, live_rect, signs):
    upper, lower, left, right = [to_index(v) for v in live_rect]
    height, breadth = (resid_ext.shape[2], resid_ext.shape[3])
    row_ids = lax.broadcasted_iota(jnp.int32, (height, 1), 0)
    col_ids = lax.broadcasted_iota(jnp.int32, (1, breadth), 1)
    live_mask = (
        (row_ids >= upper) & (row_ids < lower) & (col_ids >= left) & (col_ids < right)
    ).astype(resid_ext.dtype)
    local_res = resid_ext * live_mask
    correction = jnp.zeros_like(resid_ext)
    for sweep_index in range(SWEEPS):
        if sweep_index > 0:
            padded = jnp.pad(correction, ((0, 0), (0, 0), (1, 1), (1, 1)))
            padded = fill_ghost(padded, upper + 1, lower + 1, left + 1, right + 1, signs)
            local_res = live_mask * (resid_ext - apply_operator(padded, wave_ext, signs))
        if sweep_index % 2 == 0:
            update = along_rows(local_res, row_blocks, signs)
        else:
            update = along_cols(local_res, col_blocks, signs)
        correction = correction + live_mask * update
    return correction


def exchange(x, row_width, col_width, extra=None):
    row_count = lax.axis_size("gx")
    col_count = lax.axis_size("gy")
    height, breadth = (x.shape[-2], x.shape[-1])
    pieces = {}
    for dr in (-1, 0, 1):
        for dc in (-1, 0, 1):
            if dr == 0 and dc == 0:
                continue
            slab = x
            if dr == -1:
                slab = lax.slice_in_dim(slab, height - row_width, height, axis=x.ndim - 2)
            elif dr == 1:
                slab = lax.slice_in_dim(slab, 0, row_width, axis=x.ndim - 2)
            if dc == -1:
                slab = lax.slice_in_dim(slab, breadth - col_width, breadth, axis=x.ndim - 1)
            elif dc == 1:
                slab = lax.slice_in_dim(slab, 0, col_width, axis=x.ndim - 1)
            if extra is not None and (dr, dc) in extra:
                slab = jnp.concatenate([slab, extra[(dr, dc)]], axis=0)
            perm = []
            for r in range(row_count):
                for c in range(col_count):
                    rr, cc = (r - dr, c - dc)
                    if 0 <= rr < row_count and 0 <= cc < col_count:
                        perm.append((r * col_count + c, rr * col_count + cc))
            pieces[(dr, dc)] = lax.ppermute(slab, ("gx", "gy"), perm)
    return pieces


def exchange_axis(x, axis, dim, width, extra_lo=None, extra_hi=None):
    peers, length = (lax.axis_size(axis), x.shape[dim])
    up = [(i, i + 1) for i in range(peers - 1)]
    down = [(j, i) for i, j in up]
    last = lax.slice_in_dim(x, length - width, length, axis=dim)
    first = lax.slice_in_dim(x, 0, width, axis=dim)
    if extra_lo is not None:
        last = jnp.concatenate([last, extra_lo], axis=0)
        first = jnp.concatenate([first, extra_hi], axis=0)
    return lax.ppermute(last, axis, up), lax.ppermute(first, axis, down)


def assemble(pieces, centre, lead):
    rows = []
    for dr in (-1, 0, 1):
        row = []
        for dc in (-1, 0, 1):
            part = centre if (dr == 0 and dc == 0) else pieces[(dr, dc)][:lead]
            row.append(part)
        rows.append(jnp.concatenate(row, axis=-1))
    return jnp.concatenate(rows, axis=-2)


def grid_residual(fields_ref, data_ref, res_ref):
    height, breadth = (res_ref.shape[1], res_ref.shape[2])

    def ahead(x, step, axis):
        return pltpu.roll(x, x.shape[axis] - step, axis)

    for problem in range(res_ref.shape[0] // 2):
        sign = 1.0 - 2.0 * problem
        totals, centres = ([], [])
        for part in range(2):
            padded = fields_ref[2 * problem + part]
            outer = padded + ahead(padded, 2, 0)
            middle = ahead(padded, 1, 0)
            edge = ahead(outer, 1, 1) + middle + ahead(middle, 2, 1)
            corner = outer + ahead(outer, 2, 1)
            totals.append((4.0 * edge + corner)[:height, :breadth])
            centres.append(ahead(middle, 1, 1)[:height, :breadth])
        real_part, imag_part = centres
        wave = data_ref[4]
        lap_r = (totals[0] - 20.0 * real_part) / 6.0
        lap_i = (totals[1] - 20.0 * imag_part) / 6.0
        mass_r = real_part - sign * DAMPING * imag_part
        mass_i = imag_part + sign * DAMPING * real_part
        res_ref[2 * problem] = data_ref[2 * problem] - (-lap_r - wave * mass_r)
        res_ref[2 * problem + 1] = data_ref[2 * problem + 1] - (-lap_i - wave * mass_i)


def solve_kernel(rect_ref, resid_ref, data_ref, wrow_ref, wcol_ref, *refs, has_base, last, own_rows, own_cols, slab,
                 from_fields):
    if from_fields:
        grid_residual(resid_ref, data_ref, refs[-1])
        resid_ref = refs[-1]
        refs = refs[:-1]
    base_ref = refs[0] if has_base else None
    outs = refs[1:] if has_base else refs
    full_ref = None if last else outs[0]
    own_ref = outs[-1] if last else outs[1]
    top_ref, bottom_ref = (None, None) if last else outs[2:4]
    height, breadth = (resid_ref.shape[1], resid_ref.shape[2])
    half = height // 2
    upper, lower, left, right = (rect_ref[0], rect_ref[1], rect_ref[2], rect_ref[3])
    row_ids = lax.broadcasted_iota(jnp.int32, (height, breadth), 0)
    col_ids = lax.broadcasted_iota(jnp.int32, (height, breadth), 1)
    live = (row_ids >= upper) & (row_ids < lower) & (col_ids >= left) & (col_ids < right)
    top, bottom = (row_ids == upper, row_ids == lower - 1)
    first, last = (col_ids == left, col_ids == right - 1)
    row_flag = top.astype(jnp.float32) + bottom.astype(jnp.float32)
    col_flag = first.astype(jnp.float32) + last.astype(jnp.float32)
    edge_flag = 4.0 * (row_flag + col_flag)
    zero = jnp.zeros((height, breadth), jnp.float32)

    def mask(x):
        return jnp.where(live, x, zero)

    def rows_sum(x):
        up = jnp.where(top, x, pltpu.roll(x, 1, 0))
        down = jnp.where(bottom, x, pltpu.roll(x, height - 1, 0))
        return up + down

    def cols_sum(x):
        lft = jnp.where(first, x, pltpu.roll(x, 1, 1))
        rgt = jnp.where(last, x, pltpu.roll(x, breadth - 1, 1))
        return lft + rgt

    def stencil(x):
        vertical = rows_sum(x)
        ghost_rows = row_flag * x
        total = 4.0 * (vertical + cols_sum(x)) + cols_sum(vertical)
        ghost = edge_flag * x + cols_sum(ghost_rows) + col_flag * (vertical - ghost_rows)
        return total, ghost

    def operator(real_part, imag_part, sign):
        wave = data_ref[4]
        total_r, ghost_r = stencil(real_part)
        total_i, ghost_i = stencil(imag_part)
        lap_r = (total_r + sign * ROBIN_COEF * ghost_i - 20.0 * real_part) / 6.0
        lap_i = (total_i - sign * ROBIN_COEF * ghost_r - 20.0 * imag_part) / 6.0
        mass_r = real_part - sign * DAMPING * imag_part
        mass_i = imag_part + sign * DAMPING * real_part
        return (-lap_r - wave * mass_r, -lap_i - wave * mass_i)

    def dot(a, b):
        return jnp.dot(a, b, precision=lax.Precision.HIGH, preferred_element_type=jnp.float32)

    def dot_t(a, b):
        return lax.dot_general(
            a, b, (((1,), (1,)), ((), ())), precision=lax.Precision.HIGH, preferred_element_type=jnp.float32
        )

    def rows_apply(real_part, imag_part, sign):
        outs_r, outs_i = ([], [])
        for h in range(breadth // half):
            cols = slice(h * half, (h + 1) * half)
            prod_r = dot_t(real_part[:, cols], wrow_ref[h])
            prod_i = dot_t(imag_part[:, cols], wrow_ref[h])
            outs_r.append(prod_r[:, :half] - sign * prod_i[:, half:])
            outs_i.append(prod_i[:, :half] + sign * prod_r[:, half:])
        return (jnp.concatenate(outs_r, axis=1), jnp.concatenate(outs_i, axis=1))

    def cols_apply(real_part, imag_part, sign):
        outs_r, outs_i = ([], [])
        for h in range(height // half):
            rows = slice(h * half, (h + 1) * half)
            prod_r = dot(wcol_ref[h], real_part[rows, :])
            prod_i = dot(wcol_ref[h], imag_part[rows, :])
            outs_r.append(prod_r[:half] - sign * prod_i[half:])
            outs_i.append(prod_i[:half] + sign * prod_r[half:])
        return (jnp.concatenate(outs_r, axis=0), jnp.concatenate(outs_i, axis=0))

    def problem_body(problem, carry):
        sign = 1.0 - 2.0 * problem.astype(jnp.float32)
        up_r, up_i = rows_apply(mask(resid_ref[2 * problem]), mask(resid_ref[2 * problem + 1]), sign)
        cor_r, cor_i = (mask(up_r), mask(up_i))
        for step in range(SWEEPS - 1):
            op_r, op_i = operator(cor_r, cor_i, sign)
            loc_r, loc_i = (mask(resid_ref[2 * problem] - op_r), mask(resid_ref[2 * problem + 1] - op_i))
            apply = cols_apply if step % 2 == 0 else rows_apply
            up_r, up_i = apply(loc_r, loc_i, sign)
            cor_r, cor_i = (cor_r + mask(up_r), cor_i + mask(up_i))
        if base_ref is not None:
            cor_r, cor_i = (cor_r + base_ref[problem, 0], cor_i + base_ref[problem, 1])
        first_row = (height - own_rows) // 2
        for part, value in ((0, cor_r), (1, cor_i)):
            if full_ref is not None:
                full_ref[problem, part] = value
            own = pltpu.roll(value, breadth - (breadth - own_cols) // 2, 1)[first_row : first_row + own_rows, :own_cols]
            own_ref[problem, part] = own
            if top_ref is not None:
                top_ref[problem, part] = own[:slab]
                bottom_ref[problem, part] = own[own_rows - slab :]
        return carry

    lax.fori_loop(0, resid_ref.shape[0] // 2, problem_body, 0)


def line_matrices(row_blocks, col_blocks):
    block = row_blocks.shape[-1]

    def pairs(blocks):
        mats = []
        for h in range(blocks.shape[0] // 2):
            parts = []
            for m in range(2):
                for a in range(2):
                    parts.append(jnp.pad(blocks[2 * h + a, m], ((0, 0), (a * block, (1 - a) * block))))
            mats.append(jnp.concatenate(parts, axis=0))
        return jnp.stack(mats)

    return pairs(row_blocks), pairs(col_blocks)


def solve_local_kernel(resid_planes, data_ext, row_mats, col_mats, live_rect, own_shape, slab, base=None, last=False,
                       from_fields=False, interpret=False):
    extra = [] if base is None else [base]
    rect = jnp.stack([to_index(v) for v in live_rect])
    dtype = resid_planes.dtype
    ext_shape = data_ext.shape[1:]
    shapes = [] if last else [(2, 2) + ext_shape]
    shapes.append((2, 2) + own_shape)
    if not last:
        shapes += [(2, 2, slab, own_shape[1])] * 2
    vmem = pltpu.MemorySpace.VMEM if hasattr(pltpu, "MemorySpace") else pltpu.VMEM
    kernel = functools.partial(
        solve_kernel, has_base=base is not None, last=last, own_rows=own_shape[0], own_cols=own_shape[1], slab=slab,
        from_fields=from_fields,
    )
    scratch = [pltpu.VMEM((4,) + ext_shape, jnp.float32)] if from_fields else []
    return pl.pallas_call(
        kernel,
        out_shape=[jax.ShapeDtypeStruct(s, dtype) for s in shapes],
        in_specs=[pl.BlockSpec(memory_space=pltpu.SMEM)] + [pl.BlockSpec(memory_space=vmem)] * (4 + len(extra)),
        out_specs=[pl.BlockSpec(memory_space=vmem)] * len(shapes),
        scratch_shapes=scratch,
        interpret=interpret,
    )(rect, resid_planes, data_ext, row_mats, col_mats, *extra)


def shards(sources, wavenumber, row_inverse, col_inverse, reach_steps):
    own_rows, own_cols = (sources.shape[2], sources.shape[3])
    block = row_inverse.shape[-1]
    step_cells = block // 4
    signs = jnp.array([1.0, -1.0], dtype=sources.dtype).reshape(2, 1, 1)
    row_rank = to_index(lax.axis_index("gx"))
    col_rank = to_index(lax.axis_index("gy"))
    row_count = lax.axis_size("gx")
    col_count = lax.axis_size("gy")
    zero = to_index(0)
    widths = reach_steps.reshape(4) * step_cells
    upper_w = jnp.where(row_rank > 0, widths[0], zero)
    lower_w = jnp.where(row_rank < row_count - 1, widths[1], zero)
    left_w = jnp.where(col_rank > 0, widths[2], zero)
    right_w = jnp.where(col_rank < col_count - 1, widths[3], zero)
    live_rect = (
        block - upper_w,
        block + own_rows + lower_w,
        block - left_w,
        block + own_cols + right_w,
    )
    stacked = jnp.concatenate([sources.reshape(4, own_rows, own_cols), wavenumber[None]], axis=0)
    lead = stacked.shape[0]
    col_pair = col_inverse.shape[0]
    row_pair = row_inverse.shape[0]
    inv_rows = col_inverse.shape[1] * block * block // own_cols
    before, after = exchange_axis(
        stacked, "gx", 1, block,
        col_inverse[col_pair - 1].reshape(1, inv_rows, own_cols), col_inverse[0].reshape(1, inv_rows, own_cols),
    )
    tall = jnp.concatenate([before[:lead, :block], stacked, after[:lead, :block]], axis=1)
    def inv_slab(mats):
        flat = mats.reshape(1, -1, block)
        return jnp.pad(flat, ((0, 0), (0, tall.shape[1] - flat.shape[1]), (0, 0)))
    left, right = exchange_axis(tall, "gy", 2, block, inv_slab(row_inverse[row_pair - 1]), inv_slab(row_inverse[0]))
    stacked_ext = jnp.concatenate([left[:lead], tall, right[:lead]], axis=2)
    sources_ext = stacked_ext[:4].reshape(2, 2, own_rows + 2 * block, own_cols + 2 * block)
    wave_ext = stacked_ext[4]
    inv_shape = (1,) + row_inverse.shape[1:]
    inv_size = row_inverse.shape[1] * block * block // block
    col_blocks = jnp.concatenate(
        [before[lead:].reshape(inv_shape), col_inverse, after[lead:].reshape(inv_shape)], axis=0
    )
    row_blocks = jnp.concatenate(
        [left[lead:, :inv_size].reshape(inv_shape), row_inverse, right[lead:, :inv_size].reshape(inv_shape)], axis=0
    )
    row_mats, col_mats = line_matrices(row_blocks, col_blocks)
    width = block + 1
    edges = (row_rank == 0, row_rank == row_count - 1, col_rank == 0, col_rank == col_count - 1)
    slab = -(-width // 8) * 8
    solution = None
    base = None
    for iteration in range(ITERS):
        last = iteration == ITERS - 1
        if iteration == 0:
            resid_planes = stacked_ext
        else:
            peers = lax.axis_size("gx")
            up = [(i, i + 1) for i in range(peers - 1)]
            down = [(j, i) for i, j in up]
            before = lax.ppermute(bottom, "gx", up)[:, :, slab - width :]
            after = lax.ppermute(top, "gx", down)[:, :, :width]
            extent = (own_rows + 2 * width, own_cols + 2 * width)
            tile_rows = -(-extent[0] // 8) * 8 - extent[0]
            tile_cols = -(-extent[1] // 128) * 128 - extent[1]
            fill_rows = jnp.zeros(solution.shape[:2] + (tile_rows, own_cols), solution.dtype)
            tall = jnp.concatenate([before, solution, after, fill_rows], axis=2)
            left, right = exchange_axis(tall, "gy", 3, width)
            fill_cols = jnp.zeros(tall.shape[:3] + (tile_cols,), solution.dtype)
            padded = jnp.concatenate([left, tall, right, fill_cols], axis=3)
            padded = grid_ghost(padded, width, extent, edges, signs)
            resid_planes = padded.reshape((4,) + padded.shape[2:])
        outs = solve_local_kernel(
            resid_planes, stacked_ext, row_mats, col_mats, live_rect, (own_rows, own_cols), slab, base=base, last=last,
            from_fields=iteration > 0,
        )
        if last:
            solution = outs[0]
        else:
            base, solution, top, bottom = outs
    return solution


def solution(mesh):
    return jax.shard_map(
        shards,
        mesh=mesh,
        in_specs=(
            P(None, None, "gx", "gy"),
            P("gx", "gy"),
            P("gy", None, None, None),
            P("gx", None, None, None),
            P("gx", "gy", None),
        ),
        out_specs=P(None, None, "gx", "gy"),
        check_vma=False,
    )
```

```python
import functools

import jax
import jax.numpy as jnp
from jax import lax
from jax.sharding import PartitionSpec as P
from jax.experimental import pallas as pl
from jax.experimental.pallas import tpu as pltpu

ITERS = 2
SWEEPS = 4


DAMPING = 0.5
ROBIN_COEF = 0.5


def with_halo(shard, sides, width):
    for axis, dim in sides:
        peers, length = (lax.axis_size(axis), shard.shape[dim])
        up = [(i, (i + 1) % peers) for i in range(peers - 1)]
        down = [(j, i) for i, j in up]
        last = lax.slice_in_dim(shard, length - width, length, axis=dim)
        first = lax.slice_in_dim(shard, 0, width, axis=dim)
        before = lax.ppermute(last, axis, up)
        after = lax.ppermute(first, axis, down)
        shard = jnp.concatenate([before, shard, after], axis=dim)
    return shard


def to_index(value):
    return jnp.asarray(value).astype(jnp.int32)


def slice_line(values, start, axis):
    starts = [to_index(0) for _ in range(values.ndim)]
    starts[axis] = to_index(start)
    sizes = list(values.shape)
    sizes[axis] = 1
    return lax.dynamic_slice(values, starts, sizes)


def fill_ghost(values, upper, lower, left, right, signs):
    upper, lower, left, right = (to_index(upper), to_index(lower), to_index(left), to_index(right))
    height, breadth = (values.shape[2], values.shape[3])
    row_ids = lax.broadcasted_iota(jnp.int32, (height, 1), 0)
    col_ids = lax.broadcasted_iota(jnp.int32, (1, breadth), 1)
    upper_row = slice_line(values, upper, 2)
    lower_row = slice_line(values, lower - 1, 2)
    values = jnp.where(row_ids < upper, upper_row, jnp.where(row_ids >= lower, lower_row, values))
    left_col = slice_line(values, left, 3)
    right_col = slice_line(values, right - 1, 3)
    values = jnp.where(col_ids < left, left_col, jnp.where(col_ids >= right, right_col, values))
    inside = (row_ids >= upper) & (row_ids < lower) & (col_ids >= left) & (col_ids < right)
    real_part = values[:, 0]
    imag_part = values[:, 1]
    ghost_cycle = jnp.stack(
        [real_part + signs * ROBIN_COEF * imag_part, imag_part - signs * ROBIN_COEF * real_part],
        axis=1,
    )
    return jnp.where(inside, values, ghost_cycle)


def grid_ghost(values, width, extent, edges, signs):
    at_top, at_bottom, at_left, at_right = edges
    height, breadth = extent
    row_ids = lax.broadcasted_iota(jnp.int32, (values.shape[2], 1), 0)
    col_ids = lax.broadcasted_iota(jnp.int32, (1, values.shape[3]), 1)
    above = at_top & (row_ids < width)
    below = at_bottom & (row_ids >= height - width)
    before = at_left & (col_ids < width)
    after = at_right & (col_ids >= breadth - width)
    first_row, last_row = (width, height - width - 1)
    first_col, last_col = (width, breadth - width - 1)

    def rows_filled(part):
        return jnp.where(
            above, part[:, :, first_row : first_row + 1], jnp.where(below, part[:, :, last_row : last_row + 1], part)
        )

    filled = rows_filled(values)
    left_col = rows_filled(values[:, :, :, first_col : first_col + 1])
    right_col = rows_filled(values[:, :, :, last_col : last_col + 1])
    values = jnp.where(before, left_col, jnp.where(after, right_col, filled))
    outside = above | below | before | after
    real_part = values[:, 0]
    imag_part = values[:, 1]
    ghost_cycle = jnp.stack(
        [real_part + signs * ROBIN_COEF * imag_part, imag_part - signs * ROBIN_COEF * real_part],
        axis=1,
    )
    return jnp.where(outside, ghost_cycle, values)


def apply_operator(padded, wave_cells, signs):
    centre = padded[:, :, 1:-1, 1:-1]
    edge_sum = (
        padded[:, :, :-2, 1:-1]
        + padded[:, :, 2:, 1:-1]
        + padded[:, :, 1:-1, :-2]
        + padded[:, :, 1:-1, 2:]
    )
    corner_sum = (
        padded[:, :, :-2, :-2]
        + padded[:, :, :-2, 2:]
        + padded[:, :, 2:, :-2]
        + padded[:, :, 2:, 2:]
    )
    laplace = (4.0 * edge_sum + corner_sum - 20.0 * centre) / 6.0
    real_part = centre[:, 0]
    imag_part = centre[:, 1]
    mass_term = jnp.stack(
        [real_part - signs * DAMPING * imag_part, imag_part + signs * DAMPING * real_part], axis=1
    )
    return -laplace - wave_cells * mass_term


def combine_parts(products, signs, shape):
    real_out = products[0][:, 0] - signs[..., None] * products[1][:, 1]
    imag_out = products[0][:, 1] + signs[..., None] * products[1][:, 0]
    return jnp.stack([real_out, imag_out], axis=1).reshape(shape)


def along_rows(values, inverse, signs):
    block = inverse.shape[-1]
    blocked = values.reshape(values.shape[0], 2, values.shape[2], values.shape[3] // block, block)
    products = jnp.einsum("qmok,fchqk->mfchqo", inverse, blocked, precision=lax.Precision.HIGHEST)
    return combine_parts(products, signs, values.shape)


def along_cols(values, inverse, signs):
    block = inverse.shape[-1]
    blocked = values.reshape(values.shape[0], 2, values.shape[2] // block, block, values.shape[3])
    products = jnp.einsum("qmok,fcqkw->mfcqow", inverse, blocked, precision=lax.Precision.HIGHEST)
    return combine_parts(products, signs, values.shape)


def solve_local(resid_ext, wave_ext, row_blocks, col_blocks, live_rect, signs):
    upper, lower, left, right = [to_index(v) for v in live_rect]
    height, breadth = (resid_ext.shape[2], resid_ext.shape[3])
    row_ids = lax.broadcasted_iota(jnp.int32, (height, 1), 0)
    col_ids = lax.broadcasted_iota(jnp.int32, (1, breadth), 1)
    live_mask = (
        (row_ids >= upper) & (row_ids < lower) & (col_ids >= left) & (col_ids < right)
    ).astype(resid_ext.dtype)
    local_res = resid_ext * live_mask
    correction = jnp.zeros_like(resid_ext)
    for sweep_index in range(SWEEPS):
        if sweep_index > 0:
            padded = jnp.pad(correction, ((0, 0), (0, 0), (1, 1), (1, 1)))
            padded = fill_ghost(padded, upper + 1, lower + 1, left + 1, right + 1, signs)
            local_res = live_mask * (resid_ext - apply_operator(padded, wave_ext, signs))
        if sweep_index % 2 == 0:
            update = along_rows(local_res, row_blocks, signs)
        else:
            update = along_cols(local_res, col_blocks, signs)
        correction = correction + live_mask * update
    return correction


def exchange(x, row_width, col_width, extra=None):
    row_count = lax.axis_size("gx")
    col_count = lax.axis_size("gy")
    height, breadth = (x.shape[-2], x.shape[-1])
    pieces = {}
    for dr in (-1, 0, 1):
        for dc in (-1, 0, 1):
            if dr == 0 and dc == 0:
                continue
            slab = x
            if dr == -1:
                slab = lax.slice_in_dim(slab, height - row_width, height, axis=x.ndim - 2)
            elif dr == 1:
                slab = lax.slice_in_dim(slab, 0, row_width, axis=x.ndim - 2)
            if dc == -1:
                slab = lax.slice_in_dim(slab, breadth - col_width, breadth, axis=x.ndim - 1)
            elif dc == 1:
                slab = lax.slice_in_dim(slab, 0, col_width, axis=x.ndim - 1)
            if extra is not None and (dr, dc) in extra:
                slab = jnp.concatenate([slab, extra[(dr, dc)]], axis=0)
            perm = []
            for r in range(row_count):
                for c in range(col_count):
                    rr, cc = (r - dr, c - dc)
                    if 0 <= rr < row_count and 0 <= cc < col_count:
                        perm.append((r * col_count + c, rr * col_count + cc))
            pieces[(dr, dc)] = lax.ppermute(slab, ("gx", "gy"), perm)
    return pieces


def exchange_axis(x, axis, dim, width, extra_lo=None, extra_hi=None):
    peers, length = (lax.axis_size(axis), x.shape[dim])
    up = [(i, i + 1) for i in range(peers - 1)]
    down = [(j, i) for i, j in up]
    last = lax.slice_in_dim(x, length - width, length, axis=dim)
    first = lax.slice_in_dim(x, 0, width, axis=dim)
    if extra_lo is not None:
        last = jnp.concatenate([last, extra_lo], axis=0)
        first = jnp.concatenate([first, extra_hi], axis=0)
    return lax.ppermute(last, axis, up), lax.ppermute(first, axis, down)


def assemble(pieces, centre, lead):
    rows = []
    for dr in (-1, 0, 1):
        row = []
        for dc in (-1, 0, 1):
            part = centre if (dr == 0 and dc == 0) else pieces[(dr, dc)][:lead]
            row.append(part)
        rows.append(jnp.concatenate(row, axis=-1))
    return jnp.concatenate(rows, axis=-2)


def grid_residual(fields_ref, data_ref, res_ref):
    height, breadth = (res_ref.shape[1], res_ref.shape[2])

    def ahead(x, step, axis):
        return pltpu.roll(x, x.shape[axis] - step, axis)

    for problem in range(res_ref.shape[0] // 2):
        sign = 1.0 - 2.0 * problem
        totals, centres = ([], [])
        for part in range(2):
            padded = fields_ref[2 * problem + part]
            outer = padded + ahead(padded, 2, 0)
            middle = ahead(padded, 1, 0)
            edge = ahead(outer, 1, 1) + middle + ahead(middle, 2, 1)
            corner = outer + ahead(outer, 2, 1)
            totals.append((4.0 * edge + corner)[:height, :breadth])
            centres.append(ahead(middle, 1, 1)[:height, :breadth])
        real_part, imag_part = centres
        wave = data_ref[4]
        lap_r = (totals[0] - 20.0 * real_part) / 6.0
        lap_i = (totals[1] - 20.0 * imag_part) / 6.0
        mass_r = real_part - sign * DAMPING * imag_part
        mass_i = imag_part + sign * DAMPING * real_part
        res_ref[2 * problem] = data_ref[2 * problem] - (-lap_r - wave * mass_r)
        res_ref[2 * problem + 1] = data_ref[2 * problem + 1] - (-lap_i - wave * mass_i)


def solve_kernel(rect_ref, resid_ref, data_ref, wrow_ref, wcol_ref, *refs, has_base, last, own_rows, own_cols, slab,
                 from_fields):
    if from_fields:
        grid_residual(resid_ref, data_ref, refs[-1])
        resid_ref = refs[-1]
        refs = refs[:-1]
    base_ref = refs[0] if has_base else None
    outs = refs[1:] if has_base else refs
    full_ref = None if last else outs[0]
    own_ref = outs[-1] if last else outs[1]
    top_ref, bottom_ref = (None, None) if last else outs[2:4]
    height, breadth = (resid_ref.shape[1], resid_ref.shape[2])
    half = height // 2
    upper, lower, left, right = (rect_ref[0], rect_ref[1], rect_ref[2], rect_ref[3])
    row_ids = lax.broadcasted_iota(jnp.int32, (height, breadth), 0)
    col_ids = lax.broadcasted_iota(jnp.int32, (height, breadth), 1)
    live = (row_ids >= upper) & (row_ids < lower) & (col_ids >= left) & (col_ids < right)
    top, bottom = (row_ids == upper, row_ids == lower - 1)
    first, last = (col_ids == left, col_ids == right - 1)
    row_flag = top.astype(jnp.float32) + bottom.astype(jnp.float32)
    col_flag = first.astype(jnp.float32) + last.astype(jnp.float32)
    edge_flag = 4.0 * (row_flag + col_flag)
    zero = jnp.zeros((height, breadth), jnp.float32)

    def mask(x):
        return jnp.where(live, x, zero)

    def rows_sum(x):
        up = jnp.where(top, x, pltpu.roll(x, 1, 0))
        down = jnp.where(bottom, x, pltpu.roll(x, height - 1, 0))
        return up + down

    def cols_sum(x):
        lft = jnp.where(first, x, pltpu.roll(x, 1, 1))
        rgt = jnp.where(last, x, pltpu.roll(x, breadth - 1, 1))
        return lft + rgt

    def stencil(x):
        vertical = rows_sum(x)
        ghost_rows = row_flag * x
        total = 4.0 * (vertical + cols_sum(x)) + cols_sum(vertical)
        ghost = edge_flag * x + cols_sum(ghost_rows) + col_flag * (vertical - ghost_rows)
        return total, ghost

    def operator(real_part, imag_part, sign):
        wave = data_ref[4]
        total_r, ghost_r = stencil(real_part)
        total_i, ghost_i = stencil(imag_part)
        lap_r = (total_r + sign * ROBIN_COEF * ghost_i - 20.0 * real_part) / 6.0
        lap_i = (total_i - sign * ROBIN_COEF * ghost_r - 20.0 * imag_part) / 6.0
        mass_r = real_part - sign * DAMPING * imag_part
        mass_i = imag_part + sign * DAMPING * real_part
        return (-lap_r - wave * mass_r, -lap_i - wave * mass_i)

    def dot(a, b):
        return jnp.dot(a, b, precision=lax.Precision.HIGH, preferred_element_type=jnp.float32)

    def dot_t(a, b):
        return lax.dot_general(
            a, b, (((1,), (1,)), ((), ())), precision=lax.Precision.HIGH, preferred_element_type=jnp.float32
        )

    def rows_apply(real_part, imag_part, sign):
        outs_r, outs_i = ([], [])
        for h in range(breadth // half):
            cols = slice(h * half, (h + 1) * half)
            prod_r = dot_t(real_part[:, cols], wrow_ref[h])
            prod_i = dot_t(imag_part[:, cols], wrow_ref[h])
            outs_r.append(prod_r[:, :half] - sign * prod_i[:, half:])
            outs_i.append(prod_i[:, :half] + sign * prod_r[:, half:])
        return (jnp.concatenate(outs_r, axis=1), jnp.concatenate(outs_i, axis=1))

    def cols_apply(real_part, imag_part, sign):
        outs_r, outs_i = ([], [])
        for h in range(height // half):
            rows = slice(h * half, (h + 1) * half)
            prod_r = dot(wcol_ref[h], real_part[rows, :])
            prod_i = dot(wcol_ref[h], imag_part[rows, :])
            outs_r.append(prod_r[:half] - sign * prod_i[half:])
            outs_i.append(prod_i[:half] + sign * prod_r[half:])
        return (jnp.concatenate(outs_r, axis=0), jnp.concatenate(outs_i, axis=0))

    def problem_body(problem, carry):
        sign = 1.0 - 2.0 * problem.astype(jnp.float32)
        up_r, up_i = rows_apply(mask(resid_ref[2 * problem]), mask(resid_ref[2 * problem + 1]), sign)
        cor_r, cor_i = (mask(up_r), mask(up_i))
        for step in range(SWEEPS - 1):
            op_r, op_i = operator(cor_r, cor_i, sign)
            loc_r, loc_i = (mask(resid_ref[2 * problem] - op_r), mask(resid_ref[2 * problem + 1] - op_i))
            apply = cols_apply if step % 2 == 0 else rows_apply
            up_r, up_i = apply(loc_r, loc_i, sign)
            cor_r, cor_i = (cor_r + mask(up_r), cor_i + mask(up_i))
        if base_ref is not None:
            cor_r, cor_i = (cor_r + base_ref[problem, 0], cor_i + base_ref[problem, 1])
        first_row = (height - own_rows) // 2
        for part, value in ((0, cor_r), (1, cor_i)):
            if full_ref is not None:
                full_ref[problem, part] = value
            own = pltpu.roll(value, breadth - (breadth - own_cols) // 2, 1)[first_row : first_row + own_rows, :own_cols]
            own_ref[problem, part] = own
            if top_ref is not None:
                top_ref[problem, part] = own[:slab]
                bottom_ref[problem, part] = own[own_rows - slab :]
        return carry

    lax.fori_loop(0, resid_ref.shape[0] // 2, problem_body, 0)


def line_matrices(row_blocks, col_blocks):
    block = row_blocks.shape[-1]

    def pairs(blocks):
        mats = []
        for h in range(blocks.shape[0] // 2):
            parts = []
            for m in range(2):
                for a in range(2):
                    parts.append(jnp.pad(blocks[2 * h + a, m], ((0, 0), (a * block, (1 - a) * block))))
            mats.append(jnp.concatenate(parts, axis=0))
        return jnp.stack(mats)

    return pairs(row_blocks), pairs(col_blocks)


def solve_local_kernel(resid_planes, data_ext, row_mats, col_mats, live_rect, own_shape, slab, base=None, last=False,
                       from_fields=False, interpret=False):
    extra = [] if base is None else [base]
    rect = jnp.stack([to_index(v) for v in live_rect])
    dtype = resid_planes.dtype
    ext_shape = data_ext.shape[1:]
    shapes = [] if last else [(2, 2) + ext_shape]
    shapes.append((2, 2) + own_shape)
    if not last:
        shapes += [(2, 2, slab, own_shape[1])] * 2
    vmem = pltpu.MemorySpace.VMEM if hasattr(pltpu, "MemorySpace") else pltpu.VMEM
    kernel = functools.partial(
        solve_kernel, has_base=base is not None, last=last, own_rows=own_shape[0], own_cols=own_shape[1], slab=slab,
        from_fields=from_fields,
    )
    scratch = [pltpu.VMEM((4,) + ext_shape, jnp.float32)] if from_fields else []
    return pl.pallas_call(
        kernel,
        out_shape=[jax.ShapeDtypeStruct(s, dtype) for s in shapes],
        in_specs=[pl.BlockSpec(memory_space=pltpu.SMEM)] + [pl.BlockSpec(memory_space=vmem)] * (4 + len(extra)),
        out_specs=[pl.BlockSpec(memory_space=vmem)] * len(shapes),
        scratch_shapes=scratch,
        interpret=interpret,
    )(rect, resid_planes, data_ext, row_mats, col_mats, *extra)


def shards(sources, wavenumber, row_inverse, col_inverse, reach_steps):
    own_rows, own_cols = (sources.shape[2], sources.shape[3])
    block = row_inverse.shape[-1]
    step_cells = block // 4
    signs = jnp.array([1.0, -1.0], dtype=sources.dtype).reshape(2, 1, 1)
    row_rank = to_index(lax.axis_index("gx"))
    col_rank = to_index(lax.axis_index("gy"))
    row_count = lax.axis_size("gx")
    col_count = lax.axis_size("gy")
    zero = to_index(0)
    widths = reach_steps.reshape(4) * step_cells
    upper_w = jnp.where(row_rank > 0, widths[0], zero)
    lower_w = jnp.where(row_rank < row_count - 1, widths[1], zero)
    left_w = jnp.where(col_rank > 0, widths[2], zero)
    right_w = jnp.where(col_rank < col_count - 1, widths[3], zero)
    live_rect = (
        block - upper_w,
        block + own_rows + lower_w,
        block - left_w,
        block + own_cols + right_w,
    )
    planes = [sources.reshape(4, own_rows, own_cols), wavenumber[None]]
    lead = 5
    col_pair = col_inverse.shape[0]
    row_pair = row_inverse.shape[0]
    inv_rows = col_inverse.shape[1] * block * block // own_cols
    peers_x, peers_y = (lax.axis_size("gx"), lax.axis_size("gy"))
    up_x = [(i, i + 1) for i in range(peers_x - 1)]
    up_y = [(i, i + 1) for i in range(peers_y - 1)]
    last_rows = jnp.concatenate(
        [p[:, own_rows - block :] for p in planes] + [col_inverse[col_pair - 1].reshape(1, inv_rows, own_cols)], axis=0
    )
    first_rows = jnp.concatenate(
        [p[:, :block] for p in planes] + [col_inverse[0].reshape(1, inv_rows, own_cols)], axis=0
    )
    before = lax.ppermute(last_rows, "gx", up_x)
    after = lax.ppermute(first_rows, "gx", [(j, i) for i, j in up_x])
    column_parts = [before[:lead]] + [jnp.concatenate(planes, axis=0)] + [after[:lead]]
    ext_rows = own_rows + 2 * block

    def inv_slab(mats):
        flat = mats.reshape(1, -1, block)
        return jnp.pad(flat, ((0, 0), (0, ext_rows - flat.shape[1]), (0, 0)))

    last_cols = jnp.concatenate(
        [jnp.concatenate([p[:, :, own_cols - block :] for p in column_parts], axis=1), inv_slab(row_inverse[row_pair - 1])],
        axis=0,
    )
    first_cols = jnp.concatenate(
        [jnp.concatenate([p[:, :, :block] for p in column_parts], axis=1), inv_slab(row_inverse[0])], axis=0
    )
    left = lax.ppermute(last_cols, "gy", up_y)
    right = lax.ppermute(first_cols, "gy", [(j, i) for i, j in up_y])
    tall = jnp.concatenate(column_parts, axis=1)
    stacked_ext = jnp.concatenate([left[:lead], tall, right[:lead]], axis=2)
    inv_shape = (1,) + row_inverse.shape[1:]
    inv_size = row_inverse.shape[1] * block * block // block
    col_blocks = jnp.concatenate(
        [before[lead:].reshape(inv_shape), col_inverse, after[lead:].reshape(inv_shape)], axis=0
    )
    row_blocks = jnp.concatenate(
        [left[lead:, :inv_size].reshape(inv_shape), row_inverse, right[lead:, :inv_size].reshape(inv_shape)], axis=0
    )
    row_mats, col_mats = line_matrices(row_blocks, col_blocks)
    width = block + 1
    edges = (row_rank == 0, row_rank == row_count - 1, col_rank == 0, col_rank == col_count - 1)
    slab = -(-width // 8) * 8
    solution = None
    base = None
    for iteration in range(ITERS):
        last = iteration == ITERS - 1
        if iteration == 0:
            resid_planes = stacked_ext
        else:
            peers = lax.axis_size("gx")
            up = [(i, i + 1) for i in range(peers - 1)]
            down = [(j, i) for i, j in up]
            before = lax.ppermute(bottom, "gx", up)[:, :, slab - width :]
            after = lax.ppermute(top, "gx", down)[:, :, :width]
            extent = (own_rows + 2 * width, own_cols + 2 * width)
            tile_rows = -(-extent[0] // 8) * 8 - extent[0]
            tile_cols = -(-extent[1] // 128) * 128 - extent[1]
            fill_rows = jnp.zeros(solution.shape[:2] + (tile_rows, own_cols), solution.dtype)
            tall = jnp.concatenate([before, solution, after, fill_rows], axis=2)
            left, right = exchange_axis(tall, "gy", 3, width)
            fill_cols = jnp.zeros(tall.shape[:3] + (tile_cols,), solution.dtype)
            padded = jnp.concatenate([left, tall, right, fill_cols], axis=3)
            padded = grid_ghost(padded, width, extent, edges, signs)
            resid_planes = padded.reshape((4,) + padded.shape[2:])
        outs = solve_local_kernel(
            resid_planes, stacked_ext, row_mats, col_mats, live_rect, (own_rows, own_cols), slab, base=base, last=last,
            from_fields=iteration > 0,
        )
        if last:
            solution = outs[0]
        else:
            base, solution, top, bottom = outs
    return solution


def solution(mesh):
    return jax.shard_map(
        shards,
        mesh=mesh,
        in_specs=(
            P(None, None, "gx", "gy"),
            P("gx", "gy"),
            P("gy", None, None, None),
            P("gx", None, None, None),
            P("gx", "gy", None),
        ),
        out_specs=P(None, None, "gx", "gy"),
        check_vma=False,
    )
```

```python
import functools

import jax
import jax.numpy as jnp
from jax import lax
from jax.sharding import PartitionSpec as P
from jax.experimental import pallas as pl
from jax.experimental.pallas import tpu as pltpu

ITERS = 2
SWEEPS = 4


DAMPING = 0.5
ROBIN_COEF = 0.5


def with_halo(shard, sides, width):
    for axis, dim in sides:
        peers, length = (lax.axis_size(axis), shard.shape[dim])
        up = [(i, (i + 1) % peers) for i in range(peers - 1)]
        down = [(j, i) for i, j in up]
        last = lax.slice_in_dim(shard, length - width, length, axis=dim)
        first = lax.slice_in_dim(shard, 0, width, axis=dim)
        before = lax.ppermute(last, axis, up)
        after = lax.ppermute(first, axis, down)
        shard = jnp.concatenate([before, shard, after], axis=dim)
    return shard


def to_index(value):
    return jnp.asarray(value).astype(jnp.int32)


def slice_line(values, start, axis):
    starts = [to_index(0) for _ in range(values.ndim)]
    starts[axis] = to_index(start)
    sizes = list(values.shape)
    sizes[axis] = 1
    return lax.dynamic_slice(values, starts, sizes)


def fill_ghost(values, upper, lower, left, right, signs):
    upper, lower, left, right = (to_index(upper), to_index(lower), to_index(left), to_index(right))
    height, breadth = (values.shape[2], values.shape[3])
    row_ids = lax.broadcasted_iota(jnp.int32, (height, 1), 0)
    col_ids = lax.broadcasted_iota(jnp.int32, (1, breadth), 1)
    upper_row = slice_line(values, upper, 2)
    lower_row = slice_line(values, lower - 1, 2)
    values = jnp.where(row_ids < upper, upper_row, jnp.where(row_ids >= lower, lower_row, values))
    left_col = slice_line(values, left, 3)
    right_col = slice_line(values, right - 1, 3)
    values = jnp.where(col_ids < left, left_col, jnp.where(col_ids >= right, right_col, values))
    inside = (row_ids >= upper) & (row_ids < lower) & (col_ids >= left) & (col_ids < right)
    real_part = values[:, 0]
    imag_part = values[:, 1]
    ghost_cycle = jnp.stack(
        [real_part + signs * ROBIN_COEF * imag_part, imag_part - signs * ROBIN_COEF * real_part],
        axis=1,
    )
    return jnp.where(inside, values, ghost_cycle)


def grid_ghost(values, width, edges, signs):
    at_top, at_bottom, at_left, at_right = edges
    height, breadth = (values.shape[2], values.shape[3])
    row_ids = lax.broadcasted_iota(jnp.int32, (height, 1), 0)
    col_ids = lax.broadcasted_iota(jnp.int32, (1, breadth), 1)
    above = at_top & (row_ids < width)
    below = at_bottom & (row_ids >= height - width)
    values = jnp.where(
        above, values[:, :, width : width + 1], jnp.where(below, values[:, :, height - width - 1 : height - width], values)
    )
    before = at_left & (col_ids < width)
    after = at_right & (col_ids >= breadth - width)
    values = jnp.where(
        before, values[:, :, :, width : width + 1],
        jnp.where(after, values[:, :, :, breadth - width - 1 : breadth - width], values),
    )
    outside = above | below | before | after
    real_part = values[:, 0]
    imag_part = values[:, 1]
    ghost_cycle = jnp.stack(
        [real_part + signs * ROBIN_COEF * imag_part, imag_part - signs * ROBIN_COEF * real_part],
        axis=1,
    )
    return jnp.where(outside, ghost_cycle, values)


def apply_operator(padded, wave_cells, signs):
    centre = padded[:, :, 1:-1, 1:-1]
    edge_sum = (
        padded[:, :, :-2, 1:-1]
        + padded[:, :, 2:, 1:-1]
        + padded[:, :, 1:-1, :-2]
        + padded[:, :, 1:-1, 2:]
    )
    corner_sum = (
        padded[:, :, :-2, :-2]
        + padded[:, :, :-2, 2:]
        + padded[:, :, 2:, :-2]
        + padded[:, :, 2:, 2:]
    )
    laplace = (4.0 * edge_sum + corner_sum - 20.0 * centre) / 6.0
    real_part = centre[:, 0]
    imag_part = centre[:, 1]
    mass_term = jnp.stack(
        [real_part - signs * DAMPING * imag_part, imag_part + signs * DAMPING * real_part], axis=1
    )
    return -laplace - wave_cells * mass_term


def combine_parts(products, signs, shape):
    real_out = products[0][:, 0] - signs[..., None] * products[1][:, 1]
    imag_out = products[0][:, 1] + signs[..., None] * products[1][:, 0]
    return jnp.stack([real_out, imag_out], axis=1).reshape(shape)


def along_rows(values, inverse, signs):
    block = inverse.shape[-1]
    blocked = values.reshape(values.shape[0], 2, values.shape[2], values.shape[3] // block, block)
    products = jnp.einsum("qmok,fchqk->mfchqo", inverse, blocked, precision=lax.Precision.HIGHEST)
    return combine_parts(products, signs, values.shape)


def along_cols(values, inverse, signs):
    block = inverse.shape[-1]
    blocked = values.reshape(values.shape[0], 2, values.shape[2] // block, block, values.shape[3])
    products = jnp.einsum("qmok,fcqkw->mfcqow", inverse, blocked, precision=lax.Precision.HIGHEST)
    return combine_parts(products, signs, values.shape)


def solve_local(resid_ext, wave_ext, row_blocks, col_blocks, live_rect, signs):
    upper, lower, left, right = [to_index(v) for v in live_rect]
    height, breadth = (resid_ext.shape[2], resid_ext.shape[3])
    row_ids = lax.broadcasted_iota(jnp.int32, (height, 1), 0)
    col_ids = lax.broadcasted_iota(jnp.int32, (1, breadth), 1)
    live_mask = (
        (row_ids >= upper) & (row_ids < lower) & (col_ids >= left) & (col_ids < right)
    ).astype(resid_ext.dtype)
    local_res = resid_ext * live_mask
    correction = jnp.zeros_like(resid_ext)
    for sweep_index in range(SWEEPS):
        if sweep_index > 0:
            padded = jnp.pad(correction, ((0, 0), (0, 0), (1, 1), (1, 1)))
            padded = fill_ghost(padded, upper + 1, lower + 1, left + 1, right + 1, signs)
            local_res = live_mask * (resid_ext - apply_operator(padded, wave_ext, signs))
        if sweep_index % 2 == 0:
            update = along_rows(local_res, row_blocks, signs)
        else:
            update = along_cols(local_res, col_blocks, signs)
        correction = correction + live_mask * update
    return correction


def exchange(x, row_width, col_width, extra=None):
    row_count = lax.axis_size("gx")
    col_count = lax.axis_size("gy")
    height, breadth = (x.shape[-2], x.shape[-1])
    pieces = {}
    for dr in (-1, 0, 1):
        for dc in (-1, 0, 1):
            if dr == 0 and dc == 0:
                continue
            slab = x
            if dr == -1:
                slab = lax.slice_in_dim(slab, height - row_width, height, axis=x.ndim - 2)
            elif dr == 1:
                slab = lax.slice_in_dim(slab, 0, row_width, axis=x.ndim - 2)
            if dc == -1:
                slab = lax.slice_in_dim(slab, breadth - col_width, breadth, axis=x.ndim - 1)
            elif dc == 1:
                slab = lax.slice_in_dim(slab, 0, col_width, axis=x.ndim - 1)
            if extra is not None and (dr, dc) in extra:
                slab = jnp.concatenate([slab, extra[(dr, dc)]], axis=0)
            perm = []
            for r in range(row_count):
                for c in range(col_count):
                    rr, cc = (r - dr, c - dc)
                    if 0 <= rr < row_count and 0 <= cc < col_count:
                        perm.append((r * col_count + c, rr * col_count + cc))
            pieces[(dr, dc)] = lax.ppermute(slab, ("gx", "gy"), perm)
    return pieces


def exchange_axis(x, axis, dim, width, extra_lo=None, extra_hi=None):
    peers, length = (lax.axis_size(axis), x.shape[dim])
    up = [(i, i + 1) for i in range(peers - 1)]
    down = [(j, i) for i, j in up]
    last = lax.slice_in_dim(x, length - width, length, axis=dim)
    first = lax.slice_in_dim(x, 0, width, axis=dim)
    if extra_lo is not None:
        last = jnp.concatenate([last, extra_lo], axis=0)
        first = jnp.concatenate([first, extra_hi], axis=0)
    return lax.ppermute(last, axis, up), lax.ppermute(first, axis, down)


def assemble(pieces, centre, lead):
    rows = []
    for dr in (-1, 0, 1):
        row = []
        for dc in (-1, 0, 1):
            part = centre if (dr == 0 and dc == 0) else pieces[(dr, dc)][:lead]
            row.append(part)
        rows.append(jnp.concatenate(row, axis=-1))
    return jnp.concatenate(rows, axis=-2)


def grid_residual(fields_ref, data_ref, res_ref):
    height, breadth = (res_ref.shape[1], res_ref.shape[2])

    def ahead(x, step, axis):
        return pltpu.roll(x, x.shape[axis] - step, axis)

    for problem in range(res_ref.shape[0] // 2):
        sign = 1.0 - 2.0 * problem
        totals, centres = ([], [])
        for part in range(2):
            padded = fields_ref[2 * problem + part]
            outer = padded + ahead(padded, 2, 0)
            middle = ahead(padded, 1, 0)
            edge = ahead(outer, 1, 1) + middle + ahead(middle, 2, 1)
            corner = outer + ahead(outer, 2, 1)
            totals.append((4.0 * edge + corner)[:height, :breadth])
            centres.append(ahead(middle, 1, 1)[:height, :breadth])
        real_part, imag_part = centres
        wave = data_ref[4]
        lap_r = (totals[0] - 20.0 * real_part) / 6.0
        lap_i = (totals[1] - 20.0 * imag_part) / 6.0
        mass_r = real_part - sign * DAMPING * imag_part
        mass_i = imag_part + sign * DAMPING * real_part
        res_ref[2 * problem] = data_ref[2 * problem] - (-lap_r - wave * mass_r)
        res_ref[2 * problem + 1] = data_ref[2 * problem + 1] - (-lap_i - wave * mass_i)


def solve_kernel(rect_ref, resid_ref, data_ref, wrow_ref, wcol_ref, *refs, has_base, last, own_rows, own_cols, slab,
                 from_fields):
    if from_fields:
        grid_residual(resid_ref, data_ref, refs[-1])
        resid_ref = refs[-1]
        refs = refs[:-1]
    base_ref = refs[0] if has_base else None
    outs = refs[1:] if has_base else refs
    full_ref = None if last else outs[0]
    own_ref = outs[-1] if last else outs[1]
    top_ref, bottom_ref = (None, None) if last else outs[2:4]
    height, breadth = (resid_ref.shape[1], resid_ref.shape[2])
    half = height // 2
    upper, lower, left, right = (rect_ref[0], rect_ref[1], rect_ref[2], rect_ref[3])
    row_ids = lax.broadcasted_iota(jnp.int32, (height, breadth), 0)
    col_ids = lax.broadcasted_iota(jnp.int32, (height, breadth), 1)
    live = (row_ids >= upper) & (row_ids < lower) & (col_ids >= left) & (col_ids < right)
    top, bottom = (row_ids == upper, row_ids == lower - 1)
    first, last = (col_ids == left, col_ids == right - 1)
    row_flag = top.astype(jnp.float32) + bottom.astype(jnp.float32)
    col_flag = first.astype(jnp.float32) + last.astype(jnp.float32)
    edge_flag = 4.0 * (row_flag + col_flag)
    zero = jnp.zeros((height, breadth), jnp.float32)

    def mask(x):
        return jnp.where(live, x, zero)

    def rows_sum(x):
        up = jnp.where(top, x, pltpu.roll(x, 1, 0))
        down = jnp.where(bottom, x, pltpu.roll(x, height - 1, 0))
        return up + down

    def cols_sum(x):
        lft = jnp.where(first, x, pltpu.roll(x, 1, 1))
        rgt = jnp.where(last, x, pltpu.roll(x, breadth - 1, 1))
        return lft + rgt

    def stencil(x):
        vertical = rows_sum(x)
        ghost_rows = row_flag * x
        total = 4.0 * (vertical + cols_sum(x)) + cols_sum(vertical)
        ghost = edge_flag * x + cols_sum(ghost_rows) + col_flag * (vertical - ghost_rows)
        return total, ghost

    def operator(real_part, imag_part, sign):
        wave = data_ref[4]
        total_r, ghost_r = stencil(real_part)
        total_i, ghost_i = stencil(imag_part)
        lap_r = (total_r + sign * ROBIN_COEF * ghost_i - 20.0 * real_part) / 6.0
        lap_i = (total_i - sign * ROBIN_COEF * ghost_r - 20.0 * imag_part) / 6.0
        mass_r = real_part - sign * DAMPING * imag_part
        mass_i = imag_part + sign * DAMPING * real_part
        return (-lap_r - wave * mass_r, -lap_i - wave * mass_i)

    def dot(a, b):
        return jnp.dot(a, b, precision=lax.Precision.HIGH, preferred_element_type=jnp.float32)

    def dot_t(a, b):
        return lax.dot_general(
            a, b, (((1,), (1,)), ((), ())), precision=lax.Precision.HIGH, preferred_element_type=jnp.float32
        )

    def rows_apply(real_part, imag_part, sign):
        outs_r, outs_i = ([], [])
        for h in range(breadth // half):
            cols = slice(h * half, (h + 1) * half)
            prod_r = dot_t(real_part[:, cols], wrow_ref[h])
            prod_i = dot_t(imag_part[:, cols], wrow_ref[h])
            outs_r.append(prod_r[:, :half] - sign * prod_i[:, half:])
            outs_i.append(prod_i[:, :half] + sign * prod_r[:, half:])
        return (jnp.concatenate(outs_r, axis=1), jnp.concatenate(outs_i, axis=1))

    def cols_apply(real_part, imag_part, sign):
        outs_r, outs_i = ([], [])
        for h in range(height // half):
            rows = slice(h * half, (h + 1) * half)
            prod_r = dot(wcol_ref[h], real_part[rows, :])
            prod_i = dot(wcol_ref[h], imag_part[rows, :])
            outs_r.append(prod_r[:half] - sign * prod_i[half:])
            outs_i.append(prod_i[:half] + sign * prod_r[half:])
        return (jnp.concatenate(outs_r, axis=0), jnp.concatenate(outs_i, axis=0))

    def problem_body(problem, carry):
        sign = 1.0 - 2.0 * problem.astype(jnp.float32)
        up_r, up_i = rows_apply(mask(resid_ref[2 * problem]), mask(resid_ref[2 * problem + 1]), sign)
        cor_r, cor_i = (mask(up_r), mask(up_i))
        for step in range(SWEEPS - 1):
            op_r, op_i = operator(cor_r, cor_i, sign)
            loc_r, loc_i = (mask(resid_ref[2 * problem] - op_r), mask(resid_ref[2 * problem + 1] - op_i))
            apply = cols_apply if step % 2 == 0 else rows_apply
            up_r, up_i = apply(loc_r, loc_i, sign)
            cor_r, cor_i = (cor_r + mask(up_r), cor_i + mask(up_i))
        if base_ref is not None:
            cor_r, cor_i = (cor_r + base_ref[problem, 0], cor_i + base_ref[problem, 1])
        first_row = (height - own_rows) // 2
        for part, value in ((0, cor_r), (1, cor_i)):
            if full_ref is not None:
                full_ref[problem, part] = value
            own = pltpu.roll(value, breadth - (breadth - own_cols) // 2, 1)[first_row : first_row + own_rows, :own_cols]
            own_ref[problem, part] = own
            if top_ref is not None:
                top_ref[problem, part] = own[:slab]
                bottom_ref[problem, part] = own[own_rows - slab :]
        return carry

    lax.fori_loop(0, resid_ref.shape[0] // 2, problem_body, 0)


def line_matrices(row_blocks, col_blocks):
    block = row_blocks.shape[-1]

    def pairs(blocks):
        mats = []
        for h in range(blocks.shape[0] // 2):
            parts = []
            for m in range(2):
                for a in range(2):
                    parts.append(jnp.pad(blocks[2 * h + a, m], ((0, 0), (a * block, (1 - a) * block))))
            mats.append(jnp.concatenate(parts, axis=0))
        return jnp.stack(mats)

    return pairs(row_blocks), pairs(col_blocks)


def solve_local_kernel(resid_planes, data_ext, row_mats, col_mats, live_rect, own_shape, slab, base=None, last=False,
                       from_fields=False, interpret=False):
    extra = [] if base is None else [base]
    rect = jnp.stack([to_index(v) for v in live_rect])
    dtype = resid_planes.dtype
    ext_shape = data_ext.shape[1:]
    shapes = [] if last else [(2, 2) + ext_shape]
    shapes.append((2, 2) + own_shape)
    if not last:
        shapes += [(2, 2, slab, own_shape[1])] * 2
    vmem = pltpu.MemorySpace.VMEM if hasattr(pltpu, "MemorySpace") else pltpu.VMEM
    kernel = functools.partial(
        solve_kernel, has_base=base is not None, last=last, own_rows=own_shape[0], own_cols=own_shape[1], slab=slab,
        from_fields=from_fields,
    )
    scratch = [pltpu.VMEM((4,) + ext_shape, jnp.float32)] if from_fields else []
    return pl.pallas_call(
        kernel,
        out_shape=[jax.ShapeDtypeStruct(s, dtype) for s in shapes],
        in_specs=[pl.BlockSpec(memory_space=pltpu.SMEM)] + [pl.BlockSpec(memory_space=vmem)] * (4 + len(extra)),
        out_specs=[pl.BlockSpec(memory_space=vmem)] * len(shapes),
        scratch_shapes=scratch,
        interpret=interpret,
    )(rect, resid_planes, data_ext, row_mats, col_mats, *extra)


def shards(sources, wavenumber, row_inverse, col_inverse, reach_steps):
    own_rows, own_cols = (sources.shape[2], sources.shape[3])
    block = row_inverse.shape[-1]
    step_cells = block // 4
    signs = jnp.array([1.0, -1.0], dtype=sources.dtype).reshape(2, 1, 1)
    row_rank = to_index(lax.axis_index("gx"))
    col_rank = to_index(lax.axis_index("gy"))
    row_count = lax.axis_size("gx")
    col_count = lax.axis_size("gy")
    zero = to_index(0)
    widths = reach_steps.reshape(4) * step_cells
    upper_w = jnp.where(row_rank > 0, widths[0], zero)
    lower_w = jnp.where(row_rank < row_count - 1, widths[1], zero)
    left_w = jnp.where(col_rank > 0, widths[2], zero)
    right_w = jnp.where(col_rank < col_count - 1, widths[3], zero)
    live_rect = (
        block - upper_w,
        block + own_rows + lower_w,
        block - left_w,
        block + own_cols + right_w,
    )
    stacked = jnp.concatenate([sources.reshape(4, own_rows, own_cols), wavenumber[None]], axis=0)
    lead = stacked.shape[0]
    col_pair = col_inverse.shape[0]
    row_pair = row_inverse.shape[0]
    inv_cols = row_inverse.shape[1] * block * block // own_rows
    left, right = exchange_axis(
        stacked, "gy", 2, block,
        row_inverse[row_pair - 1].reshape(1, own_rows, inv_cols), row_inverse[0].reshape(1, own_rows, inv_cols),
    )
    wide = jnp.concatenate([left[:lead, :, :block], stacked, right[:lead, :, :block]], axis=2)

    def inv_slab(mats):
        flat = mats.reshape(1, block, -1)
        return jnp.pad(flat, ((0, 0), (0, 0), (0, wide.shape[2] - flat.shape[2])))

    before, after = exchange_axis(wide, "gx", 1, block, inv_slab(col_inverse[col_pair - 1]), inv_slab(col_inverse[0]))
    stacked_ext = jnp.concatenate([before[:lead], wide, after[:lead]], axis=1)
    inv_shape = (1,) + row_inverse.shape[1:]
    inv_size = col_inverse.shape[1] * block * block // block
    row_blocks = jnp.concatenate(
        [left[lead:].reshape(inv_shape), row_inverse, right[lead:].reshape(inv_shape)], axis=0
    )
    col_blocks = jnp.concatenate(
        [before[lead:, :, :inv_size].reshape(inv_shape), col_inverse, after[lead:, :, :inv_size].reshape(inv_shape)],
        axis=0,
    )
    row_mats, col_mats = line_matrices(row_blocks, col_blocks)
    width = block + 1
    edges = (row_rank == 0, row_rank == row_count - 1, col_rank == 0, col_rank == col_count - 1)
    slab = -(-width // 8) * 8
    solution = None
    base = None
    for iteration in range(ITERS):
        last = iteration == ITERS - 1
        if iteration == 0:
            resid_planes = stacked_ext
        else:
            peers = lax.axis_size("gx")
            up = [(i, i + 1) for i in range(peers - 1)]
            down = [(j, i) for i, j in up]
            before = lax.ppermute(bottom, "gx", up)[:, :, slab - width :]
            after = lax.ppermute(top, "gx", down)[:, :, :width]
            tall = jnp.concatenate([before, solution, after], axis=2)
            left, right = exchange_axis(tall, "gy", 3, width)
            padded = jnp.concatenate([left, tall, right], axis=3)
            padded = grid_ghost(padded, width, edges, signs)
            tile_rows = -(-padded.shape[2] // 8) * 8 - padded.shape[2]
            tile_cols = -(-padded.shape[3] // 128) * 128 - padded.shape[3]
            padded = jnp.pad(padded, ((0, 0), (0, 0), (0, tile_rows), (0, tile_cols)))
            resid_planes = padded.reshape((4,) + padded.shape[2:])
        outs = solve_local_kernel(
            resid_planes, stacked_ext, row_mats, col_mats, live_rect, (own_rows, own_cols), slab, base=base, last=last,
            from_fields=iteration > 0,
        )
        if last:
            solution = outs[0]
        else:
            base, solution, top, bottom = outs
    return solution


def solution(mesh):
    return jax.shard_map(
        shards,
        mesh=mesh,
        in_specs=(
            P(None, None, "gx", "gy"),
            P("gx", "gy"),
            P("gy", None, None, None),
            P("gx", None, None, None),
            P("gx", "gy", None),
        ),
        out_specs=P(None, None, "gx", "gy"),
        check_vma=False,
    )
```

```python
import functools

import jax
import jax.numpy as jnp
from jax import lax
from jax.sharding import PartitionSpec as P
from jax.experimental import pallas as pl
from jax.experimental.pallas import tpu as pltpu

ITERS = 2
SWEEPS = 4


DAMPING = 0.5
ROBIN_COEF = 0.5


def with_halo(shard, sides, width):
    for axis, dim in sides:
        peers, length = (lax.axis_size(axis), shard.shape[dim])
        up = [(i, (i + 1) % peers) for i in range(peers - 1)]
        down = [(j, i) for i, j in up]
        last = lax.slice_in_dim(shard, length - width, length, axis=dim)
        first = lax.slice_in_dim(shard, 0, width, axis=dim)
        before = lax.ppermute(last, axis, up)
        after = lax.ppermute(first, axis, down)
        shard = jnp.concatenate([before, shard, after], axis=dim)
    return shard


def to_index(value):
    return jnp.asarray(value).astype(jnp.int32)


def slice_line(values, start, axis):
    starts = [to_index(0) for _ in range(values.ndim)]
    starts[axis] = to_index(start)
    sizes = list(values.shape)
    sizes[axis] = 1
    return lax.dynamic_slice(values, starts, sizes)


def fill_ghost(values, upper, lower, left, right, signs):
    upper, lower, left, right = (to_index(upper), to_index(lower), to_index(left), to_index(right))
    height, breadth = (values.shape[2], values.shape[3])
    row_ids = lax.broadcasted_iota(jnp.int32, (height, 1), 0)
    col_ids = lax.broadcasted_iota(jnp.int32, (1, breadth), 1)
    upper_row = slice_line(values, upper, 2)
    lower_row = slice_line(values, lower - 1, 2)
    values = jnp.where(row_ids < upper, upper_row, jnp.where(row_ids >= lower, lower_row, values))
    left_col = slice_line(values, left, 3)
    right_col = slice_line(values, right - 1, 3)
    values = jnp.where(col_ids < left, left_col, jnp.where(col_ids >= right, right_col, values))
    inside = (row_ids >= upper) & (row_ids < lower) & (col_ids >= left) & (col_ids < right)
    real_part = values[:, 0]
    imag_part = values[:, 1]
    ghost_cycle = jnp.stack(
        [real_part + signs * ROBIN_COEF * imag_part, imag_part - signs * ROBIN_COEF * real_part],
        axis=1,
    )
    return jnp.where(inside, values, ghost_cycle)


def grid_ghost(values, width, edges, signs):
    at_top, at_bottom, at_left, at_right = edges
    height, breadth = (values.shape[2], values.shape[3])
    row_ids = lax.broadcasted_iota(jnp.int32, (height, 1), 0)
    col_ids = lax.broadcasted_iota(jnp.int32, (1, breadth), 1)
    above = at_top & (row_ids < width)
    below = at_bottom & (row_ids >= height - width)
    values = jnp.where(
        above, values[:, :, width : width + 1], jnp.where(below, values[:, :, height - width - 1 : height - width], values)
    )
    before = at_left & (col_ids < width)
    after = at_right & (col_ids >= breadth - width)
    values = jnp.where(
        before, values[:, :, :, width : width + 1],
        jnp.where(after, values[:, :, :, breadth - width - 1 : breadth - width], values),
    )
    outside = above | below | before | after
    real_part = values[:, 0]
    imag_part = values[:, 1]
    ghost_cycle = jnp.stack(
        [real_part + signs * ROBIN_COEF * imag_part, imag_part - signs * ROBIN_COEF * real_part],
        axis=1,
    )
    return jnp.where(outside, ghost_cycle, values)


def apply_operator(padded, wave_cells, signs):
    centre = padded[:, :, 1:-1, 1:-1]
    edge_sum = (
        padded[:, :, :-2, 1:-1]
        + padded[:, :, 2:, 1:-1]
        + padded[:, :, 1:-1, :-2]
        + padded[:, :, 1:-1, 2:]
    )
    corner_sum = (
        padded[:, :, :-2, :-2]
        + padded[:, :, :-2, 2:]
        + padded[:, :, 2:, :-2]
        + padded[:, :, 2:, 2:]
    )
    laplace = (4.0 * edge_sum + corner_sum - 20.0 * centre) / 6.0
    real_part = centre[:, 0]
    imag_part = centre[:, 1]
    mass_term = jnp.stack(
        [real_part - signs * DAMPING * imag_part, imag_part + signs * DAMPING * real_part], axis=1
    )
    return -laplace - wave_cells * mass_term


def combine_parts(products, signs, shape):
    real_out = products[0][:, 0] - signs[..., None] * products[1][:, 1]
    imag_out = products[0][:, 1] + signs[..., None] * products[1][:, 0]
    return jnp.stack([real_out, imag_out], axis=1).reshape(shape)


def along_rows(values, inverse, signs):
    block = inverse.shape[-1]
    blocked = values.reshape(values.shape[0], 2, values.shape[2], values.shape[3] // block, block)
    products = jnp.einsum("qmok,fchqk->mfchqo", inverse, blocked, precision=lax.Precision.HIGHEST)
    return combine_parts(products, signs, values.shape)


def along_cols(values, inverse, signs):
    block = inverse.shape[-1]
    blocked = values.reshape(values.shape[0], 2, values.shape[2] // block, block, values.shape[3])
    products = jnp.einsum("qmok,fcqkw->mfcqow", inverse, blocked, precision=lax.Precision.HIGHEST)
    return combine_parts(products, signs, values.shape)


def solve_local(resid_ext, wave_ext, row_blocks, col_blocks, live_rect, signs):
    upper, lower, left, right = [to_index(v) for v in live_rect]
    height, breadth = (resid_ext.shape[2], resid_ext.shape[3])
    row_ids = lax.broadcasted_iota(jnp.int32, (height, 1), 0)
    col_ids = lax.broadcasted_iota(jnp.int32, (1, breadth), 1)
    live_mask = (
        (row_ids >= upper) & (row_ids < lower) & (col_ids >= left) & (col_ids < right)
    ).astype(resid_ext.dtype)
    local_res = resid_ext * live_mask
    correction = jnp.zeros_like(resid_ext)
    for sweep_index in range(SWEEPS):
        if sweep_index > 0:
            padded = jnp.pad(correction, ((0, 0), (0, 0), (1, 1), (1, 1)))
            padded = fill_ghost(padded, upper + 1, lower + 1, left + 1, right + 1, signs)
            local_res = live_mask * (resid_ext - apply_operator(padded, wave_ext, signs))
        if sweep_index % 2 == 0:
            update = along_rows(local_res, row_blocks, signs)
        else:
            update = along_cols(local_res, col_blocks, signs)
        correction = correction + live_mask * update
    return correction


def exchange(x, row_width, col_width, extra=None):
    row_count = lax.axis_size("gx")
    col_count = lax.axis_size("gy")
    height, breadth = (x.shape[-2], x.shape[-1])
    pieces = {}
    for dr in (-1, 0, 1):
        for dc in (-1, 0, 1):
            if dr == 0 and dc == 0:
                continue
            slab = x
            if dr == -1:
                slab = lax.slice_in_dim(slab, height - row_width, height, axis=x.ndim - 2)
            elif dr == 1:
                slab = lax.slice_in_dim(slab, 0, row_width, axis=x.ndim - 2)
            if dc == -1:
                slab = lax.slice_in_dim(slab, breadth - col_width, breadth, axis=x.ndim - 1)
            elif dc == 1:
                slab = lax.slice_in_dim(slab, 0, col_width, axis=x.ndim - 1)
            if extra is not None and (dr, dc) in extra:
                slab = jnp.concatenate([slab, extra[(dr, dc)]], axis=0)
            perm = []
            for r in range(row_count):
                for c in range(col_count):
                    rr, cc = (r - dr, c - dc)
                    if 0 <= rr < row_count and 0 <= cc < col_count:
                        perm.append((r * col_count + c, rr * col_count + cc))
            pieces[(dr, dc)] = lax.ppermute(slab, ("gx", "gy"), perm)
    return pieces


def exchange_axis(x, axis, dim, width, extra_lo=None, extra_hi=None):
    peers, length = (lax.axis_size(axis), x.shape[dim])
    up = [(i, i + 1) for i in range(peers - 1)]
    down = [(j, i) for i, j in up]
    last = lax.slice_in_dim(x, length - width, length, axis=dim)
    first = lax.slice_in_dim(x, 0, width, axis=dim)
    if extra_lo is not None:
        last = jnp.concatenate([last, extra_lo], axis=0)
        first = jnp.concatenate([first, extra_hi], axis=0)
    return lax.ppermute(last, axis, up), lax.ppermute(first, axis, down)


def assemble(pieces, centre, lead):
    rows = []
    for dr in (-1, 0, 1):
        row = []
        for dc in (-1, 0, 1):
            part = centre if (dr == 0 and dc == 0) else pieces[(dr, dc)][:lead]
            row.append(part)
        rows.append(jnp.concatenate(row, axis=-1))
    return jnp.concatenate(rows, axis=-2)


def grid_residual(fields_ref, data_ref, res_ref):
    height, breadth = (res_ref.shape[1], res_ref.shape[2])

    def ahead(x, step, axis):
        return pltpu.roll(x, x.shape[axis] - step, axis)

    for problem in range(res_ref.shape[0] // 2):
        sign = 1.0 - 2.0 * problem
        totals, centres = ([], [])
        for part in range(2):
            padded = fields_ref[2 * problem + part]
            outer = padded + ahead(padded, 2, 0)
            middle = ahead(padded, 1, 0)
            edge = ahead(outer, 1, 1) + middle + ahead(middle, 2, 1)
            corner = outer + ahead(outer, 2, 1)
            totals.append((4.0 * edge + corner)[:height, :breadth])
            centres.append(ahead(middle, 1, 1)[:height, :breadth])
        real_part, imag_part = centres
        wave = data_ref[4]
        lap_r = (totals[0] - 20.0 * real_part) / 6.0
        lap_i = (totals[1] - 20.0 * imag_part) / 6.0
        mass_r = real_part - sign * DAMPING * imag_part
        mass_i = imag_part + sign * DAMPING * real_part
        res_ref[2 * problem] = data_ref[2 * problem] - (-lap_r - wave * mass_r)
        res_ref[2 * problem + 1] = data_ref[2 * problem + 1] - (-lap_i - wave * mass_i)


def solve_kernel(rect_ref, resid_ref, data_ref, wrow_ref, wcol_ref, *refs, has_base, last, own_rows, own_cols, slab,
                 from_fields):
    if from_fields:
        grid_residual(resid_ref, data_ref, refs[-1])
        resid_ref = refs[-1]
        refs = refs[:-1]
    base_ref = refs[0] if has_base else None
    outs = refs[1:] if has_base else refs
    own_ref = outs[0]
    top_ref, bottom_ref = (None, None) if last else outs[1:3]
    height, breadth = (resid_ref.shape[1], resid_ref.shape[2])
    half = height // 2
    upper, lower, left, right = (rect_ref[0], rect_ref[1], rect_ref[2], rect_ref[3])
    row_ids = lax.broadcasted_iota(jnp.int32, (height, breadth), 0)
    col_ids = lax.broadcasted_iota(jnp.int32, (height, breadth), 1)
    live = (row_ids >= upper) & (row_ids < lower) & (col_ids >= left) & (col_ids < right)
    top, bottom = (row_ids == upper, row_ids == lower - 1)
    first, last = (col_ids == left, col_ids == right - 1)
    row_flag = top.astype(jnp.float32) + bottom.astype(jnp.float32)
    col_flag = first.astype(jnp.float32) + last.astype(jnp.float32)
    edge_flag = 4.0 * (row_flag + col_flag)
    zero = jnp.zeros((height, breadth), jnp.float32)

    def mask(x):
        return jnp.where(live, x, zero)

    def rows_sum(x):
        up = jnp.where(top, x, pltpu.roll(x, 1, 0))
        down = jnp.where(bottom, x, pltpu.roll(x, height - 1, 0))
        return up + down

    def cols_sum(x):
        lft = jnp.where(first, x, pltpu.roll(x, 1, 1))
        rgt = jnp.where(last, x, pltpu.roll(x, breadth - 1, 1))
        return lft + rgt

    def stencil(x):
        vertical = rows_sum(x)
        ghost_rows = row_flag * x
        total = 4.0 * (vertical + cols_sum(x)) + cols_sum(vertical)
        ghost = edge_flag * x + cols_sum(ghost_rows) + col_flag * (vertical - ghost_rows)
        return total, ghost

    def operator(real_part, imag_part, sign):
        wave = data_ref[4]
        total_r, ghost_r = stencil(real_part)
        total_i, ghost_i = stencil(imag_part)
        lap_r = (total_r + sign * ROBIN_COEF * ghost_i - 20.0 * real_part) / 6.0
        lap_i = (total_i - sign * ROBIN_COEF * ghost_r - 20.0 * imag_part) / 6.0
        mass_r = real_part - sign * DAMPING * imag_part
        mass_i = imag_part + sign * DAMPING * real_part
        return (-lap_r - wave * mass_r, -lap_i - wave * mass_i)

    def dot(a, b):
        return jnp.dot(a, b, precision=lax.Precision.HIGH, preferred_element_type=jnp.float32)

    def rows_apply(real_part, imag_part, sign):
        outs_r, outs_i = ([], [])
        for h in range(breadth // half):
            cols = slice(h * half, (h + 1) * half)
            prod_r = dot(real_part[:, cols], wrow_ref[h])
            prod_i = dot(imag_part[:, cols], wrow_ref[h])
            outs_r.append(prod_r[:, :half] - sign * prod_i[:, half:])
            outs_i.append(prod_i[:, :half] + sign * prod_r[:, half:])
        return (jnp.concatenate(outs_r, axis=1), jnp.concatenate(outs_i, axis=1))

    def cols_apply(real_part, imag_part, sign):
        outs_r, outs_i = ([], [])
        for h in range(height // half):
            rows = slice(h * half, (h + 1) * half)
            prod_r = dot(wcol_ref[h], real_part[rows, :])
            prod_i = dot(wcol_ref[h], imag_part[rows, :])
            outs_r.append(prod_r[:half] - sign * prod_i[half:])
            outs_i.append(prod_i[:half] + sign * prod_r[half:])
        return (jnp.concatenate(outs_r, axis=0), jnp.concatenate(outs_i, axis=0))

    def problem_body(problem, carry):
        sign = 1.0 - 2.0 * problem.astype(jnp.float32)
        up_r, up_i = rows_apply(mask(resid_ref[2 * problem]), mask(resid_ref[2 * problem + 1]), sign)
        cor_r, cor_i = (mask(up_r), mask(up_i))
        for step in range(SWEEPS - 1):
            op_r, op_i = operator(cor_r, cor_i, sign)
            loc_r, loc_i = (mask(resid_ref[2 * problem] - op_r), mask(resid_ref[2 * problem + 1] - op_i))
            apply = cols_apply if step % 2 == 0 else rows_apply
            up_r, up_i = apply(loc_r, loc_i, sign)
            cor_r, cor_i = (cor_r + mask(up_r), cor_i + mask(up_i))
        first_row = (height - own_rows) // 2
        for part, value in ((0, cor_r), (1, cor_i)):
            own = pltpu.roll(value, breadth - (breadth - own_cols) // 2, 1)[first_row : first_row + own_rows, :own_cols]
            if base_ref is not None:
                own = own + base_ref[problem, part]
            own_ref[problem, part] = own
            if top_ref is not None:
                top_ref[problem, part] = own[:slab]
                bottom_ref[problem, part] = own[own_rows - slab :]
        return carry

    lax.fori_loop(0, resid_ref.shape[0] // 2, problem_body, 0)


def line_matrices(row_blocks, col_blocks):
    block = row_blocks.shape[-1]
    eye = jnp.eye(2, dtype=row_blocks.dtype)
    halves = row_blocks.shape[0] // 2
    rows_t = jnp.transpose(row_blocks, (0, 3, 1, 2)).reshape(halves, 2, block, 2, block)
    row_mats = jnp.einsum("hakmo,ab->hakmbo", rows_t, eye).reshape(halves, 2 * block, 4 * block)
    cols = col_blocks.reshape(halves, 2, 2, block, block)
    col_mats = jnp.einsum("hamok,ab->hmaobk", cols, eye).reshape(halves, 4 * block, 2 * block)
    return row_mats, col_mats


def solve_local_kernel(resid_planes, data_ext, row_mats, col_mats, live_rect, own_shape, slab, base=None, last=False,
                       from_fields=False, interpret=False):
    extra = [] if base is None else [base]
    rect = jnp.stack([to_index(v) for v in live_rect])
    dtype = resid_planes.dtype
    ext_shape = data_ext.shape[1:]
    shapes = [(2, 2) + own_shape]
    if not last:
        shapes += [(2, 2, slab, own_shape[1])] * 2
    vmem = pltpu.MemorySpace.VMEM if hasattr(pltpu, "MemorySpace") else pltpu.VMEM
    kernel = functools.partial(
        solve_kernel, has_base=base is not None, last=last, own_rows=own_shape[0], own_cols=own_shape[1], slab=slab,
        from_fields=from_fields,
    )
    scratch = [pltpu.VMEM((4,) + ext_shape, jnp.float32)] if from_fields else []
    return pl.pallas_call(
        kernel,
        out_shape=[jax.ShapeDtypeStruct(s, dtype) for s in shapes],
        in_specs=[pl.BlockSpec(memory_space=pltpu.SMEM)] + [pl.BlockSpec(memory_space=vmem)] * (4 + len(extra)),
        out_specs=[pl.BlockSpec(memory_space=vmem)] * len(shapes),
        scratch_shapes=scratch,
        interpret=interpret,
    )(rect, resid_planes, data_ext, row_mats, col_mats, *extra)


def shards(sources, wavenumber, row_inverse, col_inverse, reach_steps):
    own_rows, own_cols = (sources.shape[2], sources.shape[3])
    block = row_inverse.shape[-1]
    step_cells = block // 4
    signs = jnp.array([1.0, -1.0], dtype=sources.dtype).reshape(2, 1, 1)
    row_rank = to_index(lax.axis_index("gx"))
    col_rank = to_index(lax.axis_index("gy"))
    row_count = lax.axis_size("gx")
    col_count = lax.axis_size("gy")
    zero = to_index(0)
    widths = reach_steps.reshape(4) * step_cells
    upper_w = jnp.where(row_rank > 0, widths[0], zero)
    lower_w = jnp.where(row_rank < row_count - 1, widths[1], zero)
    left_w = jnp.where(col_rank > 0, widths[2], zero)
    right_w = jnp.where(col_rank < col_count - 1, widths[3], zero)
    live_rect = (
        block - upper_w,
        block + own_rows + lower_w,
        block - left_w,
        block + own_cols + right_w,
    )
    stacked = jnp.concatenate([sources.reshape(4, own_rows, own_cols), wavenumber[None]], axis=0)
    lead = stacked.shape[0]
    col_pair = col_inverse.shape[0]
    row_pair = row_inverse.shape[0]
    inv_rows = col_inverse.shape[1] * block * block // own_cols
    before, after = exchange_axis(
        stacked, "gx", 1, block,
        col_inverse[col_pair - 1].reshape(1, inv_rows, own_cols), col_inverse[0].reshape(1, inv_rows, own_cols),
    )
    tall = jnp.concatenate([before[:lead, :block], stacked, after[:lead, :block]], axis=1)
    def inv_slab(mats):
        flat = mats.reshape(1, -1, block)
        return jnp.pad(flat, ((0, 0), (0, tall.shape[1] - flat.shape[1]), (0, 0)))
    left, right = exchange_axis(tall, "gy", 2, block, inv_slab(row_inverse[row_pair - 1]), inv_slab(row_inverse[0]))
    stacked_ext = jnp.concatenate([left[:lead], tall, right[:lead]], axis=2)
    sources_ext = stacked_ext[:4].reshape(2, 2, own_rows + 2 * block, own_cols + 2 * block)
    wave_ext = stacked_ext[4]
    inv_shape = (1,) + row_inverse.shape[1:]
    inv_size = row_inverse.shape[1] * block * block // block
    col_blocks = jnp.concatenate(
        [before[lead:].reshape(inv_shape), col_inverse, after[lead:].reshape(inv_shape)], axis=0
    )
    row_blocks = jnp.concatenate(
        [left[lead:, :inv_size].reshape(inv_shape), row_inverse, right[lead:, :inv_size].reshape(inv_shape)], axis=0
    )
    row_mats, col_mats = line_matrices(row_blocks, col_blocks)
    width = block + 1
    edges = (row_rank == 0, row_rank == row_count - 1, col_rank == 0, col_rank == col_count - 1)
    slab = -(-width // 8) * 8
    solution = None
    base = None
    for iteration in range(ITERS):
        last = iteration == ITERS - 1
        if iteration == 0:
            resid_planes = stacked_ext
        else:
            peers = lax.axis_size("gx")
            up = [(i, i + 1) for i in range(peers - 1)]
            down = [(j, i) for i, j in up]
            before = lax.ppermute(bottom, "gx", up)[:, :, slab - width :]
            after = lax.ppermute(top, "gx", down)[:, :, :width]
            tall = jnp.concatenate([before, solution, after], axis=2)
            left, right = exchange_axis(tall, "gy", 3, width)
            padded = jnp.concatenate([left, tall, right], axis=3)
            padded = grid_ghost(padded, width, edges, signs)
            tile_rows = -(-padded.shape[2] // 8) * 8 - padded.shape[2]
            tile_cols = -(-padded.shape[3] // 128) * 128 - padded.shape[3]
            padded = jnp.pad(padded, ((0, 0), (0, 0), (0, tile_rows), (0, tile_cols)))
            resid_planes = padded.reshape((4,) + padded.shape[2:])
        outs = solve_local_kernel(
            resid_planes, stacked_ext, row_mats, col_mats, live_rect, (own_rows, own_cols), slab, base=base, last=last,
            from_fields=iteration > 0,
        )
        solution = outs[0]
        if not last:
            solution, top, bottom = outs
        base = solution
    return solution


def solution(mesh):
    return jax.shard_map(
        shards,
        mesh=mesh,
        in_specs=(
            P(None, None, "gx", "gy"),
            P("gx", "gy"),
            P("gy", None, None, None),
            P("gx", None, None, None),
            P("gx", "gy", None),
        ),
        out_specs=P(None, None, "gx", "gy"),
        check_vma=False,
    )
```

```python
import functools

import jax
import jax.numpy as jnp
from jax import lax
from jax.sharding import PartitionSpec as P
from jax.experimental import pallas as pl
from jax.experimental.pallas import tpu as pltpu

ITERS = 2
SWEEPS = 4


DAMPING = 0.5
ROBIN_COEF = 0.5


def with_halo(shard, sides, width):
    for axis, dim in sides:
        peers, length = (lax.axis_size(axis), shard.shape[dim])
        up = [(i, (i + 1) % peers) for i in range(peers - 1)]
        down = [(j, i) for i, j in up]
        last = lax.slice_in_dim(shard, length - width, length, axis=dim)
        first = lax.slice_in_dim(shard, 0, width, axis=dim)
        before = lax.ppermute(last, axis, up)
        after = lax.ppermute(first, axis, down)
        shard = jnp.concatenate([before, shard, after], axis=dim)
    return shard


def to_index(value):
    return jnp.asarray(value).astype(jnp.int32)


def slice_line(values, start, axis):
    starts = [to_index(0) for _ in range(values.ndim)]
    starts[axis] = to_index(start)
    sizes = list(values.shape)
    sizes[axis] = 1
    return lax.dynamic_slice(values, starts, sizes)


def fill_ghost(values, upper, lower, left, right, signs):
    upper, lower, left, right = (to_index(upper), to_index(lower), to_index(left), to_index(right))
    height, breadth = (values.shape[2], values.shape[3])
    row_ids = lax.broadcasted_iota(jnp.int32, (height, 1), 0)
    col_ids = lax.broadcasted_iota(jnp.int32, (1, breadth), 1)
    upper_row = slice_line(values, upper, 2)
    lower_row = slice_line(values, lower - 1, 2)
    values = jnp.where(row_ids < upper, upper_row, jnp.where(row_ids >= lower, lower_row, values))
    left_col = slice_line(values, left, 3)
    right_col = slice_line(values, right - 1, 3)
    values = jnp.where(col_ids < left, left_col, jnp.where(col_ids >= right, right_col, values))
    inside = (row_ids >= upper) & (row_ids < lower) & (col_ids >= left) & (col_ids < right)
    real_part = values[:, 0]
    imag_part = values[:, 1]
    ghost_cycle = jnp.stack(
        [real_part + signs * ROBIN_COEF * imag_part, imag_part - signs * ROBIN_COEF * real_part],
        axis=1,
    )
    return jnp.where(inside, values, ghost_cycle)


def grid_ghost(values, width, edges, signs):
    at_top, at_bottom, at_left, at_right = edges
    height, breadth = (values.shape[2], values.shape[3])
    row_ids = lax.broadcasted_iota(jnp.int32, (height, 1), 0)
    col_ids = lax.broadcasted_iota(jnp.int32, (1, breadth), 1)
    above = at_top & (row_ids < width)
    below = at_bottom & (row_ids >= height - width)
    values = jnp.where(
        above, values[:, :, width : width + 1], jnp.where(below, values[:, :, height - width - 1 : height - width], values)
    )
    before = at_left & (col_ids < width)
    after = at_right & (col_ids >= breadth - width)
    values = jnp.where(
        before, values[:, :, :, width : width + 1],
        jnp.where(after, values[:, :, :, breadth - width - 1 : breadth - width], values),
    )
    outside = above | below | before | after
    real_part = values[:, 0]
    imag_part = values[:, 1]
    ghost_cycle = jnp.stack(
        [real_part + signs * ROBIN_COEF * imag_part, imag_part - signs * ROBIN_COEF * real_part],
        axis=1,
    )
    return jnp.where(outside, ghost_cycle, values)


def apply_operator(padded, wave_cells, signs):
    centre = padded[:, :, 1:-1, 1:-1]
    edge_sum = (
        padded[:, :, :-2, 1:-1]
        + padded[:, :, 2:, 1:-1]
        + padded[:, :, 1:-1, :-2]
        + padded[:, :, 1:-1, 2:]
    )
    corner_sum = (
        padded[:, :, :-2, :-2]
        + padded[:, :, :-2, 2:]
        + padded[:, :, 2:, :-2]
        + padded[:, :, 2:, 2:]
    )
    laplace = (4.0 * edge_sum + corner_sum - 20.0 * centre) / 6.0
    real_part = centre[:, 0]
    imag_part = centre[:, 1]
    mass_term = jnp.stack(
        [real_part - signs * DAMPING * imag_part, imag_part + signs * DAMPING * real_part], axis=1
    )
    return -laplace - wave_cells * mass_term


def combine_parts(products, signs, shape):
    real_out = products[0][:, 0] - signs[..., None] * products[1][:, 1]
    imag_out = products[0][:, 1] + signs[..., None] * products[1][:, 0]
    return jnp.stack([real_out, imag_out], axis=1).reshape(shape)


def along_rows(values, inverse, signs):
    block = inverse.shape[-1]
    blocked = values.reshape(values.shape[0], 2, values.shape[2], values.shape[3] // block, block)
    products = jnp.einsum("qmok,fchqk->mfchqo", inverse, blocked, precision=lax.Precision.HIGHEST)
    return combine_parts(products, signs, values.shape)


def along_cols(values, inverse, signs):
    block = inverse.shape[-1]
    blocked = values.reshape(values.shape[0], 2, values.shape[2] // block, block, values.shape[3])
    products = jnp.einsum("qmok,fcqkw->mfcqow", inverse, blocked, precision=lax.Precision.HIGHEST)
    return combine_parts(products, signs, values.shape)


def solve_local(resid_ext, wave_ext, row_blocks, col_blocks, live_rect, signs):
    upper, lower, left, right = [to_index(v) for v in live_rect]
    height, breadth = (resid_ext.shape[2], resid_ext.shape[3])
    row_ids = lax.broadcasted_iota(jnp.int32, (height, 1), 0)
    col_ids = lax.broadcasted_iota(jnp.int32, (1, breadth), 1)
    live_mask = (
        (row_ids >= upper) & (row_ids < lower) & (col_ids >= left) & (col_ids < right)
    ).astype(resid_ext.dtype)
    local_res = resid_ext * live_mask
    correction = jnp.zeros_like(resid_ext)
    for sweep_index in range(SWEEPS):
        if sweep_index > 0:
            padded = jnp.pad(correction, ((0, 0), (0, 0), (1, 1), (1, 1)))
            padded = fill_ghost(padded, upper + 1, lower + 1, left + 1, right + 1, signs)
            local_res = live_mask * (resid_ext - apply_operator(padded, wave_ext, signs))
        if sweep_index % 2 == 0:
            update = along_rows(local_res, row_blocks, signs)
        else:
            update = along_cols(local_res, col_blocks, signs)
        correction = correction + live_mask * update
    return correction


def exchange(x, row_width, col_width, extra=None):
    row_count = lax.axis_size("gx")
    col_count = lax.axis_size("gy")
    height, breadth = (x.shape[-2], x.shape[-1])
    pieces = {}
    for dr in (-1, 0, 1):
        for dc in (-1, 0, 1):
            if dr == 0 and dc == 0:
                continue
            slab = x
            if dr == -1:
                slab = lax.slice_in_dim(slab, height - row_width, height, axis=x.ndim - 2)
            elif dr == 1:
                slab = lax.slice_in_dim(slab, 0, row_width, axis=x.ndim - 2)
            if dc == -1:
                slab = lax.slice_in_dim(slab, breadth - col_width, breadth, axis=x.ndim - 1)
            elif dc == 1:
                slab = lax.slice_in_dim(slab, 0, col_width, axis=x.ndim - 1)
            if extra is not None and (dr, dc) in extra:
                slab = jnp.concatenate([slab, extra[(dr, dc)]], axis=0)
            perm = []
            for r in range(row_count):
                for c in range(col_count):
                    rr, cc = (r - dr, c - dc)
                    if 0 <= rr < row_count and 0 <= cc < col_count:
                        perm.append((r * col_count + c, rr * col_count + cc))
            pieces[(dr, dc)] = lax.ppermute(slab, ("gx", "gy"), perm)
    return pieces


def exchange_axis(x, axis, dim, width, extra_lo=None, extra_hi=None):
    peers, length = (lax.axis_size(axis), x.shape[dim])
    up = [(i, i + 1) for i in range(peers - 1)]
    down = [(j, i) for i, j in up]
    last = lax.slice_in_dim(x, length - width, length, axis=dim)
    first = lax.slice_in_dim(x, 0, width, axis=dim)
    if extra_lo is not None:
        last = jnp.concatenate([last, extra_lo], axis=0)
        first = jnp.concatenate([first, extra_hi], axis=0)
    return lax.ppermute(last, axis, up), lax.ppermute(first, axis, down)


def assemble(pieces, centre, lead):
    rows = []
    for dr in (-1, 0, 1):
        row = []
        for dc in (-1, 0, 1):
            part = centre if (dr == 0 and dc == 0) else pieces[(dr, dc)][:lead]
            row.append(part)
        rows.append(jnp.concatenate(row, axis=-1))
    return jnp.concatenate(rows, axis=-2)


def grid_residual(fields_ref, data_ref, res_ref):
    height, breadth = (res_ref.shape[1], res_ref.shape[2])

    def ahead(x, step, axis):
        return pltpu.roll(x, x.shape[axis] - step, axis)

    for problem in range(res_ref.shape[0] // 2):
        sign = 1.0 - 2.0 * problem
        totals, centres = ([], [])
        for part in range(2):
            padded = fields_ref[2 * problem + part]
            outer = padded + ahead(padded, 2, 0)
            middle = ahead(padded, 1, 0)
            edge = ahead(outer, 1, 1) + middle + ahead(middle, 2, 1)
            corner = outer + ahead(outer, 2, 1)
            totals.append((4.0 * edge + corner)[:height, :breadth])
            centres.append(ahead(middle, 1, 1)[:height, :breadth])
        real_part, imag_part = centres
        wave = data_ref[4]
        lap_r = (totals[0] - 20.0 * real_part) / 6.0
        lap_i = (totals[1] - 20.0 * imag_part) / 6.0
        mass_r = real_part - sign * DAMPING * imag_part
        mass_i = imag_part + sign * DAMPING * real_part
        res_ref[2 * problem] = data_ref[2 * problem] - (-lap_r - wave * mass_r)
        res_ref[2 * problem + 1] = data_ref[2 * problem + 1] - (-lap_i - wave * mass_i)


def solve_kernel(rect_ref, resid_ref, data_ref, wrow_ref, wcol_ref, *refs, has_base, last, own_rows, own_cols, slab,
                 from_fields):
    if from_fields:
        grid_residual(resid_ref, data_ref, refs[-1])
        resid_ref = refs[-1]
        refs = refs[:-1]
    base_ref = refs[0] if has_base else None
    outs = refs[1:] if has_base else refs
    own_ref = outs[0]
    top_ref, bottom_ref = (None, None) if last else outs[1:3]
    height, breadth = (resid_ref.shape[1], resid_ref.shape[2])
    half = height // 2
    upper, lower, left, right = (rect_ref[0], rect_ref[1], rect_ref[2], rect_ref[3])
    row_ids = lax.broadcasted_iota(jnp.int32, (height, breadth), 0)
    col_ids = lax.broadcasted_iota(jnp.int32, (height, breadth), 1)
    live = (row_ids >= upper) & (row_ids < lower) & (col_ids >= left) & (col_ids < right)
    top, bottom = (row_ids == upper, row_ids == lower - 1)
    first, last = (col_ids == left, col_ids == right - 1)
    row_flag = top.astype(jnp.float32) + bottom.astype(jnp.float32)
    col_flag = first.astype(jnp.float32) + last.astype(jnp.float32)
    edge_flag = 4.0 * (row_flag + col_flag)
    zero = jnp.zeros((height, breadth), jnp.float32)

    def mask(x):
        return jnp.where(live, x, zero)

    def rows_sum(x):
        up = jnp.where(top, x, pltpu.roll(x, 1, 0))
        down = jnp.where(bottom, x, pltpu.roll(x, height - 1, 0))
        return up + down

    def cols_sum(x):
        lft = jnp.where(first, x, pltpu.roll(x, 1, 1))
        rgt = jnp.where(last, x, pltpu.roll(x, breadth - 1, 1))
        return lft + rgt

    def stencil(x):
        vertical = rows_sum(x)
        ghost_rows = row_flag * x
        total = 4.0 * (vertical + cols_sum(x)) + cols_sum(vertical)
        ghost = edge_flag * x + cols_sum(ghost_rows) + col_flag * (vertical - ghost_rows)
        return total, ghost

    def operator(real_part, imag_part, sign):
        wave = data_ref[4]
        total_r, ghost_r = stencil(real_part)
        total_i, ghost_i = stencil(imag_part)
        lap_r = (total_r + sign * ROBIN_COEF * ghost_i - 20.0 * real_part) / 6.0
        lap_i = (total_i - sign * ROBIN_COEF * ghost_r - 20.0 * imag_part) / 6.0
        mass_r = real_part - sign * DAMPING * imag_part
        mass_i = imag_part + sign * DAMPING * real_part
        return (-lap_r - wave * mass_r, -lap_i - wave * mass_i)

    def dot(a, b):
        return jnp.dot(a, b, precision=lax.Precision.HIGH, preferred_element_type=jnp.float32)

    def rows_apply(real_part, imag_part, sign):
        outs_r, outs_i = ([], [])
        for h in range(breadth // half):
            cols = slice(h * half, (h + 1) * half)
            prod_r = dot(real_part[:, cols], wrow_ref[h])
            prod_i = dot(imag_part[:, cols], wrow_ref[h])
            outs_r.append(prod_r[:, :half] - sign * prod_i[:, half:])
            outs_i.append(prod_i[:, :half] + sign * prod_r[:, half:])
        return (jnp.concatenate(outs_r, axis=1), jnp.concatenate(outs_i, axis=1))

    def cols_apply(real_part, imag_part, sign):
        outs_r, outs_i = ([], [])
        for h in range(height // half):
            rows = slice(h * half, (h + 1) * half)
            prod_r = dot(wcol_ref[h], real_part[rows, :])
            prod_i = dot(wcol_ref[h], imag_part[rows, :])
            outs_r.append(prod_r[:half] - sign * prod_i[half:])
            outs_i.append(prod_i[:half] + sign * prod_r[half:])
        return (jnp.concatenate(outs_r, axis=0), jnp.concatenate(outs_i, axis=0))

    def problem_body(problem, carry):
        sign = 1.0 - 2.0 * problem.astype(jnp.float32)
        up_r, up_i = rows_apply(mask(resid_ref[2 * problem]), mask(resid_ref[2 * problem + 1]), sign)
        cor_r, cor_i = (mask(up_r), mask(up_i))
        for step in range(SWEEPS - 1):
            op_r, op_i = operator(cor_r, cor_i, sign)
            loc_r, loc_i = (mask(resid_ref[2 * problem] - op_r), mask(resid_ref[2 * problem + 1] - op_i))
            apply = cols_apply if step % 2 == 0 else rows_apply
            up_r, up_i = apply(loc_r, loc_i, sign)
            cor_r, cor_i = (cor_r + mask(up_r), cor_i + mask(up_i))
        first_row = (height - own_rows) // 2
        for part, value in ((0, cor_r), (1, cor_i)):
            own = pltpu.roll(value, breadth - (breadth - own_cols) // 2, 1)[first_row : first_row + own_rows, :own_cols]
            if base_ref is not None:
                own = own + base_ref[problem, part]
            own_ref[problem, part] = own
            if top_ref is not None:
                top_ref[problem, part] = own[:slab]
                bottom_ref[problem, part] = own[own_rows - slab :]
        return carry

    lax.fori_loop(0, resid_ref.shape[0] // 2, problem_body, 0)


def line_matrices(row_blocks, col_blocks):
    block = row_blocks.shape[-1]
    eye = jnp.eye(2, dtype=row_blocks.dtype)
    halves = row_blocks.shape[0] // 2
    rows_t = jnp.transpose(row_blocks, (0, 3, 1, 2)).reshape(halves, 2, block, 2, block)
    row_mats = jnp.einsum("hakmo,ab->hakmbo", rows_t, eye).reshape(halves, 2 * block, 4 * block)
    cols = col_blocks.reshape(halves, 2, 2, block, block)
    col_mats = jnp.einsum("hamok,ab->hmaobk", cols, eye).reshape(halves, 4 * block, 2 * block)
    return row_mats, col_mats


def solve_local_kernel(resid_planes, data_ext, row_mats, col_mats, live_rect, own_shape, slab, base=None, last=False,
                       from_fields=False, interpret=False):
    extra = [] if base is None else [base]
    rect = jnp.stack([to_index(v) for v in live_rect])
    dtype = data_ext.dtype
    ext_shape = data_ext.shape[1:]
    shapes = [(2, 2) + own_shape]
    if not last:
        shapes += [(2, 2, slab, own_shape[1])] * 2
    vmem = pltpu.MemorySpace.VMEM if hasattr(pltpu, "MemorySpace") else pltpu.VMEM
    kernel = functools.partial(
        solve_kernel, has_base=base is not None, last=last, own_rows=own_shape[0], own_cols=own_shape[1], slab=slab,
        from_fields=from_fields,
    )
    scratch = [pltpu.VMEM((4,) + ext_shape, jnp.float32)] if from_fields else []
    operands = [data_ext, row_mats, col_mats] + extra
    if resid_planes is None:
        inner = kernel

        def kernel(rect_ref, data_ref, *refs):
            return inner(rect_ref, data_ref, data_ref, *refs)
    else:
        operands = [resid_planes] + operands
    return pl.pallas_call(
        kernel,
        out_shape=[jax.ShapeDtypeStruct(s, dtype) for s in shapes],
        in_specs=[pl.BlockSpec(memory_space=pltpu.SMEM)] + [pl.BlockSpec(memory_space=vmem)] * len(operands),
        out_specs=[pl.BlockSpec(memory_space=vmem)] * len(shapes),
        scratch_shapes=scratch,
        interpret=interpret,
    )(rect, *operands)


def shards(sources, wavenumber, row_inverse, col_inverse, reach_steps):
    own_rows, own_cols = (sources.shape[2], sources.shape[3])
    block = row_inverse.shape[-1]
    step_cells = block // 4
    signs = jnp.array([1.0, -1.0], dtype=sources.dtype).reshape(2, 1, 1)
    row_rank = to_index(lax.axis_index("gx"))
    col_rank = to_index(lax.axis_index("gy"))
    row_count = lax.axis_size("gx")
    col_count = lax.axis_size("gy")
    zero = to_index(0)
    widths = reach_steps.reshape(4) * step_cells
    upper_w = jnp.where(row_rank > 0, widths[0], zero)
    lower_w = jnp.where(row_rank < row_count - 1, widths[1], zero)
    left_w = jnp.where(col_rank > 0, widths[2], zero)
    right_w = jnp.where(col_rank < col_count - 1, widths[3], zero)
    live_rect = (
        block - upper_w,
        block + own_rows + lower_w,
        block - left_w,
        block + own_cols + right_w,
    )
    stacked = jnp.concatenate([sources.reshape(4, own_rows, own_cols), wavenumber[None]], axis=0)
    lead = stacked.shape[0]
    col_pair = col_inverse.shape[0]
    row_pair = row_inverse.shape[0]
    inv_rows = col_inverse.shape[1] * block * block // own_cols
    before, after = exchange_axis(
        stacked, "gx", 1, block,
        col_inverse[col_pair - 1].reshape(1, inv_rows, own_cols), col_inverse[0].reshape(1, inv_rows, own_cols),
    )
    tall = jnp.concatenate([before[:lead, :block], stacked, after[:lead, :block]], axis=1)
    def inv_slab(mats):
        flat = mats.reshape(1, -1, block)
        return jnp.pad(flat, ((0, 0), (0, tall.shape[1] - flat.shape[1]), (0, 0)))
    left, right = exchange_axis(tall, "gy", 2, block, inv_slab(row_inverse[row_pair - 1]), inv_slab(row_inverse[0]))
    stacked_ext = jnp.concatenate([left[:lead], tall, right[:lead]], axis=2)
    sources_ext = stacked_ext[:4].reshape(2, 2, own_rows + 2 * block, own_cols + 2 * block)
    wave_ext = stacked_ext[4]
    inv_shape = (1,) + row_inverse.shape[1:]
    inv_size = row_inverse.shape[1] * block * block // block
    col_blocks = jnp.concatenate(
        [before[lead:].reshape(inv_shape), col_inverse, after[lead:].reshape(inv_shape)], axis=0
    )
    row_blocks = jnp.concatenate(
        [left[lead:, :inv_size].reshape(inv_shape), row_inverse, right[lead:, :inv_size].reshape(inv_shape)], axis=0
    )
    row_mats, col_mats = line_matrices(row_blocks, col_blocks)
    width = block + 1
    edges = (row_rank == 0, row_rank == row_count - 1, col_rank == 0, col_rank == col_count - 1)
    slab = -(-width // 8) * 8
    solution = None
    base = None
    for iteration in range(ITERS):
        last = iteration == ITERS - 1
        if iteration == 0:
            resid_planes = None
        else:
            peers = lax.axis_size("gx")
            up = [(i, i + 1) for i in range(peers - 1)]
            down = [(j, i) for i, j in up]
            before = lax.ppermute(bottom, "gx", up)[:, :, slab - width :]
            after = lax.ppermute(top, "gx", down)[:, :, :width]
            tall = jnp.concatenate([before, solution, after], axis=2)
            left, right = exchange_axis(tall, "gy", 3, width)
            padded = jnp.concatenate([left, tall, right], axis=3)
            padded = grid_ghost(padded, width, edges, signs)
            tile_rows = -(-padded.shape[2] // 8) * 8 - padded.shape[2]
            tile_cols = -(-padded.shape[3] // 128) * 128 - padded.shape[3]
            padded = jnp.pad(padded, ((0, 0), (0, 0), (0, tile_rows), (0, tile_cols)))
            resid_planes = padded.reshape((4,) + padded.shape[2:])
        outs = solve_local_kernel(
            resid_planes, stacked_ext, row_mats, col_mats, live_rect, (own_rows, own_cols), slab, base=base, last=last,
            from_fields=iteration > 0,
        )
        solution = outs[0]
        if not last:
            solution, top, bottom = outs
        base = solution
    return solution


def solution(mesh):
    return jax.shard_map(
        shards,
        mesh=mesh,
        in_specs=(
            P(None, None, "gx", "gy"),
            P("gx", "gy"),
            P("gy", None, None, None),
            P("gx", None, None, None),
            P("gx", "gy", None),
        ),
        out_specs=P(None, None, "gx", "gy"),
        check_vma=False,
    )
```

```python
import functools

import jax
import jax.numpy as jnp
from jax import lax
from jax.sharding import PartitionSpec as P
from jax.experimental import pallas as pl
from jax.experimental.pallas import tpu as pltpu

ITERS = 2
SWEEPS = 4


DAMPING = 0.5
ROBIN_COEF = 0.5


def with_halo(shard, sides, width):
    for axis, dim in sides:
        peers, length = (lax.axis_size(axis), shard.shape[dim])
        up = [(i, (i + 1) % peers) for i in range(peers - 1)]
        down = [(j, i) for i, j in up]
        last = lax.slice_in_dim(shard, length - width, length, axis=dim)
        first = lax.slice_in_dim(shard, 0, width, axis=dim)
        before = lax.ppermute(last, axis, up)
        after = lax.ppermute(first, axis, down)
        shard = jnp.concatenate([before, shard, after], axis=dim)
    return shard


def to_index(value):
    return jnp.asarray(value).astype(jnp.int32)


def slice_line(values, start, axis):
    starts = [to_index(0) for _ in range(values.ndim)]
    starts[axis] = to_index(start)
    sizes = list(values.shape)
    sizes[axis] = 1
    return lax.dynamic_slice(values, starts, sizes)


def fill_ghost(values, upper, lower, left, right, signs):
    upper, lower, left, right = (to_index(upper), to_index(lower), to_index(left), to_index(right))
    height, breadth = (values.shape[2], values.shape[3])
    row_ids = lax.broadcasted_iota(jnp.int32, (height, 1), 0)
    col_ids = lax.broadcasted_iota(jnp.int32, (1, breadth), 1)
    upper_row = slice_line(values, upper, 2)
    lower_row = slice_line(values, lower - 1, 2)
    values = jnp.where(row_ids < upper, upper_row, jnp.where(row_ids >= lower, lower_row, values))
    left_col = slice_line(values, left, 3)
    right_col = slice_line(values, right - 1, 3)
    values = jnp.where(col_ids < left, left_col, jnp.where(col_ids >= right, right_col, values))
    inside = (row_ids >= upper) & (row_ids < lower) & (col_ids >= left) & (col_ids < right)
    real_part = values[:, 0]
    imag_part = values[:, 1]
    ghost_cycle = jnp.stack(
        [real_part + signs * ROBIN_COEF * imag_part, imag_part - signs * ROBIN_COEF * real_part],
        axis=1,
    )
    return jnp.where(inside, values, ghost_cycle)


def grid_ghost(values, width, edges, signs):
    at_top, at_bottom, at_left, at_right = edges
    height, breadth = (values.shape[2], values.shape[3])
    row_ids = lax.broadcasted_iota(jnp.int32, (height, 1), 0)
    col_ids = lax.broadcasted_iota(jnp.int32, (1, breadth), 1)
    above = at_top & (row_ids < width)
    below = at_bottom & (row_ids >= height - width)
    values = jnp.where(
        above, values[:, :, width : width + 1], jnp.where(below, values[:, :, height - width - 1 : height - width], values)
    )
    before = at_left & (col_ids < width)
    after = at_right & (col_ids >= breadth - width)
    values = jnp.where(
        before, values[:, :, :, width : width + 1],
        jnp.where(after, values[:, :, :, breadth - width - 1 : breadth - width], values),
    )
    outside = above | below | before | after
    real_part = values[:, 0]
    imag_part = values[:, 1]
    ghost_cycle = jnp.stack(
        [real_part + signs * ROBIN_COEF * imag_part, imag_part - signs * ROBIN_COEF * real_part],
        axis=1,
    )
    return jnp.where(outside, ghost_cycle, values)


def apply_operator(padded, wave_cells, signs):
    centre = padded[:, :, 1:-1, 1:-1]
    edge_sum = (
        padded[:, :, :-2, 1:-1]
        + padded[:, :, 2:, 1:-1]
        + padded[:, :, 1:-1, :-2]
        + padded[:, :, 1:-1, 2:]
    )
    corner_sum = (
        padded[:, :, :-2, :-2]
        + padded[:, :, :-2, 2:]
        + padded[:, :, 2:, :-2]
        + padded[:, :, 2:, 2:]
    )
    laplace = (4.0 * edge_sum + corner_sum - 20.0 * centre) / 6.0
    real_part = centre[:, 0]
    imag_part = centre[:, 1]
    mass_term = jnp.stack(
        [real_part - signs * DAMPING * imag_part, imag_part + signs * DAMPING * real_part], axis=1
    )
    return -laplace - wave_cells * mass_term


def combine_parts(products, signs, shape):
    real_out = products[0][:, 0] - signs[..., None] * products[1][:, 1]
    imag_out = products[0][:, 1] + signs[..., None] * products[1][:, 0]
    return jnp.stack([real_out, imag_out], axis=1).reshape(shape)


def along_rows(values, inverse, signs):
    block = inverse.shape[-1]
    blocked = values.reshape(values.shape[0], 2, values.shape[2], values.shape[3] // block, block)
    products = jnp.einsum("qmok,fchqk->mfchqo", inverse, blocked, precision=lax.Precision.HIGHEST)
    return combine_parts(products, signs, values.shape)


def along_cols(values, inverse, signs):
    block = inverse.shape[-1]
    blocked = values.reshape(values.shape[0], 2, values.shape[2] // block, block, values.shape[3])
    products = jnp.einsum("qmok,fcqkw->mfcqow", inverse, blocked, precision=lax.Precision.HIGHEST)
    return combine_parts(products, signs, values.shape)


def solve_local(resid_ext, wave_ext, row_blocks, col_blocks, live_rect, signs):
    upper, lower, left, right = [to_index(v) for v in live_rect]
    height, breadth = (resid_ext.shape[2], resid_ext.shape[3])
    row_ids = lax.broadcasted_iota(jnp.int32, (height, 1), 0)
    col_ids = lax.broadcasted_iota(jnp.int32, (1, breadth), 1)
    live_mask = (
        (row_ids >= upper) & (row_ids < lower) & (col_ids >= left) & (col_ids < right)
    ).astype(resid_ext.dtype)
    local_res = resid_ext * live_mask
    correction = jnp.zeros_like(resid_ext)
    for sweep_index in range(SWEEPS):
        if sweep_index > 0:
            padded = jnp.pad(correction, ((0, 0), (0, 0), (1, 1), (1, 1)))
            padded = fill_ghost(padded, upper + 1, lower + 1, left + 1, right + 1, signs)
            local_res = live_mask * (resid_ext - apply_operator(padded, wave_ext, signs))
        if sweep_index % 2 == 0:
            update = along_rows(local_res, row_blocks, signs)
        else:
            update = along_cols(local_res, col_blocks, signs)
        correction = correction + live_mask * update
    return correction


def exchange(x, row_width, col_width, extra=None):
    row_count = lax.axis_size("gx")
    col_count = lax.axis_size("gy")
    height, breadth = (x.shape[-2], x.shape[-1])
    pieces = {}
    for dr in (-1, 0, 1):
        for dc in (-1, 0, 1):
            if dr == 0 and dc == 0:
                continue
            slab = x
            if dr == -1:
                slab = lax.slice_in_dim(slab, height - row_width, height, axis=x.ndim - 2)
            elif dr == 1:
                slab = lax.slice_in_dim(slab, 0, row_width, axis=x.ndim - 2)
            if dc == -1:
                slab = lax.slice_in_dim(slab, breadth - col_width, breadth, axis=x.ndim - 1)
            elif dc == 1:
                slab = lax.slice_in_dim(slab, 0, col_width, axis=x.ndim - 1)
            if extra is not None and (dr, dc) in extra:
                slab = jnp.concatenate([slab, extra[(dr, dc)]], axis=0)
            perm = []
            for r in range(row_count):
                for c in range(col_count):
                    rr, cc = (r - dr, c - dc)
                    if 0 <= rr < row_count and 0 <= cc < col_count:
                        perm.append((r * col_count + c, rr * col_count + cc))
            pieces[(dr, dc)] = lax.ppermute(slab, ("gx", "gy"), perm)
    return pieces


def exchange_axis(x, axis, dim, width, extra_lo=None, extra_hi=None):
    peers, length = (lax.axis_size(axis), x.shape[dim])
    up = [(i, i + 1) for i in range(peers - 1)]
    down = [(j, i) for i, j in up]
    last = lax.slice_in_dim(x, length - width, length, axis=dim)
    first = lax.slice_in_dim(x, 0, width, axis=dim)
    if extra_lo is not None:
        last = jnp.concatenate([last, extra_lo], axis=0)
        first = jnp.concatenate([first, extra_hi], axis=0)
    return lax.ppermute(last, axis, up), lax.ppermute(first, axis, down)


def assemble(pieces, centre, lead):
    rows = []
    for dr in (-1, 0, 1):
        row = []
        for dc in (-1, 0, 1):
            part = centre if (dr == 0 and dc == 0) else pieces[(dr, dc)][:lead]
            row.append(part)
        rows.append(jnp.concatenate(row, axis=-1))
    return jnp.concatenate(rows, axis=-2)


def grid_residual(fields_ref, data_ref, res_ref):
    height, breadth = (res_ref.shape[1], res_ref.shape[2])

    def ahead(x, step, axis):
        return pltpu.roll(x, x.shape[axis] - step, axis)

    for problem in range(res_ref.shape[0] // 2):
        sign = 1.0 - 2.0 * problem
        totals, centres = ([], [])
        for part in range(2):
            padded = fields_ref[2 * problem + part]
            outer = padded + ahead(padded, 2, 0)
            middle = ahead(padded, 1, 0)
            edge = ahead(outer, 1, 1) + middle + ahead(middle, 2, 1)
            corner = outer + ahead(outer, 2, 1)
            totals.append((4.0 * edge + corner)[:height, :breadth])
            centres.append(ahead(middle, 1, 1)[:height, :breadth])
        real_part, imag_part = centres
        wave = data_ref[4]
        lap_r = (totals[0] - 20.0 * real_part) / 6.0
        lap_i = (totals[1] - 20.0 * imag_part) / 6.0
        mass_r = real_part - sign * DAMPING * imag_part
        mass_i = imag_part + sign * DAMPING * real_part
        res_ref[2 * problem] = data_ref[2 * problem] - (-lap_r - wave * mass_r)
        res_ref[2 * problem + 1] = data_ref[2 * problem + 1] - (-lap_i - wave * mass_i)


def solve_kernel(rect_ref, resid_ref, data_ref, wrow_ref, wcol_ref, *refs, has_base, last, own_rows, own_cols, slab,
                 from_fields):
    if from_fields:
        grid_residual(resid_ref, data_ref, refs[-1])
        resid_ref = refs[-1]
        refs = refs[:-1]
    base_ref = refs[0] if has_base else None
    outs = refs[1:] if has_base else refs
    own_ref = outs[0]
    top_ref, bottom_ref = (None, None) if last else outs[1:3]
    height, breadth = (resid_ref.shape[1], resid_ref.shape[2])
    half = height // 2
    upper, lower, left, right = (rect_ref[0], rect_ref[1], rect_ref[2], rect_ref[3])
    row_ids = lax.broadcasted_iota(jnp.int32, (height, breadth), 0)
    col_ids = lax.broadcasted_iota(jnp.int32, (height, breadth), 1)
    live = (row_ids >= upper) & (row_ids < lower) & (col_ids >= left) & (col_ids < right)
    top, bottom = (row_ids == upper, row_ids == lower - 1)
    first, last = (col_ids == left, col_ids == right - 1)
    row_flag = top.astype(jnp.float32) + bottom.astype(jnp.float32)
    col_flag = first.astype(jnp.float32) + last.astype(jnp.float32)
    edge_flag = 4.0 * (row_flag + col_flag)
    zero = jnp.zeros((height, breadth), jnp.float32)

    def mask(x):
        return jnp.where(live, x, zero)

    def rows_sum(x):
        up = jnp.where(top, x, pltpu.roll(x, 1, 0))
        down = jnp.where(bottom, x, pltpu.roll(x, height - 1, 0))
        return up + down

    def cols_sum(x):
        lft = jnp.where(first, x, pltpu.roll(x, 1, 1))
        rgt = jnp.where(last, x, pltpu.roll(x, breadth - 1, 1))
        return lft + rgt

    def stencil(x):
        vertical = rows_sum(x)
        ghost_rows = row_flag * x
        total = 4.0 * (vertical + cols_sum(x)) + cols_sum(vertical)
        ghost = edge_flag * x + cols_sum(ghost_rows) + col_flag * (vertical - ghost_rows)
        return total, ghost

    def operator(real_part, imag_part, sign):
        wave = data_ref[4]
        total_r, ghost_r = stencil(real_part)
        total_i, ghost_i = stencil(imag_part)
        lap_r = (total_r + sign * ROBIN_COEF * ghost_i - 20.0 * real_part) / 6.0
        lap_i = (total_i - sign * ROBIN_COEF * ghost_r - 20.0 * imag_part) / 6.0
        mass_r = real_part - sign * DAMPING * imag_part
        mass_i = imag_part + sign * DAMPING * real_part
        return (-lap_r - wave * mass_r, -lap_i - wave * mass_i)

    def dot(a, b):
        return jnp.dot(a, b, precision=lax.Precision.HIGH, preferred_element_type=jnp.float32)

    def rows_apply(real_part, imag_part, sign):
        outs_r, outs_i = ([], [])
        for h in range(breadth // half):
            cols = slice(h * half, (h + 1) * half)
            prod_r = dot(real_part[:, cols], wrow_ref[h])
            prod_i = dot(imag_part[:, cols], wrow_ref[h])
            outs_r.append(prod_r[:, :half] - sign * prod_i[:, half:])
            outs_i.append(prod_i[:, :half] + sign * prod_r[:, half:])
        return (jnp.concatenate(outs_r, axis=1), jnp.concatenate(outs_i, axis=1))

    def cols_apply(real_part, imag_part, sign):
        outs_r, outs_i = ([], [])
        for h in range(height // half):
            rows = slice(h * half, (h + 1) * half)
            prod_r = dot(wcol_ref[h], real_part[rows, :])
            prod_i = dot(wcol_ref[h], imag_part[rows, :])
            outs_r.append(prod_r[:half] - sign * prod_i[half:])
            outs_i.append(prod_i[:half] + sign * prod_r[half:])
        return (jnp.concatenate(outs_r, axis=0), jnp.concatenate(outs_i, axis=0))

    def problem_body(problem, carry):
        sign = 1.0 - 2.0 * problem.astype(jnp.float32)
        up_r, up_i = rows_apply(mask(resid_ref[2 * problem]), mask(resid_ref[2 * problem + 1]), sign)
        cor_r, cor_i = (mask(up_r), mask(up_i))
        for step in range(SWEEPS - 1):
            op_r, op_i = operator(cor_r, cor_i, sign)
            loc_r, loc_i = (mask(resid_ref[2 * problem] - op_r), mask(resid_ref[2 * problem + 1] - op_i))
            apply = cols_apply if step % 2 == 0 else rows_apply
            up_r, up_i = apply(loc_r, loc_i, sign)
            cor_r, cor_i = (cor_r + mask(up_r), cor_i + mask(up_i))
        first_row = (height - own_rows) // 2
        for part, value in ((0, cor_r), (1, cor_i)):
            own = pltpu.roll(value, breadth - (breadth - own_cols) // 2, 1)[first_row : first_row + own_rows, :own_cols]
            if base_ref is not None:
                own = own + base_ref[problem, part]
            own_ref[problem, part] = own
            if top_ref is not None:
                top_ref[problem, part] = own[:slab]
                bottom_ref[problem, part] = own[own_rows - slab :]
        return carry

    lax.fori_loop(0, resid_ref.shape[0] // 2, problem_body, 0)


def line_matrices(row_blocks, col_blocks):
    block = row_blocks.shape[-1]
    eye = jnp.eye(2, dtype=row_blocks.dtype)
    halves = row_blocks.shape[0] // 2
    rows_t = jnp.transpose(row_blocks, (0, 3, 1, 2)).reshape(halves, 2, block, 2, block)
    row_mats = jnp.einsum("hakmo,ab->hakmbo", rows_t, eye).reshape(halves, 2 * block, 4 * block)
    cols = col_blocks.reshape(halves, 2, 2, block, block)
    col_mats = jnp.einsum("hamok,ab->hmaobk", cols, eye).reshape(halves, 4 * block, 2 * block)
    return row_mats, col_mats


def solve_local_kernel(resid_planes, data_ext, row_mats, col_mats, live_rect, own_shape, slab, base=None, last=False,
                       from_fields=False, interpret=False):
    extra = [] if base is None else [base]
    rect = jnp.stack([to_index(v) for v in live_rect])
    dtype = data_ext.dtype
    ext_shape = data_ext.shape[1:]
    shapes = [(2, 2) + own_shape]
    if not last:
        shapes += [(2, 2, slab, own_shape[1])] * 2
    vmem = pltpu.MemorySpace.VMEM if hasattr(pltpu, "MemorySpace") else pltpu.VMEM
    kernel = functools.partial(
        solve_kernel, has_base=base is not None, last=last, own_rows=own_shape[0], own_cols=own_shape[1], slab=slab,
        from_fields=from_fields,
    )
    scratch = [pltpu.VMEM((4,) + ext_shape, jnp.float32)] if from_fields else []
    operands = [data_ext, row_mats, col_mats] + extra
    if resid_planes is None:
        inner = kernel

        def kernel(rect_ref, data_ref, *refs):
            return inner(rect_ref, data_ref, data_ref, *refs)
    else:
        operands = [resid_planes] + operands
    return pl.pallas_call(
        kernel,
        out_shape=[jax.ShapeDtypeStruct(s, dtype) for s in shapes],
        in_specs=[pl.BlockSpec(memory_space=pltpu.SMEM)] + [pl.BlockSpec(memory_space=vmem)] * len(operands),
        out_specs=[pl.BlockSpec(memory_space=vmem)] * len(shapes),
        scratch_shapes=scratch,
        interpret=interpret,
    )(rect, *operands)


def shards(sources, wavenumber, row_inverse, col_inverse, reach_steps):
    own_rows, own_cols = (sources.shape[2], sources.shape[3])
    block = row_inverse.shape[-1]
    step_cells = block // 4
    signs = jnp.array([1.0, -1.0], dtype=sources.dtype).reshape(2, 1, 1)
    row_rank = to_index(lax.axis_index("gx"))
    col_rank = to_index(lax.axis_index("gy"))
    row_count = lax.axis_size("gx")
    col_count = lax.axis_size("gy")
    zero = to_index(0)
    widths = reach_steps.reshape(4) * step_cells
    upper_w = jnp.where(row_rank > 0, widths[0], zero)
    lower_w = jnp.where(row_rank < row_count - 1, widths[1], zero)
    left_w = jnp.where(col_rank > 0, widths[2], zero)
    right_w = jnp.where(col_rank < col_count - 1, widths[3], zero)
    live_rect = (
        block - upper_w,
        block + own_rows + lower_w,
        block - left_w,
        block + own_cols + right_w,
    )
    stacked = jnp.concatenate([sources.reshape(4, own_rows, own_cols), wavenumber[None]], axis=0)
    lead = stacked.shape[0]
    col_pair = col_inverse.shape[0]
    row_pair = row_inverse.shape[0]
    inv_rows = col_inverse.shape[1] * block * block // own_cols
    before, after = exchange_axis(
        stacked, "gx", 1, block,
        col_inverse[col_pair - 1].reshape(1, inv_rows, own_cols), col_inverse[0].reshape(1, inv_rows, own_cols),
    )
    tall = jnp.concatenate([before[:lead, :block], stacked, after[:lead, :block]], axis=1)
    def inv_slab(mats):
        flat = mats.reshape(1, -1, block)
        return jnp.pad(flat, ((0, 0), (0, tall.shape[1] - flat.shape[1]), (0, 0)))
    left, right = exchange_axis(tall, "gy", 2, block, inv_slab(row_inverse[row_pair - 1]), inv_slab(row_inverse[0]))
    stacked_ext = jnp.concatenate([left[:lead], tall, right[:lead]], axis=2)
    sources_ext = stacked_ext[:4].reshape(2, 2, own_rows + 2 * block, own_cols + 2 * block)
    wave_ext = stacked_ext[4]
    inv_shape = (1,) + row_inverse.shape[1:]
    inv_size = row_inverse.shape[1] * block * block // block
    col_blocks = jnp.concatenate(
        [before[lead:].reshape(inv_shape), col_inverse, after[lead:].reshape(inv_shape)], axis=0
    )
    row_blocks = jnp.concatenate(
        [left[lead:, :inv_size].reshape(inv_shape), row_inverse, right[lead:, :inv_size].reshape(inv_shape)], axis=0
    )
    row_mats, col_mats = line_matrices(row_blocks, col_blocks)
    width = block + 1
    edges = (row_rank == 0, row_rank == row_count - 1, col_rank == 0, col_rank == col_count - 1)
    slab = -(-width // 8) * 8
    solution = None
    base = None
    for iteration in range(ITERS):
        last = iteration == ITERS - 1
        if iteration == 0:
            resid_planes = None
        else:
            peers = lax.axis_size("gx")
            up = [(i, i + 1) for i in range(peers - 1)]
            down = [(j, i) for i, j in up]
            before = lax.ppermute(bottom, "gx", up)[:, :, slab - width :]
            after = lax.ppermute(top, "gx", down)[:, :, :width]
            tall = jnp.concatenate([before, solution, after], axis=2)
            left, right = exchange_axis(tall, "gy", 3, width)
            padded = jnp.concatenate([left, tall, right], axis=3)
            on_edge = edges[0] | edges[1] | edges[2] | edges[3]
            padded = lax.cond(on_edge, lambda v: grid_ghost(v, width, edges, signs), lambda v: v, padded)
            tile_rows = -(-padded.shape[2] // 8) * 8 - padded.shape[2]
            tile_cols = -(-padded.shape[3] // 128) * 128 - padded.shape[3]
            padded = jnp.pad(padded, ((0, 0), (0, 0), (0, tile_rows), (0, tile_cols)))
            resid_planes = padded.reshape((4,) + padded.shape[2:])
        outs = solve_local_kernel(
            resid_planes, stacked_ext, row_mats, col_mats, live_rect, (own_rows, own_cols), slab, base=base, last=last,
            from_fields=iteration > 0,
        )
        solution = outs[0]
        if not last:
            solution, top, bottom = outs
        base = solution
    return solution


def solution(mesh):
    return jax.shard_map(
        shards,
        mesh=mesh,
        in_specs=(
            P(None, None, "gx", "gy"),
            P("gx", "gy"),
            P("gy", None, None, None),
            P("gx", None, None, None),
            P("gx", "gy", None),
        ),
        out_specs=P(None, None, "gx", "gy"),
        check_vma=False,
    )
```

```python
import functools

import jax
import jax.numpy as jnp
from jax import lax
from jax.sharding import PartitionSpec as P
from jax.experimental import pallas as pl
from jax.experimental.pallas import tpu as pltpu

ITERS = 2
SWEEPS = 4


DAMPING = 0.5
ROBIN_COEF = 0.5


def with_halo(shard, sides, width):
    for axis, dim in sides:
        peers, length = (lax.axis_size(axis), shard.shape[dim])
        up = [(i, (i + 1) % peers) for i in range(peers - 1)]
        down = [(j, i) for i, j in up]
        last = lax.slice_in_dim(shard, length - width, length, axis=dim)
        first = lax.slice_in_dim(shard, 0, width, axis=dim)
        before = lax.ppermute(last, axis, up)
        after = lax.ppermute(first, axis, down)
        shard = jnp.concatenate([before, shard, after], axis=dim)
    return shard


def to_index(value):
    return jnp.asarray(value).astype(jnp.int32)


def slice_line(values, start, axis):
    starts = [to_index(0) for _ in range(values.ndim)]
    starts[axis] = to_index(start)
    sizes = list(values.shape)
    sizes[axis] = 1
    return lax.dynamic_slice(values, starts, sizes)


def fill_ghost(values, upper, lower, left, right, signs):
    upper, lower, left, right = (to_index(upper), to_index(lower), to_index(left), to_index(right))
    height, breadth = (values.shape[2], values.shape[3])
    row_ids = lax.broadcasted_iota(jnp.int32, (height, 1), 0)
    col_ids = lax.broadcasted_iota(jnp.int32, (1, breadth), 1)
    upper_row = slice_line(values, upper, 2)
    lower_row = slice_line(values, lower - 1, 2)
    values = jnp.where(row_ids < upper, upper_row, jnp.where(row_ids >= lower, lower_row, values))
    left_col = slice_line(values, left, 3)
    right_col = slice_line(values, right - 1, 3)
    values = jnp.where(col_ids < left, left_col, jnp.where(col_ids >= right, right_col, values))
    inside = (row_ids >= upper) & (row_ids < lower) & (col_ids >= left) & (col_ids < right)
    real_part = values[:, 0]
    imag_part = values[:, 1]
    ghost_cycle = jnp.stack(
        [real_part + signs * ROBIN_COEF * imag_part, imag_part - signs * ROBIN_COEF * real_part],
        axis=1,
    )
    return jnp.where(inside, values, ghost_cycle)


def grid_ghost(values, width, edges, signs):
    at_top, at_bottom, at_left, at_right = edges
    height, breadth = (values.shape[2], values.shape[3])
    row_ids = lax.broadcasted_iota(jnp.int32, (height, 1), 0)
    col_ids = lax.broadcasted_iota(jnp.int32, (1, breadth), 1)
    above = at_top & (row_ids < width)
    below = at_bottom & (row_ids >= height - width)
    values = jnp.where(
        above, values[:, :, width : width + 1], jnp.where(below, values[:, :, height - width - 1 : height - width], values)
    )
    before = at_left & (col_ids < width)
    after = at_right & (col_ids >= breadth - width)
    values = jnp.where(
        before, values[:, :, :, width : width + 1],
        jnp.where(after, values[:, :, :, breadth - width - 1 : breadth - width], values),
    )
    outside = above | below | before | after
    real_part = values[:, 0]
    imag_part = values[:, 1]
    ghost_cycle = jnp.stack(
        [real_part + signs * ROBIN_COEF * imag_part, imag_part - signs * ROBIN_COEF * real_part],
        axis=1,
    )
    return jnp.where(outside, ghost_cycle, values)


def apply_operator(padded, wave_cells, signs):
    centre = padded[:, :, 1:-1, 1:-1]
    edge_sum = (
        padded[:, :, :-2, 1:-1]
        + padded[:, :, 2:, 1:-1]
        + padded[:, :, 1:-1, :-2]
        + padded[:, :, 1:-1, 2:]
    )
    corner_sum = (
        padded[:, :, :-2, :-2]
        + padded[:, :, :-2, 2:]
        + padded[:, :, 2:, :-2]
        + padded[:, :, 2:, 2:]
    )
    laplace = (4.0 * edge_sum + corner_sum - 20.0 * centre) / 6.0
    real_part = centre[:, 0]
    imag_part = centre[:, 1]
    mass_term = jnp.stack(
        [real_part - signs * DAMPING * imag_part, imag_part + signs * DAMPING * real_part], axis=1
    )
    return -laplace - wave_cells * mass_term


def combine_parts(products, signs, shape):
    real_out = products[0][:, 0] - signs[..., None] * products[1][:, 1]
    imag_out = products[0][:, 1] + signs[..., None] * products[1][:, 0]
    return jnp.stack([real_out, imag_out], axis=1).reshape(shape)


def along_rows(values, inverse, signs):
    block = inverse.shape[-1]
    blocked = values.reshape(values.shape[0], 2, values.shape[2], values.shape[3] // block, block)
    products = jnp.einsum("qmok,fchqk->mfchqo", inverse, blocked, precision=lax.Precision.HIGHEST)
    return combine_parts(products, signs, values.shape)


def along_cols(values, inverse, signs):
    block = inverse.shape[-1]
    blocked = values.reshape(values.shape[0], 2, values.shape[2] // block, block, values.shape[3])
    products = jnp.einsum("qmok,fcqkw->mfcqow", inverse, blocked, precision=lax.Precision.HIGHEST)
    return combine_parts(products, signs, values.shape)


def solve_local(resid_ext, wave_ext, row_blocks, col_blocks, live_rect, signs):
    upper, lower, left, right = [to_index(v) for v in live_rect]
    height, breadth = (resid_ext.shape[2], resid_ext.shape[3])
    row_ids = lax.broadcasted_iota(jnp.int32, (height, 1), 0)
    col_ids = lax.broadcasted_iota(jnp.int32, (1, breadth), 1)
    live_mask = (
        (row_ids >= upper) & (row_ids < lower) & (col_ids >= left) & (col_ids < right)
    ).astype(resid_ext.dtype)
    local_res = resid_ext * live_mask
    correction = jnp.zeros_like(resid_ext)
    for sweep_index in range(SWEEPS):
        if sweep_index > 0:
            padded = jnp.pad(correction, ((0, 0), (0, 0), (1, 1), (1, 1)))
            padded = fill_ghost(padded, upper + 1, lower + 1, left + 1, right + 1, signs)
            local_res = live_mask * (resid_ext - apply_operator(padded, wave_ext, signs))
        if sweep_index % 2 == 0:
            update = along_rows(local_res, row_blocks, signs)
        else:
            update = along_cols(local_res, col_blocks, signs)
        correction = correction + live_mask * update
    return correction


def exchange(x, row_width, col_width, extra=None):
    row_count = lax.axis_size("gx")
    col_count = lax.axis_size("gy")
    height, breadth = (x.shape[-2], x.shape[-1])
    pieces = {}
    for dr in (-1, 0, 1):
        for dc in (-1, 0, 1):
            if dr == 0 and dc == 0:
                continue
            slab = x
            if dr == -1:
                slab = lax.slice_in_dim(slab, height - row_width, height, axis=x.ndim - 2)
            elif dr == 1:
                slab = lax.slice_in_dim(slab, 0, row_width, axis=x.ndim - 2)
            if dc == -1:
                slab = lax.slice_in_dim(slab, breadth - col_width, breadth, axis=x.ndim - 1)
            elif dc == 1:
                slab = lax.slice_in_dim(slab, 0, col_width, axis=x.ndim - 1)
            if extra is not None and (dr, dc) in extra:
                slab = jnp.concatenate([slab, extra[(dr, dc)]], axis=0)
            perm = []
            for r in range(row_count):
                for c in range(col_count):
                    rr, cc = (r - dr, c - dc)
                    if 0 <= rr < row_count and 0 <= cc < col_count:
                        perm.append((r * col_count + c, rr * col_count + cc))
            pieces[(dr, dc)] = lax.ppermute(slab, ("gx", "gy"), perm)
    return pieces


def exchange_axis(x, axis, dim, width, extra_lo=None, extra_hi=None):
    peers, length = (lax.axis_size(axis), x.shape[dim])
    up = [(i, i + 1) for i in range(peers - 1)]
    down = [(j, i) for i, j in up]
    last = lax.slice_in_dim(x, length - width, length, axis=dim)
    first = lax.slice_in_dim(x, 0, width, axis=dim)
    if extra_lo is not None:
        last = jnp.concatenate([last, extra_lo], axis=0)
        first = jnp.concatenate([first, extra_hi], axis=0)
    return lax.ppermute(last, axis, up), lax.ppermute(first, axis, down)


def assemble(pieces, centre, lead):
    rows = []
    for dr in (-1, 0, 1):
        row = []
        for dc in (-1, 0, 1):
            part = centre if (dr == 0 and dc == 0) else pieces[(dr, dc)][:lead]
            row.append(part)
        rows.append(jnp.concatenate(row, axis=-1))
    return jnp.concatenate(rows, axis=-2)


def grid_residual(fields_ref, data_ref, res_ref):
    height, breadth = (res_ref.shape[1], res_ref.shape[2])

    def ahead(x, step, axis):
        return pltpu.roll(x, x.shape[axis] - step, axis)

    for problem in range(res_ref.shape[0] // 2):
        sign = 1.0 - 2.0 * problem
        totals, centres = ([], [])
        for part in range(2):
            padded = fields_ref[2 * problem + part]
            outer = padded + ahead(padded, 2, 0)
            middle = ahead(padded, 1, 0)
            edge = ahead(outer, 1, 1) + middle + ahead(middle, 2, 1)
            corner = outer + ahead(outer, 2, 1)
            totals.append((4.0 * edge + corner)[:height, :breadth])
            centres.append(ahead(middle, 1, 1)[:height, :breadth])
        real_part, imag_part = centres
        wave = data_ref[4]
        lap_r = (totals[0] - 20.0 * real_part) / 6.0
        lap_i = (totals[1] - 20.0 * imag_part) / 6.0
        mass_r = real_part - sign * DAMPING * imag_part
        mass_i = imag_part + sign * DAMPING * real_part
        res_ref[2 * problem] = data_ref[2 * problem] - (-lap_r - wave * mass_r)
        res_ref[2 * problem + 1] = data_ref[2 * problem + 1] - (-lap_i - wave * mass_i)


def solve_kernel(rect_ref, resid_ref, data_ref, wrow_ref, wcol_ref, *refs, has_base, last, own_rows, own_cols, slab,
                 from_fields):
    if from_fields:
        grid_residual(resid_ref, data_ref, refs[-1])
        resid_ref = refs[-1]
        refs = refs[:-1]
    base_ref = refs[0] if has_base else None
    outs = refs[1:] if has_base else refs
    own_ref = outs[0]
    top_ref, bottom_ref = (None, None) if last else outs[1:3]
    height, breadth = (resid_ref.shape[1], resid_ref.shape[2])
    half = height // 2
    upper, lower, left, right = (rect_ref[0], rect_ref[1], rect_ref[2], rect_ref[3])
    row_ids = lax.broadcasted_iota(jnp.int32, (height, breadth), 0)
    col_ids = lax.broadcasted_iota(jnp.int32, (height, breadth), 1)
    live = (row_ids >= upper) & (row_ids < lower) & (col_ids >= left) & (col_ids < right)
    top, bottom = (row_ids == upper, row_ids == lower - 1)
    first, last = (col_ids == left, col_ids == right - 1)
    row_flag = top.astype(jnp.float32) + bottom.astype(jnp.float32)
    col_flag = first.astype(jnp.float32) + last.astype(jnp.float32)
    edge_flag = 4.0 * (row_flag + col_flag)
    zero = jnp.zeros((height, breadth), jnp.float32)

    def mask(x):
        return jnp.where(live, x, zero)

    def rows_sum(x):
        up = jnp.where(top, x, pltpu.roll(x, 1, 0))
        down = jnp.where(bottom, x, pltpu.roll(x, height - 1, 0))
        return up + down

    def cols_sum(x):
        lft = jnp.where(first, x, pltpu.roll(x, 1, 1))
        rgt = jnp.where(last, x, pltpu.roll(x, breadth - 1, 1))
        return lft + rgt

    def stencil(x):
        vertical = rows_sum(x)
        ghost_rows = row_flag * x
        total = 4.0 * (vertical + cols_sum(x)) + cols_sum(vertical)
        ghost = edge_flag * x + cols_sum(ghost_rows) + col_flag * (vertical - ghost_rows)
        return total, ghost

    def operator(real_part, imag_part, sign):
        wave = data_ref[4]
        total_r, ghost_r = stencil(real_part)
        total_i, ghost_i = stencil(imag_part)
        lap_r = (total_r + sign * ROBIN_COEF * ghost_i - 20.0 * real_part) / 6.0
        lap_i = (total_i - sign * ROBIN_COEF * ghost_r - 20.0 * imag_part) / 6.0
        mass_r = real_part - sign * DAMPING * imag_part
        mass_i = imag_part + sign * DAMPING * real_part
        return (-lap_r - wave * mass_r, -lap_i - wave * mass_i)

    def split(x):
        high = x.astype(jnp.bfloat16)
        return high, (x - high.astype(jnp.float32)).astype(jnp.bfloat16)

    def bdot(a, b):
        return jnp.dot(a, b, preferred_element_type=jnp.float32)

    def dot_w(x, w_ref, h):
        x_hi, x_lo = split(x)
        return bdot(x_hi, w_ref[0, h]) + (bdot(x_hi, w_ref[1, h]) + bdot(x_lo, w_ref[0, h]))

    def w_dot(w_ref, h, x):
        x_hi, x_lo = split(x)
        return bdot(w_ref[0, h], x_hi) + (bdot(w_ref[1, h], x_hi) + bdot(w_ref[0, h], x_lo))

    def rows_apply(real_part, imag_part, sign):
        outs_r, outs_i = ([], [])
        for h in range(breadth // half):
            cols = slice(h * half, (h + 1) * half)
            prod_r = dot_w(real_part[:, cols], wrow_ref, h)
            prod_i = dot_w(imag_part[:, cols], wrow_ref, h)
            outs_r.append(prod_r[:, :half] - sign * prod_i[:, half:])
            outs_i.append(prod_i[:, :half] + sign * prod_r[:, half:])
        return (jnp.concatenate(outs_r, axis=1), jnp.concatenate(outs_i, axis=1))

    def cols_apply(real_part, imag_part, sign):
        outs_r, outs_i = ([], [])
        for h in range(height // half):
            rows = slice(h * half, (h + 1) * half)
            prod_r = w_dot(wcol_ref, h, real_part[rows, :])
            prod_i = w_dot(wcol_ref, h, imag_part[rows, :])
            outs_r.append(prod_r[:half] - sign * prod_i[half:])
            outs_i.append(prod_i[:half] + sign * prod_r[half:])
        return (jnp.concatenate(outs_r, axis=0), jnp.concatenate(outs_i, axis=0))

    def problem_body(problem, carry):
        sign = 1.0 - 2.0 * problem.astype(jnp.float32)
        up_r, up_i = rows_apply(mask(resid_ref[2 * problem]), mask(resid_ref[2 * problem + 1]), sign)
        cor_r, cor_i = (mask(up_r), mask(up_i))
        for step in range(SWEEPS - 1):
            op_r, op_i = operator(cor_r, cor_i, sign)
            loc_r, loc_i = (mask(resid_ref[2 * problem] - op_r), mask(resid_ref[2 * problem + 1] - op_i))
            apply = cols_apply if step % 2 == 0 else rows_apply
            up_r, up_i = apply(loc_r, loc_i, sign)
            cor_r, cor_i = (cor_r + mask(up_r), cor_i + mask(up_i))
        first_row = (height - own_rows) // 2
        for part, value in ((0, cor_r), (1, cor_i)):
            own = pltpu.roll(value, breadth - (breadth - own_cols) // 2, 1)[first_row : first_row + own_rows, :own_cols]
            if base_ref is not None:
                own = own + base_ref[problem, part]
            own_ref[problem, part] = own
            if top_ref is not None:
                top_ref[problem, part] = own[:slab]
                bottom_ref[problem, part] = own[own_rows - slab :]
        return carry

    lax.fori_loop(0, resid_ref.shape[0] // 2, problem_body, 0)


def line_matrices(row_blocks, col_blocks):
    block = row_blocks.shape[-1]
    eye = jnp.eye(2, dtype=row_blocks.dtype)
    halves = row_blocks.shape[0] // 2
    rows_t = jnp.transpose(row_blocks, (0, 3, 1, 2)).reshape(halves, 2, block, 2, block)
    row_mats = jnp.einsum("hakmo,ab->hakmbo", rows_t, eye).reshape(halves, 2 * block, 4 * block)
    cols = col_blocks.reshape(halves, 2, 2, block, block)
    col_mats = jnp.einsum("hamok,ab->hmaobk", cols, eye).reshape(halves, 4 * block, 2 * block)
    return row_mats, col_mats


def solve_local_kernel(resid_planes, data_ext, row_mats, col_mats, live_rect, own_shape, slab, base=None, last=False,
                       from_fields=False, interpret=False):
    extra = [] if base is None else [base]
    rect = jnp.stack([to_index(v) for v in live_rect])
    dtype = data_ext.dtype
    ext_shape = data_ext.shape[1:]
    shapes = [(2, 2) + own_shape]
    if not last:
        shapes += [(2, 2, slab, own_shape[1])] * 2
    vmem = pltpu.MemorySpace.VMEM if hasattr(pltpu, "MemorySpace") else pltpu.VMEM
    kernel = functools.partial(
        solve_kernel, has_base=base is not None, last=last, own_rows=own_shape[0], own_cols=own_shape[1], slab=slab,
        from_fields=from_fields,
    )
    scratch = [pltpu.VMEM((4,) + ext_shape, jnp.float32)] if from_fields else []
    operands = [data_ext, row_mats, col_mats] + extra
    if resid_planes is None:
        inner = kernel

        def kernel(rect_ref, data_ref, *refs):
            return inner(rect_ref, data_ref, data_ref, *refs)
    else:
        operands = [resid_planes] + operands
    return pl.pallas_call(
        kernel,
        out_shape=[jax.ShapeDtypeStruct(s, dtype) for s in shapes],
        in_specs=[pl.BlockSpec(memory_space=pltpu.SMEM)] + [pl.BlockSpec(memory_space=vmem)] * len(operands),
        out_specs=[pl.BlockSpec(memory_space=vmem)] * len(shapes),
        scratch_shapes=scratch,
        interpret=interpret,
    )(rect, *operands)


def shards(sources, wavenumber, row_inverse, col_inverse, reach_steps):
    own_rows, own_cols = (sources.shape[2], sources.shape[3])
    block = row_inverse.shape[-1]
    step_cells = block // 4
    signs = jnp.array([1.0, -1.0], dtype=sources.dtype).reshape(2, 1, 1)
    row_rank = to_index(lax.axis_index("gx"))
    col_rank = to_index(lax.axis_index("gy"))
    row_count = lax.axis_size("gx")
    col_count = lax.axis_size("gy")
    zero = to_index(0)
    widths = reach_steps.reshape(4) * step_cells
    upper_w = jnp.where(row_rank > 0, widths[0], zero)
    lower_w = jnp.where(row_rank < row_count - 1, widths[1], zero)
    left_w = jnp.where(col_rank > 0, widths[2], zero)
    right_w = jnp.where(col_rank < col_count - 1, widths[3], zero)
    live_rect = (
        block - upper_w,
        block + own_rows + lower_w,
        block - left_w,
        block + own_cols + right_w,
    )
    stacked = jnp.concatenate([sources.reshape(4, own_rows, own_cols), wavenumber[None]], axis=0)
    lead = stacked.shape[0]
    col_pair = col_inverse.shape[0]
    row_pair = row_inverse.shape[0]
    inv_rows = col_inverse.shape[1] * block * block // own_cols
    before, after = exchange_axis(
        stacked, "gx", 1, block,
        col_inverse[col_pair - 1].reshape(1, inv_rows, own_cols), col_inverse[0].reshape(1, inv_rows, own_cols),
    )
    tall = jnp.concatenate([before[:lead, :block], stacked, after[:lead, :block]], axis=1)
    def inv_slab(mats):
        flat = mats.reshape(1, -1, block)
        return jnp.pad(flat, ((0, 0), (0, tall.shape[1] - flat.shape[1]), (0, 0)))
    left, right = exchange_axis(tall, "gy", 2, block, inv_slab(row_inverse[row_pair - 1]), inv_slab(row_inverse[0]))
    stacked_ext = jnp.concatenate([left[:lead], tall, right[:lead]], axis=2)
    sources_ext = stacked_ext[:4].reshape(2, 2, own_rows + 2 * block, own_cols + 2 * block)
    wave_ext = stacked_ext[4]
    inv_shape = (1,) + row_inverse.shape[1:]
    inv_size = row_inverse.shape[1] * block * block // block
    col_blocks = jnp.concatenate(
        [before[lead:].reshape(inv_shape), col_inverse, after[lead:].reshape(inv_shape)], axis=0
    )
    row_blocks = jnp.concatenate(
        [left[lead:, :inv_size].reshape(inv_shape), row_inverse, right[lead:, :inv_size].reshape(inv_shape)], axis=0
    )
    row_mats, col_mats = line_matrices(row_blocks, col_blocks)

    def split_parts(mats):
        high = lax.reduce_precision(mats, exponent_bits=8, mantissa_bits=7)
        return jnp.stack([high.astype(jnp.bfloat16), (mats - high).astype(jnp.bfloat16)])

    row_mats, col_mats = (split_parts(row_mats), split_parts(col_mats))
    width = block + 1
    edges = (row_rank == 0, row_rank == row_count - 1, col_rank == 0, col_rank == col_count - 1)
    slab = -(-width // 8) * 8
    solution = None
    base = None
    for iteration in range(ITERS):
        last = iteration == ITERS - 1
        if iteration == 0:
            resid_planes = None
        else:
            peers = lax.axis_size("gx")
            up = [(i, i + 1) for i in range(peers - 1)]
            down = [(j, i) for i, j in up]
            before = lax.ppermute(bottom, "gx", up)[:, :, slab - width :]
            after = lax.ppermute(top, "gx", down)[:, :, :width]
            tall = jnp.concatenate([before, solution, after], axis=2)
            left, right = exchange_axis(tall, "gy", 3, width)
            padded = jnp.concatenate([left, tall, right], axis=3)
            padded = grid_ghost(padded, width, edges, signs)
            tile_rows = -(-padded.shape[2] // 8) * 8 - padded.shape[2]
            tile_cols = -(-padded.shape[3] // 128) * 128 - padded.shape[3]
            padded = jnp.pad(padded, ((0, 0), (0, 0), (0, tile_rows), (0, tile_cols)))
            resid_planes = padded.reshape((4,) + padded.shape[2:])
        outs = solve_local_kernel(
            resid_planes, stacked_ext, row_mats, col_mats, live_rect, (own_rows, own_cols), slab, base=base, last=last,
            from_fields=iteration > 0,
        )
        solution = outs[0]
        if not last:
            solution, top, bottom = outs
        base = solution
    return solution


def solution(mesh):
    return jax.shard_map(
        shards,
        mesh=mesh,
        in_specs=(
            P(None, None, "gx", "gy"),
            P("gx", "gy"),
            P("gy", None, None, None),
            P("gx", None, None, None),
            P("gx", "gy", None),
        ),
        out_specs=P(None, None, "gx", "gy"),
        check_vma=False,
    )
```

```python
import functools

import jax
import jax.numpy as jnp
from jax import lax
from jax.sharding import PartitionSpec as P
from jax.experimental import pallas as pl
from jax.experimental.pallas import tpu as pltpu

ITERS = 2
SWEEPS = 4


DAMPING = 0.5
ROBIN_COEF = 0.5


def with_halo(shard, sides, width):
    for axis, dim in sides:
        peers, length = (lax.axis_size(axis), shard.shape[dim])
        up = [(i, (i + 1) % peers) for i in range(peers - 1)]
        down = [(j, i) for i, j in up]
        last = lax.slice_in_dim(shard, length - width, length, axis=dim)
        first = lax.slice_in_dim(shard, 0, width, axis=dim)
        before = lax.ppermute(last, axis, up)
        after = lax.ppermute(first, axis, down)
        shard = jnp.concatenate([before, shard, after], axis=dim)
    return shard


def to_index(value):
    return jnp.asarray(value).astype(jnp.int32)


def slice_line(values, start, axis):
    starts = [to_index(0) for _ in range(values.ndim)]
    starts[axis] = to_index(start)
    sizes = list(values.shape)
    sizes[axis] = 1
    return lax.dynamic_slice(values, starts, sizes)


def fill_ghost(values, upper, lower, left, right, signs):
    upper, lower, left, right = (to_index(upper), to_index(lower), to_index(left), to_index(right))
    height, breadth = (values.shape[2], values.shape[3])
    row_ids = lax.broadcasted_iota(jnp.int32, (height, 1), 0)
    col_ids = lax.broadcasted_iota(jnp.int32, (1, breadth), 1)
    upper_row = slice_line(values, upper, 2)
    lower_row = slice_line(values, lower - 1, 2)
    values = jnp.where(row_ids < upper, upper_row, jnp.where(row_ids >= lower, lower_row, values))
    left_col = slice_line(values, left, 3)
    right_col = slice_line(values, right - 1, 3)
    values = jnp.where(col_ids < left, left_col, jnp.where(col_ids >= right, right_col, values))
    inside = (row_ids >= upper) & (row_ids < lower) & (col_ids >= left) & (col_ids < right)
    real_part = values[:, 0]
    imag_part = values[:, 1]
    ghost_cycle = jnp.stack(
        [real_part + signs * ROBIN_COEF * imag_part, imag_part - signs * ROBIN_COEF * real_part],
        axis=1,
    )
    return jnp.where(inside, values, ghost_cycle)


def grid_ghost(values, width, edges, signs):
    at_top, at_bottom, at_left, at_right = edges
    height, breadth = (values.shape[2], values.shape[3])
    row_ids = lax.broadcasted_iota(jnp.int32, (height, 1), 0)
    col_ids = lax.broadcasted_iota(jnp.int32, (1, breadth), 1)
    above = at_top & (row_ids < width)
    below = at_bottom & (row_ids >= height - width)
    values = jnp.where(
        above, values[:, :, width : width + 1], jnp.where(below, values[:, :, height - width - 1 : height - width], values)
    )
    before = at_left & (col_ids < width)
    after = at_right & (col_ids >= breadth - width)
    values = jnp.where(
        before, values[:, :, :, width : width + 1],
        jnp.where(after, values[:, :, :, breadth - width - 1 : breadth - width], values),
    )
    outside = above | below | before | after
    real_part = values[:, 0]
    imag_part = values[:, 1]
    ghost_cycle = jnp.stack(
        [real_part + signs * ROBIN_COEF * imag_part, imag_part - signs * ROBIN_COEF * real_part],
        axis=1,
    )
    return jnp.where(outside, ghost_cycle, values)


def apply_operator(padded, wave_cells, signs):
    centre = padded[:, :, 1:-1, 1:-1]
    edge_sum = (
        padded[:, :, :-2, 1:-1]
        + padded[:, :, 2:, 1:-1]
        + padded[:, :, 1:-1, :-2]
        + padded[:, :, 1:-1, 2:]
    )
    corner_sum = (
        padded[:, :, :-2, :-2]
        + padded[:, :, :-2, 2:]
        + padded[:, :, 2:, :-2]
        + padded[:, :, 2:, 2:]
    )
    laplace = (4.0 * edge_sum + corner_sum - 20.0 * centre) / 6.0
    real_part = centre[:, 0]
    imag_part = centre[:, 1]
    mass_term = jnp.stack(
        [real_part - signs * DAMPING * imag_part, imag_part + signs * DAMPING * real_part], axis=1
    )
    return -laplace - wave_cells * mass_term


def combine_parts(products, signs, shape):
    real_out = products[0][:, 0] - signs[..., None] * products[1][:, 1]
    imag_out = products[0][:, 1] + signs[..., None] * products[1][:, 0]
    return jnp.stack([real_out, imag_out], axis=1).reshape(shape)


def along_rows(values, inverse, signs):
    block = inverse.shape[-1]
    blocked = values.reshape(values.shape[0], 2, values.shape[2], values.shape[3] // block, block)
    products = jnp.einsum("qmok,fchqk->mfchqo", inverse, blocked, precision=lax.Precision.HIGHEST)
    return combine_parts(products, signs, values.shape)


def along_cols(values, inverse, signs):
    block = inverse.shape[-1]
    blocked = values.reshape(values.shape[0], 2, values.shape[2] // block, block, values.shape[3])
    products = jnp.einsum("qmok,fcqkw->mfcqow", inverse, blocked, precision=lax.Precision.HIGHEST)
    return combine_parts(products, signs, values.shape)


def solve_local(resid_ext, wave_ext, row_blocks, col_blocks, live_rect, signs):
    upper, lower, left, right = [to_index(v) for v in live_rect]
    height, breadth = (resid_ext.shape[2], resid_ext.shape[3])
    row_ids = lax.broadcasted_iota(jnp.int32, (height, 1), 0)
    col_ids = lax.broadcasted_iota(jnp.int32, (1, breadth), 1)
    live_mask = (
        (row_ids >= upper) & (row_ids < lower) & (col_ids >= left) & (col_ids < right)
    ).astype(resid_ext.dtype)
    local_res = resid_ext * live_mask
    correction = jnp.zeros_like(resid_ext)
    for sweep_index in range(SWEEPS):
        if sweep_index > 0:
            padded = jnp.pad(correction, ((0, 0), (0, 0), (1, 1), (1, 1)))
            padded = fill_ghost(padded, upper + 1, lower + 1, left + 1, right + 1, signs)
            local_res = live_mask * (resid_ext - apply_operator(padded, wave_ext, signs))
        if sweep_index % 2 == 0:
            update = along_rows(local_res, row_blocks, signs)
        else:
            update = along_cols(local_res, col_blocks, signs)
        correction = correction + live_mask * update
    return correction


def exchange(x, row_width, col_width, extra=None):
    row_count = lax.axis_size("gx")
    col_count = lax.axis_size("gy")
    height, breadth = (x.shape[-2], x.shape[-1])
    pieces = {}
    for dr in (-1, 0, 1):
        for dc in (-1, 0, 1):
            if dr == 0 and dc == 0:
                continue
            slab = x
            if dr == -1:
                slab = lax.slice_in_dim(slab, height - row_width, height, axis=x.ndim - 2)
            elif dr == 1:
                slab = lax.slice_in_dim(slab, 0, row_width, axis=x.ndim - 2)
            if dc == -1:
                slab = lax.slice_in_dim(slab, breadth - col_width, breadth, axis=x.ndim - 1)
            elif dc == 1:
                slab = lax.slice_in_dim(slab, 0, col_width, axis=x.ndim - 1)
            if extra is not None and (dr, dc) in extra:
                slab = jnp.concatenate([slab, extra[(dr, dc)]], axis=0)
            perm = []
            for r in range(row_count):
                for c in range(col_count):
                    rr, cc = (r - dr, c - dc)
                    if 0 <= rr < row_count and 0 <= cc < col_count:
                        perm.append((r * col_count + c, rr * col_count + cc))
            pieces[(dr, dc)] = lax.ppermute(slab, ("gx", "gy"), perm)
    return pieces


def exchange_axis(x, axis, dim, width, extra_lo=None, extra_hi=None):
    peers, length = (lax.axis_size(axis), x.shape[dim])
    up = [(i, i + 1) for i in range(peers - 1)]
    down = [(j, i) for i, j in up]
    last = lax.slice_in_dim(x, length - width, length, axis=dim)
    first = lax.slice_in_dim(x, 0, width, axis=dim)
    if extra_lo is not None:
        last = jnp.concatenate([last, extra_lo], axis=0)
        first = jnp.concatenate([first, extra_hi], axis=0)
    return lax.ppermute(last, axis, up), lax.ppermute(first, axis, down)


def assemble(pieces, centre, lead):
    rows = []
    for dr in (-1, 0, 1):
        row = []
        for dc in (-1, 0, 1):
            part = centre if (dr == 0 and dc == 0) else pieces[(dr, dc)][:lead]
            row.append(part)
        rows.append(jnp.concatenate(row, axis=-1))
    return jnp.concatenate(rows, axis=-2)


def grid_residual(fields_ref, data_ref, res_ref):
    height, breadth = (res_ref.shape[1], res_ref.shape[2])

    def ahead(x, step, axis):
        return pltpu.roll(x, x.shape[axis] - step, axis)

    for problem in range(res_ref.shape[0] // 2):
        sign = 1.0 - 2.0 * problem
        totals, centres = ([], [])
        for part in range(2):
            padded = fields_ref[2 * problem + part]
            outer = padded + ahead(padded, 2, 0)
            middle = ahead(padded, 1, 0)
            edge = ahead(outer, 1, 1) + middle + ahead(middle, 2, 1)
            corner = outer + ahead(outer, 2, 1)
            totals.append((4.0 * edge + corner)[:height, :breadth])
            centres.append(ahead(middle, 1, 1)[:height, :breadth])
        real_part, imag_part = centres
        wave = data_ref[4]
        lap_r = (totals[0] - 20.0 * real_part) / 6.0
        lap_i = (totals[1] - 20.0 * imag_part) / 6.0
        mass_r = real_part - sign * DAMPING * imag_part
        mass_i = imag_part + sign * DAMPING * real_part
        res_ref[2 * problem] = data_ref[2 * problem] - (-lap_r - wave * mass_r)
        res_ref[2 * problem + 1] = data_ref[2 * problem + 1] - (-lap_i - wave * mass_i)


def solve_kernel(rect_ref, resid_ref, data_ref, wrow_ref, wcol_ref, *refs, has_base, last, own_rows, own_cols, slab,
                 from_fields):
    if from_fields:
        grid_residual(resid_ref, data_ref, refs[-1])
        resid_ref = refs[-1]
        refs = refs[:-1]
    base_ref = refs[0] if has_base else None
    outs = refs[1:] if has_base else refs
    own_ref = outs[0]
    top_ref, bottom_ref = (None, None) if last else outs[1:3]
    height, breadth = (resid_ref.shape[1], resid_ref.shape[2])
    half = height // 2
    upper, lower, left, right = (rect_ref[0], rect_ref[1], rect_ref[2], rect_ref[3])
    row_ids = lax.broadcasted_iota(jnp.int32, (height, breadth), 0)
    col_ids = lax.broadcasted_iota(jnp.int32, (height, breadth), 1)
    live = (row_ids >= upper) & (row_ids < lower) & (col_ids >= left) & (col_ids < right)
    top, bottom = (row_ids == upper, row_ids == lower - 1)
    first, last = (col_ids == left, col_ids == right - 1)
    row_flag = top.astype(jnp.float32) + bottom.astype(jnp.float32)
    col_flag = first.astype(jnp.float32) + last.astype(jnp.float32)
    edge_flag = 4.0 * (row_flag + col_flag)
    zero = jnp.zeros((height, breadth), jnp.float32)

    def mask(x):
        return jnp.where(live, x, zero)

    def rows_sum(x):
        up = jnp.where(top, x, pltpu.roll(x, 1, 0))
        down = jnp.where(bottom, x, pltpu.roll(x, height - 1, 0))
        return up + down

    def cols_sum(x):
        lft = jnp.where(first, x, pltpu.roll(x, 1, 1))
        rgt = jnp.where(last, x, pltpu.roll(x, breadth - 1, 1))
        return lft + rgt

    def stencil(x):
        vertical = rows_sum(x)
        ghost_rows = row_flag * x
        total = 4.0 * (vertical + cols_sum(x)) + cols_sum(vertical)
        ghost = edge_flag * x + cols_sum(ghost_rows) + col_flag * (vertical - ghost_rows)
        return total, ghost

    def operator(real_part, imag_part, sign):
        wave = data_ref[4]
        total_r, ghost_r = stencil(real_part)
        total_i, ghost_i = stencil(imag_part)
        lap_r = (total_r + sign * ROBIN_COEF * ghost_i - 20.0 * real_part) / 6.0
        lap_i = (total_i - sign * ROBIN_COEF * ghost_r - 20.0 * imag_part) / 6.0
        mass_r = real_part - sign * DAMPING * imag_part
        mass_i = imag_part + sign * DAMPING * real_part
        return (-lap_r - wave * mass_r, -lap_i - wave * mass_i)

    def dot(a, b):
        return jnp.dot(a, b, precision=lax.Precision.HIGH, preferred_element_type=jnp.float32)

    def rows_apply(real_part, imag_part, sign):
        outs_r, outs_i = ([], [])
        for h in range(breadth // half):
            cols = slice(h * half, (h + 1) * half)
            prod_r = dot(real_part[:, cols], wrow_ref[h])
            prod_i = dot(imag_part[:, cols], wrow_ref[h])
            outs_r.append(prod_r[:, :half] - sign * prod_i[:, half:])
            outs_i.append(prod_i[:, :half] + sign * prod_r[:, half:])
        return (jnp.concatenate(outs_r, axis=1), jnp.concatenate(outs_i, axis=1))

    def cols_apply(real_part, imag_part, sign):
        outs_r, outs_i = ([], [])
        for h in range(height // half):
            rows = slice(h * half, (h + 1) * half)
            prod_r = dot(wcol_ref[h], real_part[rows, :])
            prod_i = dot(wcol_ref[h], imag_part[rows, :])
            outs_r.append(prod_r[:half] - sign * prod_i[half:])
            outs_i.append(prod_i[:half] + sign * prod_r[half:])
        return (jnp.concatenate(outs_r, axis=0), jnp.concatenate(outs_i, axis=0))

    def problem_body(problem, carry):
        sign = 1.0 - 2.0 * problem.astype(jnp.float32)
        up_r, up_i = rows_apply(mask(resid_ref[2 * problem]), mask(resid_ref[2 * problem + 1]), sign)
        cor_r, cor_i = (mask(up_r), mask(up_i))
        for step in range(SWEEPS - 1):
            op_r, op_i = operator(cor_r, cor_i, sign)
            loc_r, loc_i = (mask(resid_ref[2 * problem] - op_r), mask(resid_ref[2 * problem + 1] - op_i))
            apply = cols_apply if step % 2 == 0 else rows_apply
            up_r, up_i = apply(loc_r, loc_i, sign)
            cor_r, cor_i = (cor_r + mask(up_r), cor_i + mask(up_i))
        first_row = (height - own_rows) // 2
        for part, value in ((0, cor_r), (1, cor_i)):
            own = pltpu.roll(value, breadth - (breadth - own_cols) // 2, 1)[first_row : first_row + own_rows, :own_cols]
            if base_ref is not None:
                own = own + base_ref[problem, part]
            own_ref[problem, part] = own
            if top_ref is not None:
                top_ref[problem, part] = own[:slab]
                bottom_ref[problem, part] = own[own_rows - slab :]
        return carry

    lax.fori_loop(0, resid_ref.shape[0] // 2, problem_body, 0)


def line_matrices(row_blocks, col_blocks):
    block = row_blocks.shape[-1]
    eye = jnp.eye(2, dtype=row_blocks.dtype)
    halves = row_blocks.shape[0] // 2
    rows_t = jnp.transpose(row_blocks, (0, 3, 1, 2)).reshape(halves, 2, block, 2, block)
    row_mats = jnp.einsum("hakmo,ab->hakmbo", rows_t, eye).reshape(halves, 2 * block, 4 * block)
    cols = col_blocks.reshape(halves, 2, 2, block, block)
    col_mats = jnp.einsum("hamok,ab->hmaobk", cols, eye).reshape(halves, 4 * block, 2 * block)
    return row_mats, col_mats


def solve_local_kernel(resid_planes, data_ext, row_mats, col_mats, live_rect, own_shape, slab, base=None, last=False,
                       from_fields=False, interpret=False):
    extra = [] if base is None else [base]
    rect = jnp.stack([to_index(v) for v in live_rect])
    dtype = data_ext.dtype
    ext_shape = data_ext.shape[1:]
    shapes = [(2, 2) + own_shape]
    if not last:
        shapes += [(2, 2, slab, own_shape[1])] * 2
    vmem = pltpu.MemorySpace.VMEM if hasattr(pltpu, "MemorySpace") else pltpu.VMEM
    kernel = functools.partial(
        solve_kernel, has_base=base is not None, last=last, own_rows=own_shape[0], own_cols=own_shape[1], slab=slab,
        from_fields=from_fields,
    )
    scratch = [pltpu.VMEM((4,) + ext_shape, jnp.float32)] if from_fields else []
    operands = [data_ext, row_mats, col_mats] + extra
    if resid_planes is None:
        inner = kernel

        def kernel(rect_ref, data_ref, *refs):
            return inner(rect_ref, data_ref, data_ref, *refs)
    else:
        operands = [resid_planes] + operands
    return pl.pallas_call(
        kernel,
        out_shape=[jax.ShapeDtypeStruct(s, dtype) for s in shapes],
        in_specs=[pl.BlockSpec(memory_space=pltpu.SMEM)] + [pl.BlockSpec(memory_space=vmem)] * len(operands),
        out_specs=[pl.BlockSpec(memory_space=vmem)] * len(shapes),
        scratch_shapes=scratch,
        interpret=interpret,
    )(rect, *operands)


def shards(sources, wavenumber, row_inverse, col_inverse, reach_steps):
    own_rows, own_cols = (sources.shape[2], sources.shape[3])
    block = row_inverse.shape[-1]
    step_cells = block // 4
    signs = jnp.array([1.0, -1.0], dtype=sources.dtype).reshape(2, 1, 1)
    row_rank = to_index(lax.axis_index("gx"))
    col_rank = to_index(lax.axis_index("gy"))
    row_count = lax.axis_size("gx")
    col_count = lax.axis_size("gy")
    zero = to_index(0)
    widths = reach_steps.reshape(4) * step_cells
    upper_w = jnp.where(row_rank > 0, widths[0], zero)
    lower_w = jnp.where(row_rank < row_count - 1, widths[1], zero)
    left_w = jnp.where(col_rank > 0, widths[2], zero)
    right_w = jnp.where(col_rank < col_count - 1, widths[3], zero)
    live_rect = (
        block - upper_w,
        block + own_rows + lower_w,
        block - left_w,
        block + own_cols + right_w,
    )
    stacked = jnp.concatenate([sources.reshape(4, own_rows, own_cols), wavenumber[None]], axis=0)
    lead = stacked.shape[0]
    col_pair = col_inverse.shape[0]
    row_pair = row_inverse.shape[0]
    inv_rows = col_inverse.shape[1] * block * block // own_cols
    before, after = exchange_axis(
        stacked, "gx", 1, block,
        col_inverse[col_pair - 1].reshape(1, inv_rows, own_cols), col_inverse[0].reshape(1, inv_rows, own_cols),
    )
    tall = jnp.concatenate([before[:lead, :block], stacked, after[:lead, :block]], axis=1)
    def inv_slab(mats):
        flat = mats.reshape(1, -1, block)
        return jnp.pad(flat, ((0, 0), (0, tall.shape[1] - flat.shape[1]), (0, 0)))
    left, right = exchange_axis(tall, "gy", 2, block, inv_slab(row_inverse[row_pair - 1]), inv_slab(row_inverse[0]))
    stacked_ext = jnp.concatenate([left[:lead], tall, right[:lead]], axis=2)
    sources_ext = stacked_ext[:4].reshape(2, 2, own_rows + 2 * block, own_cols + 2 * block)
    wave_ext = stacked_ext[4]
    inv_shape = (1,) + row_inverse.shape[1:]
    inv_size = row_inverse.shape[1] * block * block // block
    col_blocks = jnp.concatenate(
        [before[lead:].reshape(inv_shape), col_inverse, after[lead:].reshape(inv_shape)], axis=0
    )
    row_blocks = jnp.concatenate(
        [left[lead:, :inv_size].reshape(inv_shape), row_inverse, right[lead:, :inv_size].reshape(inv_shape)], axis=0
    )
    row_mats, col_mats = line_matrices(row_blocks, col_blocks)
    width = block + 1
    edges = (row_rank == 0, row_rank == row_count - 1, col_rank == 0, col_rank == col_count - 1)
    slab = -(-width // 8) * 8
    solution = None
    base = None
    for iteration in range(ITERS):
        last = iteration == ITERS - 1
        if iteration == 0:
            resid_planes = None
        else:
            padded = assemble(exchange(solution, width, width), solution, 2)
            padded = grid_ghost(padded, width, edges, signs)
            tile_rows = -(-padded.shape[2] // 8) * 8 - padded.shape[2]
            tile_cols = -(-padded.shape[3] // 128) * 128 - padded.shape[3]
            padded = jnp.pad(padded, ((0, 0), (0, 0), (0, tile_rows), (0, tile_cols)))
            resid_planes = padded.reshape((4,) + padded.shape[2:])
        outs = solve_local_kernel(
            resid_planes, stacked_ext, row_mats, col_mats, live_rect, (own_rows, own_cols), slab, base=base, last=last,
            from_fields=iteration > 0,
        )
        solution = outs[0]
        if not last:
            solution, top, bottom = outs
        base = solution
    return solution


def solution(mesh):
    return jax.shard_map(
        shards,
        mesh=mesh,
        in_specs=(
            P(None, None, "gx", "gy"),
            P("gx", "gy"),
            P("gy", None, None, None),
            P("gx", None, None, None),
            P("gx", "gy", None),
        ),
        out_specs=P(None, None, "gx", "gy"),
        check_vma=False,
    )
```

```python
import functools

import jax
import jax.numpy as jnp
from jax import lax
from jax.sharding import PartitionSpec as P
from jax.experimental import pallas as pl
from jax.experimental.pallas import tpu as pltpu

ITERS = 2
SWEEPS = 4


DAMPING = 0.5
ROBIN_COEF = 0.5


def with_halo(shard, sides, width):
    for axis, dim in sides:
        peers, length = (lax.axis_size(axis), shard.shape[dim])
        up = [(i, (i + 1) % peers) for i in range(peers - 1)]
        down = [(j, i) for i, j in up]
        last = lax.slice_in_dim(shard, length - width, length, axis=dim)
        first = lax.slice_in_dim(shard, 0, width, axis=dim)
        before = lax.ppermute(last, axis, up)
        after = lax.ppermute(first, axis, down)
        shard = jnp.concatenate([before, shard, after], axis=dim)
    return shard


def to_index(value):
    return jnp.asarray(value).astype(jnp.int32)


def slice_line(values, start, axis):
    starts = [to_index(0) for _ in range(values.ndim)]
    starts[axis] = to_index(start)
    sizes = list(values.shape)
    sizes[axis] = 1
    return lax.dynamic_slice(values, starts, sizes)


def fill_ghost(values, upper, lower, left, right, signs):
    upper, lower, left, right = (to_index(upper), to_index(lower), to_index(left), to_index(right))
    height, breadth = (values.shape[2], values.shape[3])
    row_ids = lax.broadcasted_iota(jnp.int32, (height, 1), 0)
    col_ids = lax.broadcasted_iota(jnp.int32, (1, breadth), 1)
    upper_row = slice_line(values, upper, 2)
    lower_row = slice_line(values, lower - 1, 2)
    values = jnp.where(row_ids < upper, upper_row, jnp.where(row_ids >= lower, lower_row, values))
    left_col = slice_line(values, left, 3)
    right_col = slice_line(values, right - 1, 3)
    values = jnp.where(col_ids < left, left_col, jnp.where(col_ids >= right, right_col, values))
    inside = (row_ids >= upper) & (row_ids < lower) & (col_ids >= left) & (col_ids < right)
    real_part = values[:, 0]
    imag_part = values[:, 1]
    ghost_cycle = jnp.stack(
        [real_part + signs * ROBIN_COEF * imag_part, imag_part - signs * ROBIN_COEF * real_part],
        axis=1,
    )
    return jnp.where(inside, values, ghost_cycle)


def grid_ghost(values, width, edges, signs):
    at_top, at_bottom, at_left, at_right = edges
    height, breadth = (values.shape[2], values.shape[3])
    row_ids = lax.broadcasted_iota(jnp.int32, (height, 1), 0)
    col_ids = lax.broadcasted_iota(jnp.int32, (1, breadth), 1)
    above = at_top & (row_ids < width)
    below = at_bottom & (row_ids >= height - width)
    values = jnp.where(
        above, values[:, :, width : width + 1], jnp.where(below, values[:, :, height - width - 1 : height - width], values)
    )
    before = at_left & (col_ids < width)
    after = at_right & (col_ids >= breadth - width)
    values = jnp.where(
        before, values[:, :, :, width : width + 1],
        jnp.where(after, values[:, :, :, breadth - width - 1 : breadth - width], values),
    )
    outside = above | below | before | after
    real_part = values[:, 0]
    imag_part = values[:, 1]
    ghost_cycle = jnp.stack(
        [real_part + signs * ROBIN_COEF * imag_part, imag_part - signs * ROBIN_COEF * real_part],
        axis=1,
    )
    return jnp.where(outside, ghost_cycle, values)


def apply_operator(padded, wave_cells, signs):
    centre = padded[:, :, 1:-1, 1:-1]
    edge_sum = (
        padded[:, :, :-2, 1:-1]
        + padded[:, :, 2:, 1:-1]
        + padded[:, :, 1:-1, :-2]
        + padded[:, :, 1:-1, 2:]
    )
    corner_sum = (
        padded[:, :, :-2, :-2]
        + padded[:, :, :-2, 2:]
        + padded[:, :, 2:, :-2]
        + padded[:, :, 2:, 2:]
    )
    laplace = (4.0 * edge_sum + corner_sum - 20.0 * centre) / 6.0
    real_part = centre[:, 0]
    imag_part = centre[:, 1]
    mass_term = jnp.stack(
        [real_part - signs * DAMPING * imag_part, imag_part + signs * DAMPING * real_part], axis=1
    )
    return -laplace - wave_cells * mass_term


def combine_parts(products, signs, shape):
    real_out = products[0][:, 0] - signs[..., None] * products[1][:, 1]
    imag_out = products[0][:, 1] + signs[..., None] * products[1][:, 0]
    return jnp.stack([real_out, imag_out], axis=1).reshape(shape)


def along_rows(values, inverse, signs):
    block = inverse.shape[-1]
    blocked = values.reshape(values.shape[0], 2, values.shape[2], values.shape[3] // block, block)
    products = jnp.einsum("qmok,fchqk->mfchqo", inverse, blocked, precision=lax.Precision.HIGHEST)
    return combine_parts(products, signs, values.shape)


def along_cols(values, inverse, signs):
    block = inverse.shape[-1]
    blocked = values.reshape(values.shape[0], 2, values.shape[2] // block, block, values.shape[3])
    products = jnp.einsum("qmok,fcqkw->mfcqow", inverse, blocked, precision=lax.Precision.HIGHEST)
    return combine_parts(products, signs, values.shape)


def solve_local(resid_ext, wave_ext, row_blocks, col_blocks, live_rect, signs):
    upper, lower, left, right = [to_index(v) for v in live_rect]
    height, breadth = (resid_ext.shape[2], resid_ext.shape[3])
    row_ids = lax.broadcasted_iota(jnp.int32, (height, 1), 0)
    col_ids = lax.broadcasted_iota(jnp.int32, (1, breadth), 1)
    live_mask = (
        (row_ids >= upper) & (row_ids < lower) & (col_ids >= left) & (col_ids < right)
    ).astype(resid_ext.dtype)
    local_res = resid_ext * live_mask
    correction = jnp.zeros_like(resid_ext)
    for sweep_index in range(SWEEPS):
        if sweep_index > 0:
            padded = jnp.pad(correction, ((0, 0), (0, 0), (1, 1), (1, 1)))
            padded = fill_ghost(padded, upper + 1, lower + 1, left + 1, right + 1, signs)
            local_res = live_mask * (resid_ext - apply_operator(padded, wave_ext, signs))
        if sweep_index % 2 == 0:
            update = along_rows(local_res, row_blocks, signs)
        else:
            update = along_cols(local_res, col_blocks, signs)
        correction = correction + live_mask * update
    return correction


def exchange(x, row_width, col_width, extra=None):
    row_count = lax.axis_size("gx")
    col_count = lax.axis_size("gy")
    height, breadth = (x.shape[-2], x.shape[-1])
    pieces = {}
    for dr in (-1, 0, 1):
        for dc in (-1, 0, 1):
            if dr == 0 and dc == 0:
                continue
            slab = x
            if dr == -1:
                slab = lax.slice_in_dim(slab, height - row_width, height, axis=x.ndim - 2)
            elif dr == 1:
                slab = lax.slice_in_dim(slab, 0, row_width, axis=x.ndim - 2)
            if dc == -1:
                slab = lax.slice_in_dim(slab, breadth - col_width, breadth, axis=x.ndim - 1)
            elif dc == 1:
                slab = lax.slice_in_dim(slab, 0, col_width, axis=x.ndim - 1)
            if extra is not None and (dr, dc) in extra:
                slab = jnp.concatenate([slab, extra[(dr, dc)]], axis=0)
            perm = []
            for r in range(row_count):
                for c in range(col_count):
                    rr, cc = (r - dr, c - dc)
                    if 0 <= rr < row_count and 0 <= cc < col_count:
                        perm.append((r * col_count + c, rr * col_count + cc))
            pieces[(dr, dc)] = lax.ppermute(slab, ("gx", "gy"), perm)
    return pieces


def exchange_axis(x, axis, dim, width, extra_lo=None, extra_hi=None):
    peers, length = (lax.axis_size(axis), x.shape[dim])
    up = [(i, i + 1) for i in range(peers - 1)]
    down = [(j, i) for i, j in up]
    last = lax.slice_in_dim(x, length - width, length, axis=dim)
    first = lax.slice_in_dim(x, 0, width, axis=dim)
    if extra_lo is not None:
        last = jnp.concatenate([last, extra_lo], axis=0)
        first = jnp.concatenate([first, extra_hi], axis=0)
    return lax.ppermute(last, axis, up), lax.ppermute(first, axis, down)


def assemble(pieces, centre, lead):
    rows = []
    for dr in (-1, 0, 1):
        row = []
        for dc in (-1, 0, 1):
            part = centre if (dr == 0 and dc == 0) else pieces[(dr, dc)][:lead]
            row.append(part)
        rows.append(jnp.concatenate(row, axis=-1))
    return jnp.concatenate(rows, axis=-2)


def grid_residual(fields_ref, data_ref, res_ref):
    height, breadth = (res_ref.shape[1], res_ref.shape[2])

    def ahead(x, step, axis):
        return pltpu.roll(x, x.shape[axis] - step, axis)

    for problem in range(res_ref.shape[0] // 2):
        sign = 1.0 - 2.0 * problem
        totals, centres = ([], [])
        for part in range(2):
            padded = fields_ref[2 * problem + part]
            outer = padded + ahead(padded, 2, 0)
            middle = ahead(padded, 1, 0)
            edge = ahead(outer, 1, 1) + middle + ahead(middle, 2, 1)
            corner = outer + ahead(outer, 2, 1)
            totals.append((4.0 * edge + corner)[:height, :breadth])
            centres.append(ahead(middle, 1, 1)[:height, :breadth])
        real_part, imag_part = centres
        wave = data_ref[4]
        lap_r = (totals[0] - 20.0 * real_part) / 6.0
        lap_i = (totals[1] - 20.0 * imag_part) / 6.0
        mass_r = real_part - sign * DAMPING * imag_part
        mass_i = imag_part + sign * DAMPING * real_part
        res_ref[2 * problem] = data_ref[2 * problem] - (-lap_r - wave * mass_r)
        res_ref[2 * problem + 1] = data_ref[2 * problem + 1] - (-lap_i - wave * mass_i)


def solve_kernel(rect_ref, resid_ref, data_ref, wrow_ref, wcol_ref, *refs, has_base, last, own_rows, own_cols, slab,
                 from_fields):
    if from_fields:
        grid_residual(resid_ref, data_ref, refs[-1])
        resid_ref = refs[-1]
        refs = refs[:-1]
    base_ref = refs[0] if has_base else None
    outs = refs[1:] if has_base else refs
    own_ref = outs[0]
    top_ref, bottom_ref = (None, None) if last else outs[1:3]
    height, breadth = (resid_ref.shape[1], resid_ref.shape[2])
    half = height // 2
    upper, lower, left, right = (rect_ref[0], rect_ref[1], rect_ref[2], rect_ref[3])
    row_ids = lax.broadcasted_iota(jnp.int32, (height, breadth), 0)
    col_ids = lax.broadcasted_iota(jnp.int32, (height, breadth), 1)
    live = (row_ids >= upper) & (row_ids < lower) & (col_ids >= left) & (col_ids < right)
    top, bottom = (row_ids == upper, row_ids == lower - 1)
    first, last = (col_ids == left, col_ids == right - 1)
    row_flag = top.astype(jnp.float32) + bottom.astype(jnp.float32)
    col_flag = first.astype(jnp.float32) + last.astype(jnp.float32)
    edge_flag = 4.0 * (row_flag + col_flag)
    zero = jnp.zeros((height, breadth), jnp.float32)

    def mask(x):
        return jnp.where(live, x, zero)

    def rows_sum(x):
        up = jnp.where(top, x, pltpu.roll(x, 1, 0))
        down = jnp.where(bottom, x, pltpu.roll(x, height - 1, 0))
        return up + down

    def cols_sum(x):
        lft = jnp.where(first, x, pltpu.roll(x, 1, 1))
        rgt = jnp.where(last, x, pltpu.roll(x, breadth - 1, 1))
        return lft + rgt

    def stencil(x):
        vertical = rows_sum(x)
        ghost_rows = row_flag * x
        total = 4.0 * (vertical + cols_sum(x)) + cols_sum(vertical)
        ghost = edge_flag * x + cols_sum(ghost_rows) + col_flag * (vertical - ghost_rows)
        return total, ghost

    def operator(real_part, imag_part, sign):
        wave = data_ref[4]
        total_r, ghost_r = stencil(real_part)
        total_i, ghost_i = stencil(imag_part)
        lap_r = (total_r + sign * ROBIN_COEF * ghost_i - 20.0 * real_part) / 6.0
        lap_i = (total_i - sign * ROBIN_COEF * ghost_r - 20.0 * imag_part) / 6.0
        mass_r = real_part - sign * DAMPING * imag_part
        mass_i = imag_part + sign * DAMPING * real_part
        return (-lap_r - wave * mass_r, -lap_i - wave * mass_i)

    def dot(a, b):
        return jnp.dot(a, b, precision=lax.Precision.HIGH, preferred_element_type=jnp.float32)

    def dot_t(a, b):
        return lax.dot_general(
            a, b, (((1,), (1,)), ((), ())), precision=lax.Precision.HIGH, preferred_element_type=jnp.float32
        )

    def rows_apply(real_part, imag_part, sign):
        outs_r, outs_i = ([], [])
        for h in range(breadth // half):
            cols = slice(h * half, (h + 1) * half)
            prod_r = dot_t(real_part[:, cols], wrow_ref[h])
            prod_i = dot_t(imag_part[:, cols], wrow_ref[h])
            outs_r.append(prod_r[:, :half] - sign * prod_i[:, half:])
            outs_i.append(prod_i[:, :half] + sign * prod_r[:, half:])
        return (jnp.concatenate(outs_r, axis=1), jnp.concatenate(outs_i, axis=1))

    def cols_apply(real_part, imag_part, sign):
        outs_r, outs_i = ([], [])
        for h in range(height // half):
            rows = slice(h * half, (h + 1) * half)
            prod_r = dot(wcol_ref[h], real_part[rows, :])
            prod_i = dot(wcol_ref[h], imag_part[rows, :])
            outs_r.append(prod_r[:half] - sign * prod_i[half:])
            outs_i.append(prod_i[:half] + sign * prod_r[half:])
        return (jnp.concatenate(outs_r, axis=0), jnp.concatenate(outs_i, axis=0))

    def problem_body(problem, carry):
        sign = 1.0 - 2.0 * problem.astype(jnp.float32)
        up_r, up_i = rows_apply(mask(resid_ref[2 * problem]), mask(resid_ref[2 * problem + 1]), sign)
        cor_r, cor_i = (mask(up_r), mask(up_i))
        for step in range(SWEEPS - 1):
            op_r, op_i = operator(cor_r, cor_i, sign)
            loc_r, loc_i = (mask(resid_ref[2 * problem] - op_r), mask(resid_ref[2 * problem + 1] - op_i))
            apply = cols_apply if step % 2 == 0 else rows_apply
            up_r, up_i = apply(loc_r, loc_i, sign)
            cor_r, cor_i = (cor_r + mask(up_r), cor_i + mask(up_i))
        first_row = (height - own_rows) // 2
        for part, value in ((0, cor_r), (1, cor_i)):
            own = pltpu.roll(value, breadth - (breadth - own_cols) // 2, 1)[first_row : first_row + own_rows, :own_cols]
            if base_ref is not None:
                own = own + base_ref[problem, part]
            own_ref[problem, part] = own
            if top_ref is not None:
                top_ref[problem, part] = own[:slab]
                bottom_ref[problem, part] = own[own_rows - slab :]
        return carry

    lax.fori_loop(0, resid_ref.shape[0] // 2, problem_body, 0)


def line_matrices(row_blocks, col_blocks):
    block = row_blocks.shape[-1]

    def pairs(blocks):
        mats = []
        for h in range(blocks.shape[0] // 2):
            parts = []
            for m in range(2):
                for a in range(2):
                    parts.append(jnp.pad(blocks[2 * h + a, m], ((0, 0), (a * block, (1 - a) * block))))
            mats.append(jnp.concatenate(parts, axis=0))
        return jnp.stack(mats)

    return pairs(row_blocks), pairs(col_blocks)


def solve_local_kernel(resid_planes, data_ext, row_mats, col_mats, live_rect, own_shape, slab, base=None, last=False,
                       from_fields=False, interpret=False):
    extra = [] if base is None else [base]
    rect = jnp.stack([to_index(v) for v in live_rect])
    dtype = data_ext.dtype
    ext_shape = data_ext.shape[1:]
    shapes = [(2, 2) + own_shape]
    if not last:
        shapes += [(2, 2, slab, own_shape[1])] * 2
    vmem = pltpu.MemorySpace.VMEM if hasattr(pltpu, "MemorySpace") else pltpu.VMEM
    kernel = functools.partial(
        solve_kernel, has_base=base is not None, last=last, own_rows=own_shape[0], own_cols=own_shape[1], slab=slab,
        from_fields=from_fields,
    )
    scratch = [pltpu.VMEM((4,) + ext_shape, jnp.float32)] if from_fields else []
    operands = [data_ext, row_mats, col_mats] + extra
    if resid_planes is None:
        inner = kernel

        def kernel(rect_ref, data_ref, *refs):
            return inner(rect_ref, data_ref, data_ref, *refs)
    else:
        operands = [resid_planes] + operands
    return pl.pallas_call(
        kernel,
        out_shape=[jax.ShapeDtypeStruct(s, dtype) for s in shapes],
        in_specs=[pl.BlockSpec(memory_space=pltpu.SMEM)] + [pl.BlockSpec(memory_space=vmem)] * len(operands),
        out_specs=[pl.BlockSpec(memory_space=vmem)] * len(shapes),
        scratch_shapes=scratch,
        interpret=interpret,
    )(rect, *operands)


def shards(sources, wavenumber, row_inverse, col_inverse, reach_steps):
    own_rows, own_cols = (sources.shape[2], sources.shape[3])
    block = row_inverse.shape[-1]
    step_cells = block // 4
    signs = jnp.array([1.0, -1.0], dtype=sources.dtype).reshape(2, 1, 1)
    row_rank = to_index(lax.axis_index("gx"))
    col_rank = to_index(lax.axis_index("gy"))
    row_count = lax.axis_size("gx")
    col_count = lax.axis_size("gy")
    zero = to_index(0)
    widths = reach_steps.reshape(4) * step_cells
    upper_w = jnp.where(row_rank > 0, widths[0], zero)
    lower_w = jnp.where(row_rank < row_count - 1, widths[1], zero)
    left_w = jnp.where(col_rank > 0, widths[2], zero)
    right_w = jnp.where(col_rank < col_count - 1, widths[3], zero)
    live_rect = (
        block - upper_w,
        block + own_rows + lower_w,
        block - left_w,
        block + own_cols + right_w,
    )
    stacked = jnp.concatenate([sources.reshape(4, own_rows, own_cols), wavenumber[None]], axis=0)
    lead = stacked.shape[0]
    col_pair = col_inverse.shape[0]
    row_pair = row_inverse.shape[0]
    inv_rows = col_inverse.shape[1] * block * block // own_cols
    before, after = exchange_axis(
        stacked, "gx", 1, block,
        col_inverse[col_pair - 1].reshape(1, inv_rows, own_cols), col_inverse[0].reshape(1, inv_rows, own_cols),
    )
    tall = jnp.concatenate([before[:lead, :block], stacked, after[:lead, :block]], axis=1)
    def inv_slab(mats):
        flat = mats.reshape(1, -1, block)
        return jnp.pad(flat, ((0, 0), (0, tall.shape[1] - flat.shape[1]), (0, 0)))
    left, right = exchange_axis(tall, "gy", 2, block, inv_slab(row_inverse[row_pair - 1]), inv_slab(row_inverse[0]))
    stacked_ext = jnp.concatenate([left[:lead], tall, right[:lead]], axis=2)
    sources_ext = stacked_ext[:4].reshape(2, 2, own_rows + 2 * block, own_cols + 2 * block)
    wave_ext = stacked_ext[4]
    inv_shape = (1,) + row_inverse.shape[1:]
    inv_size = row_inverse.shape[1] * block * block // block
    col_blocks = jnp.concatenate(
        [before[lead:].reshape(inv_shape), col_inverse, after[lead:].reshape(inv_shape)], axis=0
    )
    row_blocks = jnp.concatenate(
        [left[lead:, :inv_size].reshape(inv_shape), row_inverse, right[lead:, :inv_size].reshape(inv_shape)], axis=0
    )
    row_mats, col_mats = line_matrices(row_blocks, col_blocks)
    width = block + 1
    edges = (row_rank == 0, row_rank == row_count - 1, col_rank == 0, col_rank == col_count - 1)
    slab = -(-width // 8) * 8
    solution = None
    base = None
    for iteration in range(ITERS):
        last = iteration == ITERS - 1
        if iteration == 0:
            resid_planes = None
        else:
            peers = lax.axis_size("gx")
            up = [(i, i + 1) for i in range(peers - 1)]
            down = [(j, i) for i, j in up]
            before = lax.ppermute(bottom, "gx", up)[:, :, slab - width :]
            after = lax.ppermute(top, "gx", down)[:, :, :width]
            tall = jnp.concatenate([before, solution, after], axis=2)
            left, right = exchange_axis(tall, "gy", 3, width)
            padded = jnp.concatenate([left, tall, right], axis=3)
            padded = grid_ghost(padded, width, edges, signs)
            tile_rows = -(-padded.shape[2] // 8) * 8 - padded.shape[2]
            tile_cols = -(-padded.shape[3] // 128) * 128 - padded.shape[3]
            padded = jnp.pad(padded, ((0, 0), (0, 0), (0, tile_rows), (0, tile_cols)))
            resid_planes = padded.reshape((4,) + padded.shape[2:])
        outs = solve_local_kernel(
            resid_planes, stacked_ext, row_mats, col_mats, live_rect, (own_rows, own_cols), slab, base=base, last=last,
            from_fields=iteration > 0,
        )
        solution = outs[0]
        if not last:
            solution, top, bottom = outs
        base = solution
    return solution


def solution(mesh):
    return jax.shard_map(
        shards,
        mesh=mesh,
        in_specs=(
            P(None, None, "gx", "gy"),
            P("gx", "gy"),
            P("gy", None, None, None),
            P("gx", None, None, None),
            P("gx", "gy", None),
        ),
        out_specs=P(None, None, "gx", "gy"),
        check_vma=False,
    )
```
